32 devices in a mesh: dp: 8 (over y, x, core), tensor: 4 (over z).
Axes of the slice: x: 2, y: 2, z: 4, core: 2. Of those that a mesh axis runs over, the one named last changes fastest.
Arguments:
- tokens: bfloat16 [24576, 768], P(('dp', 'tensor')), may hold values from -6 to 6
- lengths: int32 [40], replicated, may hold values from 257 to 1024, as said below
- dealing: int32 [40], replicated, may hold values from 0 to 39, as said below
- w_query: bfloat16 [768, 768], P('dp', 'tensor'), may hold values from -0.4375 to 0.4375
- w_key: bfloat16 [768, 768], P('dp', 'tensor'), may hold values from -0.21875 to 0.21875
- w_value: bfloat16 [768, 768], P('dp', 'tensor'), may hold values from -0.21875 to 0.21875
- w_out: bfloat16 [768, 768], P('tensor', 'dp'), may hold values from -1.75 to 1.75
- w_inner: bfloat16 [768, 3072], P('dp', 'tensor'), may hold values from -0.21875 to 0.21875
- w_outer: bfloat16 [3072, 768], P('tensor', 'dp'), may hold values from -0.109375 to 0.109375
- b_query: bfloat16 [768], replicated, may hold values from -3 to 3
- b_value: bfloat16 [768], replicated, may hold values from -3 to 3
- b_out: bfloat16 [768], replicated, may hold values from -3 to 3
- b_inner: bfloat16 [3072], replicated, may hold values from -3 to 3
- b_outer: bfloat16 [768], replicated, may hold values from -3 to 3
- gain_attn: bfloat16 [768], replicated, may hold values from 0.5 to 1.5
- shift_attn: bfloat16 [768], replicated, may hold values from -2 to 2
- gain_ffn: bfloat16 [768], replicated, may hold values from 0.5 to 1.5
- shift_ffn: bfloat16 [768], replicated, may hold values from -2 to 2
- grad_out: bfloat16 [24576, 768], P(('dp', 'tensor')), may hold values from -6 to 6
Outputs:
- layer_out: bfloat16 [24576, 768], P(('dp', 'tensor'))
- grad_tokens: float32 [24576, 768], P(('dp', 'tensor'))
- grad_w_query: float32 [768, 768], P('dp', 'tensor')
- grad_w_key: float32 [768, 768], P('dp', 'tensor')
- grad_w_value: float32 [768, 768], P('dp', 'tensor')
- grad_w_out: float32 [768, 768], P('tensor', 'dp')
- grad_w_inner: float32 [768, 3072], P('dp', 'tensor')
- grad_w_outer: float32 [3072, 768], P('tensor', 'dp')
- grad_b_query: float32 [768], P(('dp', 'tensor'))
- grad_b_value: float32 [768], P(('dp', 'tensor'))
- grad_b_out: float32 [768], P(('dp', 'tensor'))
- grad_b_inner: float32 [3072], P(('dp', 'tensor'))
- grad_b_outer: float32 [768], P(('dp', 'tensor'))
- grad_gain_attn: float32 [768], P(('dp', 'tensor'))
- grad_shift_attn: float32 [768], P(('dp', 'tensor'))
- grad_gain_ffn: float32 [768], P(('dp', 'tensor'))
- grad_shift_ffn: float32 [768], P(('dp', 'tensor'))
The draws below stay inside these ranges and needn't reach their ends.
Inputs may be any that keep to these rules, and one draw needn't show every extreme that they name: In every data group one dealt sequence has exactly 1024 tokens, and the lengths of the 5 sequences dealt to a group sum to 3072. `dealing`: A permutation of the sequences.
All inputs are finite; a program needn't handle non-finite values.
Results may differ from the reference program's by a relative error of at most 0.02.
Values may be sent and summed in bfloat16 or wider, within the bound.
No kernel may reach another device: no remote copies, remote signals or barrier semaphores. Data moves between devices by JAX's collectives and lax.ppermute only.
A program may use at most 128 MiB of HBM per device.

```python
import math
import jax
import jax.numpy as jnp
from jax import lax

D = 768
HEADS = 12
HEAD_DIM = 64
FF = 3072
LONGEST = 1024
SEQ_GRP = 5
TOK_GRP = 3072
SEQS = 40
TOKENS = 24576
N_DP = 8


def shuffle_group(one_key):
    return jax.random.permutation(one_key, SEQ_GRP)


def dealt_lengths(key):
    base = jax.random.fold_in(key, 11)
    key_spread, key_order, key_deal = jax.random.split(base, 3)
    quarter = LONGEST // 4
    groups = SEQS // SEQ_GRP
    spreads = jax.random.randint(key_spread, (groups, 2), 0, quarter, dtype=jnp.int32)
    longest = jnp.full((groups,), 4 * quarter, jnp.int32)
    table = jnp.stack([longest, 2 * quarter + spreads[:, 0], 2 * quarter - spreads[:, 0], 2 * quarter + spreads[:, 1], 2 * quarter - spreads[:, 1]], axis=1).astype(jnp.int32)
    orders = jax.vmap(shuffle_group)(jax.random.split(key_order, groups))
    table = jnp.take_along_axis(table, orders, axis=1).astype(jnp.int32)
    dealing = jax.random.permutation(key_deal, SEQS).astype(jnp.int32)
    given_lengths = jnp.zeros((SEQS,), jnp.int32).at[dealing].set(table.reshape(SEQS))
    return (given_lengths, dealing)


def draw_lengths(key, part):
    return dealt_lengths(key)[0]


def draw_dealing(key, part):
    return dealt_lengths(key)[1]


def raised(drawn, own_key, source, target, parts, factor):
    def block_of(dim):
        return (jnp.arange(drawn.shape[dim]) // (drawn.shape[dim] // parts)).reshape((-1,) + (1,) * (drawn.ndim - 1 - dim))

    one_side = jax.random.permutation(own_key, parts)[block_of(target)]
    far = (block_of(target) + parts // 2) % parts
    return jnp.where((block_of(source) == one_side) | (block_of(source) == far), factor * drawn, drawn)


def block_scale(key, dims, cuts, smallest, largest):
    loudness = 1.0
    for position, blocks in cuts:
        steps = jax.random.uniform(jax.random.fold_in(jax.random.fold_in(key, 6), position), (blocks,), jnp.float32, smallest / len(cuts), largest / len(cuts))
        loudness = loudness * jnp.repeat(jnp.exp(steps), dims[position] // blocks).reshape((-1,) + (1,) * (len(dims) - 1 - position))
    return loudness


def noise(key, shape, scale, bound, pieces=(), held_as=jnp.bfloat16):
    entries = jax.random.normal(key, shape, jnp.float32) * scale
    if len(pieces) > 0:
        entries = block_scale(key, shape, pieces, -0.22, 0.18) * entries
    return jnp.clip(entries, min=-bound, max=bound).astype(held_as)


def bell_draw_with(key, extent, scale, reach, cuts, heavy, kind=jnp.bfloat16):
    entries = scale * jax.random.normal(key, extent, jnp.float32)
    if cuts:
        entries = entries * block_scale(key, extent, cuts, -0.22, 0.18)
    return jnp.clip(raised(entries, jax.random.fold_in(key, 3), *heavy), -reach, reach).astype(kind)


def setup_inputs(seed: int = 0) -> dict:
    streams_of = jax.random.split(jax.random.key(seed), 20)
    return {
        "tokens": noise(streams_of[0], (TOKENS, D), 1.0, 6.0, ((0, 32),)),
        "lengths": draw_lengths(jax.random.fold_in(streams_of[19], 71), 0),
        "dealing": draw_dealing(jax.random.fold_in(streams_of[19], 71), 0),
        "w_query": noise(streams_of[3], (D, D), (D // 4) ** -0.5, 0.4375, ((0, 8), (1, 4))),
        "w_key": noise(streams_of[4], (D, D), D ** -0.5, 0.21875, ((0, 8), (1, 4))),
        "w_value": noise(streams_of[5], (D, D), D ** -0.5, 0.21875, ((0, 8), (1, 4))),
        "w_out": noise(streams_of[6], (D, D), (D // 64) ** -0.5, 1.75, ((0, 4), (1, 8))),
        "w_inner": noise(streams_of[7], (D, FF), D ** -0.5, 0.21875, ((0, 8), (1, 4))),
        "w_outer": noise(streams_of[8], (FF, D), FF ** -0.5, 0.109375, ((0, 4), (1, 8))),
        "b_query": noise(streams_of[9], (D,), 0.5, 3.0),
        "b_value": noise(streams_of[10], (D,), 0.5, 3.0),
        "b_out": noise(streams_of[11], (D,), 0.5, 3.0),
        "b_inner": noise(streams_of[12], (FF,), 0.5, 3.0),
        "b_outer": noise(streams_of[13], (D,), 0.5, 3.0),
        "gain_attn": jnp.clip(1.0 + 0.1 * jax.random.normal(streams_of[14], (D,), jnp.float32), 0.5, 1.5).astype(jnp.bfloat16),
        "shift_attn": noise(streams_of[15], (D,), 0.3, 2.0),
        "gain_ffn": jnp.clip(1.0 + 0.1 * jax.random.normal(streams_of[16], (D,), jnp.float32), 0.5, 1.5).astype(jnp.bfloat16),
        "shift_ffn": noise(streams_of[17], (D,), 0.3, 2.0),
        "grad_out": bell_draw_with(streams_of[18], (TOKENS, D), 1.0, 6.0, ((0, 32),), (0, 1, 32, 2.75)),
    }


@jax.custom_vjp
def low(v):
    return lax.optimization_barrier(v.astype(jnp.bfloat16)).astype(jnp.float32)

@jax.custom_vjp
def low_back(v):
    return v

def low_keep(v):
    return (low(v), None)

def low_pass(kept, grad):
    return (grad,)

def back_keep(v):
    return (v, None)

def back_low(kept, grad):
    return (low(grad),)
low.defvjp(low_keep, low_pass)
low_back.defvjp(back_keep, back_low)

def matmul(left, right):
    return jnp.dot(left, right, precision=lax.Precision.HIGHEST)

def layer_norm(values, gain, shift):
    center = lax.optimization_barrier(jnp.mean(values, axis=-1, keepdims=True))
    offsets = values - center
    spread = lax.optimization_barrier(jnp.mean(offsets * offsets, axis=-1, keepdims=True))
    return offsets * lax.rsqrt(spread + 1e-06) * gain + shift

def segments(lengths, dealing):
    group_lengths = jnp.take(lengths, dealing).reshape(N_DP, SEQ_GRP).astype(jnp.int32)
    ends = jnp.cumsum(group_lengths, axis=1).astype(jnp.int32)
    places = jnp.arange(TOK_GRP, dtype=jnp.int32)
    return lax.optimization_barrier(jnp.sum((places[None, :, None] >= ends[:, None, :]).astype(jnp.int32), axis=2)).astype(jnp.int32)

def attend(query, key_heads, value_heads, segment_ids):
    block_rows = 512 if TOK_GRP % 512 == 0 else TOK_GRP
    count = TOK_GRP // block_rows
    query_blocks = query.reshape(count, block_rows, HEADS, HEAD_DIM)
    id_blocks = segment_ids.reshape(count, block_rows)
    score_scale = 1.0 / math.sqrt(HEAD_DIM)

    @jax.checkpoint
    def one_block(element):
        query_rows, row_ids = element
        raw = jnp.einsum('qhd,khd->hqk', query_rows, key_heads, precision=lax.Precision.HIGHEST) * score_scale
        scores = low_back(raw)
        scores = jnp.where((row_ids[:, None] == segment_ids[None, :])[None], scores, -1e+30)
        probs = low(jax.nn.softmax(scores, axis=-1))
        return jnp.einsum('hqk,khd->qhd', probs, value_heads, precision=lax.Precision.HIGHEST)
    context = lax.map(one_block, (query_blocks, id_blocks))
    return context.reshape(TOK_GRP, D)

def group_layer(rows, segment_ids, params):
    w_query, w_key, w_value, w_out, w_inner, w_outer, b_query, b_value, b_out, b_inner, b_outer, gain_attn, shift_attn, gain_ffn, shift_ffn = params
    query = low_back(low(matmul(rows, w_query) + b_query))
    key_rows = low_back(low(matmul(rows, w_key)))
    value_rows = low_back(low(matmul(rows, w_value) + b_value))
    context = attend(query.reshape(TOK_GRP, HEADS, HEAD_DIM), key_rows.reshape(TOK_GRP, HEADS, HEAD_DIM), value_rows.reshape(TOK_GRP, HEADS, HEAD_DIM), segment_ids)
    context = low_back(low(context))
    attn = low_back(matmul(context, w_out) + b_out)
    hidden = layer_norm(rows + attn, gain_attn, shift_attn)
    hidden_low = low(hidden)
    pre_act = low_back(matmul(hidden_low, w_inner) + b_inner)
    act = low(jax.nn.gelu(pre_act, approximate=False))
    ffn = low_back(matmul(act, w_outer) + b_outer)
    return layer_norm(hidden + ffn, gain_ffn, shift_ffn)

def reference(tokens, lengths, dealing, w_query, w_key, w_value, w_out, w_inner, w_outer, b_query, b_value, b_out, b_inner, b_outer, gain_attn, shift_attn, gain_ffn, shift_ffn, grad_out):
    params = tuple((w.astype(jnp.float32) for w in (w_query, w_key, w_value, w_out, w_inner, w_outer, b_query, b_value, b_out, b_inner, b_outer, gain_attn, shift_attn, gain_ffn, shift_ffn)))
    segment_ids = segments(lengths, dealing)
    groups = tokens.astype(jnp.float32).reshape(N_DP, TOK_GRP, D)
    layer_fn = jax.checkpoint(group_layer)

    def whole(group_rows, *weights):

        def step(totals, element):
            rows, ids = element
            return (totals, layer_fn(rows, ids, weights))
        unused, outputs = lax.scan(step, jnp.zeros((), jnp.float32), (group_rows, segment_ids))
        return outputs
    outputs, pull = jax.vjp(whole, groups, *params)
    grads = pull(grad_out.astype(jnp.float32).reshape(N_DP, TOK_GRP, D))
    return (outputs.reshape(TOKENS, D).astype(jnp.bfloat16), grads[0].reshape(TOKENS, D), grads[1], grads[2], grads[3], grads[4], grads[5], grads[6], grads[7], grads[8], grads[9], grads[10], grads[11], grads[12], grads[13], grads[14], grads[15])
```

```python
import math

import jax
import jax.numpy as jnp
from jax import lax
from jax.experimental import pallas as pl
from jax.experimental.pallas import tpu as pltpu
from jax.sharding import PartitionSpec as P

HEAD_DIM = 64
LONGEST = 1024
BLOCK = 256

NEG = -1e30


def _fwd_kernel(lo_ref, hi_ref, q_ref, k_ref, v_ref, qs_ref, ks_ref, o_ref, lse_ref, m_sc, l_sc, acc_sc):
    i = pl.program_id(0)
    j = pl.program_id(1)
    kv = lo_ref[i] + j

    @pl.when(j == 0)
    def _():
        m_sc[...] = jnp.full_like(m_sc, NEG)
        l_sc[...] = jnp.zeros_like(l_sc)
        acc_sc[...] = jnp.zeros_like(acc_sc)

    @pl.when(kv <= hi_ref[i])
    def _():
        s = jnp.einsum("hqd,hkd->hqk", q_ref[...], k_ref[...], preferred_element_type=jnp.float32) * 0.125
        mask = (qs_ref[...] == ks_ref[...])[None]
        s = jnp.where(mask, s, NEG)
        m_old = m_sc[...]
        m_new = jnp.maximum(m_old, jnp.max(s, axis=-1, keepdims=True))
        alpha = jnp.exp(m_old - m_new)
        p = jnp.where(mask, jnp.exp(s - m_new), 0.0)
        l_sc[...] = alpha * l_sc[...] + jnp.sum(p, axis=-1, keepdims=True)
        acc_sc[...] = alpha * acc_sc[...] + jnp.einsum(
            "hqk,hkd->hqd", p.astype(jnp.bfloat16), v_ref[...], preferred_element_type=jnp.float32
        )
        m_sc[...] = m_new

    @pl.when(j == pl.num_programs(1) - 1)
    def _():
        o_ref[...] = acc_sc[...] / l_sc[...]
        lse_ref[...] = m_sc[...] + jnp.log(l_sc[...])


def _dq_kernel(lo_ref, hi_ref, q_ref, k_ref, v_ref, qs_ref, ks_ref, lse_ref, dl_ref, do_ref, dq_ref, acc_sc):
    i = pl.program_id(0)
    j = pl.program_id(1)
    kv = lo_ref[i] + j

    @pl.when(j == 0)
    def _():
        acc_sc[...] = jnp.zeros_like(acc_sc)

    @pl.when(kv <= hi_ref[i])
    def _():
        k = k_ref[...]
        s = jnp.einsum("hqd,hkd->hqk", q_ref[...], k, preferred_element_type=jnp.float32) * 0.125
        mask = (qs_ref[...] == ks_ref[...])[None]
        p = jnp.where(mask, jnp.exp(s - lse_ref[...]), 0.0)
        dp = jnp.einsum("hqd,hkd->hqk", do_ref[...], v_ref[...], preferred_element_type=jnp.float32)
        ds = (p * (dp - dl_ref[...])).astype(jnp.bfloat16)
        acc_sc[...] += jnp.einsum("hqk,hkd->hqd", ds, k, preferred_element_type=jnp.float32)

    @pl.when(j == pl.num_programs(1) - 1)
    def _():
        dq_ref[...] = acc_sc[...] * 0.125


def _dkv_kernel(lo_ref, hi_ref, q_ref, k_ref, v_ref, qs_ref, ks_ref, lse_ref, dl_ref, do_ref, dk_ref, dv_ref, dk_sc, dv_sc):
    j = pl.program_id(0)
    i = pl.program_id(1)
    qb = lo_ref[j] + i

    @pl.when(i == 0)
    def _():
        dk_sc[...] = jnp.zeros_like(dk_sc)
        dv_sc[...] = jnp.zeros_like(dv_sc)

    @pl.when(qb <= hi_ref[j])
    def _():
        q = q_ref[...]
        do = do_ref[...]
        s = jnp.einsum("hqd,hkd->hqk", q, k_ref[...], preferred_element_type=jnp.float32) * 0.125
        mask = (qs_ref[...] == ks_ref[...])[None]
        p = jnp.where(mask, jnp.exp(s - lse_ref[...]), 0.0)
        dp = jnp.einsum("hqd,hkd->hqk", do, v_ref[...], preferred_element_type=jnp.float32)
        ds = (p * (dp - dl_ref[...])).astype(jnp.bfloat16)
        dv_sc[...] += jnp.einsum("hqk,hqd->hkd", p.astype(jnp.bfloat16), do, preferred_element_type=jnp.float32)
        dk_sc[...] += jnp.einsum("hqk,hqd->hkd", ds, q, preferred_element_type=jnp.float32)

    @pl.when(i == pl.num_programs(1) - 1)
    def _():
        dk_ref[...] = dk_sc[...] * 0.125
        dv_ref[...] = dv_sc[...]


def _clamp(start, step, last):
    return jnp.minimum(start + step, jnp.maximum(last, 0))


def flash_forward(q, k, v, q_ids, k_ids, lo, hi, block_q, block_k, steps):
    heads, nq, hd = q.shape
    nk = k.shape[1]
    qs = q_ids.reshape(nq, 1)
    ks = k_ids.reshape(1, nk)

    def kv_map(i, j, lo_ref, hi_ref):
        return (0, _clamp(lo_ref[i], j, hi_ref[i]), 0)

    def ks_map(i, j, lo_ref, hi_ref):
        return (0, _clamp(lo_ref[i], j, hi_ref[i]))

    grid_spec = pltpu.PrefetchScalarGridSpec(
        num_scalar_prefetch=2,
        grid=(nq // block_q, steps),
        in_specs=[
            pl.BlockSpec((heads, block_q, hd), lambda i, j, a, b: (0, i, 0)),
            pl.BlockSpec((heads, block_k, hd), kv_map),
            pl.BlockSpec((heads, block_k, hd), kv_map),
            pl.BlockSpec((block_q, 1), lambda i, j, a, b: (i, 0)),
            pl.BlockSpec((1, block_k), ks_map),
        ],
        out_specs=[
            pl.BlockSpec((heads, block_q, hd), lambda i, j, a, b: (0, i, 0)),
            pl.BlockSpec((heads, block_q, 1), lambda i, j, a, b: (0, i, 0)),
        ],
        scratch_shapes=[
            pltpu.VMEM((heads, block_q, 1), jnp.float32),
            pltpu.VMEM((heads, block_q, 1), jnp.float32),
            pltpu.VMEM((heads, block_q, hd), jnp.float32),
        ],
    )
    return pl.pallas_call(
        _fwd_kernel,
        grid_spec=grid_spec,
        out_shape=[
            jax.ShapeDtypeStruct((heads, nq, hd), jnp.float32),
            jax.ShapeDtypeStruct((heads, nq, 1), jnp.float32),
        ],
        compiler_params=pltpu.CompilerParams(
            dimension_semantics=("arbitrary", "arbitrary"), vmem_limit_bytes=100 * 1024 * 1024 // 2
        ),
    )(lo, hi, q, k, v, qs, ks)


def flash_dq(q, k, v, q_ids, k_ids, lse, delta, do, lo, hi, block_q, block_k, steps):
    heads, nq, hd = q.shape
    nk = k.shape[1]
    qs = q_ids.reshape(nq, 1)
    ks = k_ids.reshape(1, nk)

    def kv_map(i, j, lo_ref, hi_ref):
        return (0, _clamp(lo_ref[i], j, hi_ref[i]), 0)

    def ks_map(i, j, lo_ref, hi_ref):
        return (0, _clamp(lo_ref[i], j, hi_ref[i]))

    row = lambda i, j, a, b: (0, i, 0)
    grid_spec = pltpu.PrefetchScalarGridSpec(
        num_scalar_prefetch=2,
        grid=(nq // block_q, steps),
        in_specs=[
            pl.BlockSpec((heads, block_q, hd), row),
            pl.BlockSpec((heads, block_k, hd), kv_map),
            pl.BlockSpec((heads, block_k, hd), kv_map),
            pl.BlockSpec((block_q, 1), lambda i, j, a, b: (i, 0)),
            pl.BlockSpec((1, block_k), ks_map),
            pl.BlockSpec((heads, block_q, 1), row),
            pl.BlockSpec((heads, block_q, 1), row),
            pl.BlockSpec((heads, block_q, hd), row),
        ],
        out_specs=pl.BlockSpec((heads, block_q, hd), row),
        scratch_shapes=[pltpu.VMEM((heads, block_q, hd), jnp.float32)],
    )
    return pl.pallas_call(
        _dq_kernel,
        grid_spec=grid_spec,
        out_shape=jax.ShapeDtypeStruct((heads, nq, hd), jnp.float32),
        compiler_params=pltpu.CompilerParams(
            dimension_semantics=("arbitrary", "arbitrary"), vmem_limit_bytes=100 * 1024 * 1024 // 2
        ),
    )(lo, hi, q, k, v, qs, ks, lse, delta, do)


def flash_dkv(q, k, v, q_ids, k_ids, lse, delta, do, qlo, qhi, block_q, block_k, steps):
    heads, nq, hd = q.shape
    nk = k.shape[1]
    qs = q_ids.reshape(nq, 1)
    ks = k_ids.reshape(1, nk)

    def q_map(j, i, lo_ref, hi_ref):
        return (0, _clamp(lo_ref[j], i, hi_ref[j]), 0)

    def qs_map(j, i, lo_ref, hi_ref):
        return (_clamp(lo_ref[j], i, hi_ref[j]), 0)

    col = lambda j, i, a, b: (0, j, 0)
    grid_spec = pltpu.PrefetchScalarGridSpec(
        num_scalar_prefetch=2,
        grid=(nk // block_k, steps),
        in_specs=[
            pl.BlockSpec((heads, block_q, hd), q_map),
            pl.BlockSpec((heads, block_k, hd), col),
            pl.BlockSpec((heads, block_k, hd), col),
            pl.BlockSpec((block_q, 1), qs_map),
            pl.BlockSpec((1, block_k), lambda j, i, a, b: (0, j)),
            pl.BlockSpec((heads, block_q, 1), q_map),
            pl.BlockSpec((heads, block_q, 1), q_map),
            pl.BlockSpec((heads, block_q, hd), q_map),
        ],
        out_specs=[pl.BlockSpec((heads, block_k, hd), col), pl.BlockSpec((heads, block_k, hd), col)],
        scratch_shapes=[pltpu.VMEM((heads, block_k, hd), jnp.float32), pltpu.VMEM((heads, block_k, hd), jnp.float32)],
    )
    return pl.pallas_call(
        _dkv_kernel,
        grid_spec=grid_spec,
        out_shape=[
            jax.ShapeDtypeStruct((heads, nk, hd), jnp.float32),
            jax.ShapeDtypeStruct((heads, nk, hd), jnp.float32),
        ],
        compiler_params=pltpu.CompilerParams(
            dimension_semantics=("arbitrary", "arbitrary"), vmem_limit_bytes=100 * 1024 * 1024 // 2
        ),
    )(qlo, qhi, q, k, v, qs, ks, lse, delta, do)


def block_ranges(q_ids, k_ids, q_start, q_end, block_q, block_k):
    nq = q_ids.shape[0]
    nk = k_ids.shape[0]
    nqb, nkb = nq // block_q, nk // block_k
    first = q_start.reshape(nqb, block_q)[:, 0]
    last = q_end.reshape(nqb, block_q)[:, block_q - 1]
    lo = jnp.clip(first // block_k, 0, nkb - 1).astype(jnp.int32)
    hi = jnp.clip((last - 1) // block_k, 0, nkb - 1).astype(jnp.int32)
    kb = jnp.arange(nkb, dtype=jnp.int32)
    qb = jnp.arange(nqb, dtype=jnp.int32)
    cover = (lo[:, None] <= kb[None, :]) & (kb[None, :] <= hi[:, None])
    qlo = jnp.min(jnp.where(cover, qb[:, None], nqb), axis=0).astype(jnp.int32)
    qhi = jnp.max(jnp.where(cover, qb[:, None], -1), axis=0).astype(jnp.int32)
    return lo, hi, qlo, qhi


def norm_forward(values, gain, shift):
    center = jnp.mean(values, axis=-1, keepdims=True)
    offsets = values - center
    spread = jnp.mean(offsets * offsets, axis=-1, keepdims=True)
    inverse = lax.rsqrt(spread + 1e-06)
    normed = offsets * inverse
    return (normed * gain + shift, normed, inverse)


def norm_backward(grad_y, normed, inverse, gain):
    grad_normed = grad_y * gain
    mean_one = jnp.mean(grad_normed, axis=-1, keepdims=True)
    mean_two = jnp.mean(grad_normed * normed, axis=-1, keepdims=True)
    return inverse * (grad_normed - mean_one - normed * mean_two)


def activate(values):
    return jax.nn.gelu(values, approximate=False)


def contract_last(left, right):
    return lax.dot_general(left, right, (((1,), (1,)), ((), ())), preferred_element_type=jnp.float32)


def contract_first(left, right):
    return lax.dot_general(left, right, (((0,), (0,)), ((), ())), preferred_element_type=jnp.float32)


def column_sum(values):
    return jnp.sum(values.astype(jnp.float32), axis=0)


def group_segments(lengths, dealing, group_index, group_rows, per_group):
    picked = lax.dynamic_slice_in_dim(dealing, group_index * per_group, per_group)
    match = picked[:, None] == jnp.arange(lengths.shape[0], dtype=jnp.int32)[None, :]
    chosen = jnp.sum(jnp.where(match, lengths[None, :], 0), axis=1)
    ends = jnp.cumsum(chosen)
    starts = ends - chosen
    places = jnp.arange(group_rows, dtype=jnp.int32)
    segment_ids = jnp.sum((places[:, None] >= ends[None, :]).astype(jnp.int32), axis=1)
    return (segment_ids, starts, ends)


def gather_weight(w, rows_over_dp):
    dp = lax.axis_size("dp")
    tens = lax.axis_size("tensor")
    r, c = w.shape
    full = lax.all_gather(w, ("dp", "tensor"), axis=0, tiled=False).reshape(dp, tens, r, c)
    if rows_over_dp:
        return full.transpose(0, 2, 1, 3).reshape(dp * r, tens * c)
    return full.transpose(1, 2, 0, 3).reshape(tens * r, dp * c)


def scatter_grad(g, rows_over_dp):
    dp = lax.axis_size("dp")
    tens = lax.axis_size("tensor")
    if rows_over_dp:
        r, c = g.shape[0] // dp, g.shape[1] // tens
        blocks = g.reshape(dp, r, tens, c).transpose(0, 2, 1, 3)
    else:
        r, c = g.shape[0] // tens, g.shape[1] // dp
        blocks = g.reshape(tens, r, dp, c).transpose(2, 0, 1, 3)
    blocks = blocks.reshape(dp * tens, r, c)
    return lax.psum_scatter(blocks, ("dp", "tensor"), scatter_dimension=0, tiled=True).reshape(r, c)


def scatter_vectors(vectors):
    parts = lax.axis_size("dp") * lax.axis_size("tensor")
    joined = jnp.concatenate([v.reshape(parts, -1) for v in vectors], axis=1)
    summed = lax.psum_scatter(joined, ("dp", "tensor"), scatter_dimension=0, tiled=True)[0]
    out, at = [], 0
    for v in vectors:
        n = v.shape[0] // parts
        out.append(summed[at:at + n])
        at += n
    return out


def halo_plan(rows):
    hops = -(-LONGEST // rows)
    takes = [rows] * (hops - 1) + [LONGEST - rows * (hops - 1)]
    return takes


def shift_rows(values, distance, count):
    if distance >= count:
        return jnp.zeros_like(values)
    if distance > 0:
        pairs = [(s, s + distance) for s in range(count - distance)]
    else:
        pairs = [(s - distance, s) for s in range(count + distance)]
    return lax.ppermute(values, "tensor", pairs)


def build_window(own, takes, count):
    rows = own.shape[0]
    left = [shift_rows(own[rows - take:], d + 1, count) for d, take in enumerate(takes)]
    right = [shift_rows(own[:take], -(d + 1), count) for d, take in enumerate(takes)]
    return jnp.concatenate(left[::-1] + [own] + right, axis=0)


def return_window(values, takes, count):
    rows = values.shape[0] - 2 * LONGEST
    total = values[LONGEST:LONGEST + rows]
    at = LONGEST
    for d, take in enumerate(takes):
        piece = values[at - take:at].astype(jnp.bfloat16)
        at -= take
        back = shift_rows(piece, -(d + 1), count).astype(jnp.float32)
        total = total + jnp.pad(back, ((rows - take, 0), (0, 0)))
    at = LONGEST + rows
    for d, take in enumerate(takes):
        piece = values[at:at + take].astype(jnp.bfloat16)
        at += take
        back = shift_rows(piece, d + 1, count).astype(jnp.float32)
        total = total + jnp.pad(back, ((0, rows - take), (0, 0)))
    return total


def to_heads(values):
    rows, width = values.shape
    return values.reshape(rows, width // HEAD_DIM, HEAD_DIM).transpose(1, 0, 2)


def from_heads(values):
    heads, rows, hd = values.shape
    return values.transpose(1, 0, 2).reshape(rows, heads * hd)


def shards(tokens, lengths, dealing, w_query, w_key, w_value, w_out, w_inner, w_outer, b_query, b_value, b_out, b_inner, b_outer, gain_attn, shift_attn, gain_ffn, shift_ffn, grad_out):
    count = lax.axis_size("tensor")
    tens_index = lax.axis_index("tensor")
    group_index = lax.axis_index("dp")
    rows = tokens.shape[0]
    group_rows = rows * count
    per_group = lengths.shape[0] // lax.axis_size("dp")
    takes = halo_plan(rows)
    window = rows + 2 * LONGEST
    seg, starts, ends = group_segments(lengths, dealing, group_index, group_rows, per_group)
    base = rows * tens_index - LONGEST
    places = base + jnp.arange(window, dtype=jnp.int32)
    valid = (places >= 0) & (places < group_rows)
    k_ids = jnp.where(valid, jnp.take(seg, jnp.clip(places, 0, group_rows - 1)), -1).astype(jnp.int32)
    q_ids = lax.dynamic_slice_in_dim(seg, rows * tens_index, rows)
    q_start = jnp.take(starts, q_ids) - base
    q_end = jnp.take(ends, q_ids) - base
    lo, hi, qlo, qhi = block_ranges(q_ids, k_ids, q_start, q_end, BLOCK, BLOCK)
    nkb = window // BLOCK
    kv_steps = min(nkb, (BLOCK + 2 * (LONGEST - 1)) // BLOCK + 2)
    q_steps = rows // BLOCK

    wq = gather_weight(w_query, True)
    wk = gather_weight(w_key, True)
    wv = gather_weight(w_value, True)
    wo = gather_weight(w_out, False)
    wi = gather_weight(w_inner, True)
    wf = gather_weight(w_outer, False)
    gain_one = gain_attn.astype(jnp.float32)
    gain_two = gain_ffn.astype(jnp.float32)

    x_own = tokens
    x_win = build_window(tokens, takes, count)
    query = (jnp.dot(x_own, wq, preferred_element_type=jnp.float32) + b_query.astype(jnp.float32)).astype(jnp.bfloat16)
    key_w = jnp.dot(x_win, wk, preferred_element_type=jnp.float32).astype(jnp.bfloat16)
    value_w = (jnp.dot(x_win, wv, preferred_element_type=jnp.float32) + b_value.astype(jnp.float32)).astype(jnp.bfloat16)
    q_h, k_h, v_h = to_heads(query), to_heads(key_w), to_heads(value_w)
    ctx_h, lse = flash_forward(q_h, k_h, v_h, q_ids, k_ids, lo, hi, BLOCK, BLOCK, kv_steps)
    context = from_heads(ctx_h).astype(jnp.bfloat16)
    attn = jnp.dot(context, wo, preferred_element_type=jnp.float32) + b_out.astype(jnp.float32)
    hidden, norm_one, inverse_one = norm_forward(tokens.astype(jnp.float32) + attn, gain_one, shift_attn.astype(jnp.float32))
    hidden_low = hidden.astype(jnp.bfloat16)
    pre_act = jnp.dot(hidden_low, wi, preferred_element_type=jnp.float32) + b_inner.astype(jnp.float32)
    act = activate(pre_act).astype(jnp.bfloat16)
    ffn = jnp.dot(act, wf, preferred_element_type=jnp.float32) + b_outer.astype(jnp.float32)
    output, norm_two, inverse_two = norm_forward(hidden + ffn, gain_two, shift_ffn.astype(jnp.float32))

    grad_y = grad_out.astype(jnp.float32)
    grad_resid_two = norm_backward(grad_y, norm_two, inverse_two, gain_two)
    grad_ffn = grad_resid_two.astype(jnp.bfloat16)
    grad_outer_w = contract_first(act, grad_ffn)
    grad_act = contract_last(grad_ffn, wf)
    unused, gelu_pull = jax.vjp(activate, pre_act)
    grad_pre = gelu_pull(grad_act)[0].astype(jnp.bfloat16)
    grad_inner_w = contract_first(hidden_low, grad_pre)
    grad_hidden = grad_resid_two + contract_last(grad_pre, wi)
    grad_resid_one = norm_backward(grad_hidden, norm_one, inverse_one, gain_one)
    grad_attn = grad_resid_one.astype(jnp.bfloat16)
    grad_out_w = contract_first(context, grad_attn)
    grad_context = contract_last(grad_attn, wo).astype(jnp.bfloat16)
    do_h = to_heads(grad_context)
    delta = jnp.sum(do_h.astype(jnp.float32) * ctx_h, axis=-1, keepdims=True)
    dq_h = flash_dq(q_h, k_h, v_h, q_ids, k_ids, lse, delta, do_h, lo, hi, BLOCK, BLOCK, kv_steps)
    dk_h, dv_h = flash_dkv(q_h, k_h, v_h, q_ids, k_ids, lse, delta, do_h, qlo, qhi, BLOCK, BLOCK, q_steps)
    grad_query = from_heads(dq_h).astype(jnp.bfloat16)
    grad_key = from_heads(dk_h).astype(jnp.bfloat16)
    grad_value = from_heads(dv_h).astype(jnp.bfloat16)
    grad_query_w = contract_first(x_own, grad_query)
    grad_key_w = contract_first(x_win, grad_key)
    grad_value_w = contract_first(x_win, grad_value)
    grad_win = contract_last(grad_key, wk) + contract_last(grad_value, wv)
    grad_tokens = grad_resid_one + contract_last(grad_query, wq) + return_window(grad_win, takes, count)

    summed = (
        scatter_grad(grad_query_w, True),
        scatter_grad(grad_key_w, True),
        scatter_grad(grad_value_w, True),
        scatter_grad(grad_out_w, False),
        scatter_grad(grad_inner_w, True),
        scatter_grad(grad_outer_w, False),
    )
    small = scatter_vectors([
        column_sum(grad_query),
        column_sum(grad_value),
        column_sum(grad_attn),
        column_sum(grad_pre),
        column_sum(grad_ffn),
        jnp.sum(grad_hidden * norm_one, axis=0),
        jnp.sum(grad_hidden, axis=0),
        jnp.sum(grad_y * norm_two, axis=0),
        jnp.sum(grad_y, axis=0),
    ])
    return (output.astype(jnp.bfloat16), grad_tokens) + summed + tuple(small)


def solution(mesh):
    rows = P(("dp", "tensor"), None)
    vec = P(("dp", "tensor"))
    return jax.shard_map(
        shards,
        mesh=mesh,
        in_specs=(rows, P(), P(), P("dp", "tensor"), P("dp", "tensor"), P("dp", "tensor"), P("tensor", "dp"), P("dp", "tensor"), P("tensor", "dp"), P(), P(), P(), P(), P(), P(), P(), P(), P(), rows),
        out_specs=(rows, rows, P("dp", "tensor"), P("dp", "tensor"), P("dp", "tensor"), P("tensor", "dp"), P("dp", "tensor"), P("tensor", "dp")) + (vec,) * 9,
        check_vma=False,
    )
```

```python
import math

import jax
import jax.numpy as jnp
from jax import lax
from jax.experimental import pallas as pl
from jax.experimental.pallas import tpu as pltpu
from jax.sharding import PartitionSpec as P

HEAD_DIM = 64
LONGEST = 1024
BLOCK = 256

NEG = -1e30


def _fwd_kernel(lo_ref, hi_ref, q_ref, k_ref, v_ref, qs_ref, ks_ref, o_ref, lse_ref, m_sc, l_sc, acc_sc):
    i = pl.program_id(0)
    j = pl.program_id(1)
    kv = lo_ref[i] + j

    @pl.when(j == 0)
    def _():
        m_sc[...] = jnp.full_like(m_sc, NEG)
        l_sc[...] = jnp.zeros_like(l_sc)
        acc_sc[...] = jnp.zeros_like(acc_sc)

    @pl.when(kv <= hi_ref[i])
    def _():
        s = jnp.einsum("hqd,hkd->hqk", q_ref[...], k_ref[...], preferred_element_type=jnp.float32) * 0.125
        mask = (qs_ref[...] == ks_ref[...])[None]
        s = jnp.where(mask, s, NEG)
        m_old = m_sc[...]
        m_new = jnp.maximum(m_old, jnp.max(s, axis=-1, keepdims=True))
        alpha = jnp.exp(m_old - m_new)
        p = jnp.where(mask, jnp.exp(s - m_new), 0.0)
        l_sc[...] = alpha * l_sc[...] + jnp.sum(p, axis=-1, keepdims=True)
        acc_sc[...] = alpha * acc_sc[...] + jnp.einsum(
            "hqk,hkd->hqd", p.astype(jnp.bfloat16), v_ref[...], preferred_element_type=jnp.float32
        )
        m_sc[...] = m_new

    @pl.when(j == pl.num_programs(1) - 1)
    def _():
        o_ref[...] = acc_sc[...] / l_sc[...]
        lse_ref[...] = m_sc[...] + jnp.log(l_sc[...])


def _dq_kernel(lo_ref, hi_ref, q_ref, k_ref, v_ref, qs_ref, ks_ref, lse_ref, dl_ref, do_ref, dq_ref, acc_sc):
    i = pl.program_id(0)
    j = pl.program_id(1)
    kv = lo_ref[i] + j

    @pl.when(j == 0)
    def _():
        acc_sc[...] = jnp.zeros_like(acc_sc)

    @pl.when(kv <= hi_ref[i])
    def _():
        k = k_ref[...]
        s = jnp.einsum("hqd,hkd->hqk", q_ref[...], k, preferred_element_type=jnp.float32) * 0.125
        mask = (qs_ref[...] == ks_ref[...])[None]
        p = jnp.where(mask, jnp.exp(s - lse_ref[...]), 0.0)
        dp = jnp.einsum("hqd,hkd->hqk", do_ref[...], v_ref[...], preferred_element_type=jnp.float32)
        ds = (p * (dp - dl_ref[...])).astype(jnp.bfloat16)
        acc_sc[...] += jnp.einsum("hqk,hkd->hqd", ds, k, preferred_element_type=jnp.float32)

    @pl.when(j == pl.num_programs(1) - 1)
    def _():
        dq_ref[...] = acc_sc[...] * 0.125


def _dkv_kernel(lo_ref, hi_ref, q_ref, k_ref, v_ref, qs_ref, ks_ref, lse_ref, dl_ref, do_ref, dk_ref, dv_ref, dk_sc, dv_sc):
    j = pl.program_id(0)
    i = pl.program_id(1)
    qb = lo_ref[j] + i

    @pl.when(i == 0)
    def _():
        dk_sc[...] = jnp.zeros_like(dk_sc)
        dv_sc[...] = jnp.zeros_like(dv_sc)

    @pl.when(qb <= hi_ref[j])
    def _():
        q = q_ref[...]
        do = do_ref[...]
        s = jnp.einsum("hqd,hkd->hqk", q, k_ref[...], preferred_element_type=jnp.float32) * 0.125
        mask = (qs_ref[...] == ks_ref[...])[None]
        p = jnp.where(mask, jnp.exp(s - lse_ref[...]), 0.0)
        dp = jnp.einsum("hqd,hkd->hqk", do, v_ref[...], preferred_element_type=jnp.float32)
        ds = (p * (dp - dl_ref[...])).astype(jnp.bfloat16)
        dv_sc[...] += jnp.einsum("hqk,hqd->hkd", p.astype(jnp.bfloat16), do, preferred_element_type=jnp.float32)
        dk_sc[...] += jnp.einsum("hqk,hqd->hkd", ds, q, preferred_element_type=jnp.float32)

    @pl.when(i == pl.num_programs(1) - 1)
    def _():
        dk_ref[...] = dk_sc[...] * 0.125
        dv_ref[...] = dv_sc[...]


def _clamp(start, step, last):
    return jnp.minimum(start + step, jnp.maximum(last, 0))


def flash_forward(q, k, v, q_ids, k_ids, lo, hi, block_q, block_k, steps):
    heads, nq, hd = q.shape
    nk = k.shape[1]
    qs = q_ids.reshape(nq, 1)
    ks = k_ids.reshape(1, nk)

    def kv_map(i, j, lo_ref, hi_ref):
        return (0, _clamp(lo_ref[i], j, hi_ref[i]), 0)

    def ks_map(i, j, lo_ref, hi_ref):
        return (0, _clamp(lo_ref[i], j, hi_ref[i]))

    grid_spec = pltpu.PrefetchScalarGridSpec(
        num_scalar_prefetch=2,
        grid=(nq // block_q, steps),
        in_specs=[
            pl.BlockSpec((heads, block_q, hd), lambda i, j, a, b: (0, i, 0)),
            pl.BlockSpec((heads, block_k, hd), kv_map),
            pl.BlockSpec((heads, block_k, hd), kv_map),
            pl.BlockSpec((block_q, 1), lambda i, j, a, b: (i, 0)),
            pl.BlockSpec((1, block_k), ks_map),
        ],
        out_specs=[
            pl.BlockSpec((heads, block_q, hd), lambda i, j, a, b: (0, i, 0)),
            pl.BlockSpec((heads, block_q, 1), lambda i, j, a, b: (0, i, 0)),
        ],
        scratch_shapes=[
            pltpu.VMEM((heads, block_q, 1), jnp.float32),
            pltpu.VMEM((heads, block_q, 1), jnp.float32),
            pltpu.VMEM((heads, block_q, hd), jnp.float32),
        ],
    )
    return pl.pallas_call(
        _fwd_kernel,
        grid_spec=grid_spec,
        out_shape=[
            jax.ShapeDtypeStruct((heads, nq, hd), jnp.float32),
            jax.ShapeDtypeStruct((heads, nq, 1), jnp.float32),
        ],
        compiler_params=pltpu.CompilerParams(
            dimension_semantics=("arbitrary", "arbitrary"), vmem_limit_bytes=100 * 1024 * 1024 // 2
        ),
    )(lo, hi, q, k, v, qs, ks)


def flash_dq(q, k, v, q_ids, k_ids, lse, delta, do, lo, hi, block_q, block_k, steps):
    heads, nq, hd = q.shape
    nk = k.shape[1]
    qs = q_ids.reshape(nq, 1)
    ks = k_ids.reshape(1, nk)

    def kv_map(i, j, lo_ref, hi_ref):
        return (0, _clamp(lo_ref[i], j, hi_ref[i]), 0)

    def ks_map(i, j, lo_ref, hi_ref):
        return (0, _clamp(lo_ref[i], j, hi_ref[i]))

    row = lambda i, j, a, b: (0, i, 0)
    grid_spec = pltpu.PrefetchScalarGridSpec(
        num_scalar_prefetch=2,
        grid=(nq // block_q, steps),
        in_specs=[
            pl.BlockSpec((heads, block_q, hd), row),
            pl.BlockSpec((heads, block_k, hd), kv_map),
            pl.BlockSpec((heads, block_k, hd), kv_map),
            pl.BlockSpec((block_q, 1), lambda i, j, a, b: (i, 0)),
            pl.BlockSpec((1, block_k), ks_map),
            pl.BlockSpec((heads, block_q, 1), row),
            pl.BlockSpec((heads, block_q, 1), row),
            pl.BlockSpec((heads, block_q, hd), row),
        ],
        out_specs=pl.BlockSpec((heads, block_q, hd), row),
        scratch_shapes=[pltpu.VMEM((heads, block_q, hd), jnp.float32)],
    )
    return pl.pallas_call(
        _dq_kernel,
        grid_spec=grid_spec,
        out_shape=jax.ShapeDtypeStruct((heads, nq, hd), jnp.float32),
        compiler_params=pltpu.CompilerParams(
            dimension_semantics=("arbitrary", "arbitrary"), vmem_limit_bytes=100 * 1024 * 1024 // 2
        ),
    )(lo, hi, q, k, v, qs, ks, lse, delta, do)


def flash_dkv(q, k, v, q_ids, k_ids, lse, delta, do, qlo, qhi, block_q, block_k, steps):
    heads, nq, hd = q.shape
    nk = k.shape[1]
    qs = q_ids.reshape(nq, 1)
    ks = k_ids.reshape(1, nk)

    def q_map(j, i, lo_ref, hi_ref):
        return (0, _clamp(lo_ref[j], i, hi_ref[j]), 0)

    def qs_map(j, i, lo_ref, hi_ref):
        return (_clamp(lo_ref[j], i, hi_ref[j]), 0)

    col = lambda j, i, a, b: (0, j, 0)
    grid_spec = pltpu.PrefetchScalarGridSpec(
        num_scalar_prefetch=2,
        grid=(nk // block_k, steps),
        in_specs=[
            pl.BlockSpec((heads, block_q, hd), q_map),
            pl.BlockSpec((heads, block_k, hd), col),
            pl.BlockSpec((heads, block_k, hd), col),
            pl.BlockSpec((block_q, 1), qs_map),
            pl.BlockSpec((1, block_k), lambda j, i, a, b: (0, j)),
            pl.BlockSpec((heads, block_q, 1), q_map),
            pl.BlockSpec((heads, block_q, 1), q_map),
            pl.BlockSpec((heads, block_q, hd), q_map),
        ],
        out_specs=[pl.BlockSpec((heads, block_k, hd), col), pl.BlockSpec((heads, block_k, hd), col)],
        scratch_shapes=[pltpu.VMEM((heads, block_k, hd), jnp.float32), pltpu.VMEM((heads, block_k, hd), jnp.float32)],
    )
    return pl.pallas_call(
        _dkv_kernel,
        grid_spec=grid_spec,
        out_shape=[
            jax.ShapeDtypeStruct((heads, nk, hd), jnp.float32),
            jax.ShapeDtypeStruct((heads, nk, hd), jnp.float32),
        ],
        compiler_params=pltpu.CompilerParams(
            dimension_semantics=("arbitrary", "arbitrary"), vmem_limit_bytes=100 * 1024 * 1024 // 2
        ),
    )(qlo, qhi, q, k, v, qs, ks, lse, delta, do)


def block_ranges(q_ids, k_ids, q_start, q_end, block_q, block_k):
    nq = q_ids.shape[0]
    nk = k_ids.shape[0]
    nqb, nkb = nq // block_q, nk // block_k
    first = q_start.reshape(nqb, block_q)[:, 0]
    last = q_end.reshape(nqb, block_q)[:, block_q - 1]
    lo = jnp.clip(first // block_k, 0, nkb - 1).astype(jnp.int32)
    hi = jnp.clip((last - 1) // block_k, 0, nkb - 1).astype(jnp.int32)
    kb = jnp.arange(nkb, dtype=jnp.int32)
    qb = jnp.arange(nqb, dtype=jnp.int32)
    cover = (lo[:, None] <= kb[None, :]) & (kb[None, :] <= hi[:, None])
    qlo = jnp.min(jnp.where(cover, qb[:, None], nqb), axis=0).astype(jnp.int32)
    qhi = jnp.max(jnp.where(cover, qb[:, None], -1), axis=0).astype(jnp.int32)
    return lo, hi, qlo, qhi


def norm_forward(values, gain, shift):
    center = jnp.mean(values, axis=-1, keepdims=True)
    offsets = values - center
    spread = jnp.mean(offsets * offsets, axis=-1, keepdims=True)
    inverse = lax.rsqrt(spread + 1e-06)
    normed = offsets * inverse
    return (normed * gain + shift, normed, inverse)


def norm_backward(grad_y, normed, inverse, gain):
    grad_normed = grad_y * gain
    mean_one = jnp.mean(grad_normed, axis=-1, keepdims=True)
    mean_two = jnp.mean(grad_normed * normed, axis=-1, keepdims=True)
    return inverse * (grad_normed - mean_one - normed * mean_two)


def activate(values):
    return jax.nn.gelu(values, approximate=False)


def contract_last(left, right):
    return lax.dot_general(left, right, (((1,), (1,)), ((), ())), preferred_element_type=jnp.float32)


def contract_first(left, right):
    return lax.dot_general(left, right, (((0,), (0,)), ((), ())), preferred_element_type=jnp.float32)


def column_sum(values):
    return jnp.sum(values.astype(jnp.float32), axis=0)


def group_segments(lengths, dealing, group_index, group_rows, per_group):
    picked = lax.dynamic_slice_in_dim(dealing, group_index * per_group, per_group)
    match = picked[:, None] == jnp.arange(lengths.shape[0], dtype=jnp.int32)[None, :]
    chosen = jnp.sum(jnp.where(match, lengths[None, :], 0), axis=1)
    ends = jnp.cumsum(chosen)
    starts = ends - chosen
    places = jnp.arange(group_rows, dtype=jnp.int32)
    segment_ids = jnp.sum((places[:, None] >= ends[None, :]).astype(jnp.int32), axis=1)
    return (segment_ids, starts, ends)


def _block_layout(w, rows_over_dp, dp, tens):
    if rows_over_dp:
        r, c = w.shape[0] // dp, w.shape[1] // tens
        return w.reshape(dp, r, tens, c).transpose(0, 2, 1, 3).reshape(dp * tens, r * c)
    r, c = w.shape[0] // tens, w.shape[1] // dp
    return w.reshape(tens, r, dp, c).transpose(2, 0, 1, 3).reshape(dp * tens, r * c)


def gather_weights(shards_and_kinds):
    dp = lax.axis_size("dp")
    tens = lax.axis_size("tensor")
    flat = jnp.concatenate([w.reshape(-1) for w, _ in shards_and_kinds])
    full = lax.all_gather(flat, ("dp", "tensor"), axis=0, tiled=False)
    out, at = [], 0
    for w, rows_over_dp in shards_and_kinds:
        r, c = w.shape
        part = full[:, at:at + r * c].reshape(dp, tens, r, c)
        at += r * c
        if rows_over_dp:
            out.append(part.transpose(0, 2, 1, 3).reshape(dp * r, tens * c))
        else:
            out.append(part.transpose(1, 2, 0, 3).reshape(tens * r, dp * c))
    return out


def pack_grads(grads_and_kinds, extra=()):
    dp = lax.axis_size("dp")
    tens = lax.axis_size("tensor")
    parts = dp * tens
    blocks = [_block_layout(g.astype(jnp.bfloat16), k, dp, tens) for g, k in grads_and_kinds]
    blocks += [v.astype(jnp.bfloat16).reshape(parts, -1) for v in extra]
    joined = jnp.concatenate(blocks, axis=1)
    width = joined.shape[1]
    padded = -(-width // 1024) * 1024
    return jnp.pad(joined, ((0, 0), (0, padded - width))).reshape(parts, padded // 128, 128)


def unpack_grads(joined, grads_and_kinds, extra=()):
    dp = lax.axis_size("dp")
    tens = lax.axis_size("tensor")
    parts = dp * tens
    summed = lax.psum_scatter(joined, ("dp", "tensor"), scatter_dimension=0, tiled=True)
    summed = summed.reshape(-1).astype(jnp.float32)
    out, at = [], 0
    for g, k in grads_and_kinds:
        if k:
            r, c = g.shape[0] // dp, g.shape[1] // tens
        else:
            r, c = g.shape[0] // tens, g.shape[1] // dp
        out.append(summed[at:at + r * c].reshape(r, c))
        at += r * c
    for v in extra:
        n = v.shape[0] // parts
        out.append(summed[at:at + n])
        at += n
    return out


def scatter_vectors(vectors):
    parts = lax.axis_size("dp") * lax.axis_size("tensor")
    joined = jnp.concatenate([v.reshape(parts, -1) for v in vectors], axis=1)
    width = joined.shape[1]
    padded = -(-width // 1024) * 1024
    joined = jnp.pad(joined, ((0, 0), (0, padded - width))).reshape(parts, padded // 128, 128)
    summed = lax.psum_scatter(joined, ("dp", "tensor"), scatter_dimension=0, tiled=True)
    summed = summed.reshape(padded)[:width]
    out, at = [], 0
    for v in vectors:
        n = v.shape[0] // parts
        out.append(summed[at:at + n])
        at += n
    return out


def halo_plan(rows):
    hops = -(-LONGEST // rows)
    takes = [rows] * (hops - 1) + [LONGEST - rows * (hops - 1)]
    return takes


def shift_rows(values, distance, count):
    if distance >= count:
        return jnp.zeros_like(values)
    if distance > 0:
        pairs = [(s, s + distance) for s in range(count - distance)]
    else:
        pairs = [(s - distance, s) for s in range(count + distance)]
    return lax.ppermute(values, "tensor", pairs)


def build_window(own, takes, count):
    rows = own.shape[0]
    left = [shift_rows(own[rows - take:], d + 1, count) for d, take in enumerate(takes)]
    right = [shift_rows(own[:take], -(d + 1), count) for d, take in enumerate(takes)]
    return jnp.concatenate(left[::-1] + [own] + right, axis=0)


def return_window(values, takes, count):
    rows = values.shape[0] - 2 * LONGEST
    total = values[LONGEST:LONGEST + rows]
    at = LONGEST
    for d, take in enumerate(takes):
        piece = values[at - take:at].astype(jnp.bfloat16)
        at -= take
        back = shift_rows(piece, -(d + 1), count).astype(jnp.float32)
        total = total + jnp.pad(back, ((rows - take, 0), (0, 0)))
    at = LONGEST + rows
    for d, take in enumerate(takes):
        piece = values[at:at + take].astype(jnp.bfloat16)
        at += take
        back = shift_rows(piece, d + 1, count).astype(jnp.float32)
        total = total + jnp.pad(back, ((0, rows - take), (0, 0)))
    return total


def to_heads(values):
    rows, width = values.shape
    return values.reshape(rows, width // HEAD_DIM, HEAD_DIM).transpose(1, 0, 2)


def from_heads(values):
    heads, rows, hd = values.shape
    return values.transpose(1, 0, 2).reshape(rows, heads * hd)


def shards(tokens, lengths, dealing, w_query, w_key, w_value, w_out, w_inner, w_outer, b_query, b_value, b_out, b_inner, b_outer, gain_attn, shift_attn, gain_ffn, shift_ffn, grad_out):
    count = lax.axis_size("tensor")
    tens_index = lax.axis_index("tensor")
    group_index = lax.axis_index("dp")
    rows = tokens.shape[0]
    group_rows = rows * count
    per_group = lengths.shape[0] // lax.axis_size("dp")
    takes = halo_plan(rows)
    window = rows + 2 * LONGEST
    seg, starts, ends = group_segments(lengths, dealing, group_index, group_rows, per_group)
    base = rows * tens_index - LONGEST
    places = base + jnp.arange(window, dtype=jnp.int32)
    valid = (places >= 0) & (places < group_rows)
    k_ids = jnp.where(valid, jnp.take(seg, jnp.clip(places, 0, group_rows - 1)), -1).astype(jnp.int32)
    q_ids = lax.dynamic_slice_in_dim(seg, rows * tens_index, rows)
    q_start = jnp.take(starts, q_ids) - base
    q_end = jnp.take(ends, q_ids) - base
    lo, hi, qlo, qhi = block_ranges(q_ids, k_ids, q_start, q_end, BLOCK, BLOCK)
    nkb = window // BLOCK
    kv_steps = min(nkb, (BLOCK + 2 * (LONGEST - 1)) // BLOCK + 2)
    q_steps = rows // BLOCK

    wq, wk, wv = gather_weights([(w_query, True), (w_key, True), (w_value, True)])
    wo, wi, wf = gather_weights([(w_out, False), (w_inner, True), (w_outer, False)])
    gain_one = gain_attn.astype(jnp.float32)
    gain_two = gain_ffn.astype(jnp.float32)

    x_own = tokens
    x_win = build_window(tokens, takes, count)
    query = (jnp.dot(x_own, wq, preferred_element_type=jnp.float32) + b_query.astype(jnp.float32)).astype(jnp.bfloat16)
    key_w = jnp.dot(x_win, wk, preferred_element_type=jnp.float32).astype(jnp.bfloat16)
    value_w = (jnp.dot(x_win, wv, preferred_element_type=jnp.float32) + b_value.astype(jnp.float32)).astype(jnp.bfloat16)
    q_h, k_h, v_h = to_heads(query), to_heads(key_w), to_heads(value_w)
    ctx_h, lse = flash_forward(q_h, k_h, v_h, q_ids, k_ids, lo, hi, BLOCK, BLOCK, kv_steps)
    context = from_heads(ctx_h).astype(jnp.bfloat16)
    attn = jnp.dot(context, wo, preferred_element_type=jnp.float32) + b_out.astype(jnp.float32)
    hidden, norm_one, inverse_one = norm_forward(tokens.astype(jnp.float32) + attn, gain_one, shift_attn.astype(jnp.float32))
    hidden_low = hidden.astype(jnp.bfloat16)
    pre_act = jnp.dot(hidden_low, wi, preferred_element_type=jnp.float32) + b_inner.astype(jnp.float32)
    act = activate(pre_act).astype(jnp.bfloat16)
    ffn = jnp.dot(act, wf, preferred_element_type=jnp.float32) + b_outer.astype(jnp.float32)
    output, norm_two, inverse_two = norm_forward(hidden + ffn, gain_two, shift_ffn.astype(jnp.float32))

    grad_y = grad_out.astype(jnp.float32)
    grad_resid_two = norm_backward(grad_y, norm_two, inverse_two, gain_two)
    grad_ffn = grad_resid_two.astype(jnp.bfloat16)
    grad_outer_w = contract_first(act, grad_ffn)
    grad_act = contract_last(grad_ffn, wf)
    unused, gelu_pull = jax.vjp(activate, pre_act)
    grad_pre = gelu_pull(grad_act)[0].astype(jnp.bfloat16)
    grad_inner_w = contract_first(hidden_low, grad_pre)
    grad_hidden = grad_resid_two + contract_last(grad_pre, wi)
    grad_resid_one = norm_backward(grad_hidden, norm_one, inverse_one, gain_one)
    grad_attn = grad_resid_one.astype(jnp.bfloat16)
    grad_out_w = contract_first(context, grad_attn)
    grad_context = contract_last(grad_attn, wo).astype(jnp.bfloat16)
    late = [
        column_sum(grad_attn),
        column_sum(grad_pre),
        column_sum(grad_ffn),
        jnp.sum(grad_hidden * norm_one, axis=0),
        jnp.sum(grad_hidden, axis=0),
        jnp.sum(grad_y * norm_two, axis=0),
        jnp.sum(grad_y, axis=0),
    ]
    early_kinds = [(grad_out_w, False), (grad_inner_w, True), (grad_outer_w, False)]
    early = pack_grads(early_kinds)
    grad_context, early, late = lax.optimization_barrier((grad_context, early, late))
    late = scatter_vectors(late)
    g_out, g_inner, g_outer = unpack_grads(early, early_kinds)
    do_h = to_heads(grad_context)
    delta = jnp.sum(do_h.astype(jnp.float32) * ctx_h, axis=-1, keepdims=True)
    dq_h = flash_dq(q_h, k_h, v_h, q_ids, k_ids, lse, delta, do_h, lo, hi, BLOCK, BLOCK, kv_steps)
    dk_h, dv_h = flash_dkv(q_h, k_h, v_h, q_ids, k_ids, lse, delta, do_h, qlo, qhi, BLOCK, BLOCK, q_steps)
    grad_query = from_heads(dq_h).astype(jnp.bfloat16)
    grad_key = from_heads(dk_h).astype(jnp.bfloat16)
    grad_value = from_heads(dv_h).astype(jnp.bfloat16)
    grad_query_w = contract_first(x_own, grad_query)
    grad_key_w = contract_first(x_win, grad_key)
    grad_value_w = contract_first(x_win, grad_value)
    grad_win = contract_last(grad_key, wk) + contract_last(grad_value, wv)
    grad_tokens = grad_resid_one + contract_last(grad_query, wq) + return_window(grad_win, takes, count)

    late_kinds = [(grad_query_w, True), (grad_key_w, True), (grad_value_w, True)]
    extra = (column_sum(grad_query), column_sum(grad_value))
    g_query, g_key, g_value, g_bq, g_bv = unpack_grads(pack_grads(late_kinds, extra), late_kinds, extra)
    summed = (g_query, g_key, g_value, g_out, g_inner, g_outer)
    small = [g_bq, g_bv] + late
    return (output.astype(jnp.bfloat16), grad_tokens) + summed + tuple(small)


def solution(mesh):
    rows = P(("dp", "tensor"), None)
    vec = P(("dp", "tensor"))
    return jax.shard_map(
        shards,
        mesh=mesh,
        in_specs=(rows, P(), P(), P("dp", "tensor"), P("dp", "tensor"), P("dp", "tensor"), P("tensor", "dp"), P("dp", "tensor"), P("tensor", "dp"), P(), P(), P(), P(), P(), P(), P(), P(), P(), rows),
        out_specs=(rows, rows, P("dp", "tensor"), P("dp", "tensor"), P("dp", "tensor"), P("tensor", "dp"), P("dp", "tensor"), P("tensor", "dp")) + (vec,) * 9,
        check_vma=False,
    )
```

```python
import math

import jax
import jax.numpy as jnp
from jax import lax
from jax.experimental import pallas as pl
from jax.experimental.pallas import tpu as pltpu
from jax.sharding import PartitionSpec as P

HEAD_DIM = 64
LONGEST = 1024
BLOCK = 256

NEG = -1e30


def _fwd_kernel(lo_ref, hi_ref, q_ref, k_ref, v_ref, qs_ref, ks_ref, o_ref, lse_ref, m_sc, l_sc, acc_sc):
    i = pl.program_id(0)
    j = pl.program_id(1)
    kv = lo_ref[i] + j

    @pl.when(j == 0)
    def _():
        m_sc[...] = jnp.full_like(m_sc, NEG)
        l_sc[...] = jnp.zeros_like(l_sc)
        acc_sc[...] = jnp.zeros_like(acc_sc)

    @pl.when(kv <= hi_ref[i])
    def _():
        s = jnp.einsum("hqd,hkd->hqk", q_ref[...], k_ref[...], preferred_element_type=jnp.float32) * 0.125
        mask = (qs_ref[...] == ks_ref[...])[None]
        s = jnp.where(mask, s, NEG)
        m_old = m_sc[...]
        m_new = jnp.maximum(m_old, jnp.max(s, axis=-1, keepdims=True))
        alpha = jnp.exp(m_old - m_new)
        p = jnp.where(mask, jnp.exp(s - m_new), 0.0)
        l_sc[...] = alpha * l_sc[...] + jnp.sum(p, axis=-1, keepdims=True)
        acc_sc[...] = alpha * acc_sc[...] + jnp.einsum(
            "hqk,hkd->hqd", p.astype(jnp.bfloat16), v_ref[...], preferred_element_type=jnp.float32
        )
        m_sc[...] = m_new

    @pl.when(j == pl.num_programs(1) - 1)
    def _():
        o_ref[...] = acc_sc[...] / l_sc[...]
        lse_ref[...] = m_sc[...] + jnp.log(l_sc[...])


def _dq_kernel(lo_ref, hi_ref, q_ref, k_ref, v_ref, qs_ref, ks_ref, lse_ref, dl_ref, do_ref, dq_ref, acc_sc):
    i = pl.program_id(0)
    j = pl.program_id(1)
    kv = lo_ref[i] + j

    @pl.when(j == 0)
    def _():
        acc_sc[...] = jnp.zeros_like(acc_sc)

    @pl.when(kv <= hi_ref[i])
    def _():
        k = k_ref[...]
        s = jnp.einsum("hqd,hkd->hqk", q_ref[...], k, preferred_element_type=jnp.float32) * 0.125
        mask = (qs_ref[...] == ks_ref[...])[None]
        p = jnp.where(mask, jnp.exp(s - lse_ref[...]), 0.0)
        dp = jnp.einsum("hqd,hkd->hqk", do_ref[...], v_ref[...], preferred_element_type=jnp.float32)
        ds = (p * (dp - dl_ref[...])).astype(jnp.bfloat16)
        acc_sc[...] += jnp.einsum("hqk,hkd->hqd", ds, k, preferred_element_type=jnp.float32)

    @pl.when(j == pl.num_programs(1) - 1)
    def _():
        dq_ref[...] = acc_sc[...] * 0.125


def _dkv_kernel(lo_ref, hi_ref, q_ref, k_ref, v_ref, qs_ref, ks_ref, lse_ref, dl_ref, do_ref, dk_ref, dv_ref, dk_sc, dv_sc):
    j = pl.program_id(0)
    i = pl.program_id(1)
    qb = lo_ref[j] + i

    @pl.when(i == 0)
    def _():
        dk_sc[...] = jnp.zeros_like(dk_sc)
        dv_sc[...] = jnp.zeros_like(dv_sc)

    @pl.when(qb <= hi_ref[j])
    def _():
        q = q_ref[...]
        do = do_ref[...]
        s = jnp.einsum("hqd,hkd->hqk", q, k_ref[...], preferred_element_type=jnp.float32) * 0.125
        mask = (qs_ref[...] == ks_ref[...])[None]
        p = jnp.where(mask, jnp.exp(s - lse_ref[...]), 0.0)
        dp = jnp.einsum("hqd,hkd->hqk", do, v_ref[...], preferred_element_type=jnp.float32)
        ds = (p * (dp - dl_ref[...])).astype(jnp.bfloat16)
        dv_sc[...] += jnp.einsum("hqk,hqd->hkd", p.astype(jnp.bfloat16), do, preferred_element_type=jnp.float32)
        dk_sc[...] += jnp.einsum("hqk,hqd->hkd", ds, q, preferred_element_type=jnp.float32)

    @pl.when(i == pl.num_programs(1) - 1)
    def _():
        dk_ref[...] = dk_sc[...] * 0.125
        dv_ref[...] = dv_sc[...]


def _clamp(start, step, last):
    return jnp.minimum(start + step, jnp.maximum(last, 0))


def flash_forward(q, k, v, q_ids, k_ids, lo, hi, block_q, block_k, steps):
    heads, nq, hd = q.shape
    nk = k.shape[1]
    qs = q_ids.reshape(nq, 1)
    ks = k_ids.reshape(1, nk)

    def kv_map(i, j, lo_ref, hi_ref):
        return (0, _clamp(lo_ref[i], j, hi_ref[i]), 0)

    def ks_map(i, j, lo_ref, hi_ref):
        return (0, _clamp(lo_ref[i], j, hi_ref[i]))

    grid_spec = pltpu.PrefetchScalarGridSpec(
        num_scalar_prefetch=2,
        grid=(nq // block_q, steps),
        in_specs=[
            pl.BlockSpec((heads, block_q, hd), lambda i, j, a, b: (0, i, 0)),
            pl.BlockSpec((heads, block_k, hd), kv_map),
            pl.BlockSpec((heads, block_k, hd), kv_map),
            pl.BlockSpec((block_q, 1), lambda i, j, a, b: (i, 0)),
            pl.BlockSpec((1, block_k), ks_map),
        ],
        out_specs=[
            pl.BlockSpec((heads, block_q, hd), lambda i, j, a, b: (0, i, 0)),
            pl.BlockSpec((heads, block_q, 1), lambda i, j, a, b: (0, i, 0)),
        ],
        scratch_shapes=[
            pltpu.VMEM((heads, block_q, 1), jnp.float32),
            pltpu.VMEM((heads, block_q, 1), jnp.float32),
            pltpu.VMEM((heads, block_q, hd), jnp.float32),
        ],
    )
    return pl.pallas_call(
        _fwd_kernel,
        grid_spec=grid_spec,
        out_shape=[
            jax.ShapeDtypeStruct((heads, nq, hd), jnp.float32),
            jax.ShapeDtypeStruct((heads, nq, 1), jnp.float32),
        ],
        compiler_params=pltpu.CompilerParams(
            dimension_semantics=("arbitrary", "arbitrary"), vmem_limit_bytes=100 * 1024 * 1024 // 2
        ),
    )(lo, hi, q, k, v, qs, ks)


def flash_dq(q, k, v, q_ids, k_ids, lse, delta, do, lo, hi, block_q, block_k, steps):
    heads, nq, hd = q.shape
    nk = k.shape[1]
    qs = q_ids.reshape(nq, 1)
    ks = k_ids.reshape(1, nk)

    def kv_map(i, j, lo_ref, hi_ref):
        return (0, _clamp(lo_ref[i], j, hi_ref[i]), 0)

    def ks_map(i, j, lo_ref, hi_ref):
        return (0, _clamp(lo_ref[i], j, hi_ref[i]))

    row = lambda i, j, a, b: (0, i, 0)
    grid_spec = pltpu.PrefetchScalarGridSpec(
        num_scalar_prefetch=2,
        grid=(nq // block_q, steps),
        in_specs=[
            pl.BlockSpec((heads, block_q, hd), row),
            pl.BlockSpec((heads, block_k, hd), kv_map),
            pl.BlockSpec((heads, block_k, hd), kv_map),
            pl.BlockSpec((block_q, 1), lambda i, j, a, b: (i, 0)),
            pl.BlockSpec((1, block_k), ks_map),
            pl.BlockSpec((heads, block_q, 1), row),
            pl.BlockSpec((heads, block_q, 1), row),
            pl.BlockSpec((heads, block_q, hd), row),
        ],
        out_specs=pl.BlockSpec((heads, block_q, hd), row),
        scratch_shapes=[pltpu.VMEM((heads, block_q, hd), jnp.float32)],
    )
    return pl.pallas_call(
        _dq_kernel,
        grid_spec=grid_spec,
        out_shape=jax.ShapeDtypeStruct((heads, nq, hd), jnp.float32),
        compiler_params=pltpu.CompilerParams(
            dimension_semantics=("arbitrary", "arbitrary"), vmem_limit_bytes=100 * 1024 * 1024 // 2
        ),
    )(lo, hi, q, k, v, qs, ks, lse, delta, do)


def flash_dkv(q, k, v, q_ids, k_ids, lse, delta, do, qlo, qhi, block_q, block_k, steps):
    heads, nq, hd = q.shape
    nk = k.shape[1]
    qs = q_ids.reshape(nq, 1)
    ks = k_ids.reshape(1, nk)

    def q_map(j, i, lo_ref, hi_ref):
        return (0, _clamp(lo_ref[j], i, hi_ref[j]), 0)

    def qs_map(j, i, lo_ref, hi_ref):
        return (_clamp(lo_ref[j], i, hi_ref[j]), 0)

    col = lambda j, i, a, b: (0, j, 0)
    grid_spec = pltpu.PrefetchScalarGridSpec(
        num_scalar_prefetch=2,
        grid=(nk // block_k, steps),
        in_specs=[
            pl.BlockSpec((heads, block_q, hd), q_map),
            pl.BlockSpec((heads, block_k, hd), col),
            pl.BlockSpec((heads, block_k, hd), col),
            pl.BlockSpec((block_q, 1), qs_map),
            pl.BlockSpec((1, block_k), lambda j, i, a, b: (0, j)),
            pl.BlockSpec((heads, block_q, 1), q_map),
            pl.BlockSpec((heads, block_q, 1), q_map),
            pl.BlockSpec((heads, block_q, hd), q_map),
        ],
        out_specs=[pl.BlockSpec((heads, block_k, hd), col), pl.BlockSpec((heads, block_k, hd), col)],
        scratch_shapes=[pltpu.VMEM((heads, block_k, hd), jnp.float32), pltpu.VMEM((heads, block_k, hd), jnp.float32)],
    )
    return pl.pallas_call(
        _dkv_kernel,
        grid_spec=grid_spec,
        out_shape=[
            jax.ShapeDtypeStruct((heads, nk, hd), jnp.float32),
            jax.ShapeDtypeStruct((heads, nk, hd), jnp.float32),
        ],
        compiler_params=pltpu.CompilerParams(
            dimension_semantics=("arbitrary", "arbitrary"), vmem_limit_bytes=100 * 1024 * 1024 // 2
        ),
    )(qlo, qhi, q, k, v, qs, ks, lse, delta, do)


def block_ranges(q_ids, k_ids, q_start, q_end, block_q, block_k):
    nq = q_ids.shape[0]
    nk = k_ids.shape[0]
    nqb, nkb = nq // block_q, nk // block_k
    first = q_start.reshape(nqb, block_q)[:, 0]
    last = q_end.reshape(nqb, block_q)[:, block_q - 1]
    lo = jnp.clip(first // block_k, 0, nkb - 1).astype(jnp.int32)
    hi = jnp.clip((last - 1) // block_k, 0, nkb - 1).astype(jnp.int32)
    kb = jnp.arange(nkb, dtype=jnp.int32)
    qb = jnp.arange(nqb, dtype=jnp.int32)
    cover = (lo[:, None] <= kb[None, :]) & (kb[None, :] <= hi[:, None])
    qlo = jnp.min(jnp.where(cover, qb[:, None], nqb), axis=0).astype(jnp.int32)
    qhi = jnp.max(jnp.where(cover, qb[:, None], -1), axis=0).astype(jnp.int32)
    return lo, hi, qlo, qhi


def norm_forward(values, gain, shift):
    center = jnp.mean(values, axis=-1, keepdims=True)
    offsets = values - center
    spread = jnp.mean(offsets * offsets, axis=-1, keepdims=True)
    inverse = lax.rsqrt(spread + 1e-06)
    normed = offsets * inverse
    return (normed * gain + shift, normed, inverse)


def norm_backward(grad_y, normed, inverse, gain):
    grad_normed = grad_y * gain
    mean_one = jnp.mean(grad_normed, axis=-1, keepdims=True)
    mean_two = jnp.mean(grad_normed * normed, axis=-1, keepdims=True)
    return inverse * (grad_normed - mean_one - normed * mean_two)


def activate(values):
    return jax.nn.gelu(values, approximate=False)


def contract_last(left, right):
    return lax.dot_general(left, right, (((1,), (1,)), ((), ())), preferred_element_type=jnp.float32)


def contract_first(left, right):
    return lax.dot_general(left, right, (((0,), (0,)), ((), ())), preferred_element_type=jnp.float32)


def column_sum(values):
    return jnp.sum(values.astype(jnp.float32), axis=0)


def group_segments(lengths, dealing, group_index, group_rows, per_group):
    picked = lax.dynamic_slice_in_dim(dealing, group_index * per_group, per_group)
    match = picked[:, None] == jnp.arange(lengths.shape[0], dtype=jnp.int32)[None, :]
    chosen = jnp.sum(jnp.where(match, lengths[None, :], 0), axis=1)
    ends = jnp.cumsum(chosen)
    starts = ends - chosen
    places = jnp.arange(group_rows, dtype=jnp.int32)
    segment_ids = jnp.sum((places[:, None] >= ends[None, :]).astype(jnp.int32), axis=1)
    return (segment_ids, starts, ends)


def _block_layout(w, rows_over_dp, dp, tens):
    if rows_over_dp:
        r, c = w.shape[0] // dp, w.shape[1] // tens
        return w.reshape(dp, r, tens, c).transpose(0, 2, 1, 3).reshape(dp * tens, r * c)
    r, c = w.shape[0] // tens, w.shape[1] // dp
    return w.reshape(tens, r, dp, c).transpose(2, 0, 1, 3).reshape(dp * tens, r * c)


def gather_weights(shards_and_kinds):
    dp = lax.axis_size("dp")
    tens = lax.axis_size("tensor")
    flat = jnp.concatenate([w.reshape(-1) for w, _ in shards_and_kinds])
    full = lax.all_gather(flat, ("dp", "tensor"), axis=0, tiled=False)
    out, at = [], 0
    for w, rows_over_dp in shards_and_kinds:
        r, c = w.shape
        part = full[:, at:at + r * c].reshape(dp, tens, r, c)
        at += r * c
        if rows_over_dp:
            out.append(part.transpose(0, 2, 1, 3).reshape(dp * r, tens * c))
        else:
            out.append(part.transpose(1, 2, 0, 3).reshape(tens * r, dp * c))
    return out


def pack_grads(grads_and_kinds, extra=()):
    dp = lax.axis_size("dp")
    tens = lax.axis_size("tensor")
    parts = dp * tens
    blocks = [_block_layout(g.astype(jnp.bfloat16), k, dp, tens) for g, k in grads_and_kinds]
    blocks += [v.astype(jnp.bfloat16).reshape(parts, -1) for v in extra]
    joined = jnp.concatenate(blocks, axis=1)
    width = joined.shape[1]
    padded = -(-width // 1024) * 1024
    return jnp.pad(joined, ((0, 0), (0, padded - width))).reshape(parts, padded // 128, 128)


def unpack_grads(joined, grads_and_kinds, extra=()):
    dp = lax.axis_size("dp")
    tens = lax.axis_size("tensor")
    parts = dp * tens
    summed = lax.psum_scatter(joined, ("dp", "tensor"), scatter_dimension=0, tiled=True)
    summed = summed.reshape(-1).astype(jnp.float32)
    out, at = [], 0
    for g, k in grads_and_kinds:
        if k:
            r, c = g.shape[0] // dp, g.shape[1] // tens
        else:
            r, c = g.shape[0] // tens, g.shape[1] // dp
        out.append(summed[at:at + r * c].reshape(r, c))
        at += r * c
    for v in extra:
        n = v.shape[0] // parts
        out.append(summed[at:at + n])
        at += n
    return out


def scatter_vectors(vectors):
    parts = lax.axis_size("dp") * lax.axis_size("tensor")
    joined = jnp.concatenate([v.reshape(parts, -1) for v in vectors], axis=1)
    width = joined.shape[1]
    padded = -(-width // 1024) * 1024
    joined = jnp.pad(joined, ((0, 0), (0, padded - width))).reshape(parts, padded // 128, 128)
    summed = lax.psum_scatter(joined, ("dp", "tensor"), scatter_dimension=0, tiled=True)
    summed = summed.reshape(padded)[:width]
    out, at = [], 0
    for v in vectors:
        n = v.shape[0] // parts
        out.append(summed[at:at + n])
        at += n
    return out


def halo_plan(rows):
    hops = -(-LONGEST // rows)
    takes = [rows] * (hops - 1) + [LONGEST - rows * (hops - 1)]
    return takes


def shift_rows(values, distance, count):
    if distance >= count:
        return jnp.zeros_like(values)
    if distance > 0:
        pairs = [(s, s + distance) for s in range(count - distance)]
    else:
        pairs = [(s - distance, s) for s in range(count + distance)]
    return lax.ppermute(values, "tensor", pairs)


def build_window(own, takes, count):
    rows = own.shape[0]
    left = [shift_rows(own[rows - take:], d + 1, count) for d, take in enumerate(takes)]
    right = [shift_rows(own[:take], -(d + 1), count) for d, take in enumerate(takes)]
    return jnp.concatenate(left[::-1] + [own] + right, axis=0)


def return_window(values, takes, count):
    rows = values.shape[0] - 2 * LONGEST
    total = values[LONGEST:LONGEST + rows]
    at = LONGEST
    for d, take in enumerate(takes):
        piece = values[at - take:at].astype(jnp.bfloat16)
        at -= take
        back = shift_rows(piece, -(d + 1), count).astype(jnp.float32)
        total = total + jnp.pad(back, ((rows - take, 0), (0, 0)))
    at = LONGEST + rows
    for d, take in enumerate(takes):
        piece = values[at:at + take].astype(jnp.bfloat16)
        at += take
        back = shift_rows(piece, d + 1, count).astype(jnp.float32)
        total = total + jnp.pad(back, ((0, rows - take), (0, 0)))
    return total


def to_heads(values):
    rows, width = values.shape
    return values.reshape(rows, width // HEAD_DIM, HEAD_DIM).transpose(1, 0, 2)


def from_heads(values):
    heads, rows, hd = values.shape
    return values.transpose(1, 0, 2).reshape(rows, heads * hd)


def shards(tokens, lengths, dealing, w_query, w_key, w_value, w_out, w_inner, w_outer, b_query, b_value, b_out, b_inner, b_outer, gain_attn, shift_attn, gain_ffn, shift_ffn, grad_out):
    count = lax.axis_size("tensor")
    tens_index = lax.axis_index("tensor")
    group_index = lax.axis_index("dp")
    rows = tokens.shape[0]
    group_rows = rows * count
    per_group = lengths.shape[0] // lax.axis_size("dp")
    takes = halo_plan(rows)
    window = rows + 2 * LONGEST
    seg, starts, ends = group_segments(lengths, dealing, group_index, group_rows, per_group)
    base = rows * tens_index - LONGEST
    places = base + jnp.arange(window, dtype=jnp.int32)
    valid = (places >= 0) & (places < group_rows)
    k_ids = jnp.where(valid, jnp.sum((places[:, None] >= ends[None, :]).astype(jnp.int32), axis=1), -1).astype(jnp.int32)
    q_ids = lax.dynamic_slice_in_dim(seg, rows * tens_index, rows)
    q_start = jnp.take(starts, q_ids) - base
    q_end = jnp.take(ends, q_ids) - base
    lo, hi, qlo, qhi = block_ranges(q_ids, k_ids, q_start, q_end, BLOCK, BLOCK)
    nkb = window // BLOCK
    kv_steps = min(nkb, (BLOCK + 2 * (LONGEST - 1)) // BLOCK + 2)
    q_steps = rows // BLOCK

    wq, wk, wv = gather_weights([(w_query, True), (w_key, True), (w_value, True)])
    wo, wi, wf = gather_weights([(w_out, False), (w_inner, True), (w_outer, False)])
    gain_one = gain_attn.astype(jnp.float32)
    gain_two = gain_ffn.astype(jnp.float32)

    x_own = tokens
    x_win = build_window(tokens, takes, count)
    query = (jnp.dot(x_own, wq, preferred_element_type=jnp.float32) + b_query.astype(jnp.float32)).astype(jnp.bfloat16)
    key_w = jnp.dot(x_win, wk, preferred_element_type=jnp.float32).astype(jnp.bfloat16)
    value_w = (jnp.dot(x_win, wv, preferred_element_type=jnp.float32) + b_value.astype(jnp.float32)).astype(jnp.bfloat16)
    q_h, k_h, v_h = to_heads(query), to_heads(key_w), to_heads(value_w)
    ctx_h, lse = flash_forward(q_h, k_h, v_h, q_ids, k_ids, lo, hi, BLOCK, BLOCK, kv_steps)
    context = from_heads(ctx_h).astype(jnp.bfloat16)
    attn = jnp.dot(context, wo, preferred_element_type=jnp.float32) + b_out.astype(jnp.float32)
    hidden, norm_one, inverse_one = norm_forward(tokens.astype(jnp.float32) + attn, gain_one, shift_attn.astype(jnp.float32))
    hidden_low = hidden.astype(jnp.bfloat16)
    pre_act = jnp.dot(hidden_low, wi, preferred_element_type=jnp.float32) + b_inner.astype(jnp.float32)
    act = activate(pre_act).astype(jnp.bfloat16)
    ffn = jnp.dot(act, wf, preferred_element_type=jnp.float32) + b_outer.astype(jnp.float32)
    output, norm_two, inverse_two = norm_forward(hidden + ffn, gain_two, shift_ffn.astype(jnp.float32))

    grad_y = grad_out.astype(jnp.float32)
    grad_resid_two = norm_backward(grad_y, norm_two, inverse_two, gain_two)
    grad_ffn = grad_resid_two.astype(jnp.bfloat16)
    grad_outer_w = contract_first(act, grad_ffn)
    grad_act = contract_last(grad_ffn, wf)
    unused, gelu_pull = jax.vjp(activate, pre_act)
    grad_pre = gelu_pull(grad_act)[0].astype(jnp.bfloat16)
    grad_inner_w = contract_first(hidden_low, grad_pre)
    grad_hidden = grad_resid_two + contract_last(grad_pre, wi)
    grad_resid_one = norm_backward(grad_hidden, norm_one, inverse_one, gain_one)
    grad_attn = grad_resid_one.astype(jnp.bfloat16)
    grad_out_w = contract_first(context, grad_attn)
    grad_context = contract_last(grad_attn, wo).astype(jnp.bfloat16)
    late = [
        column_sum(grad_attn),
        column_sum(grad_pre),
        column_sum(grad_ffn),
        jnp.sum(grad_hidden * norm_one, axis=0),
        jnp.sum(grad_hidden, axis=0),
        jnp.sum(grad_y * norm_two, axis=0),
        jnp.sum(grad_y, axis=0),
    ]
    early_kinds = [(grad_out_w, False), (grad_inner_w, True), (grad_outer_w, False)]
    early = pack_grads(early_kinds, late)
    grad_context, early = lax.optimization_barrier((grad_context, early))
    early_sums = unpack_grads(early, early_kinds, late)
    do_h = to_heads(grad_context)
    delta = jnp.sum(do_h.astype(jnp.float32) * ctx_h, axis=-1, keepdims=True)
    dq_h = flash_dq(q_h, k_h, v_h, q_ids, k_ids, lse, delta, do_h, lo, hi, BLOCK, BLOCK, kv_steps)
    dk_h, dv_h = flash_dkv(q_h, k_h, v_h, q_ids, k_ids, lse, delta, do_h, qlo, qhi, BLOCK, BLOCK, q_steps)
    early_sums, dq_h, dk_h, dv_h = lax.optimization_barrier((early_sums, dq_h, dk_h, dv_h))
    g_out, g_inner, g_outer = early_sums[:3]
    late = early_sums[3:]
    grad_query = from_heads(dq_h).astype(jnp.bfloat16)
    grad_key = from_heads(dk_h).astype(jnp.bfloat16)
    grad_value = from_heads(dv_h).astype(jnp.bfloat16)
    grad_query_w = contract_first(x_own, grad_query)
    grad_key_w = contract_first(x_win, grad_key)
    grad_value_w = contract_first(x_win, grad_value)
    grad_win = contract_last(grad_key, wk) + contract_last(grad_value, wv)
    grad_tokens = grad_resid_one + contract_last(grad_query, wq) + return_window(grad_win, takes, count)

    late_kinds = [(grad_query_w, True), (grad_key_w, True), (grad_value_w, True)]
    extra = (column_sum(grad_query), column_sum(grad_value))
    g_query, g_key, g_value, g_bq, g_bv = unpack_grads(pack_grads(late_kinds, extra), late_kinds, extra)
    summed = (g_query, g_key, g_value, g_out, g_inner, g_outer)
    small = [g_bq, g_bv] + late
    return (output.astype(jnp.bfloat16), grad_tokens) + summed + tuple(small)


def solution(mesh):
    rows = P(("dp", "tensor"), None)
    vec = P(("dp", "tensor"))
    return jax.shard_map(
        shards,
        mesh=mesh,
        in_specs=(rows, P(), P(), P("dp", "tensor"), P("dp", "tensor"), P("dp", "tensor"), P("tensor", "dp"), P("dp", "tensor"), P("tensor", "dp"), P(), P(), P(), P(), P(), P(), P(), P(), P(), rows),
        out_specs=(rows, rows, P("dp", "tensor"), P("dp", "tensor"), P("dp", "tensor"), P("tensor", "dp"), P("dp", "tensor"), P("tensor", "dp")) + (vec,) * 9,
        check_vma=False,
    )
```

```python
import math

import jax
import jax.numpy as jnp
from jax import lax
from jax.experimental import pallas as pl
from jax.experimental.pallas import tpu as pltpu
from jax.sharding import PartitionSpec as P

HEAD_DIM = 64
LONGEST = 1024
BLOCK = 256

NEG = -1e30


def _fwd_kernel(lo_ref, hi_ref, q_ref, k_ref, v_ref, qs_ref, ks_ref, o_ref, lse_ref, m_sc, l_sc, acc_sc):
    i = pl.program_id(0)
    j = pl.program_id(1)
    kv = lo_ref[i] + j

    @pl.when(j == 0)
    def _():
        m_sc[...] = jnp.full_like(m_sc, NEG)
        l_sc[...] = jnp.zeros_like(l_sc)
        acc_sc[...] = jnp.zeros_like(acc_sc)

    @pl.when(kv <= hi_ref[i])
    def _():
        s = jnp.einsum("hqd,hkd->hqk", q_ref[...], k_ref[...], preferred_element_type=jnp.float32) * 0.125
        mask = (qs_ref[...] == ks_ref[...])[None]
        s = jnp.where(mask, s, NEG)
        m_old = m_sc[...]
        m_new = jnp.maximum(m_old, jnp.max(s, axis=-1, keepdims=True))
        alpha = jnp.exp(m_old - m_new)
        p = jnp.where(mask, jnp.exp(s - m_new), 0.0)
        l_sc[...] = alpha * l_sc[...] + jnp.sum(p, axis=-1, keepdims=True)
        acc_sc[...] = alpha * acc_sc[...] + jnp.einsum(
            "hqk,hkd->hqd", p.astype(jnp.bfloat16), v_ref[...], preferred_element_type=jnp.float32
        )
        m_sc[...] = m_new

    @pl.when(j == pl.num_programs(1) - 1)
    def _():
        o_ref[...] = acc_sc[...] / l_sc[...]
        lse_ref[...] = m_sc[...] + jnp.log(l_sc[...])


def _dq_kernel(lo_ref, hi_ref, q_ref, k_ref, v_ref, qs_ref, ks_ref, lse_ref, dl_ref, do_ref, dq_ref, acc_sc):
    i = pl.program_id(0)
    j = pl.program_id(1)
    kv = lo_ref[i] + j

    @pl.when(j == 0)
    def _():
        acc_sc[...] = jnp.zeros_like(acc_sc)

    @pl.when(kv <= hi_ref[i])
    def _():
        k = k_ref[...]
        s = jnp.einsum("hqd,hkd->hqk", q_ref[...], k, preferred_element_type=jnp.float32) * 0.125
        mask = (qs_ref[...] == ks_ref[...])[None]
        p = jnp.where(mask, jnp.exp(s - lse_ref[...]), 0.0)
        dp = jnp.einsum("hqd,hkd->hqk", do_ref[...], v_ref[...], preferred_element_type=jnp.float32)
        ds = (p * (dp - dl_ref[...])).astype(jnp.bfloat16)
        acc_sc[...] += jnp.einsum("hqk,hkd->hqd", ds, k, preferred_element_type=jnp.float32)

    @pl.when(j == pl.num_programs(1) - 1)
    def _():
        dq_ref[...] = acc_sc[...] * 0.125


def _dkv_kernel(lo_ref, hi_ref, q_ref, k_ref, v_ref, qs_ref, ks_ref, lse_ref, dl_ref, do_ref, dk_ref, dv_ref, dk_sc, dv_sc):
    j = pl.program_id(0)
    i = pl.program_id(1)
    qb = lo_ref[j] + i

    @pl.when(i == 0)
    def _():
        dk_sc[...] = jnp.zeros_like(dk_sc)
        dv_sc[...] = jnp.zeros_like(dv_sc)

    @pl.when(qb <= hi_ref[j])
    def _():
        q = q_ref[...]
        do = do_ref[...]
        s = jnp.einsum("hqd,hkd->hqk", q, k_ref[...], preferred_element_type=jnp.float32) * 0.125
        mask = (qs_ref[...] == ks_ref[...])[None]
        p = jnp.where(mask, jnp.exp(s - lse_ref[...]), 0.0)
        dp = jnp.einsum("hqd,hkd->hqk", do, v_ref[...], preferred_element_type=jnp.float32)
        ds = (p * (dp - dl_ref[...])).astype(jnp.bfloat16)
        dv_sc[...] += jnp.einsum("hqk,hqd->hkd", p.astype(jnp.bfloat16), do, preferred_element_type=jnp.float32)
        dk_sc[...] += jnp.einsum("hqk,hqd->hkd", ds, q, preferred_element_type=jnp.float32)

    @pl.when(i == pl.num_programs(1) - 1)
    def _():
        dk_ref[...] = dk_sc[...] * 0.125
        dv_ref[...] = dv_sc[...]


def _clamp(start, step, last):
    return jnp.minimum(start + step, jnp.maximum(last, 0))


def flash_forward(q, k, v, q_ids, k_ids, lo, hi, block_q, block_k, steps):
    heads, nq, hd = q.shape
    nk = k.shape[1]
    qs = q_ids.reshape(nq, 1)
    ks = k_ids.reshape(1, nk)

    def kv_map(i, j, lo_ref, hi_ref):
        return (0, _clamp(lo_ref[i], j, hi_ref[i]), 0)

    def ks_map(i, j, lo_ref, hi_ref):
        return (0, _clamp(lo_ref[i], j, hi_ref[i]))

    grid_spec = pltpu.PrefetchScalarGridSpec(
        num_scalar_prefetch=2,
        grid=(nq // block_q, steps),
        in_specs=[
            pl.BlockSpec((heads, block_q, hd), lambda i, j, a, b: (0, i, 0)),
            pl.BlockSpec((heads, block_k, hd), kv_map),
            pl.BlockSpec((heads, block_k, hd), kv_map),
            pl.BlockSpec((block_q, 1), lambda i, j, a, b: (i, 0)),
            pl.BlockSpec((1, block_k), ks_map),
        ],
        out_specs=[
            pl.BlockSpec((heads, block_q, hd), lambda i, j, a, b: (0, i, 0)),
            pl.BlockSpec((heads, block_q, 1), lambda i, j, a, b: (0, i, 0)),
        ],
        scratch_shapes=[
            pltpu.VMEM((heads, block_q, 1), jnp.float32),
            pltpu.VMEM((heads, block_q, 1), jnp.float32),
            pltpu.VMEM((heads, block_q, hd), jnp.float32),
        ],
    )
    return pl.pallas_call(
        _fwd_kernel,
        grid_spec=grid_spec,
        out_shape=[
            jax.ShapeDtypeStruct((heads, nq, hd), jnp.float32),
            jax.ShapeDtypeStruct((heads, nq, 1), jnp.float32),
        ],
        compiler_params=pltpu.CompilerParams(
            dimension_semantics=("arbitrary", "arbitrary"), vmem_limit_bytes=100 * 1024 * 1024 // 2
        ),
    )(lo, hi, q, k, v, qs, ks)


def flash_dq(q, k, v, q_ids, k_ids, lse, delta, do, lo, hi, block_q, block_k, steps):
    heads, nq, hd = q.shape
    nk = k.shape[1]
    qs = q_ids.reshape(nq, 1)
    ks = k_ids.reshape(1, nk)

    def kv_map(i, j, lo_ref, hi_ref):
        return (0, _clamp(lo_ref[i], j, hi_ref[i]), 0)

    def ks_map(i, j, lo_ref, hi_ref):
        return (0, _clamp(lo_ref[i], j, hi_ref[i]))

    row = lambda i, j, a, b: (0, i, 0)
    grid_spec = pltpu.PrefetchScalarGridSpec(
        num_scalar_prefetch=2,
        grid=(nq // block_q, steps),
        in_specs=[
            pl.BlockSpec((heads, block_q, hd), row),
            pl.BlockSpec((heads, block_k, hd), kv_map),
            pl.BlockSpec((heads, block_k, hd), kv_map),
            pl.BlockSpec((block_q, 1), lambda i, j, a, b: (i, 0)),
            pl.BlockSpec((1, block_k), ks_map),
            pl.BlockSpec((heads, block_q, 1), row),
            pl.BlockSpec((heads, block_q, 1), row),
            pl.BlockSpec((heads, block_q, hd), row),
        ],
        out_specs=pl.BlockSpec((heads, block_q, hd), row),
        scratch_shapes=[pltpu.VMEM((heads, block_q, hd), jnp.float32)],
    )
    return pl.pallas_call(
        _dq_kernel,
        grid_spec=grid_spec,
        out_shape=jax.ShapeDtypeStruct((heads, nq, hd), jnp.float32),
        compiler_params=pltpu.CompilerParams(
            dimension_semantics=("arbitrary", "arbitrary"), vmem_limit_bytes=100 * 1024 * 1024 // 2
        ),
    )(lo, hi, q, k, v, qs, ks, lse, delta, do)


def flash_dkv(q, k, v, q_ids, k_ids, lse, delta, do, qlo, qhi, block_q, block_k, steps):
    heads, nq, hd = q.shape
    nk = k.shape[1]
    qs = q_ids.reshape(nq, 1)
    ks = k_ids.reshape(1, nk)

    def q_map(j, i, lo_ref, hi_ref):
        return (0, _clamp(lo_ref[j], i, hi_ref[j]), 0)

    def qs_map(j, i, lo_ref, hi_ref):
        return (_clamp(lo_ref[j], i, hi_ref[j]), 0)

    col = lambda j, i, a, b: (0, j, 0)
    grid_spec = pltpu.PrefetchScalarGridSpec(
        num_scalar_prefetch=2,
        grid=(nk // block_k, steps),
        in_specs=[
            pl.BlockSpec((heads, block_q, hd), q_map),
            pl.BlockSpec((heads, block_k, hd), col),
            pl.BlockSpec((heads, block_k, hd), col),
            pl.BlockSpec((block_q, 1), qs_map),
            pl.BlockSpec((1, block_k), lambda j, i, a, b: (0, j)),
            pl.BlockSpec((heads, block_q, 1), q_map),
            pl.BlockSpec((heads, block_q, 1), q_map),
            pl.BlockSpec((heads, block_q, hd), q_map),
        ],
        out_specs=[pl.BlockSpec((heads, block_k, hd), col), pl.BlockSpec((heads, block_k, hd), col)],
        scratch_shapes=[pltpu.VMEM((heads, block_k, hd), jnp.float32), pltpu.VMEM((heads, block_k, hd), jnp.float32)],
    )
    return pl.pallas_call(
        _dkv_kernel,
        grid_spec=grid_spec,
        out_shape=[
            jax.ShapeDtypeStruct((heads, nk, hd), jnp.float32),
            jax.ShapeDtypeStruct((heads, nk, hd), jnp.float32),
        ],
        compiler_params=pltpu.CompilerParams(
            dimension_semantics=("arbitrary", "arbitrary"), vmem_limit_bytes=100 * 1024 * 1024 // 2
        ),
    )(qlo, qhi, q, k, v, qs, ks, lse, delta, do)


def block_ranges(q_ids, k_ids, q_start, q_end, block_q, block_k):
    nq = q_ids.shape[0]
    nk = k_ids.shape[0]
    nqb, nkb = nq // block_q, nk // block_k
    first = q_start.reshape(nqb, block_q)[:, 0]
    last = q_end.reshape(nqb, block_q)[:, block_q - 1]
    lo = jnp.clip(first // block_k, 0, nkb - 1).astype(jnp.int32)
    hi = jnp.clip((last - 1) // block_k, 0, nkb - 1).astype(jnp.int32)
    kb = jnp.arange(nkb, dtype=jnp.int32)
    qb = jnp.arange(nqb, dtype=jnp.int32)
    cover = (lo[:, None] <= kb[None, :]) & (kb[None, :] <= hi[:, None])
    qlo = jnp.min(jnp.where(cover, qb[:, None], nqb), axis=0).astype(jnp.int32)
    qhi = jnp.max(jnp.where(cover, qb[:, None], -1), axis=0).astype(jnp.int32)
    return lo, hi, qlo, qhi


def norm_forward(values, gain, shift):
    center = jnp.mean(values, axis=-1, keepdims=True)
    offsets = values - center
    spread = jnp.mean(offsets * offsets, axis=-1, keepdims=True)
    inverse = lax.rsqrt(spread + 1e-06)
    normed = offsets * inverse
    return (normed * gain + shift, normed, inverse)


def norm_backward(grad_y, normed, inverse, gain):
    grad_normed = grad_y * gain
    mean_one = jnp.mean(grad_normed, axis=-1, keepdims=True)
    mean_two = jnp.mean(grad_normed * normed, axis=-1, keepdims=True)
    return inverse * (grad_normed - mean_one - normed * mean_two)


def activate(values):
    return jax.nn.gelu(values, approximate=False)


def contract_last(left, right):
    return lax.dot_general(left, right, (((1,), (1,)), ((), ())), preferred_element_type=jnp.float32)


def contract_first(left, right):
    return lax.dot_general(left, right, (((0,), (0,)), ((), ())), preferred_element_type=jnp.float32)


def column_sum(values):
    return jnp.sum(values.astype(jnp.float32), axis=0)


def group_segments(lengths, dealing, group_index, group_rows, per_group):
    picked = lax.dynamic_slice_in_dim(dealing, group_index * per_group, per_group)
    match = picked[:, None] == jnp.arange(lengths.shape[0], dtype=jnp.int32)[None, :]
    chosen = jnp.sum(jnp.where(match, lengths[None, :], 0), axis=1)
    ends = jnp.cumsum(chosen)
    starts = ends - chosen
    places = jnp.arange(group_rows, dtype=jnp.int32)
    segment_ids = jnp.sum((places[:, None] >= ends[None, :]).astype(jnp.int32), axis=1)
    return (segment_ids, starts, ends)


def cyclic_pieces(piece):
    count = lax.axis_size("tensor")
    me = lax.axis_index("tensor")
    got = [piece]
    for k in range(1, count):
        got.append(lax.ppermute(piece, "tensor", [(s, (s + k) % count) for s in range(count)]))
    order = (me - jnp.arange(count, dtype=jnp.int32)) % count
    return jnp.take(jnp.stack(got), order, axis=0)


def gather_weights(blocks):
    count = lax.axis_size("tensor")
    widths = [b.shape[1] for b in blocks]
    piece = jnp.concatenate(blocks, axis=1)
    parts = cyclic_pieces(piece)
    cols, at = [], 0
    for w in widths:
        cols.extend(parts[t, :, at:at + w] for t in range(count))
        at += w
    strip = jnp.concatenate(cols, axis=1)
    full = lax.all_gather(strip, "dp", axis=0, tiled=True)
    out, at = [], 0
    for w in widths:
        out.append(full[:, at:at + w * count])
        at += w * count
    return out


def vector_rows(v, rows):
    dp = lax.axis_size("dp")
    slab = rows // dp
    spread = v.reshape(dp, 1, -1)
    return jnp.pad(spread, ((0, 0), (0, slab - 1), (0, 0))).reshape(rows, -1)


def pack_grads(grads, vectors):
    count = lax.axis_size("tensor")
    me = lax.axis_index("tensor")
    rows = grads[0].shape[0]
    mats = [g.astype(jnp.bfloat16) for g in grads] + [vector_rows(v.astype(jnp.bfloat16), rows) for v in vectors]
    widths = [m.shape[1] // count for m in mats]
    cat = jnp.concatenate(mats, axis=1)
    return widths, cat


def reduce_dp(cat):
    return lax.psum_scatter(cat, "dp", scatter_dimension=0, tiled=True)


def reduce_tensor(strip, widths, n_grads):
    count = lax.axis_size("tensor")
    me = lax.axis_index("tensor")
    strip = strip.astype(jnp.float32)
    per_t = []
    for t in range(count):
        at, cols = 0, []
        for w in widths:
            cols.append(strip[:, at + t * w:at + (t + 1) * w])
            at += w * count
        per_t.append(jnp.concatenate(cols, axis=1))
    stacked = jnp.stack(per_t)
    total = jnp.take(stacked, me, axis=0)
    for k in range(1, count):
        send = jnp.take(stacked, (me + k) % count, axis=0)
        total = total + lax.ppermute(send, "tensor", [(s, (s + k) % count) for s in range(count)])
    out, at = [], 0
    for i, w in enumerate(widths):
        block = total[:, at:at + w]
        at += w
        out.append(block if i < n_grads else block[0])
    return out


def halo_plan(rows):
    hops = -(-LONGEST // rows)
    takes = [rows] * (hops - 1) + [LONGEST - rows * (hops - 1)]
    return takes


def shift_rows(values, distance, count):
    if distance >= count:
        return jnp.zeros_like(values)
    if distance > 0:
        pairs = [(s, s + distance) for s in range(count - distance)]
    else:
        pairs = [(s - distance, s) for s in range(count + distance)]
    return lax.ppermute(values, "tensor", pairs)


def build_window(own, takes, count):
    rows = own.shape[0]
    left = [shift_rows(own[rows - take:], d + 1, count) for d, take in enumerate(takes)]
    right = [shift_rows(own[:take], -(d + 1), count) for d, take in enumerate(takes)]
    return jnp.concatenate(left[::-1] + [own] + right, axis=0)


def return_window(values, takes, count):
    rows = values.shape[0] - 2 * LONGEST
    total = values[LONGEST:LONGEST + rows]
    at = LONGEST
    for d, take in enumerate(takes):
        piece = values[at - take:at].astype(jnp.bfloat16)
        at -= take
        back = shift_rows(piece, -(d + 1), count).astype(jnp.float32)
        total = total + jnp.pad(back, ((rows - take, 0), (0, 0)))
    at = LONGEST + rows
    for d, take in enumerate(takes):
        piece = values[at:at + take].astype(jnp.bfloat16)
        at += take
        back = shift_rows(piece, d + 1, count).astype(jnp.float32)
        total = total + jnp.pad(back, ((0, rows - take), (0, 0)))
    return total


def to_heads(values):
    rows, width = values.shape
    return values.reshape(rows, width // HEAD_DIM, HEAD_DIM).transpose(1, 0, 2)


def from_heads(values):
    heads, rows, hd = values.shape
    return values.transpose(1, 0, 2).reshape(rows, heads * hd)


def shards(tokens, lengths, dealing, w_query, w_key, w_value, w_out, w_inner, w_outer, b_query, b_value, b_out, b_inner, b_outer, gain_attn, shift_attn, gain_ffn, shift_ffn, grad_out):
    count = lax.axis_size("tensor")
    tens_index = lax.axis_index("tensor")
    group_index = lax.axis_index("dp")
    rows = tokens.shape[0]
    group_rows = rows * count
    per_group = lengths.shape[0] // lax.axis_size("dp")
    takes = halo_plan(rows)
    window = rows + 2 * LONGEST
    seg, starts, ends = group_segments(lengths, dealing, group_index, group_rows, per_group)
    base = rows * tens_index - LONGEST
    places = base + jnp.arange(window, dtype=jnp.int32)
    valid = (places >= 0) & (places < group_rows)
    k_ids = jnp.where(valid, jnp.sum((places[:, None] >= ends[None, :]).astype(jnp.int32), axis=1), -1).astype(jnp.int32)
    q_ids = lax.dynamic_slice_in_dim(seg, rows * tens_index, rows)
    q_start = jnp.take(starts, q_ids) - base
    q_end = jnp.take(ends, q_ids) - base
    lo, hi, qlo, qhi = block_ranges(q_ids, k_ids, q_start, q_end, BLOCK, BLOCK)
    nkb = window // BLOCK
    kv_steps = min(nkb, (BLOCK + 2 * (LONGEST - 1)) // BLOCK + 2)
    q_steps = rows // BLOCK

    wq, wk, wv = gather_weights([w_query, w_key, w_value])
    wo_t, wi, wf_t = gather_weights([w_out.T, w_inner, w_outer.T])
    gain_one = gain_attn.astype(jnp.float32)
    gain_two = gain_ffn.astype(jnp.float32)

    x_own = tokens
    x_win = build_window(tokens, takes, count)
    query = (jnp.dot(x_own, wq, preferred_element_type=jnp.float32) + b_query.astype(jnp.float32)).astype(jnp.bfloat16)
    key_w = jnp.dot(x_win, wk, preferred_element_type=jnp.float32).astype(jnp.bfloat16)
    value_w = (jnp.dot(x_win, wv, preferred_element_type=jnp.float32) + b_value.astype(jnp.float32)).astype(jnp.bfloat16)
    q_h, k_h, v_h = to_heads(query), to_heads(key_w), to_heads(value_w)
    ctx_h, lse = flash_forward(q_h, k_h, v_h, q_ids, k_ids, lo, hi, BLOCK, BLOCK, kv_steps)
    context = from_heads(ctx_h).astype(jnp.bfloat16)
    attn = contract_last(context, wo_t) + b_out.astype(jnp.float32)
    hidden, norm_one, inverse_one = norm_forward(tokens.astype(jnp.float32) + attn, gain_one, shift_attn.astype(jnp.float32))
    hidden_low = hidden.astype(jnp.bfloat16)
    pre_act = jnp.dot(hidden_low, wi, preferred_element_type=jnp.float32) + b_inner.astype(jnp.float32)
    act = activate(pre_act).astype(jnp.bfloat16)
    ffn = contract_last(act, wf_t) + b_outer.astype(jnp.float32)
    output, norm_two, inverse_two = norm_forward(hidden + ffn, gain_two, shift_ffn.astype(jnp.float32))

    grad_y = grad_out.astype(jnp.float32)
    grad_resid_two = norm_backward(grad_y, norm_two, inverse_two, gain_two)
    grad_ffn = grad_resid_two.astype(jnp.bfloat16)
    grad_outer_t = contract_first(grad_ffn, act)
    grad_act = jnp.dot(grad_ffn, wf_t, preferred_element_type=jnp.float32)
    unused, gelu_pull = jax.vjp(activate, pre_act)
    grad_pre = gelu_pull(grad_act)[0].astype(jnp.bfloat16)
    grad_inner_w = contract_first(hidden_low, grad_pre)
    grad_hidden = grad_resid_two + contract_last(grad_pre, wi)
    grad_resid_one = norm_backward(grad_hidden, norm_one, inverse_one, gain_one)
    grad_attn = grad_resid_one.astype(jnp.bfloat16)
    grad_out_t = contract_first(grad_attn, context)
    grad_context = jnp.dot(grad_attn, wo_t, preferred_element_type=jnp.float32).astype(jnp.bfloat16)
    late = [
        column_sum(grad_attn),
        column_sum(grad_pre),
        column_sum(grad_ffn),
        jnp.sum(grad_hidden * norm_one, axis=0),
        jnp.sum(grad_hidden, axis=0),
        jnp.sum(grad_y * norm_two, axis=0),
        jnp.sum(grad_y, axis=0),
    ]
    early_widths, early_cat = pack_grads([grad_out_t, grad_inner_w, grad_outer_t], late)
    grad_context, early_cat = lax.optimization_barrier((grad_context, early_cat))
    early_strip = reduce_dp(early_cat)
    do_h = to_heads(grad_context)
    delta = jnp.sum(do_h.astype(jnp.float32) * ctx_h, axis=-1, keepdims=True)
    dq_h = flash_dq(q_h, k_h, v_h, q_ids, k_ids, lse, delta, do_h, lo, hi, BLOCK, BLOCK, kv_steps)
    dk_h, dv_h = flash_dkv(q_h, k_h, v_h, q_ids, k_ids, lse, delta, do_h, qlo, qhi, BLOCK, BLOCK, q_steps)
    early_strip, dq_h, dk_h, dv_h = lax.optimization_barrier((early_strip, dq_h, dk_h, dv_h))
    early_sums = reduce_tensor(early_strip, early_widths, 3)
    g_out_t, g_inner, g_outer_t = early_sums[:3]
    late = early_sums[3:]
    grad_query = from_heads(dq_h).astype(jnp.bfloat16)
    grad_key = from_heads(dk_h).astype(jnp.bfloat16)
    grad_value = from_heads(dv_h).astype(jnp.bfloat16)
    grad_query_w = contract_first(x_own, grad_query)
    grad_key_w = contract_first(x_win, grad_key)
    grad_value_w = contract_first(x_win, grad_value)
    grad_win = contract_last(grad_key, wk) + contract_last(grad_value, wv)
    grad_tokens = grad_resid_one + contract_last(grad_query, wq) + return_window(grad_win, takes, count)

    late_widths, late_cat = pack_grads(
        [grad_query_w, grad_key_w, grad_value_w], [column_sum(grad_query), column_sum(grad_value)]
    )
    g_query, g_key, g_value, g_bq, g_bv = reduce_tensor(reduce_dp(late_cat), late_widths, 3)
    summed = (g_query, g_key, g_value, g_out_t.T, g_inner, g_outer_t.T)
    small = [g_bq, g_bv] + late
    return (output.astype(jnp.bfloat16), grad_tokens) + summed + tuple(small)


def solution(mesh):
    rows = P(("dp", "tensor"), None)
    vec = P(("dp", "tensor"))
    return jax.shard_map(
        shards,
        mesh=mesh,
        in_specs=(rows, P(), P(), P("dp", "tensor"), P("dp", "tensor"), P("dp", "tensor"), P("tensor", "dp"), P("dp", "tensor"), P("tensor", "dp"), P(), P(), P(), P(), P(), P(), P(), P(), P(), rows),
        out_specs=(rows, rows, P("dp", "tensor"), P("dp", "tensor"), P("dp", "tensor"), P("tensor", "dp"), P("dp", "tensor"), P("tensor", "dp")) + (vec,) * 9,
        check_vma=False,
    )
```

```python
import math

import jax
import jax.numpy as jnp
from jax import lax
from jax.experimental import pallas as pl
from jax.experimental.pallas import tpu as pltpu
from jax.sharding import PartitionSpec as P

HEAD_DIM = 64
LONGEST = 1024
BLOCK = 256

NEG = -1e30
LANES = 128


def _lanes(rows):
    return lax.broadcasted_iota(jnp.int32, (rows, LANES), 1) < LANES // 2


def _pick(first, second, lanes):
    return jnp.where(lanes, first, second)


def _nt(a, b):
    return lax.dot_general(a, b, (((1,), (1,)), ((), ())), preferred_element_type=jnp.float32)


def _tn(a, b):
    return lax.dot_general(a, b, (((0,), (0,)), ((), ())), preferred_element_type=jnp.float32)


def _nn(a, b):
    return lax.dot_general(a, b, (((1,), (0,)), ((), ())), preferred_element_type=jnp.float32)


def _attn_fwd(lo_ref, hi_ref, q_ref, k_ref, v_ref, qs_ref, ks_ref, o_ref, lse_ref, m_sc, l_sc, acc_sc):
    i = pl.program_id(0)
    j = pl.program_id(1)
    kv = lo_ref[i] + j
    pairs = q_ref.shape[1] // LANES
    bq = q_ref.shape[0]

    @pl.when(j == 0)
    def _():
        m_sc[...] = jnp.full_like(m_sc, NEG)
        l_sc[...] = jnp.zeros_like(l_sc)
        acc_sc[...] = jnp.zeros_like(acc_sc)

    @pl.when(kv <= hi_ref[i])
    def _():
        mask = qs_ref[...] == ks_ref[...]
        lanes = _lanes(bq)

        def pair(p, carry):
            cols = pl.ds(pl.multiple_of(p * LANES, LANES), LANES)
            q2 = q_ref[:, cols]
            k2 = k_ref[:, cols]
            v2 = v_ref[:, cols]
            zero = jnp.zeros_like(q2)
            alphas, pvs = [], []
            for h in range(2):
                hq = _pick(q2, zero, lanes) if h == 0 else _pick(zero, q2, lanes)
                s = jnp.where(mask, _nt(hq, k2) * 0.125, NEG)
                m_old = m_sc[2 * p + h]
                m_new = jnp.maximum(m_old, jnp.max(s, axis=-1, keepdims=True))
                alpha = jnp.exp(m_old - m_new)
                e = jnp.where(mask, jnp.exp(s - m_new), 0.0)
                l_sc[2 * p + h] = alpha * l_sc[2 * p + h] + jnp.sum(e, axis=-1, keepdims=True)
                m_sc[2 * p + h] = m_new
                alphas.append(alpha)
                pvs.append(_nn(e.astype(jnp.bfloat16), v2))
            acc_sc[:, cols] = _pick(alphas[0], alphas[1], lanes) * acc_sc[:, cols] + _pick(pvs[0], pvs[1], lanes)
            return carry

        lax.fori_loop(0, pairs, pair, 0)

    @pl.when(j == pl.num_programs(1) - 1)
    def _():
        lanes = _lanes(bq)

        def pair(p, carry):
            cols = pl.ds(pl.multiple_of(p * LANES, LANES), LANES)
            l0, l1 = l_sc[2 * p], l_sc[2 * p + 1]
            o_ref[:, cols] = acc_sc[:, cols] / _pick(l0, l1, lanes)
            lse_ref[2 * p] = m_sc[2 * p] + jnp.log(l0)
            lse_ref[2 * p + 1] = m_sc[2 * p + 1] + jnp.log(l1)
            return carry

        lax.fori_loop(0, pairs, pair, 0)


def _attn_dq(lo_ref, hi_ref, q_ref, k_ref, v_ref, qs_ref, ks_ref, lse_ref, dl_ref, do_ref, dq_ref, acc_sc):
    i = pl.program_id(0)
    j = pl.program_id(1)
    kv = lo_ref[i] + j
    pairs = q_ref.shape[1] // LANES
    bq = q_ref.shape[0]

    @pl.when(j == 0)
    def _():
        acc_sc[...] = jnp.zeros_like(acc_sc)

    @pl.when(kv <= hi_ref[i])
    def _():
        mask = qs_ref[...] == ks_ref[...]
        lanes = _lanes(bq)

        def pair(p, carry):
            cols = pl.ds(pl.multiple_of(p * LANES, LANES), LANES)
            q2 = q_ref[:, cols]
            k2 = k_ref[:, cols]
            v2 = v_ref[:, cols]
            do2 = do_ref[:, cols]
            zero = jnp.zeros_like(q2)
            parts = []
            for h in range(2):
                sel = (lambda a: _pick(a, zero, lanes)) if h == 0 else (lambda a: _pick(zero, a, lanes))
                s = _nt(sel(q2), k2) * 0.125
                e = jnp.where(mask, jnp.exp(s - lse_ref[2 * p + h]), 0.0)
                dp = _nt(sel(do2), v2)
                ds = (e * (dp - dl_ref[2 * p + h])).astype(jnp.bfloat16)
                parts.append(_nn(ds, k2))
            acc_sc[:, cols] += _pick(parts[0], parts[1], lanes)
            return carry

        lax.fori_loop(0, pairs, pair, 0)

    @pl.when(j == pl.num_programs(1) - 1)
    def _():
        dq_ref[...] = acc_sc[...] * 0.125


def _attn_dkv(lo_ref, hi_ref, q_ref, k_ref, v_ref, qs_ref, ks_ref, lse_ref, dl_ref, do_ref, dk_ref, dv_ref, dk_sc, dv_sc):
    j = pl.program_id(0)
    i = pl.program_id(1)
    qb = lo_ref[j] + i
    pairs = q_ref.shape[1] // LANES
    bq = q_ref.shape[0]
    bk = k_ref.shape[0]

    @pl.when(i == 0)
    def _():
        dk_sc[...] = jnp.zeros_like(dk_sc)
        dv_sc[...] = jnp.zeros_like(dv_sc)

    @pl.when(qb <= hi_ref[j])
    def _():
        mask = qs_ref[...] == ks_ref[...]
        lanes_q = _lanes(bq)
        lanes_k = _lanes(bk)

        def pair(p, carry):
            cols = pl.ds(pl.multiple_of(p * LANES, LANES), LANES)
            q2 = q_ref[:, cols]
            k2 = k_ref[:, cols]
            v2 = v_ref[:, cols]
            do2 = do_ref[:, cols]
            zero = jnp.zeros_like(q2)
            dks, dvs = [], []
            for h in range(2):
                sel = (lambda a: _pick(a, zero, lanes_q)) if h == 0 else (lambda a: _pick(zero, a, lanes_q))
                s = _nt(sel(q2), k2) * 0.125
                e = jnp.where(mask, jnp.exp(s - lse_ref[2 * p + h]), 0.0)
                dp = _nt(sel(do2), v2)
                ds = (e * (dp - dl_ref[2 * p + h])).astype(jnp.bfloat16)
                dvs.append(_tn(e.astype(jnp.bfloat16), do2))
                dks.append(_tn(ds, q2))
            dv_sc[:, cols] += _pick(dvs[0], dvs[1], lanes_k)
            dk_sc[:, cols] += _pick(dks[0], dks[1], lanes_k)
            return carry

        lax.fori_loop(0, pairs, pair, 0)

    @pl.when(i == pl.num_programs(1) - 1)
    def _():
        dk_ref[...] = dk_sc[...] * 0.125
        dv_ref[...] = dv_sc[...]


def _clamp(start, step, last):
    return jnp.minimum(start + step, jnp.maximum(last, 0))


def _params():
    return pltpu.CompilerParams(dimension_semantics=("arbitrary", "arbitrary"), vmem_limit_bytes=48 * 1024 * 1024)


def flash_forward(q, k, v, q_ids, k_ids, lo, hi, block_q, block_k, steps):
    nq, width = q.shape
    nk = k.shape[0]
    heads = width // 64
    kv_map = lambda i, j, a, b: (_clamp(a[i], j, b[i]), 0)
    ks_map = lambda i, j, a, b: (0, _clamp(a[i], j, b[i]))
    row = lambda i, j, a, b: (i, 0)
    grid_spec = pltpu.PrefetchScalarGridSpec(
        num_scalar_prefetch=2,
        grid=(nq // block_q, steps),
        in_specs=[
            pl.BlockSpec((block_q, width), row),
            pl.BlockSpec((block_k, width), kv_map),
            pl.BlockSpec((block_k, width), kv_map),
            pl.BlockSpec((block_q, 1), row),
            pl.BlockSpec((1, block_k), ks_map),
        ],
        out_specs=[
            pl.BlockSpec((block_q, width), row),
            pl.BlockSpec((heads, block_q, 1), lambda i, j, a, b: (0, i, 0)),
        ],
        scratch_shapes=[
            pltpu.VMEM((heads, block_q, 1), jnp.float32),
            pltpu.VMEM((heads, block_q, 1), jnp.float32),
            pltpu.VMEM((block_q, width), jnp.float32),
        ],
    )
    return pl.pallas_call(
        _attn_fwd,
        grid_spec=grid_spec,
        out_shape=[jax.ShapeDtypeStruct((nq, width), jnp.float32), jax.ShapeDtypeStruct((heads, nq, 1), jnp.float32)],
        compiler_params=_params(),
    )(lo, hi, q, k, v, q_ids.reshape(nq, 1), k_ids.reshape(1, nk))


def flash_dq(q, k, v, q_ids, k_ids, lse, delta, do, lo, hi, block_q, block_k, steps):
    nq, width = q.shape
    nk = k.shape[0]
    heads = width // 64
    kv_map = lambda i, j, a, b: (_clamp(a[i], j, b[i]), 0)
    ks_map = lambda i, j, a, b: (0, _clamp(a[i], j, b[i]))
    row = lambda i, j, a, b: (i, 0)
    hrow = lambda i, j, a, b: (0, i, 0)
    grid_spec = pltpu.PrefetchScalarGridSpec(
        num_scalar_prefetch=2,
        grid=(nq // block_q, steps),
        in_specs=[
            pl.BlockSpec((block_q, width), row),
            pl.BlockSpec((block_k, width), kv_map),
            pl.BlockSpec((block_k, width), kv_map),
            pl.BlockSpec((block_q, 1), row),
            pl.BlockSpec((1, block_k), ks_map),
            pl.BlockSpec((heads, block_q, 1), hrow),
            pl.BlockSpec((heads, block_q, 1), hrow),
            pl.BlockSpec((block_q, width), row),
        ],
        out_specs=pl.BlockSpec((block_q, width), row),
        scratch_shapes=[pltpu.VMEM((block_q, width), jnp.float32)],
    )
    return pl.pallas_call(
        _attn_dq,
        grid_spec=grid_spec,
        out_shape=jax.ShapeDtypeStruct((nq, width), jnp.float32),
        compiler_params=_params(),
    )(lo, hi, q, k, v, q_ids.reshape(nq, 1), k_ids.reshape(1, nk), lse, delta, do)


def flash_dkv(q, k, v, q_ids, k_ids, lse, delta, do, qlo, qhi, block_q, block_k, steps):
    nq, width = q.shape
    nk = k.shape[0]
    heads = width // 64
    q_map = lambda j, i, a, b: (_clamp(a[j], i, b[j]), 0)
    h_map = lambda j, i, a, b: (0, _clamp(a[j], i, b[j]), 0)
    col = lambda j, i, a, b: (j, 0)
    grid_spec = pltpu.PrefetchScalarGridSpec(
        num_scalar_prefetch=2,
        grid=(nk // block_k, steps),
        in_specs=[
            pl.BlockSpec((block_q, width), q_map),
            pl.BlockSpec((block_k, width), col),
            pl.BlockSpec((block_k, width), col),
            pl.BlockSpec((block_q, 1), q_map),
            pl.BlockSpec((1, block_k), lambda j, i, a, b: (0, j)),
            pl.BlockSpec((heads, block_q, 1), h_map),
            pl.BlockSpec((heads, block_q, 1), h_map),
            pl.BlockSpec((block_q, width), q_map),
        ],
        out_specs=[pl.BlockSpec((block_k, width), col), pl.BlockSpec((block_k, width), col)],
        scratch_shapes=[pltpu.VMEM((block_k, width), jnp.float32), pltpu.VMEM((block_k, width), jnp.float32)],
    )
    return pl.pallas_call(
        _attn_dkv,
        grid_spec=grid_spec,
        out_shape=[jax.ShapeDtypeStruct((nk, width), jnp.float32), jax.ShapeDtypeStruct((nk, width), jnp.float32)],
        compiler_params=_params(),
    )(qlo, qhi, q, k, v, q_ids.reshape(nq, 1), k_ids.reshape(1, nk), lse, delta, do)


def block_ranges(q_ids, k_ids, q_start, q_end, block_q, block_k):
    nq = q_ids.shape[0]
    nk = k_ids.shape[0]
    nqb, nkb = nq // block_q, nk // block_k
    first = q_start.reshape(nqb, block_q)[:, 0]
    last = q_end.reshape(nqb, block_q)[:, block_q - 1]
    lo = jnp.clip(first // block_k, 0, nkb - 1).astype(jnp.int32)
    hi = jnp.clip((last - 1) // block_k, 0, nkb - 1).astype(jnp.int32)
    kb = jnp.arange(nkb, dtype=jnp.int32)
    qb = jnp.arange(nqb, dtype=jnp.int32)
    cover = (lo[:, None] <= kb[None, :]) & (kb[None, :] <= hi[:, None])
    qlo = jnp.min(jnp.where(cover, qb[:, None], nqb), axis=0).astype(jnp.int32)
    qhi = jnp.max(jnp.where(cover, qb[:, None], -1), axis=0).astype(jnp.int32)
    return lo, hi, qlo, qhi


def norm_forward(values, gain, shift):
    center = jnp.mean(values, axis=-1, keepdims=True)
    offsets = values - center
    spread = jnp.mean(offsets * offsets, axis=-1, keepdims=True)
    inverse = lax.rsqrt(spread + 1e-06)
    normed = offsets * inverse
    return (normed * gain + shift, normed, inverse)


def norm_backward(grad_y, normed, inverse, gain):
    grad_normed = grad_y * gain
    mean_one = jnp.mean(grad_normed, axis=-1, keepdims=True)
    mean_two = jnp.mean(grad_normed * normed, axis=-1, keepdims=True)
    return inverse * (grad_normed - mean_one - normed * mean_two)


def activate(values):
    return jax.nn.gelu(values, approximate=False)


def contract_last(left, right):
    return lax.dot_general(left, right, (((1,), (1,)), ((), ())), preferred_element_type=jnp.float32)


def contract_first(left, right):
    return lax.dot_general(left, right, (((0,), (0,)), ((), ())), preferred_element_type=jnp.float32)


def column_sum(values):
    return jnp.sum(values.astype(jnp.float32), axis=0)


def group_segments(lengths, dealing, group_index, group_rows, per_group):
    picked = lax.dynamic_slice_in_dim(dealing, group_index * per_group, per_group)
    match = picked[:, None] == jnp.arange(lengths.shape[0], dtype=jnp.int32)[None, :]
    chosen = jnp.sum(jnp.where(match, lengths[None, :], 0), axis=1)
    ends = jnp.cumsum(chosen)
    starts = ends - chosen
    places = jnp.arange(group_rows, dtype=jnp.int32)
    segment_ids = jnp.sum((places[:, None] >= ends[None, :]).astype(jnp.int32), axis=1)
    return (segment_ids, starts, ends)


def cyclic_pieces(piece):
    count = lax.axis_size("tensor")
    me = lax.axis_index("tensor")
    got = [piece]
    for k in range(1, count):
        got.append(lax.ppermute(piece, "tensor", [(s, (s + k) % count) for s in range(count)]))
    order = (me - jnp.arange(count, dtype=jnp.int32)) % count
    return jnp.take(jnp.stack(got), order, axis=0)


def gather_weights(blocks):
    count = lax.axis_size("tensor")
    widths = [b.shape[1] for b in blocks]
    piece = jnp.concatenate(blocks, axis=1)
    parts = cyclic_pieces(piece)
    cols, at = [], 0
    for w in widths:
        cols.extend(parts[t, :, at:at + w] for t in range(count))
        at += w
    strip = jnp.concatenate(cols, axis=1)
    full = lax.all_gather(strip, "dp", axis=0, tiled=True)
    out, at = [], 0
    for w in widths:
        out.append(full[:, at:at + w * count])
        at += w * count
    return out


def vector_rows(v, rows):
    dp = lax.axis_size("dp")
    slab = rows // dp
    spread = v.reshape(dp, 1, -1)
    return jnp.pad(spread, ((0, 0), (0, slab - 1), (0, 0))).reshape(rows, -1)


def pack_grads(grads, vectors):
    count = lax.axis_size("tensor")
    me = lax.axis_index("tensor")
    rows = grads[0].shape[0]
    mats = [g.astype(jnp.bfloat16) for g in grads] + [vector_rows(v.astype(jnp.bfloat16), rows) for v in vectors]
    widths = [m.shape[1] // count for m in mats]
    cat = jnp.concatenate(mats, axis=1)
    return widths, cat


def reduce_dp(cat):
    return lax.psum_scatter(cat, "dp", scatter_dimension=0, tiled=True)


def reduce_tensor(strip, widths, n_grads):
    count = lax.axis_size("tensor")
    me = lax.axis_index("tensor")
    strip = strip.astype(jnp.float32)
    per_t = []
    for t in range(count):
        at, cols = 0, []
        for w in widths:
            cols.append(strip[:, at + t * w:at + (t + 1) * w])
            at += w * count
        per_t.append(jnp.concatenate(cols, axis=1))
    stacked = jnp.stack(per_t)
    total = jnp.take(stacked, me, axis=0)
    for k in range(1, count):
        send = jnp.take(stacked, (me + k) % count, axis=0)
        total = total + lax.ppermute(send, "tensor", [(s, (s + k) % count) for s in range(count)])
    out, at = [], 0
    for i, w in enumerate(widths):
        block = total[:, at:at + w]
        at += w
        out.append(block if i < n_grads else block[0])
    return out


def halo_plan(rows):
    hops = -(-LONGEST // rows)
    takes = [rows] * (hops - 1) + [LONGEST - rows * (hops - 1)]
    return takes


def shift_rows(values, distance, count):
    if distance >= count:
        return jnp.zeros_like(values)
    if distance > 0:
        pairs = [(s, s + distance) for s in range(count - distance)]
    else:
        pairs = [(s - distance, s) for s in range(count + distance)]
    return lax.ppermute(values, "tensor", pairs)


def build_window(own, takes, count):
    rows = own.shape[0]
    left = [shift_rows(own[rows - take:], d + 1, count) for d, take in enumerate(takes)]
    right = [shift_rows(own[:take], -(d + 1), count) for d, take in enumerate(takes)]
    return jnp.concatenate(left[::-1] + [own] + right, axis=0)


def return_window(values, takes, count):
    rows = values.shape[0] - 2 * LONGEST
    total = values[LONGEST:LONGEST + rows]
    at = LONGEST
    for d, take in enumerate(takes):
        piece = values[at - take:at].astype(jnp.bfloat16)
        at -= take
        back = shift_rows(piece, -(d + 1), count).astype(jnp.float32)
        total = total + jnp.pad(back, ((rows - take, 0), (0, 0)))
    at = LONGEST + rows
    for d, take in enumerate(takes):
        piece = values[at:at + take].astype(jnp.bfloat16)
        at += take
        back = shift_rows(piece, d + 1, count).astype(jnp.float32)
        total = total + jnp.pad(back, ((0, rows - take), (0, 0)))
    return total


def to_heads(values):
    rows, width = values.shape
    return values.reshape(rows, width // HEAD_DIM, HEAD_DIM).transpose(1, 0, 2)


def from_heads(values):
    heads, rows, hd = values.shape
    return values.transpose(1, 0, 2).reshape(rows, heads * hd)


def shards(tokens, lengths, dealing, w_query, w_key, w_value, w_out, w_inner, w_outer, b_query, b_value, b_out, b_inner, b_outer, gain_attn, shift_attn, gain_ffn, shift_ffn, grad_out):
    count = lax.axis_size("tensor")
    tens_index = lax.axis_index("tensor")
    group_index = lax.axis_index("dp")
    rows = tokens.shape[0]
    group_rows = rows * count
    per_group = lengths.shape[0] // lax.axis_size("dp")
    takes = halo_plan(rows)
    window = rows + 2 * LONGEST
    seg, starts, ends = group_segments(lengths, dealing, group_index, group_rows, per_group)
    base = rows * tens_index - LONGEST
    places = base + jnp.arange(window, dtype=jnp.int32)
    valid = (places >= 0) & (places < group_rows)
    k_ids = jnp.where(valid, jnp.sum((places[:, None] >= ends[None, :]).astype(jnp.int32), axis=1), -1).astype(jnp.int32)
    q_ids = lax.dynamic_slice_in_dim(seg, rows * tens_index, rows)
    q_start = jnp.take(starts, q_ids) - base
    q_end = jnp.take(ends, q_ids) - base
    lo, hi, qlo, qhi = block_ranges(q_ids, k_ids, q_start, q_end, BLOCK, BLOCK)
    nkb = window // BLOCK
    kv_steps = min(nkb, (BLOCK + 2 * (LONGEST - 1)) // BLOCK + 2)
    q_steps = rows // BLOCK

    wq, wk, wv = gather_weights([w_query, w_key, w_value])
    wo_t, wi, wf_t = gather_weights([w_out.T, w_inner, w_outer.T])
    gain_one = gain_attn.astype(jnp.float32)
    gain_two = gain_ffn.astype(jnp.float32)

    x_own = tokens
    x_win = build_window(tokens, takes, count)
    query = (jnp.dot(x_own, wq, preferred_element_type=jnp.float32) + b_query.astype(jnp.float32)).astype(jnp.bfloat16)
    key_w = jnp.dot(x_win, wk, preferred_element_type=jnp.float32).astype(jnp.bfloat16)
    value_w = (jnp.dot(x_win, wv, preferred_element_type=jnp.float32) + b_value.astype(jnp.float32)).astype(jnp.bfloat16)
    ctx32, lse = flash_forward(query, key_w, value_w, q_ids, k_ids, lo, hi, BLOCK, BLOCK, kv_steps)
    context = ctx32.astype(jnp.bfloat16)
    attn = contract_last(context, wo_t) + b_out.astype(jnp.float32)
    hidden, norm_one, inverse_one = norm_forward(tokens.astype(jnp.float32) + attn, gain_one, shift_attn.astype(jnp.float32))
    hidden_low = hidden.astype(jnp.bfloat16)
    pre_act = jnp.dot(hidden_low, wi, preferred_element_type=jnp.float32) + b_inner.astype(jnp.float32)
    act = activate(pre_act).astype(jnp.bfloat16)
    ffn = contract_last(act, wf_t) + b_outer.astype(jnp.float32)
    output, norm_two, inverse_two = norm_forward(hidden + ffn, gain_two, shift_ffn.astype(jnp.float32))

    grad_y = grad_out.astype(jnp.float32)
    grad_resid_two = norm_backward(grad_y, norm_two, inverse_two, gain_two)
    grad_ffn = grad_resid_two.astype(jnp.bfloat16)
    grad_outer_t = contract_first(grad_ffn, act)
    grad_act = jnp.dot(grad_ffn, wf_t, preferred_element_type=jnp.float32)
    unused, gelu_pull = jax.vjp(activate, pre_act)
    grad_pre = gelu_pull(grad_act)[0].astype(jnp.bfloat16)
    grad_inner_w = contract_first(hidden_low, grad_pre)
    grad_hidden = grad_resid_two + contract_last(grad_pre, wi)
    grad_resid_one = norm_backward(grad_hidden, norm_one, inverse_one, gain_one)
    grad_attn = grad_resid_one.astype(jnp.bfloat16)
    grad_out_t = contract_first(grad_attn, context)
    grad_context = jnp.dot(grad_attn, wo_t, preferred_element_type=jnp.float32).astype(jnp.bfloat16)
    late = [
        column_sum(grad_attn),
        column_sum(grad_pre),
        column_sum(grad_ffn),
        jnp.sum(grad_hidden * norm_one, axis=0),
        jnp.sum(grad_hidden, axis=0),
        jnp.sum(grad_y * norm_two, axis=0),
        jnp.sum(grad_y, axis=0),
    ]
    early_widths, early_cat = pack_grads([grad_out_t, grad_inner_w, grad_outer_t], late)
    grad_context, early_cat = lax.optimization_barrier((grad_context, early_cat))
    early_strip = reduce_dp(early_cat)
    heads = query.shape[1] // HEAD_DIM
    delta = jnp.sum((grad_context.astype(jnp.float32) * ctx32).reshape(rows, heads, HEAD_DIM), axis=-1)
    delta = delta.T.reshape(heads, rows, 1)
    dq_h = flash_dq(query, key_w, value_w, q_ids, k_ids, lse, delta, grad_context, lo, hi, BLOCK, BLOCK, kv_steps)
    dk_h, dv_h = flash_dkv(query, key_w, value_w, q_ids, k_ids, lse, delta, grad_context, qlo, qhi, BLOCK, BLOCK, q_steps)
    early_strip, dq_h, dk_h, dv_h = lax.optimization_barrier((early_strip, dq_h, dk_h, dv_h))
    early_sums = reduce_tensor(early_strip, early_widths, 3)
    g_out_t, g_inner, g_outer_t = early_sums[:3]
    late = early_sums[3:]
    grad_query = dq_h.astype(jnp.bfloat16)
    grad_key = dk_h.astype(jnp.bfloat16)
    grad_value = dv_h.astype(jnp.bfloat16)
    grad_query_w = contract_first(x_own, grad_query)
    grad_key_w = contract_first(x_win, grad_key)
    grad_value_w = contract_first(x_win, grad_value)
    grad_win = contract_last(grad_key, wk) + contract_last(grad_value, wv)
    grad_tokens = grad_resid_one + contract_last(grad_query, wq) + return_window(grad_win, takes, count)

    late_widths, late_cat = pack_grads(
        [grad_query_w, grad_key_w, grad_value_w], [column_sum(grad_query), column_sum(grad_value)]
    )
    g_query, g_key, g_value, g_bq, g_bv = reduce_tensor(reduce_dp(late_cat), late_widths, 3)
    summed = (g_query, g_key, g_value, g_out_t.T, g_inner, g_outer_t.T)
    small = [g_bq, g_bv] + late
    return (output.astype(jnp.bfloat16), grad_tokens) + summed + tuple(small)


def solution(mesh):
    rows = P(("dp", "tensor"), None)
    vec = P(("dp", "tensor"))
    return jax.shard_map(
        shards,
        mesh=mesh,
        in_specs=(rows, P(), P(), P("dp", "tensor"), P("dp", "tensor"), P("dp", "tensor"), P("tensor", "dp"), P("dp", "tensor"), P("tensor", "dp"), P(), P(), P(), P(), P(), P(), P(), P(), P(), rows),
        out_specs=(rows, rows, P("dp", "tensor"), P("dp", "tensor"), P("dp", "tensor"), P("tensor", "dp"), P("dp", "tensor"), P("tensor", "dp")) + (vec,) * 9,
        check_vma=False,
    )
```

```python
import math

import jax
import jax.numpy as jnp
from jax import lax
from jax.experimental import pallas as pl
from jax.experimental.pallas import tpu as pltpu
from jax.sharding import PartitionSpec as P

HEAD_DIM = 64
LONGEST = 1024
BLOCK = 256

NEG = -1e30
LANES = 128


def _lanes(rows):
    return lax.broadcasted_iota(jnp.int32, (rows, LANES), 1) < LANES // 2


def _pick(first, second, lanes):
    return jnp.where(lanes, first, second)


def _nt(a, b):
    return lax.dot_general(a, b, (((1,), (1,)), ((), ())), preferred_element_type=jnp.float32)


def _tn(a, b):
    return lax.dot_general(a, b, (((0,), (0,)), ((), ())), preferred_element_type=jnp.float32)


def _nn(a, b):
    return lax.dot_general(a, b, (((1,), (0,)), ((), ())), preferred_element_type=jnp.float32)


def _attn_fwd(lo_ref, hi_ref, q_ref, k_ref, v_ref, qs_ref, ks_ref, o_ref, lse_ref, m_sc, l_sc, acc_sc):
    i = pl.program_id(0)
    j = pl.program_id(1)
    kv = lo_ref[i] + j
    pairs = q_ref.shape[1] // LANES
    bq = q_ref.shape[0]

    @pl.when(j == 0)
    def _():
        m_sc[...] = jnp.full_like(m_sc, NEG)
        l_sc[...] = jnp.zeros_like(l_sc)
        acc_sc[...] = jnp.zeros_like(acc_sc)

    @pl.when(kv <= hi_ref[i])
    def _():
        mask = qs_ref[...] == ks_ref[...]
        lanes = _lanes(bq)

        def pair(p, carry):
            cols = pl.ds(p * LANES, LANES)
            q2 = q_ref[:, cols]
            k2 = k_ref[:, cols]
            v2 = v_ref[:, cols]
            zero = jnp.zeros_like(q2)
            alphas, pvs = [], []
            for h in range(2):
                hq = _pick(q2, zero, lanes) if h == 0 else _pick(zero, q2, lanes)
                s = jnp.where(mask, _nt(hq, k2), NEG)
                m_old = m_sc[2 * p + h]
                m_new = jnp.maximum(m_old, jnp.max(s, axis=-1, keepdims=True))
                alpha = jnp.exp(m_old - m_new)
                e = jnp.exp(s - m_new)
                l_sc[2 * p + h] = alpha * l_sc[2 * p + h] + jnp.sum(e, axis=-1, keepdims=True)
                m_sc[2 * p + h] = m_new
                alphas.append(alpha)
                pvs.append(_nn(e.astype(jnp.bfloat16), v2))
            acc_sc[:, cols] = _pick(alphas[0], alphas[1], lanes) * acc_sc[:, cols] + _pick(pvs[0], pvs[1], lanes)
            return carry

        for p in range(pairs):
            pair(p, 0)

    @pl.when(j == pl.num_programs(1) - 1)
    def _():
        lanes = _lanes(bq)

        def pair(p, carry):
            cols = pl.ds(p * LANES, LANES)
            l0, l1 = l_sc[2 * p], l_sc[2 * p + 1]
            o_ref[:, cols] = acc_sc[:, cols] / _pick(l0, l1, lanes)
            lse_ref[2 * p] = m_sc[2 * p] + jnp.log(l0)
            lse_ref[2 * p + 1] = m_sc[2 * p + 1] + jnp.log(l1)
            return carry

        for p in range(pairs):
            pair(p, 0)


def _attn_dq(lo_ref, hi_ref, q_ref, k_ref, v_ref, qs_ref, ks_ref, lse_ref, dl_ref, do_ref, dq_ref, acc_sc):
    i = pl.program_id(0)
    j = pl.program_id(1)
    kv = lo_ref[i] + j
    pairs = q_ref.shape[1] // LANES
    bq = q_ref.shape[0]

    @pl.when(j == 0)
    def _():
        acc_sc[...] = jnp.zeros_like(acc_sc)

    @pl.when(kv <= hi_ref[i])
    def _():
        mask = qs_ref[...] == ks_ref[...]
        lanes = _lanes(bq)

        def pair(p, carry):
            cols = pl.ds(p * LANES, LANES)
            q2 = q_ref[:, cols]
            k2 = k_ref[:, cols]
            v2 = v_ref[:, cols]
            do2 = do_ref[:, cols]
            zero = jnp.zeros_like(q2)
            parts = []
            for h in range(2):
                sel = (lambda a: _pick(a, zero, lanes)) if h == 0 else (lambda a: _pick(zero, a, lanes))
                s = _nt(sel(q2), k2)
                e = jnp.where(mask, jnp.exp(s - lse_ref[2 * p + h]), 0.0)
                dp = _nt(sel(do2), v2)
                ds = (e * (dp - dl_ref[2 * p + h])).astype(jnp.bfloat16)
                parts.append(_nn(ds, k2))
            acc_sc[:, cols] += _pick(parts[0], parts[1], lanes)
            return carry

        for p in range(pairs):
            pair(p, 0)

    @pl.when(j == pl.num_programs(1) - 1)
    def _():
        dq_ref[...] = acc_sc[...] * 0.125


def _attn_dkv(lo_ref, hi_ref, q_ref, k_ref, v_ref, qs_ref, ks_ref, lse_ref, dl_ref, do_ref, dk_ref, dv_ref, dk_sc, dv_sc):
    j = pl.program_id(0)
    i = pl.program_id(1)
    qb = lo_ref[j] + i
    pairs = q_ref.shape[1] // LANES
    bq = q_ref.shape[0]
    bk = k_ref.shape[0]

    @pl.when(i == 0)
    def _():
        dk_sc[...] = jnp.zeros_like(dk_sc)
        dv_sc[...] = jnp.zeros_like(dv_sc)

    @pl.when(qb <= hi_ref[j])
    def _():
        mask = qs_ref[...] == ks_ref[...]
        lanes_q = _lanes(bq)
        lanes_k = _lanes(bk)

        def pair(p, carry):
            cols = pl.ds(p * LANES, LANES)
            q2 = q_ref[:, cols]
            k2 = k_ref[:, cols]
            v2 = v_ref[:, cols]
            do2 = do_ref[:, cols]
            zero = jnp.zeros_like(q2)
            dks, dvs = [], []
            for h in range(2):
                sel = (lambda a: _pick(a, zero, lanes_q)) if h == 0 else (lambda a: _pick(zero, a, lanes_q))
                s = _nt(sel(q2), k2)
                e = jnp.where(mask, jnp.exp(s - lse_ref[2 * p + h]), 0.0)
                dp = _nt(sel(do2), v2)
                ds = (e * (dp - dl_ref[2 * p + h])).astype(jnp.bfloat16)
                dvs.append(_tn(e.astype(jnp.bfloat16), do2))
                dks.append(_tn(ds, q2))
            dv_sc[:, cols] += _pick(dvs[0], dvs[1], lanes_k)
            dk_sc[:, cols] += _pick(dks[0], dks[1], lanes_k)
            return carry

        for p in range(pairs):
            pair(p, 0)

    @pl.when(i == pl.num_programs(1) - 1)
    def _():
        dk_ref[...] = dk_sc[...]
        dv_ref[...] = dv_sc[...]


def _clamp(start, step, last):
    return jnp.minimum(start + step, jnp.maximum(last, 0))


def _params():
    return pltpu.CompilerParams(dimension_semantics=("arbitrary", "arbitrary"), vmem_limit_bytes=48 * 1024 * 1024)


def flash_forward(q, k, v, q_ids, k_ids, lo, hi, block_q, block_k, steps):
    nq, width = q.shape
    nk = k.shape[0]
    heads = width // 64
    kv_map = lambda i, j, a, b: (_clamp(a[i], j, b[i]), 0)
    ks_map = lambda i, j, a, b: (0, _clamp(a[i], j, b[i]))
    row = lambda i, j, a, b: (i, 0)
    grid_spec = pltpu.PrefetchScalarGridSpec(
        num_scalar_prefetch=2,
        grid=(nq // block_q, steps),
        in_specs=[
            pl.BlockSpec((block_q, width), row),
            pl.BlockSpec((block_k, width), kv_map),
            pl.BlockSpec((block_k, width), kv_map),
            pl.BlockSpec((block_q, 1), row),
            pl.BlockSpec((1, block_k), ks_map),
        ],
        out_specs=[
            pl.BlockSpec((block_q, width), row),
            pl.BlockSpec((heads, block_q, 1), lambda i, j, a, b: (0, i, 0)),
        ],
        scratch_shapes=[
            pltpu.VMEM((heads, block_q, 1), jnp.float32),
            pltpu.VMEM((heads, block_q, 1), jnp.float32),
            pltpu.VMEM((block_q, width), jnp.float32),
        ],
    )
    return pl.pallas_call(
        _attn_fwd,
        grid_spec=grid_spec,
        out_shape=[jax.ShapeDtypeStruct((nq, width), jnp.float32), jax.ShapeDtypeStruct((heads, nq, 1), jnp.float32)],
        compiler_params=_params(),
    )(lo, hi, q, k, v, q_ids.reshape(nq, 1), k_ids.reshape(1, nk))


def flash_dq(q, k, v, q_ids, k_ids, lse, delta, do, lo, hi, block_q, block_k, steps):
    nq, width = q.shape
    nk = k.shape[0]
    heads = width // 64
    kv_map = lambda i, j, a, b: (_clamp(a[i], j, b[i]), 0)
    ks_map = lambda i, j, a, b: (0, _clamp(a[i], j, b[i]))
    row = lambda i, j, a, b: (i, 0)
    hrow = lambda i, j, a, b: (0, i, 0)
    grid_spec = pltpu.PrefetchScalarGridSpec(
        num_scalar_prefetch=2,
        grid=(nq // block_q, steps),
        in_specs=[
            pl.BlockSpec((block_q, width), row),
            pl.BlockSpec((block_k, width), kv_map),
            pl.BlockSpec((block_k, width), kv_map),
            pl.BlockSpec((block_q, 1), row),
            pl.BlockSpec((1, block_k), ks_map),
            pl.BlockSpec((heads, block_q, 1), hrow),
            pl.BlockSpec((heads, block_q, 1), hrow),
            pl.BlockSpec((block_q, width), row),
        ],
        out_specs=pl.BlockSpec((block_q, width), row),
        scratch_shapes=[pltpu.VMEM((block_q, width), jnp.float32)],
    )
    return pl.pallas_call(
        _attn_dq,
        grid_spec=grid_spec,
        out_shape=jax.ShapeDtypeStruct((nq, width), jnp.float32),
        compiler_params=_params(),
    )(lo, hi, q, k, v, q_ids.reshape(nq, 1), k_ids.reshape(1, nk), lse, delta, do)


def flash_dkv(q, k, v, q_ids, k_ids, lse, delta, do, qlo, qhi, block_q, block_k, steps):
    nq, width = q.shape
    nk = k.shape[0]
    heads = width // 64
    q_map = lambda j, i, a, b: (_clamp(a[j], i, b[j]), 0)
    h_map = lambda j, i, a, b: (0, _clamp(a[j], i, b[j]), 0)
    col = lambda j, i, a, b: (j, 0)
    grid_spec = pltpu.PrefetchScalarGridSpec(
        num_scalar_prefetch=2,
        grid=(nk // block_k, steps),
        in_specs=[
            pl.BlockSpec((block_q, width), q_map),
            pl.BlockSpec((block_k, width), col),
            pl.BlockSpec((block_k, width), col),
            pl.BlockSpec((block_q, 1), q_map),
            pl.BlockSpec((1, block_k), lambda j, i, a, b: (0, j)),
            pl.BlockSpec((heads, block_q, 1), h_map),
            pl.BlockSpec((heads, block_q, 1), h_map),
            pl.BlockSpec((block_q, width), q_map),
        ],
        out_specs=[pl.BlockSpec((block_k, width), col), pl.BlockSpec((block_k, width), col)],
        scratch_shapes=[pltpu.VMEM((block_k, width), jnp.float32), pltpu.VMEM((block_k, width), jnp.float32)],
    )
    return pl.pallas_call(
        _attn_dkv,
        grid_spec=grid_spec,
        out_shape=[jax.ShapeDtypeStruct((nk, width), jnp.float32), jax.ShapeDtypeStruct((nk, width), jnp.float32)],
        compiler_params=_params(),
    )(qlo, qhi, q, k, v, q_ids.reshape(nq, 1), k_ids.reshape(1, nk), lse, delta, do)


def block_ranges(q_ids, k_ids, q_start, q_end, block_q, block_k):
    nq = q_ids.shape[0]
    nk = k_ids.shape[0]
    nqb, nkb = nq // block_q, nk // block_k
    first = q_start.reshape(nqb, block_q)[:, 0]
    last = q_end.reshape(nqb, block_q)[:, block_q - 1]
    lo = jnp.clip(first // block_k, 0, nkb - 1).astype(jnp.int32)
    hi = jnp.clip((last - 1) // block_k, 0, nkb - 1).astype(jnp.int32)
    kb = jnp.arange(nkb, dtype=jnp.int32)
    qb = jnp.arange(nqb, dtype=jnp.int32)
    cover = (lo[:, None] <= kb[None, :]) & (kb[None, :] <= hi[:, None])
    qlo = jnp.min(jnp.where(cover, qb[:, None], nqb), axis=0).astype(jnp.int32)
    qhi = jnp.max(jnp.where(cover, qb[:, None], -1), axis=0).astype(jnp.int32)
    return lo, hi, qlo, qhi


def norm_forward(values, gain, shift):
    center = jnp.mean(values, axis=-1, keepdims=True)
    offsets = values - center
    spread = jnp.mean(offsets * offsets, axis=-1, keepdims=True)
    inverse = lax.rsqrt(spread + 1e-06)
    normed = offsets * inverse
    return (normed * gain + shift, normed, inverse)


def norm_backward(grad_y, normed, inverse, gain):
    grad_normed = grad_y * gain
    mean_one = jnp.mean(grad_normed, axis=-1, keepdims=True)
    mean_two = jnp.mean(grad_normed * normed, axis=-1, keepdims=True)
    return inverse * (grad_normed - mean_one - normed * mean_two)


def activate(values):
    return jax.nn.gelu(values, approximate=False)


def contract_last(left, right):
    return lax.dot_general(left, right, (((1,), (1,)), ((), ())), preferred_element_type=jnp.float32)


def contract_first(left, right):
    return lax.dot_general(left, right, (((0,), (0,)), ((), ())), preferred_element_type=jnp.float32)


def column_sum(values):
    return jnp.sum(values.astype(jnp.float32), axis=0)


def group_segments(lengths, dealing, group_index, group_rows, per_group):
    picked = lax.dynamic_slice_in_dim(dealing, group_index * per_group, per_group)
    match = picked[:, None] == jnp.arange(lengths.shape[0], dtype=jnp.int32)[None, :]
    chosen = jnp.sum(jnp.where(match, lengths[None, :], 0), axis=1)
    ends = jnp.cumsum(chosen)
    starts = ends - chosen
    places = jnp.arange(group_rows, dtype=jnp.int32)
    segment_ids = jnp.sum((places[:, None] >= ends[None, :]).astype(jnp.int32), axis=1)
    return (segment_ids, starts, ends)


def cyclic_pieces(piece):
    count = lax.axis_size("tensor")
    me = lax.axis_index("tensor")
    got = [piece]
    for k in range(1, count):
        got.append(lax.ppermute(piece, "tensor", [(s, (s + k) % count) for s in range(count)]))
    order = (me - jnp.arange(count, dtype=jnp.int32)) % count
    return jnp.take(jnp.stack(got), order, axis=0)


def gather_weights(blocks):
    count = lax.axis_size("tensor")
    widths = [b.shape[1] for b in blocks]
    piece = jnp.concatenate(blocks, axis=1)
    parts = cyclic_pieces(piece)
    cols, at = [], 0
    for w in widths:
        cols.extend(parts[t, :, at:at + w] for t in range(count))
        at += w
    strip = jnp.concatenate(cols, axis=1)
    full = lax.all_gather(strip, "dp", axis=0, tiled=True)
    out, at = [], 0
    for w in widths:
        out.append(full[:, at:at + w * count])
        at += w * count
    return out


def vector_rows(v, rows):
    dp = lax.axis_size("dp")
    slab = rows // dp
    spread = v.reshape(dp, 1, -1)
    return jnp.pad(spread, ((0, 0), (0, slab - 1), (0, 0))).reshape(rows, -1)


def pack_grads(grads, vectors):
    count = lax.axis_size("tensor")
    me = lax.axis_index("tensor")
    rows = grads[0].shape[0]
    mats = [g.astype(jnp.bfloat16) for g in grads] + [vector_rows(v.astype(jnp.bfloat16), rows) for v in vectors]
    widths = [m.shape[1] // count for m in mats]
    cat = jnp.concatenate(mats, axis=1)
    return widths, cat


def reduce_dp(cat):
    return lax.psum_scatter(cat, "dp", scatter_dimension=0, tiled=True)


def reduce_tensor(strip, widths, n_grads):
    count = lax.axis_size("tensor")
    me = lax.axis_index("tensor")
    strip = strip.astype(jnp.float32)
    per_t = []
    for t in range(count):
        at, cols = 0, []
        for w in widths:
            cols.append(strip[:, at + t * w:at + (t + 1) * w])
            at += w * count
        per_t.append(jnp.concatenate(cols, axis=1))
    stacked = jnp.stack(per_t)
    total = jnp.take(stacked, me, axis=0)
    for k in range(1, count):
        send = jnp.take(stacked, (me + k) % count, axis=0)
        total = total + lax.ppermute(send, "tensor", [(s, (s + k) % count) for s in range(count)])
    out, at = [], 0
    for i, w in enumerate(widths):
        block = total[:, at:at + w]
        at += w
        out.append(block if i < n_grads else block[0])
    return out


def halo_plan(rows):
    hops = -(-LONGEST // rows)
    takes = [rows] * (hops - 1) + [LONGEST - rows * (hops - 1)]
    return takes


def shift_rows(values, distance, count):
    if distance >= count:
        return jnp.zeros_like(values)
    if distance > 0:
        pairs = [(s, s + distance) for s in range(count - distance)]
    else:
        pairs = [(s - distance, s) for s in range(count + distance)]
    return lax.ppermute(values, "tensor", pairs)


def build_window(own, takes, count):
    rows = own.shape[0]
    left = [shift_rows(own[rows - take:], d + 1, count) for d, take in enumerate(takes)]
    right = [shift_rows(own[:take], -(d + 1), count) for d, take in enumerate(takes)]
    return jnp.concatenate(left[::-1] + [own] + right, axis=0)


def return_window(values, takes, count):
    rows = values.shape[0] - 2 * LONGEST
    total = values[LONGEST:LONGEST + rows]
    at = LONGEST
    for d, take in enumerate(takes):
        piece = values[at - take:at].astype(jnp.bfloat16)
        at -= take
        back = shift_rows(piece, -(d + 1), count).astype(jnp.float32)
        total = total + jnp.pad(back, ((rows - take, 0), (0, 0)))
    at = LONGEST + rows
    for d, take in enumerate(takes):
        piece = values[at:at + take].astype(jnp.bfloat16)
        at += take
        back = shift_rows(piece, d + 1, count).astype(jnp.float32)
        total = total + jnp.pad(back, ((0, rows - take), (0, 0)))
    return total


def to_heads(values):
    rows, width = values.shape
    return values.reshape(rows, width // HEAD_DIM, HEAD_DIM).transpose(1, 0, 2)


def from_heads(values):
    heads, rows, hd = values.shape
    return values.transpose(1, 0, 2).reshape(rows, heads * hd)


def shards(tokens, lengths, dealing, w_query, w_key, w_value, w_out, w_inner, w_outer, b_query, b_value, b_out, b_inner, b_outer, gain_attn, shift_attn, gain_ffn, shift_ffn, grad_out):
    count = lax.axis_size("tensor")
    tens_index = lax.axis_index("tensor")
    group_index = lax.axis_index("dp")
    rows = tokens.shape[0]
    group_rows = rows * count
    per_group = lengths.shape[0] // lax.axis_size("dp")
    takes = halo_plan(rows)
    window = rows + 2 * LONGEST
    seg, starts, ends = group_segments(lengths, dealing, group_index, group_rows, per_group)
    base = rows * tens_index - LONGEST
    places = base + jnp.arange(window, dtype=jnp.int32)
    valid = (places >= 0) & (places < group_rows)
    k_ids = jnp.where(valid, jnp.sum((places[:, None] >= ends[None, :]).astype(jnp.int32), axis=1), -1).astype(jnp.int32)
    q_ids = lax.dynamic_slice_in_dim(seg, rows * tens_index, rows)
    q_start = jnp.take(starts, q_ids) - base
    q_end = jnp.take(ends, q_ids) - base
    lo, hi, qlo, qhi = block_ranges(q_ids, k_ids, q_start, q_end, BLOCK, BLOCK)
    nkb = window // BLOCK
    kv_steps = min(nkb, (BLOCK + 2 * (LONGEST - 1)) // BLOCK + 2)
    q_steps = rows // BLOCK

    wq, wk, wv = gather_weights([w_query, w_key, w_value])
    wo_t, wi, wf_t = gather_weights([w_out.T, w_inner, w_outer.T])
    gain_one = gain_attn.astype(jnp.float32)
    gain_two = gain_ffn.astype(jnp.float32)

    x_own = tokens
    x_win = build_window(tokens, takes, count)
    query = (jnp.dot(x_own, wq, preferred_element_type=jnp.float32) + b_query.astype(jnp.float32)).astype(jnp.bfloat16)
    key_w = jnp.dot(x_win, wk, preferred_element_type=jnp.float32).astype(jnp.bfloat16)
    value_w = (jnp.dot(x_win, wv, preferred_element_type=jnp.float32) + b_value.astype(jnp.float32)).astype(jnp.bfloat16)
    scaled = query * jnp.asarray(1.0 / math.sqrt(HEAD_DIM), jnp.bfloat16)
    ctx32, lse = flash_forward(scaled, key_w, value_w, q_ids, k_ids, lo, hi, BLOCK, BLOCK, kv_steps)
    context = ctx32.astype(jnp.bfloat16)
    attn = contract_last(context, wo_t) + b_out.astype(jnp.float32)
    hidden, norm_one, inverse_one = norm_forward(tokens.astype(jnp.float32) + attn, gain_one, shift_attn.astype(jnp.float32))
    hidden_low = hidden.astype(jnp.bfloat16)
    pre_act = jnp.dot(hidden_low, wi, preferred_element_type=jnp.float32) + b_inner.astype(jnp.float32)
    act = activate(pre_act).astype(jnp.bfloat16)
    ffn = contract_last(act, wf_t) + b_outer.astype(jnp.float32)
    output, norm_two, inverse_two = norm_forward(hidden + ffn, gain_two, shift_ffn.astype(jnp.float32))

    grad_y = grad_out.astype(jnp.float32)
    grad_resid_two = norm_backward(grad_y, norm_two, inverse_two, gain_two)
    grad_ffn = grad_resid_two.astype(jnp.bfloat16)
    grad_outer_t = contract_first(grad_ffn, act)
    grad_act = jnp.dot(grad_ffn, wf_t, preferred_element_type=jnp.float32)
    unused, gelu_pull = jax.vjp(activate, pre_act)
    grad_pre = gelu_pull(grad_act)[0].astype(jnp.bfloat16)
    grad_inner_w = contract_first(hidden_low, grad_pre)
    grad_hidden = grad_resid_two + contract_last(grad_pre, wi)
    grad_resid_one = norm_backward(grad_hidden, norm_one, inverse_one, gain_one)
    grad_attn = grad_resid_one.astype(jnp.bfloat16)
    grad_out_t = contract_first(grad_attn, context)
    grad_context = jnp.dot(grad_attn, wo_t, preferred_element_type=jnp.float32).astype(jnp.bfloat16)
    late = [
        column_sum(grad_attn),
        column_sum(grad_pre),
        column_sum(grad_ffn),
        jnp.sum(grad_hidden * norm_one, axis=0),
        jnp.sum(grad_hidden, axis=0),
        jnp.sum(grad_y * norm_two, axis=0),
        jnp.sum(grad_y, axis=0),
    ]
    early_widths, early_cat = pack_grads([grad_out_t, grad_inner_w, grad_outer_t], late)
    grad_context, early_cat = lax.optimization_barrier((grad_context, early_cat))
    early_strip = reduce_dp(early_cat)
    heads = query.shape[1] // HEAD_DIM
    delta = jnp.sum((grad_context.astype(jnp.float32) * ctx32).reshape(rows, heads, HEAD_DIM), axis=-1)
    delta = delta.T.reshape(heads, rows, 1)
    dq_h = flash_dq(scaled, key_w, value_w, q_ids, k_ids, lse, delta, grad_context, lo, hi, BLOCK, BLOCK, kv_steps)
    dk_h, dv_h = flash_dkv(scaled, key_w, value_w, q_ids, k_ids, lse, delta, grad_context, qlo, qhi, BLOCK, BLOCK, q_steps)
    early_strip, dq_h, dk_h, dv_h = lax.optimization_barrier((early_strip, dq_h, dk_h, dv_h))
    early_sums = reduce_tensor(early_strip, early_widths, 3)
    g_out_t, g_inner, g_outer_t = early_sums[:3]
    late = early_sums[3:]
    grad_query = dq_h.astype(jnp.bfloat16)
    grad_key = dk_h.astype(jnp.bfloat16)
    grad_value = dv_h.astype(jnp.bfloat16)
    grad_query_w = contract_first(x_own, grad_query)
    grad_key_w = contract_first(x_win, grad_key)
    grad_value_w = contract_first(x_win, grad_value)
    grad_win = contract_last(grad_key, wk) + contract_last(grad_value, wv)
    grad_tokens = grad_resid_one + contract_last(grad_query, wq) + return_window(grad_win, takes, count)

    late_widths, late_cat = pack_grads(
        [grad_query_w, grad_key_w, grad_value_w], [column_sum(grad_query), column_sum(grad_value)]
    )
    g_query, g_key, g_value, g_bq, g_bv = reduce_tensor(reduce_dp(late_cat), late_widths, 3)
    summed = (g_query, g_key, g_value, g_out_t.T, g_inner, g_outer_t.T)
    small = [g_bq, g_bv] + late
    return (output.astype(jnp.bfloat16), grad_tokens) + summed + tuple(small)


def solution(mesh):
    rows = P(("dp", "tensor"), None)
    vec = P(("dp", "tensor"))
    return jax.shard_map(
        shards,
        mesh=mesh,
        in_specs=(rows, P(), P(), P("dp", "tensor"), P("dp", "tensor"), P("dp", "tensor"), P("tensor", "dp"), P("dp", "tensor"), P("tensor", "dp"), P(), P(), P(), P(), P(), P(), P(), P(), P(), rows),
        out_specs=(rows, rows, P("dp", "tensor"), P("dp", "tensor"), P("dp", "tensor"), P("tensor", "dp"), P("dp", "tensor"), P("tensor", "dp")) + (vec,) * 9,
        check_vma=False,
    )
```

```python
import math

import jax
import jax.numpy as jnp
from jax import lax
from jax.experimental import pallas as pl
from jax.experimental.pallas import tpu as pltpu
from jax.sharding import PartitionSpec as P

HEAD_DIM = 64
LONGEST = 1024
BLOCK = 256

NEG = -1e30
LANES = 128


def _lanes(rows):
    return lax.broadcasted_iota(jnp.int32, (rows, LANES), 1) < LANES // 2


def _pick(first, second, lanes):
    return jnp.where(lanes, first, second)


def _nt(a, b):
    return lax.dot_general(a, b, (((1,), (1,)), ((), ())), preferred_element_type=jnp.float32)


def _tn(a, b):
    return lax.dot_general(a, b, (((0,), (0,)), ((), ())), preferred_element_type=jnp.float32)


def _nn(a, b):
    return lax.dot_general(a, b, (((1,), (0,)), ((), ())), preferred_element_type=jnp.float32)


def _attn_fwd(lo_ref, hi_ref, q_ref, k_ref, v_ref, qs_ref, ks_ref, o_ref, lse_ref, m_sc, l_sc, acc_sc):
    i = pl.program_id(0)
    j = pl.program_id(1)
    kv = lo_ref[i] + j
    pairs = q_ref.shape[1] // LANES
    bq = q_ref.shape[0]

    @pl.when(j == 0)
    def _():
        m_sc[...] = jnp.full_like(m_sc, NEG)
        l_sc[...] = jnp.zeros_like(l_sc)
        acc_sc[...] = jnp.zeros_like(acc_sc)

    @pl.when(kv <= hi_ref[i])
    def _():
        mask = qs_ref[...] == ks_ref[...]
        lanes = _lanes(bq)

        def pair(p, carry):
            cols = pl.ds(p * LANES, LANES)
            q2 = q_ref[:, cols]
            k2 = k_ref[:, cols]
            v2 = v_ref[:, cols]
            zero = jnp.zeros_like(q2)
            alphas, pvs = [], []
            for h in range(2):
                hq = _pick(q2, zero, lanes) if h == 0 else _pick(zero, q2, lanes)
                s = jnp.where(mask, _nt(hq, k2), NEG)
                m_old = m_sc[2 * p + h]
                m_new = jnp.maximum(m_old, jnp.max(s, axis=-1, keepdims=True))
                alpha = jnp.exp(m_old - m_new)
                e = jnp.exp(s - m_new)
                l_sc[2 * p + h] = alpha * l_sc[2 * p + h] + jnp.sum(e, axis=-1, keepdims=True)
                m_sc[2 * p + h] = m_new
                alphas.append(alpha)
                pvs.append(_nn(e.astype(jnp.bfloat16), v2))
            acc_sc[:, cols] = _pick(alphas[0], alphas[1], lanes) * acc_sc[:, cols] + _pick(pvs[0], pvs[1], lanes)
            return carry

        for p in range(pairs):
            pair(p, 0)

    @pl.when(j == pl.num_programs(1) - 1)
    def _():
        lanes = _lanes(bq)

        def pair(p, carry):
            cols = pl.ds(p * LANES, LANES)
            l0, l1 = l_sc[2 * p], l_sc[2 * p + 1]
            o_ref[:, cols] = acc_sc[:, cols] / _pick(l0, l1, lanes)
            lse_ref[2 * p] = m_sc[2 * p] + jnp.log(l0)
            lse_ref[2 * p + 1] = m_sc[2 * p + 1] + jnp.log(l1)
            return carry

        for p in range(pairs):
            pair(p, 0)


def _attn_dq(lo_ref, hi_ref, q_ref, k_ref, v_ref, qs_ref, ks_ref, lse_ref, dl_ref, do_ref, dq_ref, acc_sc):
    i = pl.program_id(0)
    j = pl.program_id(1)
    kv = lo_ref[i] + j
    pairs = q_ref.shape[1] // LANES
    bq = q_ref.shape[0]

    @pl.when(j == 0)
    def _():
        acc_sc[...] = jnp.zeros_like(acc_sc)

    @pl.when(kv <= hi_ref[i])
    def _():
        mask = qs_ref[...] == ks_ref[...]
        lanes = _lanes(bq)

        def pair(p, carry):
            cols = pl.ds(p * LANES, LANES)
            q2 = q_ref[:, cols]
            k2 = k_ref[:, cols]
            v2 = v_ref[:, cols]
            do2 = do_ref[:, cols]
            zero = jnp.zeros_like(q2)
            parts = []
            for h in range(2):
                sel = (lambda a: _pick(a, zero, lanes)) if h == 0 else (lambda a: _pick(zero, a, lanes))
                s = _nt(sel(q2), k2)
                e = jnp.where(mask, jnp.exp(s - lse_ref[2 * p + h]), 0.0)
                dp = _nt(sel(do2), v2)
                ds = (e * (dp - dl_ref[2 * p + h])).astype(jnp.bfloat16)
                parts.append(_nn(ds, k2))
            acc_sc[:, cols] += _pick(parts[0], parts[1], lanes)
            return carry

        for p in range(pairs):
            pair(p, 0)

    @pl.when(j == pl.num_programs(1) - 1)
    def _():
        dq_ref[...] = acc_sc[...] * 0.125


def _attn_dkv(lo_ref, hi_ref, q_ref, k_ref, v_ref, qs_ref, ks_ref, lse_ref, dl_ref, do_ref, dk_ref, dv_ref, dk_sc, dv_sc):
    j = pl.program_id(0)
    i = pl.program_id(1)
    qb = lo_ref[j] + i
    pairs = q_ref.shape[1] // LANES
    bq = q_ref.shape[0]
    bk = k_ref.shape[0]

    @pl.when(i == 0)
    def _():
        dk_sc[...] = jnp.zeros_like(dk_sc)
        dv_sc[...] = jnp.zeros_like(dv_sc)

    @pl.when(qb <= hi_ref[j])
    def _():
        mask = qs_ref[...] == ks_ref[...]
        lanes_q = _lanes(bq)
        lanes_k = _lanes(bk)

        def pair(p, carry):
            cols = pl.ds(p * LANES, LANES)
            q2 = q_ref[:, cols]
            k2 = k_ref[:, cols]
            v2 = v_ref[:, cols]
            do2 = do_ref[:, cols]
            zero = jnp.zeros_like(q2)
            dks, dvs = [], []
            for h in range(2):
                sel = (lambda a: _pick(a, zero, lanes_q)) if h == 0 else (lambda a: _pick(zero, a, lanes_q))
                s = _nt(sel(q2), k2)
                e = jnp.where(mask, jnp.exp(s - lse_ref[2 * p + h]), 0.0)
                dp = _nt(sel(do2), v2)
                ds = (e * (dp - dl_ref[2 * p + h])).astype(jnp.bfloat16)
                dvs.append(_tn(e.astype(jnp.bfloat16), do2))
                dks.append(_tn(ds, q2))
            dv_sc[:, cols] += _pick(dvs[0], dvs[1], lanes_k)
            dk_sc[:, cols] += _pick(dks[0], dks[1], lanes_k)
            return carry

        for p in range(pairs):
            pair(p, 0)

    @pl.when(i == pl.num_programs(1) - 1)
    def _():
        dk_ref[...] = dk_sc[...]
        dv_ref[...] = dv_sc[...]


def _clamp(start, step, last):
    return jnp.minimum(start + step, jnp.maximum(last, 0))


def _params():
    return pltpu.CompilerParams(dimension_semantics=("arbitrary", "arbitrary"), vmem_limit_bytes=48 * 1024 * 1024)


def flash_forward(q, k, v, q_ids, k_ids, lo, hi, block_q, block_k, steps):
    nq, width = q.shape
    nk = k.shape[0]
    heads = width // 64
    kv_map = lambda i, j, a, b: (_clamp(a[i], j, b[i]), 0)
    ks_map = lambda i, j, a, b: (0, _clamp(a[i], j, b[i]))
    row = lambda i, j, a, b: (i, 0)
    grid_spec = pltpu.PrefetchScalarGridSpec(
        num_scalar_prefetch=2,
        grid=(nq // block_q, steps),
        in_specs=[
            pl.BlockSpec((block_q, width), row),
            pl.BlockSpec((block_k, width), kv_map),
            pl.BlockSpec((block_k, width), kv_map),
            pl.BlockSpec((block_q, 1), row),
            pl.BlockSpec((1, block_k), ks_map),
        ],
        out_specs=[
            pl.BlockSpec((block_q, width), row),
            pl.BlockSpec((heads, block_q, 1), lambda i, j, a, b: (0, i, 0)),
        ],
        scratch_shapes=[
            pltpu.VMEM((heads, block_q, 1), jnp.float32),
            pltpu.VMEM((heads, block_q, 1), jnp.float32),
            pltpu.VMEM((block_q, width), jnp.float32),
        ],
    )
    return pl.pallas_call(
        _attn_fwd,
        grid_spec=grid_spec,
        out_shape=[jax.ShapeDtypeStruct((nq, width), jnp.float32), jax.ShapeDtypeStruct((heads, nq, 1), jnp.float32)],
        compiler_params=_params(),
    )(lo, hi, q, k, v, q_ids.reshape(nq, 1), k_ids.reshape(1, nk))


def flash_dq(q, k, v, q_ids, k_ids, lse, delta, do, lo, hi, block_q, block_k, steps):
    nq, width = q.shape
    nk = k.shape[0]
    heads = width // 64
    kv_map = lambda i, j, a, b: (_clamp(a[i], j, b[i]), 0)
    ks_map = lambda i, j, a, b: (0, _clamp(a[i], j, b[i]))
    row = lambda i, j, a, b: (i, 0)
    hrow = lambda i, j, a, b: (0, i, 0)
    grid_spec = pltpu.PrefetchScalarGridSpec(
        num_scalar_prefetch=2,
        grid=(nq // block_q, steps),
        in_specs=[
            pl.BlockSpec((block_q, width), row),
            pl.BlockSpec((block_k, width), kv_map),
            pl.BlockSpec((block_k, width), kv_map),
            pl.BlockSpec((block_q, 1), row),
            pl.BlockSpec((1, block_k), ks_map),
            pl.BlockSpec((heads, block_q, 1), hrow),
            pl.BlockSpec((heads, block_q, 1), hrow),
            pl.BlockSpec((block_q, width), row),
        ],
        out_specs=pl.BlockSpec((block_q, width), row),
        scratch_shapes=[pltpu.VMEM((block_q, width), jnp.float32)],
    )
    return pl.pallas_call(
        _attn_dq,
        grid_spec=grid_spec,
        out_shape=jax.ShapeDtypeStruct((nq, width), jnp.float32),
        compiler_params=_params(),
    )(lo, hi, q, k, v, q_ids.reshape(nq, 1), k_ids.reshape(1, nk), lse, delta, do)


def flash_dkv(q, k, v, q_ids, k_ids, lse, delta, do, qlo, qhi, block_q, block_k, steps):
    nq, width = q.shape
    nk = k.shape[0]
    heads = width // 64
    q_map = lambda j, i, a, b: (_clamp(a[j], i, b[j]), 0)
    h_map = lambda j, i, a, b: (0, _clamp(a[j], i, b[j]), 0)
    col = lambda j, i, a, b: (j, 0)
    grid_spec = pltpu.PrefetchScalarGridSpec(
        num_scalar_prefetch=2,
        grid=(nk // block_k, steps),
        in_specs=[
            pl.BlockSpec((block_q, width), q_map),
            pl.BlockSpec((block_k, width), col),
            pl.BlockSpec((block_k, width), col),
            pl.BlockSpec((block_q, 1), q_map),
            pl.BlockSpec((1, block_k), lambda j, i, a, b: (0, j)),
            pl.BlockSpec((heads, block_q, 1), h_map),
            pl.BlockSpec((heads, block_q, 1), h_map),
            pl.BlockSpec((block_q, width), q_map),
        ],
        out_specs=[pl.BlockSpec((block_k, width), col), pl.BlockSpec((block_k, width), col)],
        scratch_shapes=[pltpu.VMEM((block_k, width), jnp.float32), pltpu.VMEM((block_k, width), jnp.float32)],
    )
    return pl.pallas_call(
        _attn_dkv,
        grid_spec=grid_spec,
        out_shape=[jax.ShapeDtypeStruct((nk, width), jnp.float32), jax.ShapeDtypeStruct((nk, width), jnp.float32)],
        compiler_params=_params(),
    )(qlo, qhi, q, k, v, q_ids.reshape(nq, 1), k_ids.reshape(1, nk), lse, delta, do)


def block_ranges(q_ids, k_ids, q_start, q_end, block_q, block_k):
    nq = q_ids.shape[0]
    nk = k_ids.shape[0]
    nqb, nkb = nq // block_q, nk // block_k
    first = q_start.reshape(nqb, block_q)[:, 0]
    last = q_end.reshape(nqb, block_q)[:, block_q - 1]
    lo = jnp.clip(first // block_k, 0, nkb - 1).astype(jnp.int32)
    hi = jnp.clip((last - 1) // block_k, 0, nkb - 1).astype(jnp.int32)
    kb = jnp.arange(nkb, dtype=jnp.int32)
    qb = jnp.arange(nqb, dtype=jnp.int32)
    cover = (lo[:, None] <= kb[None, :]) & (kb[None, :] <= hi[:, None])
    qlo = jnp.min(jnp.where(cover, qb[:, None], nqb), axis=0).astype(jnp.int32)
    qhi = jnp.max(jnp.where(cover, qb[:, None], -1), axis=0).astype(jnp.int32)
    return lo, hi, qlo, qhi


def norm_forward(values, gain, shift):
    center = jnp.mean(values, axis=-1, keepdims=True)
    offsets = values - center
    spread = jnp.mean(offsets * offsets, axis=-1, keepdims=True)
    inverse = lax.rsqrt(spread + 1e-06)
    normed = offsets * inverse
    return (normed * gain + shift, normed, inverse)


def norm_backward(grad_y, normed, inverse, gain):
    grad_normed = grad_y * gain
    mean_one = jnp.mean(grad_normed, axis=-1, keepdims=True)
    mean_two = jnp.mean(grad_normed * normed, axis=-1, keepdims=True)
    return inverse * (grad_normed - mean_one - normed * mean_two)


def activate(values):
    return jax.nn.gelu(values, approximate=False)


def contract_last(left, right):
    return lax.dot_general(left, right, (((1,), (1,)), ((), ())), preferred_element_type=jnp.float32)


def contract_first(left, right):
    return lax.dot_general(left, right, (((0,), (0,)), ((), ())), preferred_element_type=jnp.float32)


def column_sum(values):
    return jnp.sum(values.astype(jnp.float32), axis=0)


def group_segments(lengths, dealing, group_index, group_rows, per_group):
    picked = lax.dynamic_slice_in_dim(dealing, group_index * per_group, per_group)
    match = picked[:, None] == jnp.arange(lengths.shape[0], dtype=jnp.int32)[None, :]
    chosen = jnp.sum(jnp.where(match, lengths[None, :], 0), axis=1)
    ends = jnp.cumsum(chosen)
    starts = ends - chosen
    places = jnp.arange(group_rows, dtype=jnp.int32)
    segment_ids = jnp.sum((places[:, None] >= ends[None, :]).astype(jnp.int32), axis=1)
    return (segment_ids, starts, ends)


def cyclic(values, k):
    count = lax.axis_size("tensor")
    return lax.ppermute(values, "tensor", [(s, (s + k) % count) for s in range(count)])


def halo_sizes(rows, takes, count, k):
    hops = len(takes)
    near = takes[k - 1] if k <= hops else 0
    far = takes[count - k - 1] if count - k <= hops else 0
    return near, far


def halo_piece(tokens, takes, k):
    count = lax.axis_size("tensor")
    me = lax.axis_index("tensor")
    rows = tokens.shape[0]
    near, far = halo_sizes(rows, takes, count, k)
    size = max(near, far)
    last = jnp.pad(tokens[rows - near:], ((0, size - near), (0, 0)))
    first = jnp.pad(tokens[:far], ((0, size - far), (0, 0)))
    if near == 0:
        return first
    if far == 0:
        return last
    return jnp.where(me + k < count, last, first)


def flat_rows(piece, width):
    flat = piece.reshape(-1)
    padded = -(-flat.shape[0] // width) * width
    return jnp.pad(flat, (0, padded - flat.shape[0])).reshape(-1, width)


def start_exchange(tokens, groups, takes):
    count = lax.axis_size("tensor")
    me = lax.axis_index("tensor")
    rows, width = tokens.shape
    pieces = [jnp.concatenate(blocks, axis=1) for blocks in groups]
    packed = [flat_rows(p, width) for p in pieces]
    received, halos = [pieces], {}
    for k in range(1, count):
        halo = halo_piece(tokens, takes, k)
        got = cyclic(jnp.concatenate([halo] + packed, axis=0), k)
        halos[k] = got[:halo.shape[0]]
        at, mine = halo.shape[0], []
        for p, q in zip(pieces, packed):
            mine.append(got[at:at + q.shape[0]].reshape(-1)[:p.size].reshape(p.shape))
            at += q.shape[0]
        received.append(mine)
    order = (me - jnp.arange(count, dtype=jnp.int32)) % count
    fulls = []
    for g, blocks in enumerate(groups):
        parts = jnp.take(jnp.stack([r[g] for r in received]), order, axis=0)
        widths = [b.shape[1] for b in blocks]
        cols, at = [], 0
        for w in widths:
            cols.extend(parts[t, :, at:at + w] for t in range(count))
            at += w
        strip = jnp.concatenate(cols, axis=1)
        full = lax.all_gather(strip, "dp", axis=0, tiled=True)
        out, at = [], 0
        for w in widths:
            out.append(full[:, at:at + w * count])
            at += w * count
        fulls.append(out)
    left, right = [], []
    for d, take in enumerate(takes, start=1):
        left.append(halos[d][:take] if d < count else jnp.zeros((take, width), tokens.dtype))
        right.append(halos[count - d][:take] if d < count else jnp.zeros((take, width), tokens.dtype))
    window = jnp.concatenate(left[::-1] + [tokens] + right, axis=0)
    return fulls, window


def return_exchange(values, takes):
    count = lax.axis_size("tensor")
    me = lax.axis_index("tensor")
    hops = len(takes)
    rows = values.shape[0] - 2 * sum(takes)
    halo = sum(takes)
    total = values[halo:halo + rows]
    starts_left, at = {}, halo
    for d, take in enumerate(takes, start=1):
        at -= take
        starts_left[d] = at
    starts_right, at = {}, halo + rows
    for d, take in enumerate(takes, start=1):
        starts_right[d] = at
        at += take
    for k in range(1, count):
        near, far = halo_sizes(rows, takes, count, k)
        size = max(near, far)
        back = jnp.zeros((size, values.shape[1]), jnp.float32)
        if near:
            s = starts_left[k]
            back = back + jnp.pad(values[s:s + near], ((0, size - near), (0, 0)))
        if far:
            s = starts_right[count - k]
            back = back + jnp.pad(values[s:s + far], ((0, size - far), (0, 0)))
        got = cyclic(back.astype(jnp.bfloat16), count - k).astype(jnp.float32)
        add_last = jnp.pad(got[:near], ((rows - near, 0), (0, 0))) if near else None
        add_first = jnp.pad(got[:far], ((0, rows - far), (0, 0))) if far else None
        if near and far:
            total = total + jnp.where(me + k < count, add_last, add_first)
        elif near:
            total = total + add_last
        else:
            total = total + add_first
    return total


def vector_rows(v, rows):
    dp = lax.axis_size("dp")
    slab = rows // dp
    spread = v.reshape(dp, 1, -1)
    return jnp.pad(spread, ((0, 0), (0, slab - 1), (0, 0))).reshape(rows, -1)


def pack_grads(grads, vectors):
    count = lax.axis_size("tensor")
    me = lax.axis_index("tensor")
    rows = grads[0].shape[0]
    mats = [g.astype(jnp.bfloat16) for g in grads] + [vector_rows(v.astype(jnp.bfloat16), rows) for v in vectors]
    widths = [m.shape[1] // count for m in mats]
    cat = jnp.concatenate(mats, axis=1)
    return widths, cat


def reduce_dp(cat):
    return lax.psum_scatter(cat, "dp", scatter_dimension=0, tiled=True)


def reduce_tensor(strip, widths, n_grads):
    count = lax.axis_size("tensor")
    me = lax.axis_index("tensor")
    strip = strip.astype(jnp.float32)
    per_t = []
    for t in range(count):
        at, cols = 0, []
        for w in widths:
            cols.append(strip[:, at + t * w:at + (t + 1) * w])
            at += w * count
        per_t.append(jnp.concatenate(cols, axis=1))
    stacked = jnp.stack(per_t)
    total = jnp.take(stacked, me, axis=0)
    for k in range(1, count):
        send = jnp.take(stacked, (me + k) % count, axis=0)
        total = total + lax.ppermute(send, "tensor", [(s, (s + k) % count) for s in range(count)])
    out, at = [], 0
    for i, w in enumerate(widths):
        block = total[:, at:at + w]
        at += w
        out.append(block if i < n_grads else block[0])
    return out


def halo_plan(rows):
    hops = -(-LONGEST // rows)
    takes = [rows] * (hops - 1) + [LONGEST - rows * (hops - 1)]
    return takes


def shift_rows(values, distance, count):
    if distance >= count:
        return jnp.zeros_like(values)
    if distance > 0:
        pairs = [(s, s + distance) for s in range(count - distance)]
    else:
        pairs = [(s - distance, s) for s in range(count + distance)]
    return lax.ppermute(values, "tensor", pairs)


def build_window(own, takes, count):
    rows = own.shape[0]
    left = [shift_rows(own[rows - take:], d + 1, count) for d, take in enumerate(takes)]
    right = [shift_rows(own[:take], -(d + 1), count) for d, take in enumerate(takes)]
    return jnp.concatenate(left[::-1] + [own] + right, axis=0)


def return_window(values, takes, count):
    rows = values.shape[0] - 2 * LONGEST
    total = values[LONGEST:LONGEST + rows]
    at = LONGEST
    for d, take in enumerate(takes):
        piece = values[at - take:at].astype(jnp.bfloat16)
        at -= take
        back = shift_rows(piece, -(d + 1), count).astype(jnp.float32)
        total = total + jnp.pad(back, ((rows - take, 0), (0, 0)))
    at = LONGEST + rows
    for d, take in enumerate(takes):
        piece = values[at:at + take].astype(jnp.bfloat16)
        at += take
        back = shift_rows(piece, d + 1, count).astype(jnp.float32)
        total = total + jnp.pad(back, ((0, rows - take), (0, 0)))
    return total


def to_heads(values):
    rows, width = values.shape
    return values.reshape(rows, width // HEAD_DIM, HEAD_DIM).transpose(1, 0, 2)


def from_heads(values):
    heads, rows, hd = values.shape
    return values.transpose(1, 0, 2).reshape(rows, heads * hd)


def shards(tokens, lengths, dealing, w_query, w_key, w_value, w_out, w_inner, w_outer, b_query, b_value, b_out, b_inner, b_outer, gain_attn, shift_attn, gain_ffn, shift_ffn, grad_out):
    count = lax.axis_size("tensor")
    tens_index = lax.axis_index("tensor")
    group_index = lax.axis_index("dp")
    rows = tokens.shape[0]
    group_rows = rows * count
    per_group = lengths.shape[0] // lax.axis_size("dp")
    takes = halo_plan(rows)
    window = rows + 2 * LONGEST
    seg, starts, ends = group_segments(lengths, dealing, group_index, group_rows, per_group)
    base = rows * tens_index - LONGEST
    places = base + jnp.arange(window, dtype=jnp.int32)
    valid = (places >= 0) & (places < group_rows)
    k_ids = jnp.where(valid, jnp.sum((places[:, None] >= ends[None, :]).astype(jnp.int32), axis=1), -1).astype(jnp.int32)
    q_ids = lax.dynamic_slice_in_dim(seg, rows * tens_index, rows)
    q_start = jnp.take(starts, q_ids) - base
    q_end = jnp.take(ends, q_ids) - base
    lo, hi, qlo, qhi = block_ranges(q_ids, k_ids, q_start, q_end, BLOCK, BLOCK)
    nkb = window // BLOCK
    kv_steps = min(nkb, (BLOCK + 2 * (LONGEST - 1)) // BLOCK + 2)
    q_steps = rows // BLOCK

    ((wq, wk, wv), (wo_t, wi, wf_t)), x_win = start_exchange(
        tokens, [[w_query, w_key, w_value], [w_out.T, w_inner, w_outer.T]], takes
    )
    gain_one = gain_attn.astype(jnp.float32)
    gain_two = gain_ffn.astype(jnp.float32)

    x_own = tokens
    query = (jnp.dot(x_own, wq, preferred_element_type=jnp.float32) + b_query.astype(jnp.float32)).astype(jnp.bfloat16)
    key_w = jnp.dot(x_win, wk, preferred_element_type=jnp.float32).astype(jnp.bfloat16)
    value_w = (jnp.dot(x_win, wv, preferred_element_type=jnp.float32) + b_value.astype(jnp.float32)).astype(jnp.bfloat16)
    scaled = query * jnp.asarray(1.0 / math.sqrt(HEAD_DIM), jnp.bfloat16)
    ctx32, lse = flash_forward(scaled, key_w, value_w, q_ids, k_ids, lo, hi, BLOCK, BLOCK, kv_steps)
    context = ctx32.astype(jnp.bfloat16)
    attn = contract_last(context, wo_t) + b_out.astype(jnp.float32)
    hidden, norm_one, inverse_one = norm_forward(tokens.astype(jnp.float32) + attn, gain_one, shift_attn.astype(jnp.float32))
    hidden_low = hidden.astype(jnp.bfloat16)
    pre_act = jnp.dot(hidden_low, wi, preferred_element_type=jnp.float32) + b_inner.astype(jnp.float32)
    act = activate(pre_act).astype(jnp.bfloat16)
    ffn = contract_last(act, wf_t) + b_outer.astype(jnp.float32)
    output, norm_two, inverse_two = norm_forward(hidden + ffn, gain_two, shift_ffn.astype(jnp.float32))

    grad_y = grad_out.astype(jnp.float32)
    grad_resid_two = norm_backward(grad_y, norm_two, inverse_two, gain_two)
    grad_ffn = grad_resid_two.astype(jnp.bfloat16)
    grad_outer_t = contract_first(grad_ffn, act)
    grad_act = jnp.dot(grad_ffn, wf_t, preferred_element_type=jnp.float32)
    unused, gelu_pull = jax.vjp(activate, pre_act)
    grad_pre = gelu_pull(grad_act)[0].astype(jnp.bfloat16)
    grad_inner_w = contract_first(hidden_low, grad_pre)
    grad_hidden = grad_resid_two + contract_last(grad_pre, wi)
    grad_resid_one = norm_backward(grad_hidden, norm_one, inverse_one, gain_one)
    grad_attn = grad_resid_one.astype(jnp.bfloat16)
    grad_out_t = contract_first(grad_attn, context)
    grad_context = jnp.dot(grad_attn, wo_t, preferred_element_type=jnp.float32).astype(jnp.bfloat16)
    late = [
        column_sum(grad_attn),
        column_sum(grad_pre),
        column_sum(grad_ffn),
        jnp.sum(grad_hidden * norm_one, axis=0),
        jnp.sum(grad_hidden, axis=0),
        jnp.sum(grad_y * norm_two, axis=0),
        jnp.sum(grad_y, axis=0),
    ]
    early_widths, early_cat = pack_grads([grad_out_t, grad_inner_w, grad_outer_t], late)
    grad_context, early_cat = lax.optimization_barrier((grad_context, early_cat))
    early_strip = reduce_dp(early_cat)
    heads = query.shape[1] // HEAD_DIM
    delta = jnp.sum((grad_context.astype(jnp.float32) * ctx32).reshape(rows, heads, HEAD_DIM), axis=-1)
    delta = delta.T.reshape(heads, rows, 1)
    dq_h = flash_dq(scaled, key_w, value_w, q_ids, k_ids, lse, delta, grad_context, lo, hi, BLOCK, BLOCK, kv_steps)
    dk_h, dv_h = flash_dkv(scaled, key_w, value_w, q_ids, k_ids, lse, delta, grad_context, qlo, qhi, BLOCK, BLOCK, q_steps)
    early_strip, dq_h, dk_h, dv_h = lax.optimization_barrier((early_strip, dq_h, dk_h, dv_h))
    early_sums = reduce_tensor(early_strip, early_widths, 3)
    g_out_t, g_inner, g_outer_t = early_sums[:3]
    late = early_sums[3:]
    grad_query = dq_h.astype(jnp.bfloat16)
    grad_key = dk_h.astype(jnp.bfloat16)
    grad_value = dv_h.astype(jnp.bfloat16)
    grad_query_w = contract_first(x_own, grad_query)
    grad_key_w = contract_first(x_win, grad_key)
    grad_value_w = contract_first(x_win, grad_value)
    grad_win = contract_last(grad_key, wk) + contract_last(grad_value, wv)
    grad_tokens = grad_resid_one + contract_last(grad_query, wq) + return_exchange(grad_win, takes)

    late_widths, late_cat = pack_grads(
        [grad_query_w, grad_key_w, grad_value_w], [column_sum(grad_query), column_sum(grad_value)]
    )
    g_query, g_key, g_value, g_bq, g_bv = reduce_tensor(reduce_dp(late_cat), late_widths, 3)
    summed = (g_query, g_key, g_value, g_out_t.T, g_inner, g_outer_t.T)
    small = [g_bq, g_bv] + late
    return (output.astype(jnp.bfloat16), grad_tokens) + summed + tuple(small)


def solution(mesh):
    rows = P(("dp", "tensor"), None)
    vec = P(("dp", "tensor"))
    return jax.shard_map(
        shards,
        mesh=mesh,
        in_specs=(rows, P(), P(), P("dp", "tensor"), P("dp", "tensor"), P("dp", "tensor"), P("tensor", "dp"), P("dp", "tensor"), P("tensor", "dp"), P(), P(), P(), P(), P(), P(), P(), P(), P(), rows),
        out_specs=(rows, rows, P("dp", "tensor"), P("dp", "tensor"), P("dp", "tensor"), P("tensor", "dp"), P("dp", "tensor"), P("tensor", "dp")) + (vec,) * 9,
        check_vma=False,
    )
```

```python
import math

import jax
import jax.numpy as jnp
from jax import lax
from jax.experimental import pallas as pl
from jax.experimental.pallas import tpu as pltpu
from jax.sharding import PartitionSpec as P

HEAD_DIM = 64
LONGEST = 1024
BLOCK = 256

NEG = -1e30
LANES = 128


def _lanes(rows):
    return lax.broadcasted_iota(jnp.int32, (rows, LANES), 1) < LANES // 2


def _pick(first, second, lanes):
    return jnp.where(lanes, first, second)


def _nt(a, b):
    return lax.dot_general(a, b, (((1,), (1,)), ((), ())), preferred_element_type=jnp.float32)


def _tn(a, b):
    return lax.dot_general(a, b, (((0,), (0,)), ((), ())), preferred_element_type=jnp.float32)


def _nn(a, b):
    return lax.dot_general(a, b, (((1,), (0,)), ((), ())), preferred_element_type=jnp.float32)


def _attn_fwd(lo_ref, hi_ref, q_ref, k_ref, v_ref, qs_ref, ks_ref, o_ref, lse_ref, m_sc, l_sc, acc_sc):
    i = pl.program_id(0)
    j = pl.program_id(1)
    kv = lo_ref[i] + j
    pairs = q_ref.shape[1] // LANES
    bq = q_ref.shape[0]

    @pl.when(j == 0)
    def _():
        m_sc[...] = jnp.full_like(m_sc, NEG)
        l_sc[...] = jnp.zeros_like(l_sc)
        acc_sc[...] = jnp.zeros_like(acc_sc)

    @pl.when(kv <= hi_ref[i])
    def _():
        mask = qs_ref[...] == ks_ref[...]
        lanes = _lanes(bq)

        def pair(p, carry):
            cols = pl.ds(p * LANES, LANES)
            q2 = q_ref[:, cols]
            k2 = k_ref[:, cols]
            v2 = v_ref[:, cols]
            zero = jnp.zeros_like(q2)
            alphas, pvs = [], []
            for h in range(2):
                hq = _pick(q2, zero, lanes) if h == 0 else _pick(zero, q2, lanes)
                s = jnp.where(mask, _nt(hq, k2), NEG)
                m_old = m_sc[2 * p + h]
                m_new = jnp.maximum(m_old, jnp.max(s, axis=-1, keepdims=True))
                alpha = jnp.exp(m_old - m_new)
                e = jnp.exp(s - m_new)
                l_sc[2 * p + h] = alpha * l_sc[2 * p + h] + jnp.sum(e, axis=-1, keepdims=True)
                m_sc[2 * p + h] = m_new
                alphas.append(alpha)
                pvs.append(_nn(e.astype(jnp.bfloat16), v2))
            acc_sc[:, cols] = _pick(alphas[0], alphas[1], lanes) * acc_sc[:, cols] + _pick(pvs[0], pvs[1], lanes)
            return carry

        for p in range(pairs):
            pair(p, 0)

    @pl.when(j == pl.num_programs(1) - 1)
    def _():
        lanes = _lanes(bq)

        def pair(p, carry):
            cols = pl.ds(p * LANES, LANES)
            l0, l1 = l_sc[2 * p], l_sc[2 * p + 1]
            o_ref[:, cols] = acc_sc[:, cols] / _pick(l0, l1, lanes)
            lse_ref[2 * p] = m_sc[2 * p] + jnp.log(l0)
            lse_ref[2 * p + 1] = m_sc[2 * p + 1] + jnp.log(l1)
            return carry

        for p in range(pairs):
            pair(p, 0)


def _attn_dq(lo_ref, hi_ref, q_ref, k_ref, v_ref, qs_ref, ks_ref, lse_ref, dl_ref, do_ref, dq_ref, acc_sc):
    i = pl.program_id(0)
    j = pl.program_id(1)
    kv = lo_ref[i] + j
    pairs = q_ref.shape[1] // LANES
    bq = q_ref.shape[0]

    @pl.when(j == 0)
    def _():
        acc_sc[...] = jnp.zeros_like(acc_sc)

    @pl.when(kv <= hi_ref[i])
    def _():
        mask = qs_ref[...] == ks_ref[...]
        lanes = _lanes(bq)

        def pair(p, carry):
            cols = pl.ds(p * LANES, LANES)
            q2 = q_ref[:, cols]
            k2 = k_ref[:, cols]
            v2 = v_ref[:, cols]
            do2 = do_ref[:, cols]
            zero = jnp.zeros_like(q2)
            parts = []
            for h in range(2):
                sel = (lambda a: _pick(a, zero, lanes)) if h == 0 else (lambda a: _pick(zero, a, lanes))
                s = _nt(sel(q2), k2)
                e = jnp.where(mask, jnp.exp(s - lse_ref[2 * p + h]), 0.0)
                dp = _nt(sel(do2), v2)
                ds = (e * (dp - dl_ref[2 * p + h])).astype(jnp.bfloat16)
                parts.append(_nn(ds, k2))
            acc_sc[:, cols] += _pick(parts[0], parts[1], lanes)
            return carry

        for p in range(pairs):
            pair(p, 0)

    @pl.when(j == pl.num_programs(1) - 1)
    def _():
        dq_ref[...] = acc_sc[...] * 0.125


def _attn_dkv(lo_ref, hi_ref, q_ref, k_ref, v_ref, qs_ref, ks_ref, lse_ref, dl_ref, do_ref, dk_ref, dv_ref, dk_sc, dv_sc):
    j = pl.program_id(0)
    i = pl.program_id(1)
    qb = lo_ref[j] + i
    pairs = q_ref.shape[1] // LANES
    bq = q_ref.shape[0]
    bk = k_ref.shape[0]

    @pl.when(i == 0)
    def _():
        dk_sc[...] = jnp.zeros_like(dk_sc)
        dv_sc[...] = jnp.zeros_like(dv_sc)

    @pl.when(qb <= hi_ref[j])
    def _():
        mask = qs_ref[...] == ks_ref[...]
        lanes_q = _lanes(bq)
        lanes_k = _lanes(bk)

        def pair(p, carry):
            cols = pl.ds(p * LANES, LANES)
            q2 = q_ref[:, cols]
            k2 = k_ref[:, cols]
            v2 = v_ref[:, cols]
            do2 = do_ref[:, cols]
            zero = jnp.zeros_like(q2)
            dks, dvs = [], []
            for h in range(2):
                sel = (lambda a: _pick(a, zero, lanes_q)) if h == 0 else (lambda a: _pick(zero, a, lanes_q))
                s = _nt(sel(q2), k2)
                e = jnp.where(mask, jnp.exp(s - lse_ref[2 * p + h]), 0.0)
                dp = _nt(sel(do2), v2)
                ds = (e * (dp - dl_ref[2 * p + h])).astype(jnp.bfloat16)
                dvs.append(_tn(e.astype(jnp.bfloat16), do2))
                dks.append(_tn(ds, q2))
            dv_sc[:, cols] += _pick(dvs[0], dvs[1], lanes_k)
            dk_sc[:, cols] += _pick(dks[0], dks[1], lanes_k)
            return carry

        for p in range(pairs):
            pair(p, 0)

    @pl.when(i == pl.num_programs(1) - 1)
    def _():
        dk_ref[...] = dk_sc[...]
        dv_ref[...] = dv_sc[...]


def _clamp(start, step, last):
    return jnp.minimum(start + step, jnp.maximum(last, 0))


def _params():
    return pltpu.CompilerParams(dimension_semantics=("arbitrary", "arbitrary"), vmem_limit_bytes=48 * 1024 * 1024)


def flash_forward(q, k, v, q_ids, k_ids, lo, hi, block_q, block_k, steps):
    nq, width = q.shape
    nk = k.shape[0]
    heads = width // 64
    kv_map = lambda i, j, a, b: (_clamp(a[i], j, b[i]), 0)
    ks_map = lambda i, j, a, b: (0, _clamp(a[i], j, b[i]))
    row = lambda i, j, a, b: (i, 0)
    grid_spec = pltpu.PrefetchScalarGridSpec(
        num_scalar_prefetch=2,
        grid=(nq // block_q, steps),
        in_specs=[
            pl.BlockSpec((block_q, width), row),
            pl.BlockSpec((block_k, width), kv_map),
            pl.BlockSpec((block_k, width), kv_map),
            pl.BlockSpec((block_q, 1), row),
            pl.BlockSpec((1, block_k), ks_map),
        ],
        out_specs=[
            pl.BlockSpec((block_q, width), row),
            pl.BlockSpec((heads, block_q, 1), lambda i, j, a, b: (0, i, 0)),
        ],
        scratch_shapes=[
            pltpu.VMEM((heads, block_q, 1), jnp.float32),
            pltpu.VMEM((heads, block_q, 1), jnp.float32),
            pltpu.VMEM((block_q, width), jnp.float32),
        ],
    )
    return pl.pallas_call(
        _attn_fwd,
        grid_spec=grid_spec,
        out_shape=[jax.ShapeDtypeStruct((nq, width), jnp.float32), jax.ShapeDtypeStruct((heads, nq, 1), jnp.float32)],
        compiler_params=_params(),
    )(lo, hi, q, k, v, q_ids.reshape(nq, 1), k_ids.reshape(1, nk))


def flash_dq(q, k, v, q_ids, k_ids, lse, delta, do, lo, hi, block_q, block_k, steps):
    nq, width = q.shape
    nk = k.shape[0]
    heads = width // 64
    kv_map = lambda i, j, a, b: (_clamp(a[i], j, b[i]), 0)
    ks_map = lambda i, j, a, b: (0, _clamp(a[i], j, b[i]))
    row = lambda i, j, a, b: (i, 0)
    hrow = lambda i, j, a, b: (0, i, 0)
    grid_spec = pltpu.PrefetchScalarGridSpec(
        num_scalar_prefetch=2,
        grid=(nq // block_q, steps),
        in_specs=[
            pl.BlockSpec((block_q, width), row),
            pl.BlockSpec((block_k, width), kv_map),
            pl.BlockSpec((block_k, width), kv_map),
            pl.BlockSpec((block_q, 1), row),
            pl.BlockSpec((1, block_k), ks_map),
            pl.BlockSpec((heads, block_q, 1), hrow),
            pl.BlockSpec((heads, block_q, 1), hrow),
            pl.BlockSpec((block_q, width), row),
        ],
        out_specs=pl.BlockSpec((block_q, width), row),
        scratch_shapes=[pltpu.VMEM((block_q, width), jnp.float32)],
    )
    return pl.pallas_call(
        _attn_dq,
        grid_spec=grid_spec,
        out_shape=jax.ShapeDtypeStruct((nq, width), jnp.float32),
        compiler_params=_params(),
    )(lo, hi, q, k, v, q_ids.reshape(nq, 1), k_ids.reshape(1, nk), lse, delta, do)


def flash_dkv(q, k, v, q_ids, k_ids, lse, delta, do, qlo, qhi, block_q, block_k, steps):
    nq, width = q.shape
    nk = k.shape[0]
    heads = width // 64
    q_map = lambda j, i, a, b: (_clamp(a[j], i, b[j]), 0)
    h_map = lambda j, i, a, b: (0, _clamp(a[j], i, b[j]), 0)
    col = lambda j, i, a, b: (j, 0)
    grid_spec = pltpu.PrefetchScalarGridSpec(
        num_scalar_prefetch=2,
        grid=(nk // block_k, steps),
        in_specs=[
            pl.BlockSpec((block_q, width), q_map),
            pl.BlockSpec((block_k, width), col),
            pl.BlockSpec((block_k, width), col),
            pl.BlockSpec((block_q, 1), q_map),
            pl.BlockSpec((1, block_k), lambda j, i, a, b: (0, j)),
            pl.BlockSpec((heads, block_q, 1), h_map),
            pl.BlockSpec((heads, block_q, 1), h_map),
            pl.BlockSpec((block_q, width), q_map),
        ],
        out_specs=[pl.BlockSpec((block_k, width), col), pl.BlockSpec((block_k, width), col)],
        scratch_shapes=[pltpu.VMEM((block_k, width), jnp.float32), pltpu.VMEM((block_k, width), jnp.float32)],
    )
    return pl.pallas_call(
        _attn_dkv,
        grid_spec=grid_spec,
        out_shape=[jax.ShapeDtypeStruct((nk, width), jnp.float32), jax.ShapeDtypeStruct((nk, width), jnp.float32)],
        compiler_params=_params(),
    )(qlo, qhi, q, k, v, q_ids.reshape(nq, 1), k_ids.reshape(1, nk), lse, delta, do)


def block_ranges(q_ids, k_ids, q_start, q_end, block_q, block_k):
    nq = q_ids.shape[0]
    nk = k_ids.shape[0]
    nqb, nkb = nq // block_q, nk // block_k
    first = q_start.reshape(nqb, block_q)[:, 0]
    last = q_end.reshape(nqb, block_q)[:, block_q - 1]
    lo = jnp.clip(first // block_k, 0, nkb - 1).astype(jnp.int32)
    hi = jnp.clip((last - 1) // block_k, 0, nkb - 1).astype(jnp.int32)
    kb = jnp.arange(nkb, dtype=jnp.int32)
    qb = jnp.arange(nqb, dtype=jnp.int32)
    cover = (lo[:, None] <= kb[None, :]) & (kb[None, :] <= hi[:, None])
    qlo = jnp.min(jnp.where(cover, qb[:, None], nqb), axis=0).astype(jnp.int32)
    qhi = jnp.max(jnp.where(cover, qb[:, None], -1), axis=0).astype(jnp.int32)
    return lo, hi, qlo, qhi


def norm_forward(values, gain, shift):
    center = jnp.mean(values, axis=-1, keepdims=True)
    offsets = values - center
    spread = jnp.mean(offsets * offsets, axis=-1, keepdims=True)
    inverse = lax.rsqrt(spread + 1e-06)
    normed = offsets * inverse
    return (normed * gain + shift, normed, inverse)


def norm_backward(grad_y, normed, inverse, gain):
    grad_normed = grad_y * gain
    mean_one = jnp.mean(grad_normed, axis=-1, keepdims=True)
    mean_two = jnp.mean(grad_normed * normed, axis=-1, keepdims=True)
    return inverse * (grad_normed - mean_one - normed * mean_two)


def activate(values):
    return jax.nn.gelu(values, approximate=False)


def contract_last(left, right):
    return lax.dot_general(left, right, (((1,), (1,)), ((), ())), preferred_element_type=jnp.float32)


def contract_first(left, right):
    return lax.dot_general(left, right, (((0,), (0,)), ((), ())), preferred_element_type=jnp.float32)


def column_sum(values):
    return jnp.sum(values.astype(jnp.float32), axis=0)


def group_segments(lengths, dealing, group_index, group_rows, per_group):
    picked = lax.dynamic_slice_in_dim(dealing, group_index * per_group, per_group)
    match = picked[:, None] == jnp.arange(lengths.shape[0], dtype=jnp.int32)[None, :]
    chosen = jnp.sum(jnp.where(match, lengths[None, :], 0), axis=1)
    ends = jnp.cumsum(chosen)
    starts = ends - chosen
    places = jnp.arange(group_rows, dtype=jnp.int32)
    segment_ids = jnp.sum((places[:, None] >= ends[None, :]).astype(jnp.int32), axis=1)
    return (segment_ids, starts, ends)


def cyclic(values, k):
    count = lax.axis_size("tensor")
    return lax.ppermute(values, "tensor", [(s, (s + k) % count) for s in range(count)])


def halo_sizes(rows, takes, count, k):
    hops = len(takes)
    near = takes[k - 1] if k <= hops else 0
    far = takes[count - k - 1] if count - k <= hops else 0
    return near, far


def halo_piece(tokens, takes, k):
    count = lax.axis_size("tensor")
    me = lax.axis_index("tensor")
    rows = tokens.shape[0]
    near, far = halo_sizes(rows, takes, count, k)
    size = max(near, far)
    last = jnp.pad(tokens[rows - near:], ((0, size - near), (0, 0)))
    first = jnp.pad(tokens[:far], ((0, size - far), (0, 0)))
    if near == 0:
        return first
    if far == 0:
        return last
    return jnp.where(me + k < count, last, first)


def flat_rows(piece, width):
    flat = piece.reshape(-1)
    padded = -(-flat.shape[0] // width) * width
    return jnp.pad(flat, (0, padded - flat.shape[0])).reshape(-1, width)


def start_exchange(tokens, groups, takes):
    count = lax.axis_size("tensor")
    me = lax.axis_index("tensor")
    rows, width = tokens.shape
    pieces = [jnp.concatenate(blocks, axis=1) for blocks in groups]
    packed = [flat_rows(p, width) for p in pieces]
    by_shift, left, right = {0: pieces}, {}, {}
    for s in list(range(1, count)) + list(range(-1, -count, -1)):
        d = abs(s)
        send = list(packed)
        take = takes[d - 1] if d <= len(takes) else 0
        if take:
            send = [tokens[rows - take:] if s > 0 else tokens[:take]] + send
        got = shift_rows(jnp.concatenate(send, axis=0), s, count)
        at = 0
        if take:
            (left if s > 0 else right)[d] = got[:take]
            at = take
        mine = []
        for p, q in zip(pieces, packed):
            mine.append(got[at:at + q.shape[0]].reshape(-1)[:p.size].reshape(p.shape))
            at += q.shape[0]
        by_shift[s] = mine
    order = me - jnp.arange(count, dtype=jnp.int32) + (count - 1)
    fulls = []
    for g, blocks in enumerate(groups):
        stacked = jnp.stack([by_shift[s][g] for s in range(-(count - 1), count)])
        parts = jnp.take(stacked, order, axis=0)
        widths = [b.shape[1] for b in blocks]
        cols, at = [], 0
        for w in widths:
            cols.extend(parts[t, :, at:at + w] for t in range(count))
            at += w
        strip = jnp.concatenate(cols, axis=1)
        full = lax.all_gather(strip, "dp", axis=0, tiled=True)
        out, at = [], 0
        for w in widths:
            out.append(full[:, at:at + w * count])
            at += w * count
        fulls.append(out)
    lefts, rights = [], []
    for d, take in enumerate(takes, start=1):
        lefts.append(left.get(d, jnp.zeros((take, width), tokens.dtype)))
        rights.append(right.get(d, jnp.zeros((take, width), tokens.dtype)))
    window = jnp.concatenate(lefts[::-1] + [tokens] + rights, axis=0)
    return fulls, window


def return_exchange(values, takes):
    count = lax.axis_size("tensor")
    me = lax.axis_index("tensor")
    hops = len(takes)
    rows = values.shape[0] - 2 * sum(takes)
    halo = sum(takes)
    total = values[halo:halo + rows]
    starts_left, at = {}, halo
    for d, take in enumerate(takes, start=1):
        at -= take
        starts_left[d] = at
    starts_right, at = {}, halo + rows
    for d, take in enumerate(takes, start=1):
        starts_right[d] = at
        at += take
    for k in range(1, count):
        near, far = halo_sizes(rows, takes, count, k)
        size = max(near, far)
        back = jnp.zeros((size, values.shape[1]), jnp.float32)
        if near:
            s = starts_left[k]
            back = back + jnp.pad(values[s:s + near], ((0, size - near), (0, 0)))
        if far:
            s = starts_right[count - k]
            back = back + jnp.pad(values[s:s + far], ((0, size - far), (0, 0)))
        got = cyclic(back.astype(jnp.bfloat16), count - k).astype(jnp.float32)
        add_last = jnp.pad(got[:near], ((rows - near, 0), (0, 0))) if near else None
        add_first = jnp.pad(got[:far], ((0, rows - far), (0, 0))) if far else None
        if near and far:
            total = total + jnp.where(me + k < count, add_last, add_first)
        elif near:
            total = total + add_last
        else:
            total = total + add_first
    return total


def vector_rows(v, rows):
    dp = lax.axis_size("dp")
    slab = rows // dp
    spread = v.reshape(dp, 1, -1)
    return jnp.pad(spread, ((0, 0), (0, slab - 1), (0, 0))).reshape(rows, -1)


def pack_grads(grads, vectors):
    count = lax.axis_size("tensor")
    me = lax.axis_index("tensor")
    rows = grads[0].shape[0]
    mats = [g.astype(jnp.bfloat16) for g in grads] + [vector_rows(v.astype(jnp.bfloat16), rows) for v in vectors]
    widths = [m.shape[1] // count for m in mats]
    cat = jnp.concatenate(mats, axis=1)
    return widths, cat


def reduce_dp(cat):
    return lax.psum_scatter(cat, "dp", scatter_dimension=0, tiled=True)


def reduce_tensor(strip, widths, n_grads):
    count = lax.axis_size("tensor")
    me = lax.axis_index("tensor")
    strip = strip.astype(jnp.float32)
    per_t = []
    for t in range(count):
        at, cols = 0, []
        for w in widths:
            cols.append(strip[:, at + t * w:at + (t + 1) * w])
            at += w * count
        per_t.append(jnp.concatenate(cols, axis=1))
    stacked = jnp.stack(per_t)
    total = jnp.take(stacked, me, axis=0)
    for k in range(1, count):
        send = jnp.take(stacked, (me + k) % count, axis=0)
        total = total + lax.ppermute(send, "tensor", [(s, (s + k) % count) for s in range(count)])
    out, at = [], 0
    for i, w in enumerate(widths):
        block = total[:, at:at + w]
        at += w
        out.append(block if i < n_grads else block[0])
    return out


def halo_plan(rows):
    hops = -(-LONGEST // rows)
    takes = [rows] * (hops - 1) + [LONGEST - rows * (hops - 1)]
    return takes


def shift_rows(values, distance, count):
    if distance >= count:
        return jnp.zeros_like(values)
    if distance > 0:
        pairs = [(s, s + distance) for s in range(count - distance)]
    else:
        pairs = [(s - distance, s) for s in range(count + distance)]
    return lax.ppermute(values, "tensor", pairs)


def build_window(own, takes, count):
    rows = own.shape[0]
    left = [shift_rows(own[rows - take:], d + 1, count) for d, take in enumerate(takes)]
    right = [shift_rows(own[:take], -(d + 1), count) for d, take in enumerate(takes)]
    return jnp.concatenate(left[::-1] + [own] + right, axis=0)


def return_window(values, takes, count):
    rows = values.shape[0] - 2 * LONGEST
    total = values[LONGEST:LONGEST + rows]
    at = LONGEST
    for d, take in enumerate(takes):
        piece = values[at - take:at].astype(jnp.bfloat16)
        at -= take
        back = shift_rows(piece, -(d + 1), count).astype(jnp.float32)
        total = total + jnp.pad(back, ((rows - take, 0), (0, 0)))
    at = LONGEST + rows
    for d, take in enumerate(takes):
        piece = values[at:at + take].astype(jnp.bfloat16)
        at += take
        back = shift_rows(piece, d + 1, count).astype(jnp.float32)
        total = total + jnp.pad(back, ((0, rows - take), (0, 0)))
    return total


def to_heads(values):
    rows, width = values.shape
    return values.reshape(rows, width // HEAD_DIM, HEAD_DIM).transpose(1, 0, 2)


def from_heads(values):
    heads, rows, hd = values.shape
    return values.transpose(1, 0, 2).reshape(rows, heads * hd)


def shards(tokens, lengths, dealing, w_query, w_key, w_value, w_out, w_inner, w_outer, b_query, b_value, b_out, b_inner, b_outer, gain_attn, shift_attn, gain_ffn, shift_ffn, grad_out):
    count = lax.axis_size("tensor")
    tens_index = lax.axis_index("tensor")
    group_index = lax.axis_index("dp")
    rows = tokens.shape[0]
    group_rows = rows * count
    per_group = lengths.shape[0] // lax.axis_size("dp")
    takes = halo_plan(rows)
    window = rows + 2 * LONGEST
    seg, starts, ends = group_segments(lengths, dealing, group_index, group_rows, per_group)
    base = rows * tens_index - LONGEST
    places = base + jnp.arange(window, dtype=jnp.int32)
    valid = (places >= 0) & (places < group_rows)
    k_ids = jnp.where(valid, jnp.sum((places[:, None] >= ends[None, :]).astype(jnp.int32), axis=1), -1).astype(jnp.int32)
    q_ids = lax.dynamic_slice_in_dim(seg, rows * tens_index, rows)
    q_start = jnp.take(starts, q_ids) - base
    q_end = jnp.take(ends, q_ids) - base
    lo, hi, qlo, qhi = block_ranges(q_ids, k_ids, q_start, q_end, BLOCK, BLOCK)
    nkb = window // BLOCK
    kv_steps = min(nkb, (BLOCK + 2 * (LONGEST - 1)) // BLOCK + 2)
    q_steps = rows // BLOCK

    ((wq, wk, wv), (wo_t, wi, wf_t)), x_win = start_exchange(
        tokens, [[w_query, w_key, w_value], [w_out.T, w_inner, w_outer.T]], takes
    )
    gain_one = gain_attn.astype(jnp.float32)
    gain_two = gain_ffn.astype(jnp.float32)

    x_own = tokens
    query = (jnp.dot(x_own, wq, preferred_element_type=jnp.float32) + b_query.astype(jnp.float32)).astype(jnp.bfloat16)
    key_w = jnp.dot(x_win, wk, preferred_element_type=jnp.float32).astype(jnp.bfloat16)
    value_w = (jnp.dot(x_win, wv, preferred_element_type=jnp.float32) + b_value.astype(jnp.float32)).astype(jnp.bfloat16)
    scaled = query * jnp.asarray(1.0 / math.sqrt(HEAD_DIM), jnp.bfloat16)
    ctx32, lse = flash_forward(scaled, key_w, value_w, q_ids, k_ids, lo, hi, BLOCK, BLOCK, kv_steps)
    context = ctx32.astype(jnp.bfloat16)
    attn = contract_last(context, wo_t) + b_out.astype(jnp.float32)
    hidden, norm_one, inverse_one = norm_forward(tokens.astype(jnp.float32) + attn, gain_one, shift_attn.astype(jnp.float32))
    hidden_low = hidden.astype(jnp.bfloat16)
    pre_act = jnp.dot(hidden_low, wi, preferred_element_type=jnp.float32) + b_inner.astype(jnp.float32)
    act = activate(pre_act).astype(jnp.bfloat16)
    ffn = contract_last(act, wf_t) + b_outer.astype(jnp.float32)
    output, norm_two, inverse_two = norm_forward(hidden + ffn, gain_two, shift_ffn.astype(jnp.float32))

    grad_y = grad_out.astype(jnp.float32)
    grad_resid_two = norm_backward(grad_y, norm_two, inverse_two, gain_two)
    grad_ffn = grad_resid_two.astype(jnp.bfloat16)
    grad_outer_t = contract_first(grad_ffn, act)
    grad_act = jnp.dot(grad_ffn, wf_t, preferred_element_type=jnp.float32)
    unused, gelu_pull = jax.vjp(activate, pre_act)
    grad_pre = gelu_pull(grad_act)[0].astype(jnp.bfloat16)
    grad_inner_w = contract_first(hidden_low, grad_pre)
    grad_hidden = grad_resid_two + contract_last(grad_pre, wi)
    grad_resid_one = norm_backward(grad_hidden, norm_one, inverse_one, gain_one)
    grad_attn = grad_resid_one.astype(jnp.bfloat16)
    grad_out_t = contract_first(grad_attn, context)
    grad_context = jnp.dot(grad_attn, wo_t, preferred_element_type=jnp.float32).astype(jnp.bfloat16)
    late = [
        column_sum(grad_attn),
        column_sum(grad_pre),
        column_sum(grad_ffn),
        jnp.sum(grad_hidden * norm_one, axis=0),
        jnp.sum(grad_hidden, axis=0),
        jnp.sum(grad_y * norm_two, axis=0),
        jnp.sum(grad_y, axis=0),
    ]
    early_widths, early_cat = pack_grads([grad_out_t, grad_inner_w, grad_outer_t], late)
    grad_context, early_cat = lax.optimization_barrier((grad_context, early_cat))
    early_strip = reduce_dp(early_cat)
    heads = query.shape[1] // HEAD_DIM
    delta = jnp.sum((grad_context.astype(jnp.float32) * ctx32).reshape(rows, heads, HEAD_DIM), axis=-1)
    delta = delta.T.reshape(heads, rows, 1)
    dq_h = flash_dq(scaled, key_w, value_w, q_ids, k_ids, lse, delta, grad_context, lo, hi, BLOCK, BLOCK, kv_steps)
    dk_h, dv_h = flash_dkv(scaled, key_w, value_w, q_ids, k_ids, lse, delta, grad_context, qlo, qhi, BLOCK, BLOCK, q_steps)
    early_strip, dq_h, dk_h, dv_h = lax.optimization_barrier((early_strip, dq_h, dk_h, dv_h))
    early_sums = reduce_tensor(early_strip, early_widths, 3)
    g_out_t, g_inner, g_outer_t = early_sums[:3]
    late = early_sums[3:]
    grad_query = dq_h.astype(jnp.bfloat16)
    grad_key = dk_h.astype(jnp.bfloat16)
    grad_value = dv_h.astype(jnp.bfloat16)
    grad_query_w = contract_first(x_own, grad_query)
    grad_key_w = contract_first(x_win, grad_key)
    grad_value_w = contract_first(x_win, grad_value)
    grad_win = contract_last(grad_key, wk) + contract_last(grad_value, wv)
    grad_tokens = grad_resid_one + contract_last(grad_query, wq) + return_window(grad_win, takes, count)

    late_widths, late_cat = pack_grads(
        [grad_query_w, grad_key_w, grad_value_w], [column_sum(grad_query), column_sum(grad_value)]
    )
    g_query, g_key, g_value, g_bq, g_bv = reduce_tensor(reduce_dp(late_cat), late_widths, 3)
    summed = (g_query, g_key, g_value, g_out_t.T, g_inner, g_outer_t.T)
    small = [g_bq, g_bv] + late
    return (output.astype(jnp.bfloat16), grad_tokens) + summed + tuple(small)


def solution(mesh):
    rows = P(("dp", "tensor"), None)
    vec = P(("dp", "tensor"))
    return jax.shard_map(
        shards,
        mesh=mesh,
        in_specs=(rows, P(), P(), P("dp", "tensor"), P("dp", "tensor"), P("dp", "tensor"), P("tensor", "dp"), P("dp", "tensor"), P("tensor", "dp"), P(), P(), P(), P(), P(), P(), P(), P(), P(), rows),
        out_specs=(rows, rows, P("dp", "tensor"), P("dp", "tensor"), P("dp", "tensor"), P("tensor", "dp"), P("dp", "tensor"), P("tensor", "dp")) + (vec,) * 9,
        check_vma=False,
    )
```

```python
import math

import jax
import jax.numpy as jnp
from jax import lax
from jax.experimental import pallas as pl
from jax.experimental.pallas import tpu as pltpu
from jax.sharding import PartitionSpec as P

HEAD_DIM = 64
LONGEST = 1024
BLOCK = 256

NEG = -1e30
LANES = 128


def _lanes(rows):
    return lax.broadcasted_iota(jnp.int32, (rows, LANES), 1) < LANES // 2


def _pick(first, second, lanes):
    return jnp.where(lanes, first, second)


def _nt(a, b):
    return lax.dot_general(a, b, (((1,), (1,)), ((), ())), preferred_element_type=jnp.float32)


def _tn(a, b):
    return lax.dot_general(a, b, (((0,), (0,)), ((), ())), preferred_element_type=jnp.float32)


def _nn(a, b):
    return lax.dot_general(a, b, (((1,), (0,)), ((), ())), preferred_element_type=jnp.float32)


def _attn_fwd(lo_ref, hi_ref, q_ref, k_ref, v_ref, qs_ref, ks_ref, o_ref, lse_ref, m_sc, l_sc, acc_sc):
    i = pl.program_id(0)
    j = pl.program_id(1)
    kv = lo_ref[i] + j
    pairs = q_ref.shape[1] // LANES
    bq = q_ref.shape[0]

    @pl.when(j == 0)
    def _():
        m_sc[...] = jnp.full_like(m_sc, NEG)
        l_sc[...] = jnp.zeros_like(l_sc)
        acc_sc[...] = jnp.zeros_like(acc_sc)

    @pl.when(kv <= hi_ref[i])
    def _():
        mask = qs_ref[...] == ks_ref[...]
        lanes = _lanes(bq)

        def pair(p, carry):
            cols = pl.ds(p * LANES, LANES)
            q2 = q_ref[:, cols]
            k2 = k_ref[:, cols]
            v2 = v_ref[:, cols]
            zero = jnp.zeros_like(q2)
            alphas, pvs = [], []
            for h in range(2):
                hq = _pick(q2, zero, lanes) if h == 0 else _pick(zero, q2, lanes)
                s = jnp.where(mask, _nt(hq, k2), NEG)
                m_old = m_sc[2 * p + h]
                m_new = jnp.maximum(m_old, jnp.max(s, axis=-1, keepdims=True))
                alpha = jnp.exp(m_old - m_new)
                e = jnp.exp(s - m_new)
                l_sc[2 * p + h] = alpha * l_sc[2 * p + h] + jnp.sum(e, axis=-1, keepdims=True)
                m_sc[2 * p + h] = m_new
                alphas.append(alpha)
                pvs.append(_nn(e.astype(jnp.bfloat16), v2))
            acc_sc[:, cols] = _pick(alphas[0], alphas[1], lanes) * acc_sc[:, cols] + _pick(pvs[0], pvs[1], lanes)
            return carry

        for p in range(pairs):
            pair(p, 0)

    @pl.when(j == pl.num_programs(1) - 1)
    def _():
        lanes = _lanes(bq)

        def pair(p, carry):
            cols = pl.ds(p * LANES, LANES)
            l0, l1 = l_sc[2 * p], l_sc[2 * p + 1]
            o_ref[:, cols] = acc_sc[:, cols] / _pick(l0, l1, lanes)
            lse_ref[2 * p] = m_sc[2 * p] + jnp.log(l0)
            lse_ref[2 * p + 1] = m_sc[2 * p + 1] + jnp.log(l1)
            return carry

        for p in range(pairs):
            pair(p, 0)


def _attn_dq(lo_ref, hi_ref, q_ref, k_ref, v_ref, qs_ref, ks_ref, lse_ref, dl_ref, do_ref, dq_ref, acc_sc):
    i = pl.program_id(0)
    j = pl.program_id(1)
    kv = lo_ref[i] + j
    pairs = q_ref.shape[1] // LANES
    bq = q_ref.shape[0]

    @pl.when(j == 0)
    def _():
        acc_sc[...] = jnp.zeros_like(acc_sc)

    @pl.when(kv <= hi_ref[i])
    def _():
        mask = qs_ref[...] == ks_ref[...]
        lanes = _lanes(bq)

        def pair(p, carry):
            cols = pl.ds(p * LANES, LANES)
            q2 = q_ref[:, cols]
            k2 = k_ref[:, cols]
            v2 = v_ref[:, cols]
            do2 = do_ref[:, cols]
            zero = jnp.zeros_like(q2)
            parts = []
            for h in range(2):
                sel = (lambda a: _pick(a, zero, lanes)) if h == 0 else (lambda a: _pick(zero, a, lanes))
                s = _nt(sel(q2), k2)
                e = jnp.where(mask, jnp.exp(s - lse_ref[2 * p + h]), 0.0)
                dp = _nt(sel(do2), v2)
                ds = (e * (dp - dl_ref[2 * p + h])).astype(jnp.bfloat16)
                parts.append(_nn(ds, k2))
            acc_sc[:, cols] += _pick(parts[0], parts[1], lanes)
            return carry

        for p in range(pairs):
            pair(p, 0)

    @pl.when(j == pl.num_programs(1) - 1)
    def _():
        dq_ref[...] = acc_sc[...] * 0.125


def _attn_dkv(lo_ref, hi_ref, q_ref, k_ref, v_ref, qs_ref, ks_ref, lse_ref, dl_ref, do_ref, dk_ref, dv_ref, dk_sc, dv_sc):
    j = pl.program_id(0)
    i = pl.program_id(1)
    qb = lo_ref[j] + i
    pairs = q_ref.shape[1] // LANES
    bq = q_ref.shape[0]
    bk = k_ref.shape[0]

    @pl.when(i == 0)
    def _():
        dk_sc[...] = jnp.zeros_like(dk_sc)
        dv_sc[...] = jnp.zeros_like(dv_sc)

    @pl.when(qb <= hi_ref[j])
    def _():
        mask = qs_ref[...] == ks_ref[...]
        lanes_q = _lanes(bq)
        lanes_k = _lanes(bk)

        def pair(p, carry):
            cols = pl.ds(p * LANES, LANES)
            q2 = q_ref[:, cols]
            k2 = k_ref[:, cols]
            v2 = v_ref[:, cols]
            do2 = do_ref[:, cols]
            zero = jnp.zeros_like(q2)
            dks, dvs = [], []
            for h in range(2):
                sel = (lambda a: _pick(a, zero, lanes_q)) if h == 0 else (lambda a: _pick(zero, a, lanes_q))
                s = _nt(sel(q2), k2)
                e = jnp.where(mask, jnp.exp(s - lse_ref[2 * p + h]), 0.0)
                dp = _nt(sel(do2), v2)
                ds = (e * (dp - dl_ref[2 * p + h])).astype(jnp.bfloat16)
                dvs.append(_tn(e.astype(jnp.bfloat16), do2))
                dks.append(_tn(ds, q2))
            dv_sc[:, cols] += _pick(dvs[0], dvs[1], lanes_k)
            dk_sc[:, cols] += _pick(dks[0], dks[1], lanes_k)
            return carry

        for p in range(pairs):
            pair(p, 0)

    @pl.when(i == pl.num_programs(1) - 1)
    def _():
        dk_ref[...] = dk_sc[...]
        dv_ref[...] = dv_sc[...]


def _clamp(start, step, last):
    return jnp.minimum(start + step, jnp.maximum(last, 0))


def _params():
    return pltpu.CompilerParams(dimension_semantics=("arbitrary", "arbitrary"), vmem_limit_bytes=48 * 1024 * 1024)


def flash_forward(q, k, v, q_ids, k_ids, lo, hi, block_q, block_k, steps):
    nq, width = q.shape
    nk = k.shape[0]
    heads = width // 64
    kv_map = lambda i, j, a, b: (_clamp(a[i], j, b[i]), 0)
    ks_map = lambda i, j, a, b: (0, _clamp(a[i], j, b[i]))
    row = lambda i, j, a, b: (i, 0)
    grid_spec = pltpu.PrefetchScalarGridSpec(
        num_scalar_prefetch=2,
        grid=(nq // block_q, steps),
        in_specs=[
            pl.BlockSpec((block_q, width), row),
            pl.BlockSpec((block_k, width), kv_map),
            pl.BlockSpec((block_k, width), kv_map),
            pl.BlockSpec((block_q, 1), row),
            pl.BlockSpec((1, block_k), ks_map),
        ],
        out_specs=[
            pl.BlockSpec((block_q, width), row),
            pl.BlockSpec((heads, block_q, 1), lambda i, j, a, b: (0, i, 0)),
        ],
        scratch_shapes=[
            pltpu.VMEM((heads, block_q, 1), jnp.float32),
            pltpu.VMEM((heads, block_q, 1), jnp.float32),
            pltpu.VMEM((block_q, width), jnp.float32),
        ],
    )
    return pl.pallas_call(
        _attn_fwd,
        grid_spec=grid_spec,
        out_shape=[jax.ShapeDtypeStruct((nq, width), jnp.float32), jax.ShapeDtypeStruct((heads, nq, 1), jnp.float32)],
        compiler_params=_params(),
    )(lo, hi, q, k, v, q_ids.reshape(nq, 1), k_ids.reshape(1, nk))


def flash_dq(q, k, v, q_ids, k_ids, lse, delta, do, lo, hi, block_q, block_k, steps):
    nq, width = q.shape
    nk = k.shape[0]
    heads = width // 64
    kv_map = lambda i, j, a, b: (_clamp(a[i], j, b[i]), 0)
    ks_map = lambda i, j, a, b: (0, _clamp(a[i], j, b[i]))
    row = lambda i, j, a, b: (i, 0)
    hrow = lambda i, j, a, b: (0, i, 0)
    grid_spec = pltpu.PrefetchScalarGridSpec(
        num_scalar_prefetch=2,
        grid=(nq // block_q, steps),
        in_specs=[
            pl.BlockSpec((block_q, width), row),
            pl.BlockSpec((block_k, width), kv_map),
            pl.BlockSpec((block_k, width), kv_map),
            pl.BlockSpec((block_q, 1), row),
            pl.BlockSpec((1, block_k), ks_map),
            pl.BlockSpec((heads, block_q, 1), hrow),
            pl.BlockSpec((heads, block_q, 1), hrow),
            pl.BlockSpec((block_q, width), row),
        ],
        out_specs=pl.BlockSpec((block_q, width), row),
        scratch_shapes=[pltpu.VMEM((block_q, width), jnp.float32)],
    )
    return pl.pallas_call(
        _attn_dq,
        grid_spec=grid_spec,
        out_shape=jax.ShapeDtypeStruct((nq, width), jnp.float32),
        compiler_params=_params(),
    )(lo, hi, q, k, v, q_ids.reshape(nq, 1), k_ids.reshape(1, nk), lse, delta, do)


def flash_dkv(q, k, v, q_ids, k_ids, lse, delta, do, qlo, qhi, block_q, block_k, steps):
    nq, width = q.shape
    nk = k.shape[0]
    heads = width // 64
    q_map = lambda j, i, a, b: (_clamp(a[j], i, b[j]), 0)
    h_map = lambda j, i, a, b: (0, _clamp(a[j], i, b[j]), 0)
    col = lambda j, i, a, b: (j, 0)
    grid_spec = pltpu.PrefetchScalarGridSpec(
        num_scalar_prefetch=2,
        grid=(nk // block_k, steps),
        in_specs=[
            pl.BlockSpec((block_q, width), q_map),
            pl.BlockSpec((block_k, width), col),
            pl.BlockSpec((block_k, width), col),
            pl.BlockSpec((block_q, 1), q_map),
            pl.BlockSpec((1, block_k), lambda j, i, a, b: (0, j)),
            pl.BlockSpec((heads, block_q, 1), h_map),
            pl.BlockSpec((heads, block_q, 1), h_map),
            pl.BlockSpec((block_q, width), q_map),
        ],
        out_specs=[pl.BlockSpec((block_k, width), col), pl.BlockSpec((block_k, width), col)],
        scratch_shapes=[pltpu.VMEM((block_k, width), jnp.float32), pltpu.VMEM((block_k, width), jnp.float32)],
    )
    return pl.pallas_call(
        _attn_dkv,
        grid_spec=grid_spec,
        out_shape=[jax.ShapeDtypeStruct((nk, width), jnp.float32), jax.ShapeDtypeStruct((nk, width), jnp.float32)],
        compiler_params=_params(),
    )(qlo, qhi, q, k, v, q_ids.reshape(nq, 1), k_ids.reshape(1, nk), lse, delta, do)


def block_ranges(q_ids, k_ids, q_start, q_end, block_q, block_k):
    nq = q_ids.shape[0]
    nk = k_ids.shape[0]
    nqb, nkb = nq // block_q, nk // block_k
    first = q_start.reshape(nqb, block_q)[:, 0]
    last = q_end.reshape(nqb, block_q)[:, block_q - 1]
    lo = jnp.clip(first // block_k, 0, nkb - 1).astype(jnp.int32)
    hi = jnp.clip((last - 1) // block_k, 0, nkb - 1).astype(jnp.int32)
    kb = jnp.arange(nkb, dtype=jnp.int32)
    qb = jnp.arange(nqb, dtype=jnp.int32)
    cover = (lo[:, None] <= kb[None, :]) & (kb[None, :] <= hi[:, None])
    qlo = jnp.min(jnp.where(cover, qb[:, None], nqb), axis=0).astype(jnp.int32)
    qhi = jnp.max(jnp.where(cover, qb[:, None], -1), axis=0).astype(jnp.int32)
    return lo, hi, qlo, qhi


def norm_forward(values, gain, shift):
    center = jnp.mean(values, axis=-1, keepdims=True)
    offsets = values - center
    spread = jnp.mean(offsets * offsets, axis=-1, keepdims=True)
    inverse = lax.rsqrt(spread + 1e-06)
    normed = offsets * inverse
    return (normed * gain + shift, normed, inverse)


def norm_backward(grad_y, normed, inverse, gain):
    grad_normed = grad_y * gain
    mean_one = jnp.mean(grad_normed, axis=-1, keepdims=True)
    mean_two = jnp.mean(grad_normed * normed, axis=-1, keepdims=True)
    return inverse * (grad_normed - mean_one - normed * mean_two)


def activate(values):
    return jax.nn.gelu(values, approximate=False)


def contract_last(left, right):
    return lax.dot_general(left, right, (((1,), (1,)), ((), ())), preferred_element_type=jnp.float32)


def contract_first(left, right):
    return lax.dot_general(left, right, (((0,), (0,)), ((), ())), preferred_element_type=jnp.float32)


def column_sum(values):
    return jnp.sum(values.astype(jnp.float32), axis=0)


def group_segments(lengths, dealing, group_index, group_rows, per_group):
    picked = lax.dynamic_slice_in_dim(dealing, group_index * per_group, per_group)
    match = picked[:, None] == jnp.arange(lengths.shape[0], dtype=jnp.int32)[None, :]
    chosen = jnp.sum(jnp.where(match, lengths[None, :], 0), axis=1)
    ends = jnp.cumsum(chosen)
    starts = ends - chosen
    places = jnp.arange(group_rows, dtype=jnp.int32)
    segment_ids = jnp.sum((places[:, None] >= ends[None, :]).astype(jnp.int32), axis=1)
    return (segment_ids, starts, ends)


def cyclic_pieces(piece):
    count = lax.axis_size("tensor")
    me = lax.axis_index("tensor")
    got = [piece]
    for k in range(1, count):
        got.append(lax.ppermute(piece, "tensor", [(s, (s + k) % count) for s in range(count)]))
    order = (me - jnp.arange(count, dtype=jnp.int32)) % count
    return jnp.take(jnp.stack(got), order, axis=0)


def gather_weights(blocks):
    count = lax.axis_size("tensor")
    widths = [b.shape[1] for b in blocks]
    piece = jnp.concatenate(blocks, axis=1)
    parts = cyclic_pieces(piece)
    cols, at = [], 0
    for w in widths:
        cols.extend(parts[t, :, at:at + w] for t in range(count))
        at += w
    strip = jnp.concatenate(cols, axis=1)
    full = lax.all_gather(strip, "dp", axis=0, tiled=True)
    out, at = [], 0
    for w in widths:
        out.append(full[:, at:at + w * count])
        at += w * count
    return out


def vector_rows(v, rows):
    dp = lax.axis_size("dp")
    slab = rows // dp
    spread = v.reshape(dp, 1, -1)
    return jnp.pad(spread, ((0, 0), (0, slab - 1), (0, 0))).reshape(rows, -1)


def pack_grads(grads, vectors):
    count = lax.axis_size("tensor")
    me = lax.axis_index("tensor")
    rows = grads[0].shape[0]
    mats = [g.astype(jnp.bfloat16) for g in grads] + [vector_rows(v.astype(jnp.bfloat16), rows) for v in vectors]
    widths = [m.shape[1] // count for m in mats]
    cat = jnp.concatenate(mats, axis=1)
    return widths, cat


def reduce_dp(cat):
    return lax.psum_scatter(cat, "dp", scatter_dimension=0, tiled=True)


def reduce_dp_by_halves(cat):
    dp = lax.axis_size("dp")
    me = lax.axis_index("dp")
    slab = cat.shape[0] // dp
    part = cat.astype(jnp.float32).reshape(dp, slab, cat.shape[1])
    bit = 0
    while (1 << bit) < dp:
        mine = (me >> bit) % 2
        halves = part.reshape(part.shape[0] // 2, 2, slab, cat.shape[1])
        keep = lax.dynamic_index_in_dim(halves, mine, axis=1, keepdims=False)
        send = lax.dynamic_index_in_dim(halves, 1 - mine, axis=1, keepdims=False)
        pairs = [(i, i ^ (1 << bit)) for i in range(dp)]
        part = keep + lax.ppermute(send.astype(jnp.bfloat16), "dp", pairs).astype(jnp.float32)
        bit += 1
    return part.reshape(slab, cat.shape[1])


def reduce_tensor(strip, widths, n_grads):
    count = lax.axis_size("tensor")
    me = lax.axis_index("tensor")
    strip = strip.astype(jnp.float32)
    per_t = []
    for t in range(count):
        at, cols = 0, []
        for w in widths:
            cols.append(strip[:, at + t * w:at + (t + 1) * w])
            at += w * count
        per_t.append(jnp.concatenate(cols, axis=1))
    stacked = jnp.stack(per_t)
    total = jnp.take(stacked, me, axis=0)
    for k in range(1, count):
        send = jnp.take(stacked, (me + k) % count, axis=0)
        total = total + lax.ppermute(send, "tensor", [(s, (s + k) % count) for s in range(count)])
    out, at = [], 0
    for i, w in enumerate(widths):
        block = total[:, at:at + w]
        at += w
        out.append(block if i < n_grads else block[0])
    return out


def halo_plan(rows):
    hops = -(-LONGEST // rows)
    takes = [rows] * (hops - 1) + [LONGEST - rows * (hops - 1)]
    return takes


def shift_rows(values, distance, count):
    if distance >= count:
        return jnp.zeros_like(values)
    if distance > 0:
        pairs = [(s, s + distance) for s in range(count - distance)]
    else:
        pairs = [(s - distance, s) for s in range(count + distance)]
    return lax.ppermute(values, "tensor", pairs)


def build_window(own, takes, count):
    rows = own.shape[0]
    left = [shift_rows(own[rows - take:], d + 1, count) for d, take in enumerate(takes)]
    right = [shift_rows(own[:take], -(d + 1), count) for d, take in enumerate(takes)]
    return jnp.concatenate(left[::-1] + [own] + right, axis=0)


def return_window(values, takes, count):
    rows = values.shape[0] - 2 * LONGEST
    total = values[LONGEST:LONGEST + rows]
    at = LONGEST
    for d, take in enumerate(takes):
        piece = values[at - take:at].astype(jnp.bfloat16)
        at -= take
        back = shift_rows(piece, -(d + 1), count).astype(jnp.float32)
        total = total + jnp.pad(back, ((rows - take, 0), (0, 0)))
    at = LONGEST + rows
    for d, take in enumerate(takes):
        piece = values[at:at + take].astype(jnp.bfloat16)
        at += take
        back = shift_rows(piece, d + 1, count).astype(jnp.float32)
        total = total + jnp.pad(back, ((0, rows - take), (0, 0)))
    return total


def to_heads(values):
    rows, width = values.shape
    return values.reshape(rows, width // HEAD_DIM, HEAD_DIM).transpose(1, 0, 2)


def from_heads(values):
    heads, rows, hd = values.shape
    return values.transpose(1, 0, 2).reshape(rows, heads * hd)


def shards(tokens, lengths, dealing, w_query, w_key, w_value, w_out, w_inner, w_outer, b_query, b_value, b_out, b_inner, b_outer, gain_attn, shift_attn, gain_ffn, shift_ffn, grad_out):
    count = lax.axis_size("tensor")
    tens_index = lax.axis_index("tensor")
    group_index = lax.axis_index("dp")
    rows = tokens.shape[0]
    group_rows = rows * count
    per_group = lengths.shape[0] // lax.axis_size("dp")
    takes = halo_plan(rows)
    window = rows + 2 * LONGEST
    seg, starts, ends = group_segments(lengths, dealing, group_index, group_rows, per_group)
    base = rows * tens_index - LONGEST
    places = base + jnp.arange(window, dtype=jnp.int32)
    valid = (places >= 0) & (places < group_rows)
    k_ids = jnp.where(valid, jnp.sum((places[:, None] >= ends[None, :]).astype(jnp.int32), axis=1), -1).astype(jnp.int32)
    q_ids = lax.dynamic_slice_in_dim(seg, rows * tens_index, rows)
    q_start = jnp.take(starts, q_ids) - base
    q_end = jnp.take(ends, q_ids) - base
    lo, hi, qlo, qhi = block_ranges(q_ids, k_ids, q_start, q_end, BLOCK, BLOCK)
    nkb = window // BLOCK
    kv_steps = min(nkb, (BLOCK + 2 * (LONGEST - 1)) // BLOCK + 2)
    q_steps = rows // BLOCK

    wq, wk, wv = gather_weights([w_query, w_key, w_value])
    wo_t, wi, wf_t = gather_weights([w_out.T, w_inner, w_outer.T])
    gain_one = gain_attn.astype(jnp.float32)
    gain_two = gain_ffn.astype(jnp.float32)

    x_own = tokens
    x_win = build_window(tokens, takes, count)
    query = (jnp.dot(x_own, wq, preferred_element_type=jnp.float32) + b_query.astype(jnp.float32)).astype(jnp.bfloat16)
    key_w = jnp.dot(x_win, wk, preferred_element_type=jnp.float32).astype(jnp.bfloat16)
    value_w = (jnp.dot(x_win, wv, preferred_element_type=jnp.float32) + b_value.astype(jnp.float32)).astype(jnp.bfloat16)
    scaled = query * jnp.asarray(1.0 / math.sqrt(HEAD_DIM), jnp.bfloat16)
    ctx32, lse = flash_forward(scaled, key_w, value_w, q_ids, k_ids, lo, hi, BLOCK, BLOCK, kv_steps)
    context = ctx32.astype(jnp.bfloat16)
    attn = contract_last(context, wo_t) + b_out.astype(jnp.float32)
    hidden, norm_one, inverse_one = norm_forward(tokens.astype(jnp.float32) + attn, gain_one, shift_attn.astype(jnp.float32))
    hidden_low = hidden.astype(jnp.bfloat16)
    pre_act = jnp.dot(hidden_low, wi, preferred_element_type=jnp.float32) + b_inner.astype(jnp.float32)
    act = activate(pre_act).astype(jnp.bfloat16)
    ffn = contract_last(act, wf_t) + b_outer.astype(jnp.float32)
    output, norm_two, inverse_two = norm_forward(hidden + ffn, gain_two, shift_ffn.astype(jnp.float32))

    grad_y = grad_out.astype(jnp.float32)
    grad_resid_two = norm_backward(grad_y, norm_two, inverse_two, gain_two)
    grad_ffn = grad_resid_two.astype(jnp.bfloat16)
    grad_outer_t = contract_first(grad_ffn, act)
    grad_act = jnp.dot(grad_ffn, wf_t, preferred_element_type=jnp.float32)
    unused, gelu_pull = jax.vjp(activate, pre_act)
    grad_pre = gelu_pull(grad_act)[0].astype(jnp.bfloat16)
    grad_inner_w = contract_first(hidden_low, grad_pre)
    grad_hidden = grad_resid_two + contract_last(grad_pre, wi)
    grad_resid_one = norm_backward(grad_hidden, norm_one, inverse_one, gain_one)
    grad_attn = grad_resid_one.astype(jnp.bfloat16)
    grad_out_t = contract_first(grad_attn, context)
    grad_context = jnp.dot(grad_attn, wo_t, preferred_element_type=jnp.float32).astype(jnp.bfloat16)
    late = [
        column_sum(grad_attn),
        column_sum(grad_pre),
        column_sum(grad_ffn),
        jnp.sum(grad_hidden * norm_one, axis=0),
        jnp.sum(grad_hidden, axis=0),
        jnp.sum(grad_y * norm_two, axis=0),
        jnp.sum(grad_y, axis=0),
    ]
    early_widths, early_cat = pack_grads([grad_out_t, grad_inner_w, grad_outer_t], late)
    grad_context, early_cat = lax.optimization_barrier((grad_context, early_cat))
    early_strip = reduce_dp(early_cat)
    heads = query.shape[1] // HEAD_DIM
    delta = jnp.sum((grad_context.astype(jnp.float32) * ctx32).reshape(rows, heads, HEAD_DIM), axis=-1)
    delta = delta.T.reshape(heads, rows, 1)
    dq_h = flash_dq(scaled, key_w, value_w, q_ids, k_ids, lse, delta, grad_context, lo, hi, BLOCK, BLOCK, kv_steps)
    dk_h, dv_h = flash_dkv(scaled, key_w, value_w, q_ids, k_ids, lse, delta, grad_context, qlo, qhi, BLOCK, BLOCK, q_steps)
    early_strip, dq_h, dk_h, dv_h = lax.optimization_barrier((early_strip, dq_h, dk_h, dv_h))
    early_sums = reduce_tensor(early_strip, early_widths, 3)
    g_out_t, g_inner, g_outer_t = early_sums[:3]
    late = early_sums[3:]
    grad_query = dq_h.astype(jnp.bfloat16)
    grad_key = dk_h.astype(jnp.bfloat16)
    grad_value = dv_h.astype(jnp.bfloat16)
    grad_query_w = contract_first(x_own, grad_query)
    grad_key_w = contract_first(x_win, grad_key)
    grad_value_w = contract_first(x_win, grad_value)
    grad_win = contract_last(grad_key, wk) + contract_last(grad_value, wv)
    grad_tokens = grad_resid_one + contract_last(grad_query, wq) + return_window(grad_win, takes, count)

    late_widths, late_cat = pack_grads(
        [grad_query_w, grad_key_w, grad_value_w], [column_sum(grad_query), column_sum(grad_value)]
    )
    g_query, g_key, g_value, g_bq, g_bv = reduce_tensor(reduce_dp_by_halves(late_cat), late_widths, 3)
    summed = (g_query, g_key, g_value, g_out_t.T, g_inner, g_outer_t.T)
    small = [g_bq, g_bv] + late
    return (output.astype(jnp.bfloat16), grad_tokens) + summed + tuple(small)


def solution(mesh):
    rows = P(("dp", "tensor"), None)
    vec = P(("dp", "tensor"))
    return jax.shard_map(
        shards,
        mesh=mesh,
        in_specs=(rows, P(), P(), P("dp", "tensor"), P("dp", "tensor"), P("dp", "tensor"), P("tensor", "dp"), P("dp", "tensor"), P("tensor", "dp"), P(), P(), P(), P(), P(), P(), P(), P(), P(), rows),
        out_specs=(rows, rows, P("dp", "tensor"), P("dp", "tensor"), P("dp", "tensor"), P("tensor", "dp"), P("dp", "tensor"), P("tensor", "dp")) + (vec,) * 9,
        check_vma=False,
    )
```

```python
import math

import jax
import jax.numpy as jnp
from jax import lax
from jax.experimental import pallas as pl
from jax.experimental.pallas import tpu as pltpu
from jax.sharding import PartitionSpec as P

HEAD_DIM = 64
LONGEST = 1024
BLOCK = 256

NEG = -1e30
LANES = 128


def _lanes(rows):
    return lax.broadcasted_iota(jnp.int32, (rows, LANES), 1) < LANES // 2


def _pick(first, second, lanes):
    return jnp.where(lanes, first, second)


def _nt(a, b):
    return lax.dot_general(a, b, (((1,), (1,)), ((), ())), preferred_element_type=jnp.float32)


def _tn(a, b):
    return lax.dot_general(a, b, (((0,), (0,)), ((), ())), preferred_element_type=jnp.float32)


def _nn(a, b):
    return lax.dot_general(a, b, (((1,), (0,)), ((), ())), preferred_element_type=jnp.float32)


def _attn_fwd(lo_ref, hi_ref, q_ref, k_ref, v_ref, qs_ref, ks_ref, o_ref, lse_ref, m_sc, l_sc, acc_sc):
    i = pl.program_id(0)
    j = pl.program_id(1)
    kv = lo_ref[i] + j
    pairs = q_ref.shape[1] // LANES
    bq = q_ref.shape[0]

    @pl.when(j == 0)
    def _():
        m_sc[...] = jnp.full_like(m_sc, NEG)
        l_sc[...] = jnp.zeros_like(l_sc)
        acc_sc[...] = jnp.zeros_like(acc_sc)

    @pl.when(kv <= hi_ref[i])
    def _():
        mask = qs_ref[...] == ks_ref[...]
        lanes = _lanes(bq)

        def pair(p, carry):
            cols = pl.ds(p * LANES, LANES)
            q2 = q_ref[:, cols]
            k2 = k_ref[:, cols]
            v2 = v_ref[:, cols]
            zero = jnp.zeros_like(q2)
            alphas, pvs = [], []
            for h in range(2):
                hq = _pick(q2, zero, lanes) if h == 0 else _pick(zero, q2, lanes)
                s = jnp.where(mask, _nt(hq, k2), NEG)
                m_old = m_sc[2 * p + h]
                m_new = jnp.maximum(m_old, jnp.max(s, axis=-1, keepdims=True))
                alpha = jnp.exp(m_old - m_new)
                e = jnp.exp(s - m_new)
                l_sc[2 * p + h] = alpha * l_sc[2 * p + h] + jnp.sum(e, axis=-1, keepdims=True)
                m_sc[2 * p + h] = m_new
                alphas.append(alpha)
                pvs.append(_nn(e.astype(jnp.bfloat16), v2))
            acc_sc[:, cols] = _pick(alphas[0], alphas[1], lanes) * acc_sc[:, cols] + _pick(pvs[0], pvs[1], lanes)
            return carry

        for p in range(pairs):
            pair(p, 0)

    @pl.when(j == pl.num_programs(1) - 1)
    def _():
        lanes = _lanes(bq)

        def pair(p, carry):
            cols = pl.ds(p * LANES, LANES)
            l0, l1 = l_sc[2 * p], l_sc[2 * p + 1]
            o_ref[:, cols] = acc_sc[:, cols] / _pick(l0, l1, lanes)
            lse_ref[2 * p] = m_sc[2 * p] + jnp.log(l0)
            lse_ref[2 * p + 1] = m_sc[2 * p + 1] + jnp.log(l1)
            return carry

        for p in range(pairs):
            pair(p, 0)


def _attn_dq(lo_ref, hi_ref, q_ref, k_ref, v_ref, qs_ref, ks_ref, lse_ref, dl_ref, do_ref, dq_ref, acc_sc):
    i = pl.program_id(0)
    j = pl.program_id(1)
    kv = lo_ref[i] + j
    pairs = q_ref.shape[1] // LANES
    bq = q_ref.shape[0]

    @pl.when(j == 0)
    def _():
        acc_sc[...] = jnp.zeros_like(acc_sc)

    @pl.when(kv <= hi_ref[i])
    def _():
        mask = qs_ref[...] == ks_ref[...]
        lanes = _lanes(bq)

        def pair(p, carry):
            cols = pl.ds(p * LANES, LANES)
            q2 = q_ref[:, cols]
            k2 = k_ref[:, cols]
            v2 = v_ref[:, cols]
            do2 = do_ref[:, cols]
            zero = jnp.zeros_like(q2)
            parts = []
            for h in range(2):
                sel = (lambda a: _pick(a, zero, lanes)) if h == 0 else (lambda a: _pick(zero, a, lanes))
                s = _nt(sel(q2), k2)
                e = jnp.where(mask, jnp.exp(s - lse_ref[2 * p + h]), 0.0)
                dp = _nt(sel(do2), v2)
                ds = (e * (dp - dl_ref[2 * p + h])).astype(jnp.bfloat16)
                parts.append(_nn(ds, k2))
            acc_sc[:, cols] += _pick(parts[0], parts[1], lanes)
            return carry

        for p in range(pairs):
            pair(p, 0)

    @pl.when(j == pl.num_programs(1) - 1)
    def _():
        dq_ref[...] = acc_sc[...] * 0.125


def _attn_dkv(lo_ref, hi_ref, q_ref, k_ref, v_ref, qs_ref, ks_ref, lse_ref, dl_ref, do_ref, dk_ref, dv_ref, dk_sc, dv_sc):
    j = pl.program_id(0)
    i = pl.program_id(1)
    qb = lo_ref[j] + i
    pairs = q_ref.shape[1] // LANES
    bq = q_ref.shape[0]
    bk = k_ref.shape[0]

    @pl.when(i == 0)
    def _():
        dk_sc[...] = jnp.zeros_like(dk_sc)
        dv_sc[...] = jnp.zeros_like(dv_sc)

    @pl.when(qb <= hi_ref[j])
    def _():
        mask = qs_ref[...] == ks_ref[...]
        lanes_q = _lanes(bq)
        lanes_k = _lanes(bk)

        def pair(p, carry):
            cols = pl.ds(p * LANES, LANES)
            q2 = q_ref[:, cols]
            k2 = k_ref[:, cols]
            v2 = v_ref[:, cols]
            do2 = do_ref[:, cols]
            zero = jnp.zeros_like(q2)
            dks, dvs = [], []
            for h in range(2):
                sel = (lambda a: _pick(a, zero, lanes_q)) if h == 0 else (lambda a: _pick(zero, a, lanes_q))
                s = _nt(sel(q2), k2)
                e = jnp.where(mask, jnp.exp(s - lse_ref[2 * p + h]), 0.0)
                dp = _nt(sel(do2), v2)
                ds = (e * (dp - dl_ref[2 * p + h])).astype(jnp.bfloat16)
                dvs.append(_tn(e.astype(jnp.bfloat16), do2))
                dks.append(_tn(ds, q2))
            dv_sc[:, cols] += _pick(dvs[0], dvs[1], lanes_k)
            dk_sc[:, cols] += _pick(dks[0], dks[1], lanes_k)
            return carry

        for p in range(pairs):
            pair(p, 0)

    @pl.when(i == pl.num_programs(1) - 1)
    def _():
        dk_ref[...] = dk_sc[...]
        dv_ref[...] = dv_sc[...]


def _clamp(start, step, last):
    return jnp.minimum(start + step, jnp.maximum(last, 0))


def _params():
    return pltpu.CompilerParams(dimension_semantics=("arbitrary", "arbitrary"), vmem_limit_bytes=48 * 1024 * 1024)


def flash_forward(q, k, v, q_ids, k_ids, lo, hi, block_q, block_k, steps):
    nq, width = q.shape
    nk = k.shape[0]
    heads = width // 64
    kv_map = lambda i, j, a, b: (_clamp(a[i], j, b[i]), 0)
    ks_map = lambda i, j, a, b: (0, _clamp(a[i], j, b[i]))
    row = lambda i, j, a, b: (i, 0)
    grid_spec = pltpu.PrefetchScalarGridSpec(
        num_scalar_prefetch=2,
        grid=(nq // block_q, steps),
        in_specs=[
            pl.BlockSpec((block_q, width), row),
            pl.BlockSpec((block_k, width), kv_map),
            pl.BlockSpec((block_k, width), kv_map),
            pl.BlockSpec((block_q, 1), row),
            pl.BlockSpec((1, block_k), ks_map),
        ],
        out_specs=[
            pl.BlockSpec((block_q, width), row),
            pl.BlockSpec((heads, block_q, 1), lambda i, j, a, b: (0, i, 0)),
        ],
        scratch_shapes=[
            pltpu.VMEM((heads, block_q, 1), jnp.float32),
            pltpu.VMEM((heads, block_q, 1), jnp.float32),
            pltpu.VMEM((block_q, width), jnp.float32),
        ],
    )
    return pl.pallas_call(
        _attn_fwd,
        grid_spec=grid_spec,
        out_shape=[jax.ShapeDtypeStruct((nq, width), jnp.float32), jax.ShapeDtypeStruct((heads, nq, 1), jnp.float32)],
        compiler_params=_params(),
    )(lo, hi, q, k, v, q_ids.reshape(nq, 1), k_ids.reshape(1, nk))


def flash_dq(q, k, v, q_ids, k_ids, lse, delta, do, lo, hi, block_q, block_k, steps):
    nq, width = q.shape
    nk = k.shape[0]
    heads = width // 64
    kv_map = lambda i, j, a, b: (_clamp(a[i], j, b[i]), 0)
    ks_map = lambda i, j, a, b: (0, _clamp(a[i], j, b[i]))
    row = lambda i, j, a, b: (i, 0)
    hrow = lambda i, j, a, b: (0, i, 0)
    grid_spec = pltpu.PrefetchScalarGridSpec(
        num_scalar_prefetch=2,
        grid=(nq // block_q, steps),
        in_specs=[
            pl.BlockSpec((block_q, width), row),
            pl.BlockSpec((block_k, width), kv_map),
            pl.BlockSpec((block_k, width), kv_map),
            pl.BlockSpec((block_q, 1), row),
            pl.BlockSpec((1, block_k), ks_map),
            pl.BlockSpec((heads, block_q, 1), hrow),
            pl.BlockSpec((heads, block_q, 1), hrow),
            pl.BlockSpec((block_q, width), row),
        ],
        out_specs=pl.BlockSpec((block_q, width), row),
        scratch_shapes=[pltpu.VMEM((block_q, width), jnp.float32)],
    )
    return pl.pallas_call(
        _attn_dq,
        grid_spec=grid_spec,
        out_shape=jax.ShapeDtypeStruct((nq, width), jnp.float32),
        compiler_params=_params(),
    )(lo, hi, q, k, v, q_ids.reshape(nq, 1), k_ids.reshape(1, nk), lse, delta, do)


def flash_dkv(q, k, v, q_ids, k_ids, lse, delta, do, qlo, qhi, block_q, block_k, steps):
    nq, width = q.shape
    nk = k.shape[0]
    heads = width // 64
    q_map = lambda j, i, a, b: (_clamp(a[j], i, b[j]), 0)
    h_map = lambda j, i, a, b: (0, _clamp(a[j], i, b[j]), 0)
    col = lambda j, i, a, b: (j, 0)
    grid_spec = pltpu.PrefetchScalarGridSpec(
        num_scalar_prefetch=2,
        grid=(nk // block_k, steps),
        in_specs=[
            pl.BlockSpec((block_q, width), q_map),
            pl.BlockSpec((block_k, width), col),
            pl.BlockSpec((block_k, width), col),
            pl.BlockSpec((block_q, 1), q_map),
            pl.BlockSpec((1, block_k), lambda j, i, a, b: (0, j)),
            pl.BlockSpec((heads, block_q, 1), h_map),
            pl.BlockSpec((heads, block_q, 1), h_map),
            pl.BlockSpec((block_q, width), q_map),
        ],
        out_specs=[pl.BlockSpec((block_k, width), col), pl.BlockSpec((block_k, width), col)],
        scratch_shapes=[pltpu.VMEM((block_k, width), jnp.float32), pltpu.VMEM((block_k, width), jnp.float32)],
    )
    return pl.pallas_call(
        _attn_dkv,
        grid_spec=grid_spec,
        out_shape=[jax.ShapeDtypeStruct((nk, width), jnp.float32), jax.ShapeDtypeStruct((nk, width), jnp.float32)],
        compiler_params=_params(),
    )(qlo, qhi, q, k, v, q_ids.reshape(nq, 1), k_ids.reshape(1, nk), lse, delta, do)


def block_ranges(q_ids, k_ids, q_start, q_end, block_q, block_k):
    nq = q_ids.shape[0]
    nk = k_ids.shape[0]
    nqb, nkb = nq // block_q, nk // block_k
    first = q_start.reshape(nqb, block_q)[:, 0]
    last = q_end.reshape(nqb, block_q)[:, block_q - 1]
    lo = jnp.clip(first // block_k, 0, nkb - 1).astype(jnp.int32)
    hi = jnp.clip((last - 1) // block_k, 0, nkb - 1).astype(jnp.int32)
    kb = jnp.arange(nkb, dtype=jnp.int32)
    qb = jnp.arange(nqb, dtype=jnp.int32)
    cover = (lo[:, None] <= kb[None, :]) & (kb[None, :] <= hi[:, None])
    qlo = jnp.min(jnp.where(cover, qb[:, None], nqb), axis=0).astype(jnp.int32)
    qhi = jnp.max(jnp.where(cover, qb[:, None], -1), axis=0).astype(jnp.int32)
    return lo, hi, qlo, qhi


def norm_forward(values, gain, shift):
    center = jnp.mean(values, axis=-1, keepdims=True)
    offsets = values - center
    spread = jnp.mean(offsets * offsets, axis=-1, keepdims=True)
    inverse = lax.rsqrt(spread + 1e-06)
    normed = offsets * inverse
    return (normed * gain + shift, normed, inverse)


def norm_backward(grad_y, normed, inverse, gain):
    grad_normed = grad_y * gain
    mean_one = jnp.mean(grad_normed, axis=-1, keepdims=True)
    mean_two = jnp.mean(grad_normed * normed, axis=-1, keepdims=True)
    return inverse * (grad_normed - mean_one - normed * mean_two)


def activate(values):
    return jax.nn.gelu(values, approximate=False)


def contract_last(left, right):
    return lax.dot_general(left, right, (((1,), (1,)), ((), ())), preferred_element_type=jnp.float32)


def contract_first(left, right):
    return lax.dot_general(left, right, (((0,), (0,)), ((), ())), preferred_element_type=jnp.float32)


def column_sum(values):
    return jnp.sum(values.astype(jnp.float32), axis=0)


def group_segments(lengths, dealing, group_index, group_rows, per_group):
    picked = lax.dynamic_slice_in_dim(dealing, group_index * per_group, per_group)
    match = picked[:, None] == jnp.arange(lengths.shape[0], dtype=jnp.int32)[None, :]
    chosen = jnp.sum(jnp.where(match, lengths[None, :], 0), axis=1)
    ends = jnp.cumsum(chosen)
    starts = ends - chosen
    places = jnp.arange(group_rows, dtype=jnp.int32)
    segment_ids = jnp.sum((places[:, None] >= ends[None, :]).astype(jnp.int32), axis=1)
    return (segment_ids, starts, ends)


def cyclic_pieces(piece):
    count = lax.axis_size("tensor")
    me = lax.axis_index("tensor")
    got = [piece]
    for k in range(1, count):
        got.append(lax.ppermute(piece, "tensor", [(s, (s + k) % count) for s in range(count)]))
    order = (me - jnp.arange(count, dtype=jnp.int32)) % count
    return jnp.take(jnp.stack(got), order, axis=0)


def gather_weights(blocks):
    count = lax.axis_size("tensor")
    widths = [b.shape[1] for b in blocks]
    piece = jnp.concatenate(blocks, axis=1)
    parts = cyclic_pieces(piece)
    cols, at = [], 0
    for w in widths:
        cols.extend(parts[t, :, at:at + w] for t in range(count))
        at += w
    strip = jnp.concatenate(cols, axis=1)
    full = lax.all_gather(strip, "dp", axis=0, tiled=True)
    out, at = [], 0
    for w in widths:
        out.append(full[:, at:at + w * count])
        at += w * count
    return out


def vector_rows(v, rows):
    dp = lax.axis_size("dp")
    slab = rows // dp
    spread = v.reshape(dp, 1, -1)
    return jnp.pad(spread, ((0, 0), (0, slab - 1), (0, 0))).reshape(rows, -1)


def pack_grads(grads, vectors):
    count = lax.axis_size("tensor")
    me = lax.axis_index("tensor")
    rows = grads[0].shape[0]
    mats = [g.astype(jnp.bfloat16) for g in grads] + [vector_rows(v.astype(jnp.bfloat16), rows) for v in vectors]
    widths = [m.shape[1] // count for m in mats]
    cat = jnp.concatenate(mats, axis=1)
    return widths, cat


def reduce_dp(cat):
    return lax.psum_scatter(cat, "dp", scatter_dimension=0, tiled=True)


def reduce_dp_by_halves(cat):
    dp = lax.axis_size("dp")
    me = lax.axis_index("dp")
    slab = cat.shape[0] // dp
    part = cat.astype(jnp.float32).reshape(dp, slab, cat.shape[1])
    bit = 0
    while (1 << bit) < dp:
        mine = (me >> bit) % 2
        halves = part.reshape(part.shape[0] // 2, 2, slab, cat.shape[1])
        keep = lax.dynamic_index_in_dim(halves, mine, axis=1, keepdims=False)
        send = lax.dynamic_index_in_dim(halves, 1 - mine, axis=1, keepdims=False)
        pairs = [(i, i ^ (1 << bit)) for i in range(dp)]
        part = keep + lax.ppermute(send.astype(jnp.bfloat16), "dp", pairs).astype(jnp.float32)
        bit += 1
    return part.reshape(slab, cat.shape[1])


def reduce_tensor(strip, widths, n_grads):
    count = lax.axis_size("tensor")
    me = lax.axis_index("tensor")
    strip = strip.astype(jnp.float32)
    per_t = []
    for t in range(count):
        at, cols = 0, []
        for w in widths:
            cols.append(strip[:, at + t * w:at + (t + 1) * w])
            at += w * count
        per_t.append(jnp.concatenate(cols, axis=1))
    stacked = jnp.stack(per_t)
    total = jnp.take(stacked, me, axis=0)
    for k in range(1, count):
        send = jnp.take(stacked, (me + k) % count, axis=0)
        total = total + lax.ppermute(send, "tensor", [(s, (s + k) % count) for s in range(count)])
    out, at = [], 0
    for i, w in enumerate(widths):
        block = total[:, at:at + w]
        at += w
        out.append(block if i < n_grads else block[0])
    return out


def halo_plan(rows):
    hops = -(-LONGEST // rows)
    takes = [rows] * (hops - 1) + [LONGEST - rows * (hops - 1)]
    return takes


def shift_rows(values, distance, count):
    if distance >= count:
        return jnp.zeros_like(values)
    if distance > 0:
        pairs = [(s, s + distance) for s in range(count - distance)]
    else:
        pairs = [(s - distance, s) for s in range(count + distance)]
    return lax.ppermute(values, "tensor", pairs)


def build_window(own, takes, count):
    rows = own.shape[0]
    left = [shift_rows(own[rows - take:], d + 1, count) for d, take in enumerate(takes)]
    right = [shift_rows(own[:take], -(d + 1), count) for d, take in enumerate(takes)]
    return jnp.concatenate(left[::-1] + [own] + right, axis=0)


def return_window(values, takes, count):
    rows = values.shape[0] - 2 * LONGEST
    total = values[LONGEST:LONGEST + rows]
    at = LONGEST
    for d, take in enumerate(takes):
        piece = values[at - take:at].astype(jnp.bfloat16)
        at -= take
        back = shift_rows(piece, -(d + 1), count).astype(jnp.float32)
        total = total + jnp.pad(back, ((rows - take, 0), (0, 0)))
    at = LONGEST + rows
    for d, take in enumerate(takes):
        piece = values[at:at + take].astype(jnp.bfloat16)
        at += take
        back = shift_rows(piece, d + 1, count).astype(jnp.float32)
        total = total + jnp.pad(back, ((0, rows - take), (0, 0)))
    return total


def to_heads(values):
    rows, width = values.shape
    return values.reshape(rows, width // HEAD_DIM, HEAD_DIM).transpose(1, 0, 2)


def from_heads(values):
    heads, rows, hd = values.shape
    return values.transpose(1, 0, 2).reshape(rows, heads * hd)


def shards(tokens, lengths, dealing, w_query, w_key, w_value, w_out, w_inner, w_outer, b_query, b_value, b_out, b_inner, b_outer, gain_attn, shift_attn, gain_ffn, shift_ffn, grad_out):
    count = lax.axis_size("tensor")
    tens_index = lax.axis_index("tensor")
    group_index = lax.axis_index("dp")
    rows = tokens.shape[0]
    group_rows = rows * count
    per_group = lengths.shape[0] // lax.axis_size("dp")
    takes = halo_plan(rows)
    window = rows + 2 * LONGEST
    seg, starts, ends = group_segments(lengths, dealing, group_index, group_rows, per_group)
    base = rows * tens_index - LONGEST
    places = base + jnp.arange(window, dtype=jnp.int32)
    valid = (places >= 0) & (places < group_rows)
    k_ids = jnp.where(valid, jnp.sum((places[:, None] >= ends[None, :]).astype(jnp.int32), axis=1), -1).astype(jnp.int32)
    q_ids = lax.dynamic_slice_in_dim(seg, rows * tens_index, rows)
    q_start = jnp.take(starts, q_ids) - base
    q_end = jnp.take(ends, q_ids) - base
    lo, hi, qlo, qhi = block_ranges(q_ids, k_ids, q_start, q_end, BLOCK, BLOCK)
    nkb = window // BLOCK
    kv_steps = min(nkb, (BLOCK + 2 * (LONGEST - 1)) // BLOCK + 2)
    q_steps = rows // BLOCK

    x_win = build_window(tokens, takes, count)
    wq, wk, wv = gather_weights([w_query, w_key, w_value])
    later = (w_out.T, w_inner, w_outer.T)
    x_win, later = lax.optimization_barrier((x_win, later))
    wo_t, wi, wf_t = gather_weights(list(later))
    gain_one = gain_attn.astype(jnp.float32)
    gain_two = gain_ffn.astype(jnp.float32)

    x_own = tokens
    query = (jnp.dot(x_own, wq, preferred_element_type=jnp.float32) + b_query.astype(jnp.float32)).astype(jnp.bfloat16)
    key_w = jnp.dot(x_win, wk, preferred_element_type=jnp.float32).astype(jnp.bfloat16)
    value_w = (jnp.dot(x_win, wv, preferred_element_type=jnp.float32) + b_value.astype(jnp.float32)).astype(jnp.bfloat16)
    scaled = query * jnp.asarray(1.0 / math.sqrt(HEAD_DIM), jnp.bfloat16)
    ctx32, lse = flash_forward(scaled, key_w, value_w, q_ids, k_ids, lo, hi, BLOCK, BLOCK, kv_steps)
    context = ctx32.astype(jnp.bfloat16)
    attn = contract_last(context, wo_t) + b_out.astype(jnp.float32)
    hidden, norm_one, inverse_one = norm_forward(tokens.astype(jnp.float32) + attn, gain_one, shift_attn.astype(jnp.float32))
    hidden_low = hidden.astype(jnp.bfloat16)
    pre_act = jnp.dot(hidden_low, wi, preferred_element_type=jnp.float32) + b_inner.astype(jnp.float32)
    act = activate(pre_act).astype(jnp.bfloat16)
    ffn = contract_last(act, wf_t) + b_outer.astype(jnp.float32)
    output, norm_two, inverse_two = norm_forward(hidden + ffn, gain_two, shift_ffn.astype(jnp.float32))

    grad_y = grad_out.astype(jnp.float32)
    grad_resid_two = norm_backward(grad_y, norm_two, inverse_two, gain_two)
    grad_ffn = grad_resid_two.astype(jnp.bfloat16)
    grad_outer_t = contract_first(grad_ffn, act)
    grad_act = jnp.dot(grad_ffn, wf_t, preferred_element_type=jnp.float32)
    unused, gelu_pull = jax.vjp(activate, pre_act)
    grad_pre = gelu_pull(grad_act)[0].astype(jnp.bfloat16)
    grad_inner_w = contract_first(hidden_low, grad_pre)
    grad_hidden = grad_resid_two + contract_last(grad_pre, wi)
    grad_resid_one = norm_backward(grad_hidden, norm_one, inverse_one, gain_one)
    grad_attn = grad_resid_one.astype(jnp.bfloat16)
    grad_out_t = contract_first(grad_attn, context)
    grad_context = jnp.dot(grad_attn, wo_t, preferred_element_type=jnp.float32).astype(jnp.bfloat16)
    late = [
        column_sum(grad_attn),
        column_sum(grad_pre),
        column_sum(grad_ffn),
        jnp.sum(grad_hidden * norm_one, axis=0),
        jnp.sum(grad_hidden, axis=0),
        jnp.sum(grad_y * norm_two, axis=0),
        jnp.sum(grad_y, axis=0),
    ]
    early_widths, early_cat = pack_grads([grad_out_t, grad_inner_w, grad_outer_t], late)
    grad_context, early_cat = lax.optimization_barrier((grad_context, early_cat))
    early_strip = reduce_dp(early_cat)
    heads = query.shape[1] // HEAD_DIM
    delta = jnp.sum((grad_context.astype(jnp.float32) * ctx32).reshape(rows, heads, HEAD_DIM), axis=-1)
    delta = delta.T.reshape(heads, rows, 1)
    dq_h = flash_dq(scaled, key_w, value_w, q_ids, k_ids, lse, delta, grad_context, lo, hi, BLOCK, BLOCK, kv_steps)
    dk_h, dv_h = flash_dkv(scaled, key_w, value_w, q_ids, k_ids, lse, delta, grad_context, qlo, qhi, BLOCK, BLOCK, q_steps)
    early_strip, dq_h, dk_h, dv_h = lax.optimization_barrier((early_strip, dq_h, dk_h, dv_h))
    early_sums = reduce_tensor(early_strip, early_widths, 3)
    g_out_t, g_inner, g_outer_t = early_sums[:3]
    late = early_sums[3:]
    grad_query = dq_h.astype(jnp.bfloat16)
    grad_key = dk_h.astype(jnp.bfloat16)
    grad_value = dv_h.astype(jnp.bfloat16)
    grad_query_w = contract_first(x_own, grad_query)
    grad_key_w = contract_first(x_win, grad_key)
    grad_value_w = contract_first(x_win, grad_value)
    grad_win = contract_last(grad_key, wk) + contract_last(grad_value, wv)
    grad_tokens = grad_resid_one + contract_last(grad_query, wq) + return_window(grad_win, takes, count)

    late_widths, late_cat = pack_grads(
        [grad_query_w, grad_key_w, grad_value_w], [column_sum(grad_query), column_sum(grad_value)]
    )
    g_query, g_key, g_value, g_bq, g_bv = reduce_tensor(reduce_dp_by_halves(late_cat), late_widths, 3)
    summed = (g_query, g_key, g_value, g_out_t.T, g_inner, g_outer_t.T)
    small = [g_bq, g_bv] + late
    return (output.astype(jnp.bfloat16), grad_tokens) + summed + tuple(small)


def solution(mesh):
    rows = P(("dp", "tensor"), None)
    vec = P(("dp", "tensor"))
    return jax.shard_map(
        shards,
        mesh=mesh,
        in_specs=(rows, P(), P(), P("dp", "tensor"), P("dp", "tensor"), P("dp", "tensor"), P("tensor", "dp"), P("dp", "tensor"), P("tensor", "dp"), P(), P(), P(), P(), P(), P(), P(), P(), P(), rows),
        out_specs=(rows, rows, P("dp", "tensor"), P("dp", "tensor"), P("dp", "tensor"), P("tensor", "dp"), P("dp", "tensor"), P("tensor", "dp")) + (vec,) * 9,
        check_vma=False,
    )
```

```python
import math

import jax
import jax.numpy as jnp
from jax import lax
from jax.experimental import pallas as pl
from jax.experimental.pallas import tpu as pltpu
from jax.sharding import PartitionSpec as P

HEAD_DIM = 64
LONGEST = 1024
BLOCK = 256

NEG = -1e30
LANES = 128


def _lanes(rows):
    return lax.broadcasted_iota(jnp.int32, (rows, LANES), 1) < LANES // 2


def _pick(first, second, lanes):
    return jnp.where(lanes, first, second)


def _nt(a, b):
    return lax.dot_general(a, b, (((1,), (1,)), ((), ())), preferred_element_type=jnp.float32)


def _tn(a, b):
    return lax.dot_general(a, b, (((0,), (0,)), ((), ())), preferred_element_type=jnp.float32)


def _nn(a, b):
    return lax.dot_general(a, b, (((1,), (0,)), ((), ())), preferred_element_type=jnp.float32)


def _attn_fwd(lo_ref, hi_ref, q_ref, k_ref, v_ref, qs_ref, ks_ref, o_ref, lse_ref, m_sc, l_sc, acc_sc):
    i = pl.program_id(0)
    j = pl.program_id(1)
    kv = lo_ref[i] + j
    pairs = q_ref.shape[1] // LANES
    bq = q_ref.shape[0]

    @pl.when(j == 0)
    def _():
        m_sc[...] = jnp.full_like(m_sc, NEG)
        l_sc[...] = jnp.zeros_like(l_sc)
        acc_sc[...] = jnp.zeros_like(acc_sc)

    @pl.when(kv <= hi_ref[i])
    def _():
        mask = qs_ref[...] == ks_ref[...]
        lanes = _lanes(bq)

        def pair(p, carry):
            cols = pl.ds(p * LANES, LANES)
            q2 = q_ref[:, cols]
            k2 = k_ref[:, cols]
            v2 = v_ref[:, cols]
            zero = jnp.zeros_like(q2)
            alphas, pvs = [], []
            for h in range(2):
                hq = _pick(q2, zero, lanes) if h == 0 else _pick(zero, q2, lanes)
                s = jnp.where(mask, _nt(hq, k2), NEG)
                m_old = m_sc[2 * p + h]
                m_new = jnp.maximum(m_old, jnp.max(s, axis=-1, keepdims=True))
                alpha = jnp.exp(m_old - m_new)
                e = jnp.exp(s - m_new)
                l_sc[2 * p + h] = alpha * l_sc[2 * p + h] + jnp.sum(e, axis=-1, keepdims=True)
                m_sc[2 * p + h] = m_new
                alphas.append(alpha)
                pvs.append(_nn(e.astype(jnp.bfloat16), v2))
            acc_sc[:, cols] = _pick(alphas[0], alphas[1], lanes) * acc_sc[:, cols] + _pick(pvs[0], pvs[1], lanes)
            return carry

        for p in range(pairs):
            pair(p, 0)

    @pl.when(j == pl.num_programs(1) - 1)
    def _():
        lanes = _lanes(bq)

        def pair(p, carry):
            cols = pl.ds(p * LANES, LANES)
            l0, l1 = l_sc[2 * p], l_sc[2 * p + 1]
            o_ref[:, cols] = acc_sc[:, cols] / _pick(l0, l1, lanes)
            lse_ref[2 * p] = m_sc[2 * p] + jnp.log(l0)
            lse_ref[2 * p + 1] = m_sc[2 * p + 1] + jnp.log(l1)
            return carry

        for p in range(pairs):
            pair(p, 0)


def _attn_dq(lo_ref, hi_ref, q_ref, k_ref, v_ref, qs_ref, ks_ref, lse_ref, dl_ref, do_ref, dq_ref, acc_sc):
    i = pl.program_id(0)
    j = pl.program_id(1)
    kv = lo_ref[i] + j
    pairs = q_ref.shape[1] // LANES
    bq = q_ref.shape[0]

    @pl.when(j == 0)
    def _():
        acc_sc[...] = jnp.zeros_like(acc_sc)

    @pl.when(kv <= hi_ref[i])
    def _():
        mask = qs_ref[...] == ks_ref[...]
        lanes = _lanes(bq)

        def pair(p, carry):
            cols = pl.ds(p * LANES, LANES)
            q2 = q_ref[:, cols]
            k2 = k_ref[:, cols]
            v2 = v_ref[:, cols]
            do2 = do_ref[:, cols]
            zero = jnp.zeros_like(q2)
            parts = []
            for h in range(2):
                sel = (lambda a: _pick(a, zero, lanes)) if h == 0 else (lambda a: _pick(zero, a, lanes))
                s = _nt(sel(q2), k2)
                e = jnp.where(mask, jnp.exp(s - lse_ref[2 * p + h]), 0.0)
                dp = _nt(sel(do2), v2)
                ds = (e * (dp - dl_ref[2 * p + h])).astype(jnp.bfloat16)
                parts.append(_nn(ds, k2))
            acc_sc[:, cols] += _pick(parts[0], parts[1], lanes)
            return carry

        for p in range(pairs):
            pair(p, 0)

    @pl.when(j == pl.num_programs(1) - 1)
    def _():
        dq_ref[...] = acc_sc[...] * 0.125


def _attn_dkv(lo_ref, hi_ref, q_ref, k_ref, v_ref, qs_ref, ks_ref, lse_ref, dl_ref, do_ref, dk_ref, dv_ref, dk_sc, dv_sc):
    j = pl.program_id(0)
    i = pl.program_id(1)
    qb = lo_ref[j] + i
    pairs = q_ref.shape[1] // LANES
    bq = q_ref.shape[0]
    bk = k_ref.shape[0]

    @pl.when(i == 0)
    def _():
        dk_sc[...] = jnp.zeros_like(dk_sc)
        dv_sc[...] = jnp.zeros_like(dv_sc)

    @pl.when(qb <= hi_ref[j])
    def _():
        mask = qs_ref[...] == ks_ref[...]
        lanes_q = _lanes(bq)
        lanes_k = _lanes(bk)

        def pair(p, carry):
            cols = pl.ds(p * LANES, LANES)
            q2 = q_ref[:, cols]
            k2 = k_ref[:, cols]
            v2 = v_ref[:, cols]
            do2 = do_ref[:, cols]
            zero = jnp.zeros_like(q2)
            dks, dvs = [], []
            for h in range(2):
                sel = (lambda a: _pick(a, zero, lanes_q)) if h == 0 else (lambda a: _pick(zero, a, lanes_q))
                s = _nt(sel(q2), k2)
                e = jnp.where(mask, jnp.exp(s - lse_ref[2 * p + h]), 0.0)
                dp = _nt(sel(do2), v2)
                ds = (e * (dp - dl_ref[2 * p + h])).astype(jnp.bfloat16)
                dvs.append(_tn(e.astype(jnp.bfloat16), do2))
                dks.append(_tn(ds, q2))
            dv_sc[:, cols] += _pick(dvs[0], dvs[1], lanes_k)
            dk_sc[:, cols] += _pick(dks[0], dks[1], lanes_k)
            return carry

        for p in range(pairs):
            pair(p, 0)

    @pl.when(i == pl.num_programs(1) - 1)
    def _():
        dk_ref[...] = dk_sc[...]
        dv_ref[...] = dv_sc[...]


def _clamp(start, step, last):
    return jnp.minimum(start + step, jnp.maximum(last, 0))


def _params():
    return pltpu.CompilerParams(dimension_semantics=("arbitrary", "arbitrary"), vmem_limit_bytes=48 * 1024 * 1024)


def flash_forward(q, k, v, q_ids, k_ids, lo, hi, block_q, block_k, steps):
    nq, width = q.shape
    nk = k.shape[0]
    heads = width // 64
    kv_map = lambda i, j, a, b: (_clamp(a[i], j, b[i]), 0)
    ks_map = lambda i, j, a, b: (0, _clamp(a[i], j, b[i]))
    row = lambda i, j, a, b: (i, 0)
    grid_spec = pltpu.PrefetchScalarGridSpec(
        num_scalar_prefetch=2,
        grid=(nq // block_q, steps),
        in_specs=[
            pl.BlockSpec((block_q, width), row),
            pl.BlockSpec((block_k, width), kv_map),
            pl.BlockSpec((block_k, width), kv_map),
            pl.BlockSpec((block_q, 1), row),
            pl.BlockSpec((1, block_k), ks_map),
        ],
        out_specs=[
            pl.BlockSpec((block_q, width), row),
            pl.BlockSpec((heads, block_q, 1), lambda i, j, a, b: (0, i, 0)),
        ],
        scratch_shapes=[
            pltpu.VMEM((heads, block_q, 1), jnp.float32),
            pltpu.VMEM((heads, block_q, 1), jnp.float32),
            pltpu.VMEM((block_q, width), jnp.float32),
        ],
    )
    return pl.pallas_call(
        _attn_fwd,
        grid_spec=grid_spec,
        out_shape=[jax.ShapeDtypeStruct((nq, width), jnp.float32), jax.ShapeDtypeStruct((heads, nq, 1), jnp.float32)],
        compiler_params=_params(),
    )(lo, hi, q, k, v, q_ids.reshape(nq, 1), k_ids.reshape(1, nk))


def flash_dq(q, k, v, q_ids, k_ids, lse, delta, do, lo, hi, block_q, block_k, steps):
    nq, width = q.shape
    nk = k.shape[0]
    heads = width // 64
    kv_map = lambda i, j, a, b: (_clamp(a[i], j, b[i]), 0)
    ks_map = lambda i, j, a, b: (0, _clamp(a[i], j, b[i]))
    row = lambda i, j, a, b: (i, 0)
    hrow = lambda i, j, a, b: (0, i, 0)
    grid_spec = pltpu.PrefetchScalarGridSpec(
        num_scalar_prefetch=2,
        grid=(nq // block_q, steps),
        in_specs=[
            pl.BlockSpec((block_q, width), row),
            pl.BlockSpec((block_k, width), kv_map),
            pl.BlockSpec((block_k, width), kv_map),
            pl.BlockSpec((block_q, 1), row),
            pl.BlockSpec((1, block_k), ks_map),
            pl.BlockSpec((heads, block_q, 1), hrow),
            pl.BlockSpec((heads, block_q, 1), hrow),
            pl.BlockSpec((block_q, width), row),
        ],
        out_specs=pl.BlockSpec((block_q, width), row),
        scratch_shapes=[pltpu.VMEM((block_q, width), jnp.float32)],
    )
    return pl.pallas_call(
        _attn_dq,
        grid_spec=grid_spec,
        out_shape=jax.ShapeDtypeStruct((nq, width), jnp.float32),
        compiler_params=_params(),
    )(lo, hi, q, k, v, q_ids.reshape(nq, 1), k_ids.reshape(1, nk), lse, delta, do)


def flash_dkv(q, k, v, q_ids, k_ids, lse, delta, do, qlo, qhi, block_q, block_k, steps):
    nq, width = q.shape
    nk = k.shape[0]
    heads = width // 64
    q_map = lambda j, i, a, b: (_clamp(a[j], i, b[j]), 0)
    h_map = lambda j, i, a, b: (0, _clamp(a[j], i, b[j]), 0)
    col = lambda j, i, a, b: (j, 0)
    grid_spec = pltpu.PrefetchScalarGridSpec(
        num_scalar_prefetch=2,
        grid=(nk // block_k, steps),
        in_specs=[
            pl.BlockSpec((block_q, width), q_map),
            pl.BlockSpec((block_k, width), col),
            pl.BlockSpec((block_k, width), col),
            pl.BlockSpec((block_q, 1), q_map),
            pl.BlockSpec((1, block_k), lambda j, i, a, b: (0, j)),
            pl.BlockSpec((heads, block_q, 1), h_map),
            pl.BlockSpec((heads, block_q, 1), h_map),
            pl.BlockSpec((block_q, width), q_map),
        ],
        out_specs=[pl.BlockSpec((block_k, width), col), pl.BlockSpec((block_k, width), col)],
        scratch_shapes=[pltpu.VMEM((block_k, width), jnp.float32), pltpu.VMEM((block_k, width), jnp.float32)],
    )
    return pl.pallas_call(
        _attn_dkv,
        grid_spec=grid_spec,
        out_shape=[jax.ShapeDtypeStruct((nk, width), jnp.float32), jax.ShapeDtypeStruct((nk, width), jnp.float32)],
        compiler_params=_params(),
    )(qlo, qhi, q, k, v, q_ids.reshape(nq, 1), k_ids.reshape(1, nk), lse, delta, do)


def block_ranges(q_ids, k_ids, q_start, q_end, block_q, block_k):
    nq = q_ids.shape[0]
    nk = k_ids.shape[0]
    nqb, nkb = nq // block_q, nk // block_k
    first = q_start.reshape(nqb, block_q)[:, 0]
    last = q_end.reshape(nqb, block_q)[:, block_q - 1]
    lo = jnp.clip(first // block_k, 0, nkb - 1).astype(jnp.int32)
    hi = jnp.clip((last - 1) // block_k, 0, nkb - 1).astype(jnp.int32)
    kb = jnp.arange(nkb, dtype=jnp.int32)
    qb = jnp.arange(nqb, dtype=jnp.int32)
    cover = (lo[:, None] <= kb[None, :]) & (kb[None, :] <= hi[:, None])
    qlo = jnp.min(jnp.where(cover, qb[:, None], nqb), axis=0).astype(jnp.int32)
    qhi = jnp.max(jnp.where(cover, qb[:, None], -1), axis=0).astype(jnp.int32)
    return lo, hi, qlo, qhi


def norm_forward(values, gain, shift):
    center = jnp.mean(values, axis=-1, keepdims=True)
    offsets = values - center
    spread = jnp.mean(offsets * offsets, axis=-1, keepdims=True)
    inverse = lax.rsqrt(spread + 1e-06)
    normed = offsets * inverse
    return (normed * gain + shift, normed, inverse)


def norm_backward(grad_y, normed, inverse, gain):
    grad_normed = grad_y * gain
    mean_one = jnp.mean(grad_normed, axis=-1, keepdims=True)
    mean_two = jnp.mean(grad_normed * normed, axis=-1, keepdims=True)
    return inverse * (grad_normed - mean_one - normed * mean_two)


def activate(values):
    return jax.nn.gelu(values, approximate=False)


def contract_last(left, right):
    return lax.dot_general(left, right, (((1,), (1,)), ((), ())), preferred_element_type=jnp.float32)


def contract_first(left, right):
    return lax.dot_general(left, right, (((0,), (0,)), ((), ())), preferred_element_type=jnp.float32)


def column_sum(values):
    return jnp.sum(values.astype(jnp.float32), axis=0)


def group_segments(lengths, dealing, group_index, group_rows, per_group):
    picked = lax.dynamic_slice_in_dim(dealing, group_index * per_group, per_group)
    match = picked[:, None] == jnp.arange(lengths.shape[0], dtype=jnp.int32)[None, :]
    chosen = jnp.sum(jnp.where(match, lengths[None, :], 0), axis=1)
    ends = jnp.cumsum(chosen)
    starts = ends - chosen
    places = jnp.arange(group_rows, dtype=jnp.int32)
    segment_ids = jnp.sum((places[:, None] >= ends[None, :]).astype(jnp.int32), axis=1)
    return (segment_ids, starts, ends)


def cyclic_pieces(piece):
    count = lax.axis_size("tensor")
    me = lax.axis_index("tensor")
    got = [piece]
    for k in range(1, count):
        got.append(lax.ppermute(piece, "tensor", [(s, (s + k) % count) for s in range(count)]))
    order = (me - jnp.arange(count, dtype=jnp.int32)) % count
    return jnp.take(jnp.stack(got), order, axis=0)


def gather_weights(blocks):
    count = lax.axis_size("tensor")
    widths = [b.shape[1] for b in blocks]
    piece = jnp.concatenate(blocks, axis=1)
    parts = cyclic_pieces(piece)
    cols, at = [], 0
    for w in widths:
        cols.extend(parts[t, :, at:at + w] for t in range(count))
        at += w
    strip = jnp.concatenate(cols, axis=1)
    full = lax.all_gather(strip, "dp", axis=0, tiled=True)
    out, at = [], 0
    for w in widths:
        out.append(full[:, at:at + w * count])
        at += w * count
    return out


def vector_rows(v, rows):
    dp = lax.axis_size("dp")
    slab = rows // dp
    spread = v.reshape(dp, 1, -1)
    return jnp.pad(spread, ((0, 0), (0, slab - 1), (0, 0))).reshape(rows, -1)


def pack_grads(grads, vectors):
    count = lax.axis_size("tensor")
    me = lax.axis_index("tensor")
    rows = grads[0].shape[0]
    mats = [g.astype(jnp.bfloat16) for g in grads] + [vector_rows(v.astype(jnp.bfloat16), rows) for v in vectors]
    widths = [m.shape[1] // count for m in mats]
    cat = jnp.concatenate(mats, axis=1)
    return widths, cat


def reduce_dp(cat):
    return lax.psum_scatter(cat, "dp", scatter_dimension=0, tiled=True)


def reduce_dp_by_halves(cat):
    dp = lax.axis_size("dp")
    me = lax.axis_index("dp")
    slab = cat.shape[0] // dp
    part = cat.astype(jnp.float32).reshape(dp, slab, cat.shape[1])
    bit = 0
    while (1 << bit) < dp:
        mine = (me >> bit) % 2
        halves = part.reshape(part.shape[0] // 2, 2, slab, cat.shape[1])
        keep = lax.dynamic_index_in_dim(halves, mine, axis=1, keepdims=False)
        send = lax.dynamic_index_in_dim(halves, 1 - mine, axis=1, keepdims=False)
        pairs = [(i, i ^ (1 << bit)) for i in range(dp)]
        part = keep + lax.ppermute(send.astype(jnp.bfloat16), "dp", pairs).astype(jnp.float32)
        bit += 1
    return part.reshape(slab, cat.shape[1])


def reduce_tensor(strip, widths, n_grads):
    count = lax.axis_size("tensor")
    me = lax.axis_index("tensor")
    strip = strip.astype(jnp.float32)
    per_t = []
    for t in range(count):
        at, cols = 0, []
        for w in widths:
            cols.append(strip[:, at + t * w:at + (t + 1) * w])
            at += w * count
        per_t.append(jnp.concatenate(cols, axis=1))
    stacked = jnp.stack(per_t)
    total = jnp.take(stacked, me, axis=0)
    for k in range(1, count):
        send = jnp.take(stacked, (me + k) % count, axis=0)
        got = lax.ppermute(send.astype(jnp.bfloat16), "tensor", [(s, (s + k) % count) for s in range(count)])
        total = total + got.astype(jnp.float32)
    out, at = [], 0
    for i, w in enumerate(widths):
        block = total[:, at:at + w]
        at += w
        out.append(block if i < n_grads else block[0])
    return out


def halo_plan(rows):
    hops = -(-LONGEST // rows)
    takes = [rows] * (hops - 1) + [LONGEST - rows * (hops - 1)]
    return takes


def shift_rows(values, distance, count):
    if distance >= count:
        return jnp.zeros_like(values)
    if distance > 0:
        pairs = [(s, s + distance) for s in range(count - distance)]
    else:
        pairs = [(s - distance, s) for s in range(count + distance)]
    return lax.ppermute(values, "tensor", pairs)


def build_window(own, takes, count):
    rows = own.shape[0]
    left = [shift_rows(own[rows - take:], d + 1, count) for d, take in enumerate(takes)]
    right = [shift_rows(own[:take], -(d + 1), count) for d, take in enumerate(takes)]
    return jnp.concatenate(left[::-1] + [own] + right, axis=0)


def return_window(values, takes, count):
    rows = values.shape[0] - 2 * LONGEST
    total = values[LONGEST:LONGEST + rows]
    at = LONGEST
    for d, take in enumerate(takes):
        piece = values[at - take:at].astype(jnp.bfloat16)
        at -= take
        back = shift_rows(piece, -(d + 1), count).astype(jnp.float32)
        total = total + jnp.pad(back, ((rows - take, 0), (0, 0)))
    at = LONGEST + rows
    for d, take in enumerate(takes):
        piece = values[at:at + take].astype(jnp.bfloat16)
        at += take
        back = shift_rows(piece, d + 1, count).astype(jnp.float32)
        total = total + jnp.pad(back, ((0, rows - take), (0, 0)))
    return total


def to_heads(values):
    rows, width = values.shape
    return values.reshape(rows, width // HEAD_DIM, HEAD_DIM).transpose(1, 0, 2)


def from_heads(values):
    heads, rows, hd = values.shape
    return values.transpose(1, 0, 2).reshape(rows, heads * hd)


def shards(tokens, lengths, dealing, w_query, w_key, w_value, w_out, w_inner, w_outer, b_query, b_value, b_out, b_inner, b_outer, gain_attn, shift_attn, gain_ffn, shift_ffn, grad_out):
    count = lax.axis_size("tensor")
    tens_index = lax.axis_index("tensor")
    group_index = lax.axis_index("dp")
    rows = tokens.shape[0]
    group_rows = rows * count
    per_group = lengths.shape[0] // lax.axis_size("dp")
    takes = halo_plan(rows)
    window = rows + 2 * LONGEST
    seg, starts, ends = group_segments(lengths, dealing, group_index, group_rows, per_group)
    base = rows * tens_index - LONGEST
    places = base + jnp.arange(window, dtype=jnp.int32)
    valid = (places >= 0) & (places < group_rows)
    k_ids = jnp.where(valid, jnp.sum((places[:, None] >= ends[None, :]).astype(jnp.int32), axis=1), -1).astype(jnp.int32)
    q_ids = lax.dynamic_slice_in_dim(seg, rows * tens_index, rows)
    q_start = jnp.take(starts, q_ids) - base
    q_end = jnp.take(ends, q_ids) - base
    lo, hi, qlo, qhi = block_ranges(q_ids, k_ids, q_start, q_end, BLOCK, BLOCK)
    nkb = window // BLOCK
    kv_steps = min(nkb, (BLOCK + 2 * (LONGEST - 1)) // BLOCK + 2)
    q_steps = rows // BLOCK

    wq, wk, wv = gather_weights([w_query, w_key, w_value])
    wo_t, wi, wf_t = gather_weights([w_out.T, w_inner, w_outer.T])
    gain_one = gain_attn.astype(jnp.float32)
    gain_two = gain_ffn.astype(jnp.float32)

    x_own = tokens
    x_win = build_window(tokens, takes, count)
    query = (jnp.dot(x_own, wq, preferred_element_type=jnp.float32) + b_query.astype(jnp.float32)).astype(jnp.bfloat16)
    key_w = jnp.dot(x_win, wk, preferred_element_type=jnp.float32).astype(jnp.bfloat16)
    value_w = (jnp.dot(x_win, wv, preferred_element_type=jnp.float32) + b_value.astype(jnp.float32)).astype(jnp.bfloat16)
    scaled = query * jnp.asarray(1.0 / math.sqrt(HEAD_DIM), jnp.bfloat16)
    ctx32, lse = flash_forward(scaled, key_w, value_w, q_ids, k_ids, lo, hi, BLOCK, BLOCK, kv_steps)
    context = ctx32.astype(jnp.bfloat16)
    attn = contract_last(context, wo_t) + b_out.astype(jnp.float32)
    hidden, norm_one, inverse_one = norm_forward(tokens.astype(jnp.float32) + attn, gain_one, shift_attn.astype(jnp.float32))
    hidden_low = hidden.astype(jnp.bfloat16)
    pre_act = jnp.dot(hidden_low, wi, preferred_element_type=jnp.float32) + b_inner.astype(jnp.float32)
    act = activate(pre_act).astype(jnp.bfloat16)
    ffn = contract_last(act, wf_t) + b_outer.astype(jnp.float32)
    output, norm_two, inverse_two = norm_forward(hidden + ffn, gain_two, shift_ffn.astype(jnp.float32))

    grad_y = grad_out.astype(jnp.float32)
    grad_resid_two = norm_backward(grad_y, norm_two, inverse_two, gain_two)
    grad_ffn = grad_resid_two.astype(jnp.bfloat16)
    grad_outer_t = contract_first(grad_ffn, act)
    grad_act = jnp.dot(grad_ffn, wf_t, preferred_element_type=jnp.float32)
    unused, gelu_pull = jax.vjp(activate, pre_act)
    grad_pre = gelu_pull(grad_act)[0].astype(jnp.bfloat16)
    grad_inner_w = contract_first(hidden_low, grad_pre)
    grad_hidden = grad_resid_two + contract_last(grad_pre, wi)
    grad_resid_one = norm_backward(grad_hidden, norm_one, inverse_one, gain_one)
    grad_attn = grad_resid_one.astype(jnp.bfloat16)
    grad_out_t = contract_first(grad_attn, context)
    grad_context = jnp.dot(grad_attn, wo_t, preferred_element_type=jnp.float32).astype(jnp.bfloat16)
    late = [
        column_sum(grad_attn),
        column_sum(grad_pre),
        column_sum(grad_ffn),
        jnp.sum(grad_hidden * norm_one, axis=0),
        jnp.sum(grad_hidden, axis=0),
        jnp.sum(grad_y * norm_two, axis=0),
        jnp.sum(grad_y, axis=0),
    ]
    early_widths, early_cat = pack_grads([grad_out_t, grad_inner_w, grad_outer_t], late)
    grad_context, early_cat = lax.optimization_barrier((grad_context, early_cat))
    early_strip = reduce_dp(early_cat)
    heads = query.shape[1] // HEAD_DIM
    delta = jnp.sum((grad_context.astype(jnp.float32) * ctx32).reshape(rows, heads, HEAD_DIM), axis=-1)
    delta = delta.T.reshape(heads, rows, 1)
    dq_h = flash_dq(scaled, key_w, value_w, q_ids, k_ids, lse, delta, grad_context, lo, hi, BLOCK, BLOCK, kv_steps)
    dk_h, dv_h = flash_dkv(scaled, key_w, value_w, q_ids, k_ids, lse, delta, grad_context, qlo, qhi, BLOCK, BLOCK, q_steps)
    early_strip, dq_h, dk_h, dv_h = lax.optimization_barrier((early_strip, dq_h, dk_h, dv_h))
    early_sums = reduce_tensor(early_strip, early_widths, 3)
    g_out_t, g_inner, g_outer_t = early_sums[:3]
    late = early_sums[3:]
    grad_query = dq_h.astype(jnp.bfloat16)
    grad_key = dk_h.astype(jnp.bfloat16)
    grad_value = dv_h.astype(jnp.bfloat16)
    grad_query_w = contract_first(x_own, grad_query)
    grad_key_w = contract_first(x_win, grad_key)
    grad_value_w = contract_first(x_win, grad_value)
    grad_win = contract_last(grad_key, wk) + contract_last(grad_value, wv)
    grad_tokens = grad_resid_one + contract_last(grad_query, wq) + return_window(grad_win, takes, count)

    late_widths, late_cat = pack_grads(
        [grad_query_w, grad_key_w, grad_value_w], [column_sum(grad_query), column_sum(grad_value)]
    )
    g_query, g_key, g_value, g_bq, g_bv = reduce_tensor(reduce_dp_by_halves(late_cat), late_widths, 3)
    summed = (g_query, g_key, g_value, g_out_t.T, g_inner, g_outer_t.T)
    small = [g_bq, g_bv] + late
    return (output.astype(jnp.bfloat16), grad_tokens) + summed + tuple(small)


def solution(mesh):
    rows = P(("dp", "tensor"), None)
    vec = P(("dp", "tensor"))
    return jax.shard_map(
        shards,
        mesh=mesh,
        in_specs=(rows, P(), P(), P("dp", "tensor"), P("dp", "tensor"), P("dp", "tensor"), P("tensor", "dp"), P("dp", "tensor"), P("tensor", "dp"), P(), P(), P(), P(), P(), P(), P(), P(), P(), rows),
        out_specs=(rows, rows, P("dp", "tensor"), P("dp", "tensor"), P("dp", "tensor"), P("tensor", "dp"), P("dp", "tensor"), P("tensor", "dp")) + (vec,) * 9,
        check_vma=False,
    )
```

```python
import math

import jax
import jax.numpy as jnp
from jax import lax
from jax.experimental import pallas as pl
from jax.experimental.pallas import tpu as pltpu
from jax.sharding import PartitionSpec as P

HEAD_DIM = 64
LONGEST = 1024
BLOCK = 256

NEG = -1e30
LANES = 128


def _lanes(rows):
    return lax.broadcasted_iota(jnp.int32, (rows, LANES), 1) < LANES // 2


def _pick(first, second, lanes):
    return jnp.where(lanes, first, second)


def _nt(a, b):
    return lax.dot_general(a, b, (((1,), (1,)), ((), ())), preferred_element_type=jnp.float32)


def _tn(a, b):
    return lax.dot_general(a, b, (((0,), (0,)), ((), ())), preferred_element_type=jnp.float32)


def _nn(a, b):
    return lax.dot_general(a, b, (((1,), (0,)), ((), ())), preferred_element_type=jnp.float32)


def _attn_fwd(lo_ref, hi_ref, q_ref, k_ref, v_ref, qs_ref, ks_ref, o_ref, lse_ref, m_sc, l_sc, acc_sc):
    i = pl.program_id(0)
    j = pl.program_id(1)
    kv = lo_ref[i] + j
    pairs = q_ref.shape[1] // LANES
    bq = q_ref.shape[0]

    @pl.when(j == 0)
    def _():
        m_sc[...] = jnp.full_like(m_sc, NEG)
        l_sc[...] = jnp.zeros_like(l_sc)
        acc_sc[...] = jnp.zeros_like(acc_sc)

    @pl.when(kv <= hi_ref[i])
    def _():
        mask = qs_ref[...] == ks_ref[...]
        lanes = _lanes(bq)

        def pair(p, carry):
            cols = pl.ds(p * LANES, LANES)
            q2 = q_ref[:, cols]
            k2 = k_ref[:, cols]
            v2 = v_ref[:, cols]
            zero = jnp.zeros_like(q2)
            alphas, pvs = [], []
            for h in range(2):
                hq = _pick(q2, zero, lanes) if h == 0 else _pick(zero, q2, lanes)
                s = jnp.where(mask, _nt(hq, k2), NEG)
                m_old = m_sc[2 * p + h]
                m_new = jnp.maximum(m_old, jnp.max(s, axis=-1, keepdims=True))
                alpha = jnp.exp(m_old - m_new)
                e = jnp.exp(s - m_new)
                l_sc[2 * p + h] = alpha * l_sc[2 * p + h] + jnp.sum(e, axis=-1, keepdims=True)
                m_sc[2 * p + h] = m_new
                alphas.append(alpha)
                pvs.append(_nn(e.astype(jnp.bfloat16), v2))
            acc_sc[:, cols] = _pick(alphas[0], alphas[1], lanes) * acc_sc[:, cols] + _pick(pvs[0], pvs[1], lanes)
            return carry

        for p in range(pairs):
            pair(p, 0)

    @pl.when(j == pl.num_programs(1) - 1)
    def _():
        lanes = _lanes(bq)

        def pair(p, carry):
            cols = pl.ds(p * LANES, LANES)
            l0, l1 = l_sc[2 * p], l_sc[2 * p + 1]
            o_ref[:, cols] = acc_sc[:, cols] / _pick(l0, l1, lanes)
            lse_ref[2 * p] = m_sc[2 * p] + jnp.log(l0)
            lse_ref[2 * p + 1] = m_sc[2 * p + 1] + jnp.log(l1)
            return carry

        for p in range(pairs):
            pair(p, 0)


def _attn_dq(lo_ref, hi_ref, q_ref, k_ref, v_ref, qs_ref, ks_ref, lse_ref, dl_ref, do_ref, dq_ref, acc_sc):
    i = pl.program_id(0)
    j = pl.program_id(1)
    kv = lo_ref[i] + j
    pairs = q_ref.shape[1] // LANES
    bq = q_ref.shape[0]

    @pl.when(j == 0)
    def _():
        acc_sc[...] = jnp.zeros_like(acc_sc)

    @pl.when(kv <= hi_ref[i])
    def _():
        mask = qs_ref[...] == ks_ref[...]
        lanes = _lanes(bq)

        def pair(p, carry):
            cols = pl.ds(p * LANES, LANES)
            q2 = q_ref[:, cols]
            k2 = k_ref[:, cols]
            v2 = v_ref[:, cols]
            do2 = do_ref[:, cols]
            zero = jnp.zeros_like(q2)
            parts = []
            for h in range(2):
                sel = (lambda a: _pick(a, zero, lanes)) if h == 0 else (lambda a: _pick(zero, a, lanes))
                s = _nt(sel(q2), k2)
                e = jnp.where(mask, jnp.exp(s - lse_ref[2 * p + h]), 0.0)
                dp = _nt(sel(do2), v2)
                ds = (e * (dp - dl_ref[2 * p + h])).astype(jnp.bfloat16)
                parts.append(_nn(ds, k2))
            acc_sc[:, cols] += _pick(parts[0], parts[1], lanes)
            return carry

        for p in range(pairs):
            pair(p, 0)

    @pl.when(j == pl.num_programs(1) - 1)
    def _():
        dq_ref[...] = acc_sc[...] * 0.125


def _attn_dkv(lo_ref, hi_ref, q_ref, k_ref, v_ref, qs_ref, ks_ref, lse_ref, dl_ref, do_ref, dk_ref, dv_ref, dk_sc, dv_sc):
    j = pl.program_id(0)
    i = pl.program_id(1)
    qb = lo_ref[j] + i
    pairs = q_ref.shape[1] // LANES
    bq = q_ref.shape[0]
    bk = k_ref.shape[0]

    @pl.when(i == 0)
    def _():
        dk_sc[...] = jnp.zeros_like(dk_sc)
        dv_sc[...] = jnp.zeros_like(dv_sc)

    @pl.when(qb <= hi_ref[j])
    def _():
        mask = qs_ref[...] == ks_ref[...]
        lanes_q = _lanes(bq)
        lanes_k = _lanes(bk)

        def pair(p, carry):
            cols = pl.ds(p * LANES, LANES)
            q2 = q_ref[:, cols]
            k2 = k_ref[:, cols]
            v2 = v_ref[:, cols]
            do2 = do_ref[:, cols]
            zero = jnp.zeros_like(q2)
            dks, dvs = [], []
            for h in range(2):
                sel = (lambda a: _pick(a, zero, lanes_q)) if h == 0 else (lambda a: _pick(zero, a, lanes_q))
                s = _nt(sel(q2), k2)
                e = jnp.where(mask, jnp.exp(s - lse_ref[2 * p + h]), 0.0)
                dp = _nt(sel(do2), v2)
                ds = (e * (dp - dl_ref[2 * p + h])).astype(jnp.bfloat16)
                dvs.append(_tn(e.astype(jnp.bfloat16), do2))
                dks.append(_tn(ds, q2))
            dv_sc[:, cols] += _pick(dvs[0], dvs[1], lanes_k)
            dk_sc[:, cols] += _pick(dks[0], dks[1], lanes_k)
            return carry

        for p in range(pairs):
            pair(p, 0)

    @pl.when(i == pl.num_programs(1) - 1)
    def _():
        dk_ref[...] = dk_sc[...]
        dv_ref[...] = dv_sc[...]


def _attn_bwd(lo_ref, hi_ref, q_ref, k_ref, v_ref, qs_ref, ks_ref, lse_ref, dl_ref, do_ref, dk_ref, dv_ref, dq_ref, dk_sc, dv_sc):
    j = pl.program_id(0)
    i = pl.program_id(1)
    qb = lo_ref[j] + i
    pairs = q_ref.shape[1] // LANES
    bq = q_ref.shape[0]
    bk = k_ref.shape[0]

    @pl.when((j == 0) & (i == 0))
    def _():
        dq_ref[...] = jnp.zeros_like(dq_ref)

    @pl.when(i == 0)
    def _():
        dk_sc[...] = jnp.zeros_like(dk_sc)
        dv_sc[...] = jnp.zeros_like(dv_sc)

    @pl.when(qb <= hi_ref[j])
    def _():
        mask = qs_ref[...] == ks_ref[...]
        lanes_q = _lanes(bq)
        lanes_k = _lanes(bk)
        rows = pl.ds(pl.multiple_of(qb * bq, bq), bq)
        for p in range(pairs):
            cols = pl.ds(p * LANES, LANES)
            q2 = q_ref[:, cols]
            k2 = k_ref[:, cols]
            v2 = v_ref[:, cols]
            do2 = do_ref[:, cols]
            zero = jnp.zeros_like(q2)
            dks, dvs, dqs = [], [], []
            for h in range(2):
                sel = (lambda a: _pick(a, zero, lanes_q)) if h == 0 else (lambda a: _pick(zero, a, lanes_q))
                s = _nt(sel(q2), k2)
                e = jnp.where(mask, jnp.exp(s - lse_ref[2 * p + h]), 0.0)
                dp = _nt(sel(do2), v2)
                ds = (e * (dp - dl_ref[2 * p + h])).astype(jnp.bfloat16)
                dvs.append(_tn(e.astype(jnp.bfloat16), do2))
                dks.append(_tn(ds, q2))
                dqs.append(_nn(ds, k2))
            dv_sc[:, cols] += _pick(dvs[0], dvs[1], lanes_k)
            dk_sc[:, cols] += _pick(dks[0], dks[1], lanes_k)
            dq_ref[rows, cols] += _pick(dqs[0], dqs[1], lanes_q)

    @pl.when(i == pl.num_programs(1) - 1)
    def _():
        dk_ref[...] = dk_sc[...]
        dv_ref[...] = dv_sc[...]

    @pl.when((i == pl.num_programs(1) - 1) & (j == pl.num_programs(0) - 1))
    def _():
        dq_ref[...] = dq_ref[...] * 0.125


def _clamp(start, step, last):
    return jnp.minimum(start + step, jnp.maximum(last, 0))


def _params():
    return pltpu.CompilerParams(dimension_semantics=("arbitrary", "arbitrary"), vmem_limit_bytes=48 * 1024 * 1024)


def flash_forward(q, k, v, q_ids, k_ids, lo, hi, block_q, block_k, steps):
    nq, width = q.shape
    nk = k.shape[0]
    heads = width // 64
    kv_map = lambda i, j, a, b: (_clamp(a[i], j, b[i]), 0)
    ks_map = lambda i, j, a, b: (0, _clamp(a[i], j, b[i]))
    row = lambda i, j, a, b: (i, 0)
    grid_spec = pltpu.PrefetchScalarGridSpec(
        num_scalar_prefetch=2,
        grid=(nq // block_q, steps),
        in_specs=[
            pl.BlockSpec((block_q, width), row),
            pl.BlockSpec((block_k, width), kv_map),
            pl.BlockSpec((block_k, width), kv_map),
            pl.BlockSpec((block_q, 1), row),
            pl.BlockSpec((1, block_k), ks_map),
        ],
        out_specs=[
            pl.BlockSpec((block_q, width), row),
            pl.BlockSpec((heads, block_q, 1), lambda i, j, a, b: (0, i, 0)),
        ],
        scratch_shapes=[
            pltpu.VMEM((heads, block_q, 1), jnp.float32),
            pltpu.VMEM((heads, block_q, 1), jnp.float32),
            pltpu.VMEM((block_q, width), jnp.float32),
        ],
    )
    return pl.pallas_call(
        _attn_fwd,
        grid_spec=grid_spec,
        out_shape=[jax.ShapeDtypeStruct((nq, width), jnp.float32), jax.ShapeDtypeStruct((heads, nq, 1), jnp.float32)],
        compiler_params=_params(),
    )(lo, hi, q, k, v, q_ids.reshape(nq, 1), k_ids.reshape(1, nk))


def flash_dq(q, k, v, q_ids, k_ids, lse, delta, do, lo, hi, block_q, block_k, steps):
    nq, width = q.shape
    nk = k.shape[0]
    heads = width // 64
    kv_map = lambda i, j, a, b: (_clamp(a[i], j, b[i]), 0)
    ks_map = lambda i, j, a, b: (0, _clamp(a[i], j, b[i]))
    row = lambda i, j, a, b: (i, 0)
    hrow = lambda i, j, a, b: (0, i, 0)
    grid_spec = pltpu.PrefetchScalarGridSpec(
        num_scalar_prefetch=2,
        grid=(nq // block_q, steps),
        in_specs=[
            pl.BlockSpec((block_q, width), row),
            pl.BlockSpec((block_k, width), kv_map),
            pl.BlockSpec((block_k, width), kv_map),
            pl.BlockSpec((block_q, 1), row),
            pl.BlockSpec((1, block_k), ks_map),
            pl.BlockSpec((heads, block_q, 1), hrow),
            pl.BlockSpec((heads, block_q, 1), hrow),
            pl.BlockSpec((block_q, width), row),
        ],
        out_specs=pl.BlockSpec((block_q, width), row),
        scratch_shapes=[pltpu.VMEM((block_q, width), jnp.float32)],
    )
    return pl.pallas_call(
        _attn_dq,
        grid_spec=grid_spec,
        out_shape=jax.ShapeDtypeStruct((nq, width), jnp.float32),
        compiler_params=_params(),
    )(lo, hi, q, k, v, q_ids.reshape(nq, 1), k_ids.reshape(1, nk), lse, delta, do)


def flash_dkv(q, k, v, q_ids, k_ids, lse, delta, do, qlo, qhi, block_q, block_k, steps):
    nq, width = q.shape
    nk = k.shape[0]
    heads = width // 64
    q_map = lambda j, i, a, b: (_clamp(a[j], i, b[j]), 0)
    h_map = lambda j, i, a, b: (0, _clamp(a[j], i, b[j]), 0)
    col = lambda j, i, a, b: (j, 0)
    grid_spec = pltpu.PrefetchScalarGridSpec(
        num_scalar_prefetch=2,
        grid=(nk // block_k, steps),
        in_specs=[
            pl.BlockSpec((block_q, width), q_map),
            pl.BlockSpec((block_k, width), col),
            pl.BlockSpec((block_k, width), col),
            pl.BlockSpec((block_q, 1), q_map),
            pl.BlockSpec((1, block_k), lambda j, i, a, b: (0, j)),
            pl.BlockSpec((heads, block_q, 1), h_map),
            pl.BlockSpec((heads, block_q, 1), h_map),
            pl.BlockSpec((block_q, width), q_map),
        ],
        out_specs=[pl.BlockSpec((block_k, width), col), pl.BlockSpec((block_k, width), col)],
        scratch_shapes=[pltpu.VMEM((block_k, width), jnp.float32), pltpu.VMEM((block_k, width), jnp.float32)],
    )
    return pl.pallas_call(
        _attn_dkv,
        grid_spec=grid_spec,
        out_shape=[jax.ShapeDtypeStruct((nk, width), jnp.float32), jax.ShapeDtypeStruct((nk, width), jnp.float32)],
        compiler_params=_params(),
    )(qlo, qhi, q, k, v, q_ids.reshape(nq, 1), k_ids.reshape(1, nk), lse, delta, do)


def flash_backward(q, k, v, q_ids, k_ids, lse, delta, do, qlo, qhi, block_q, block_k, steps):
    nq, width = q.shape
    nk = k.shape[0]
    heads = width // 64
    q_map = lambda j, i, a, b: (_clamp(a[j], i, b[j]), 0)
    h_map = lambda j, i, a, b: (0, _clamp(a[j], i, b[j]), 0)
    col = lambda j, i, a, b: (j, 0)
    grid_spec = pltpu.PrefetchScalarGridSpec(
        num_scalar_prefetch=2,
        grid=(nk // block_k, steps),
        in_specs=[
            pl.BlockSpec((block_q, width), q_map),
            pl.BlockSpec((block_k, width), col),
            pl.BlockSpec((block_k, width), col),
            pl.BlockSpec((block_q, 1), q_map),
            pl.BlockSpec((1, block_k), lambda j, i, a, b: (0, j)),
            pl.BlockSpec((heads, block_q, 1), h_map),
            pl.BlockSpec((heads, block_q, 1), h_map),
            pl.BlockSpec((block_q, width), q_map),
        ],
        out_specs=[
            pl.BlockSpec((block_k, width), col),
            pl.BlockSpec((block_k, width), col),
            pl.BlockSpec((nq, width), lambda j, i, a, b: (0, 0)),
        ],
        scratch_shapes=[pltpu.VMEM((block_k, width), jnp.float32), pltpu.VMEM((block_k, width), jnp.float32)],
    )
    return pl.pallas_call(
        _attn_bwd,
        grid_spec=grid_spec,
        out_shape=[
            jax.ShapeDtypeStruct((nk, width), jnp.float32),
            jax.ShapeDtypeStruct((nk, width), jnp.float32),
            jax.ShapeDtypeStruct((nq, width), jnp.float32),
        ],
        compiler_params=_params(),
    )(qlo, qhi, q, k, v, q_ids.reshape(nq, 1), k_ids.reshape(1, nk), lse, delta, do)


def block_ranges(q_ids, k_ids, q_start, q_end, block_q, block_k):
    nq = q_ids.shape[0]
    nk = k_ids.shape[0]
    nqb, nkb = nq // block_q, nk // block_k
    first = q_start.reshape(nqb, block_q)[:, 0]
    last = q_end.reshape(nqb, block_q)[:, block_q - 1]
    lo = jnp.clip(first // block_k, 0, nkb - 1).astype(jnp.int32)
    hi = jnp.clip((last - 1) // block_k, 0, nkb - 1).astype(jnp.int32)
    kb = jnp.arange(nkb, dtype=jnp.int32)
    qb = jnp.arange(nqb, dtype=jnp.int32)
    cover = (lo[:, None] <= kb[None, :]) & (kb[None, :] <= hi[:, None])
    qlo = jnp.min(jnp.where(cover, qb[:, None], nqb), axis=0).astype(jnp.int32)
    qhi = jnp.max(jnp.where(cover, qb[:, None], -1), axis=0).astype(jnp.int32)
    return lo, hi, qlo, qhi


def norm_forward(values, gain, shift):
    center = jnp.mean(values, axis=-1, keepdims=True)
    offsets = values - center
    spread = jnp.mean(offsets * offsets, axis=-1, keepdims=True)
    inverse = lax.rsqrt(spread + 1e-06)
    normed = offsets * inverse
    return (normed * gain + shift, normed, inverse)


def norm_backward(grad_y, normed, inverse, gain):
    grad_normed = grad_y * gain
    mean_one = jnp.mean(grad_normed, axis=-1, keepdims=True)
    mean_two = jnp.mean(grad_normed * normed, axis=-1, keepdims=True)
    return inverse * (grad_normed - mean_one - normed * mean_two)


def activate(values):
    return jax.nn.gelu(values, approximate=False)


def contract_last(left, right):
    return lax.dot_general(left, right, (((1,), (1,)), ((), ())), preferred_element_type=jnp.float32)


def contract_first(left, right):
    return lax.dot_general(left, right, (((0,), (0,)), ((), ())), preferred_element_type=jnp.float32)


def column_sum(values):
    return jnp.sum(values.astype(jnp.float32), axis=0)


def group_segments(lengths, dealing, group_index, group_rows, per_group):
    picked = lax.dynamic_slice_in_dim(dealing, group_index * per_group, per_group)
    match = picked[:, None] == jnp.arange(lengths.shape[0], dtype=jnp.int32)[None, :]
    chosen = jnp.sum(jnp.where(match, lengths[None, :], 0), axis=1)
    ends = jnp.cumsum(chosen)
    starts = ends - chosen
    places = jnp.arange(group_rows, dtype=jnp.int32)
    segment_ids = jnp.sum((places[:, None] >= ends[None, :]).astype(jnp.int32), axis=1)
    return (segment_ids, starts, ends)


def cyclic_pieces(piece):
    count = lax.axis_size("tensor")
    me = lax.axis_index("tensor")
    got = [piece]
    for k in range(1, count):
        got.append(lax.ppermute(piece, "tensor", [(s, (s + k) % count) for s in range(count)]))
    order = (me - jnp.arange(count, dtype=jnp.int32)) % count
    return jnp.take(jnp.stack(got), order, axis=0)


def gather_weights(blocks):
    count = lax.axis_size("tensor")
    widths = [b.shape[1] for b in blocks]
    piece = jnp.concatenate(blocks, axis=1)
    parts = cyclic_pieces(piece)
    cols, at = [], 0
    for w in widths:
        cols.extend(parts[t, :, at:at + w] for t in range(count))
        at += w
    strip = jnp.concatenate(cols, axis=1)
    full = lax.all_gather(strip, "dp", axis=0, tiled=True)
    out, at = [], 0
    for w in widths:
        out.append(full[:, at:at + w * count])
        at += w * count
    return out


def vector_rows(v, rows):
    dp = lax.axis_size("dp")
    slab = rows // dp
    spread = v.reshape(dp, 1, -1)
    return jnp.pad(spread, ((0, 0), (0, slab - 1), (0, 0))).reshape(rows, -1)


def pack_grads(grads, vectors):
    count = lax.axis_size("tensor")
    me = lax.axis_index("tensor")
    rows = grads[0].shape[0]
    mats = [g.astype(jnp.bfloat16) for g in grads] + [vector_rows(v.astype(jnp.bfloat16), rows) for v in vectors]
    widths = [m.shape[1] // count for m in mats]
    cat = jnp.concatenate(mats, axis=1)
    return widths, cat


def reduce_dp(cat):
    return lax.psum_scatter(cat, "dp", scatter_dimension=0, tiled=True)


def reduce_dp_by_halves(cat):
    dp = lax.axis_size("dp")
    me = lax.axis_index("dp")
    slab = cat.shape[0] // dp
    part = cat.astype(jnp.float32).reshape(dp, slab, cat.shape[1])
    bit = 0
    while (1 << bit) < dp:
        mine = (me >> bit) % 2
        halves = part.reshape(part.shape[0] // 2, 2, slab, cat.shape[1])
        keep = lax.dynamic_index_in_dim(halves, mine, axis=1, keepdims=False)
        send = lax.dynamic_index_in_dim(halves, 1 - mine, axis=1, keepdims=False)
        pairs = [(i, i ^ (1 << bit)) for i in range(dp)]
        part = keep + lax.ppermute(send.astype(jnp.bfloat16), "dp", pairs).astype(jnp.float32)
        bit += 1
    return part.reshape(slab, cat.shape[1])


def reduce_tensor(strip, widths, n_grads):
    count = lax.axis_size("tensor")
    me = lax.axis_index("tensor")
    strip = strip.astype(jnp.float32)
    per_t = []
    for t in range(count):
        at, cols = 0, []
        for w in widths:
            cols.append(strip[:, at + t * w:at + (t + 1) * w])
            at += w * count
        per_t.append(jnp.concatenate(cols, axis=1))
    stacked = jnp.stack(per_t)
    total = jnp.take(stacked, me, axis=0)
    for k in range(1, count):
        send = jnp.take(stacked, (me + k) % count, axis=0)
        total = total + lax.ppermute(send, "tensor", [(s, (s + k) % count) for s in range(count)])
    out, at = [], 0
    for i, w in enumerate(widths):
        block = total[:, at:at + w]
        at += w
        out.append(block if i < n_grads else block[0])
    return out


def halo_plan(rows):
    hops = -(-LONGEST // rows)
    takes = [rows] * (hops - 1) + [LONGEST - rows * (hops - 1)]
    return takes


def shift_rows(values, distance, count):
    if distance >= count:
        return jnp.zeros_like(values)
    if distance > 0:
        pairs = [(s, s + distance) for s in range(count - distance)]
    else:
        pairs = [(s - distance, s) for s in range(count + distance)]
    return lax.ppermute(values, "tensor", pairs)


def build_window(own, takes, count):
    rows = own.shape[0]
    left = [shift_rows(own[rows - take:], d + 1, count) for d, take in enumerate(takes)]
    right = [shift_rows(own[:take], -(d + 1), count) for d, take in enumerate(takes)]
    return jnp.concatenate(left[::-1] + [own] + right, axis=0)


def return_window(values, takes, count):
    rows = values.shape[0] - 2 * LONGEST
    total = values[LONGEST:LONGEST + rows]
    at = LONGEST
    for d, take in enumerate(takes):
        piece = values[at - take:at].astype(jnp.bfloat16)
        at -= take
        back = shift_rows(piece, -(d + 1), count).astype(jnp.float32)
        total = total + jnp.pad(back, ((rows - take, 0), (0, 0)))
    at = LONGEST + rows
    for d, take in enumerate(takes):
        piece = values[at:at + take].astype(jnp.bfloat16)
        at += take
        back = shift_rows(piece, d + 1, count).astype(jnp.float32)
        total = total + jnp.pad(back, ((0, rows - take), (0, 0)))
    return total


def to_heads(values):
    rows, width = values.shape
    return values.reshape(rows, width // HEAD_DIM, HEAD_DIM).transpose(1, 0, 2)


def from_heads(values):
    heads, rows, hd = values.shape
    return values.transpose(1, 0, 2).reshape(rows, heads * hd)


def shards(tokens, lengths, dealing, w_query, w_key, w_value, w_out, w_inner, w_outer, b_query, b_value, b_out, b_inner, b_outer, gain_attn, shift_attn, gain_ffn, shift_ffn, grad_out):
    count = lax.axis_size("tensor")
    tens_index = lax.axis_index("tensor")
    group_index = lax.axis_index("dp")
    rows = tokens.shape[0]
    group_rows = rows * count
    per_group = lengths.shape[0] // lax.axis_size("dp")
    takes = halo_plan(rows)
    window = rows + 2 * LONGEST
    seg, starts, ends = group_segments(lengths, dealing, group_index, group_rows, per_group)
    base = rows * tens_index - LONGEST
    places = base + jnp.arange(window, dtype=jnp.int32)
    valid = (places >= 0) & (places < group_rows)
    k_ids = jnp.where(valid, jnp.sum((places[:, None] >= ends[None, :]).astype(jnp.int32), axis=1), -1).astype(jnp.int32)
    q_ids = lax.dynamic_slice_in_dim(seg, rows * tens_index, rows)
    q_start = jnp.take(starts, q_ids) - base
    q_end = jnp.take(ends, q_ids) - base
    lo, hi, qlo, qhi = block_ranges(q_ids, k_ids, q_start, q_end, BLOCK, BLOCK)
    nkb = window // BLOCK
    kv_steps = min(nkb, (BLOCK + 2 * (LONGEST - 1)) // BLOCK + 2)
    q_steps = rows // BLOCK

    wq, wk, wv = gather_weights([w_query, w_key, w_value])
    wo_t, wi, wf_t = gather_weights([w_out.T, w_inner, w_outer.T])
    gain_one = gain_attn.astype(jnp.float32)
    gain_two = gain_ffn.astype(jnp.float32)

    x_own = tokens
    x_win = build_window(tokens, takes, count)
    query = (jnp.dot(x_own, wq, preferred_element_type=jnp.float32) + b_query.astype(jnp.float32)).astype(jnp.bfloat16)
    key_w = jnp.dot(x_win, wk, preferred_element_type=jnp.float32).astype(jnp.bfloat16)
    value_w = (jnp.dot(x_win, wv, preferred_element_type=jnp.float32) + b_value.astype(jnp.float32)).astype(jnp.bfloat16)
    scaled = query * jnp.asarray(1.0 / math.sqrt(HEAD_DIM), jnp.bfloat16)
    ctx32, lse = flash_forward(scaled, key_w, value_w, q_ids, k_ids, lo, hi, BLOCK, BLOCK, kv_steps)
    context = ctx32.astype(jnp.bfloat16)
    attn = contract_last(context, wo_t) + b_out.astype(jnp.float32)
    hidden, norm_one, inverse_one = norm_forward(tokens.astype(jnp.float32) + attn, gain_one, shift_attn.astype(jnp.float32))
    hidden_low = hidden.astype(jnp.bfloat16)
    pre_act = jnp.dot(hidden_low, wi, preferred_element_type=jnp.float32) + b_inner.astype(jnp.float32)
    act = activate(pre_act).astype(jnp.bfloat16)
    ffn = contract_last(act, wf_t) + b_outer.astype(jnp.float32)
    output, norm_two, inverse_two = norm_forward(hidden + ffn, gain_two, shift_ffn.astype(jnp.float32))

    grad_y = grad_out.astype(jnp.float32)
    grad_resid_two = norm_backward(grad_y, norm_two, inverse_two, gain_two)
    grad_ffn = grad_resid_two.astype(jnp.bfloat16)
    grad_outer_t = contract_first(grad_ffn, act)
    grad_act = jnp.dot(grad_ffn, wf_t, preferred_element_type=jnp.float32)
    unused, gelu_pull = jax.vjp(activate, pre_act)
    grad_pre = gelu_pull(grad_act)[0].astype(jnp.bfloat16)
    grad_inner_w = contract_first(hidden_low, grad_pre)
    grad_hidden = grad_resid_two + contract_last(grad_pre, wi)
    grad_resid_one = norm_backward(grad_hidden, norm_one, inverse_one, gain_one)
    grad_attn = grad_resid_one.astype(jnp.bfloat16)
    grad_out_t = contract_first(grad_attn, context)
    grad_context = jnp.dot(grad_attn, wo_t, preferred_element_type=jnp.float32).astype(jnp.bfloat16)
    late = [
        column_sum(grad_attn),
        column_sum(grad_pre),
        column_sum(grad_ffn),
        jnp.sum(grad_hidden * norm_one, axis=0),
        jnp.sum(grad_hidden, axis=0),
        jnp.sum(grad_y * norm_two, axis=0),
        jnp.sum(grad_y, axis=0),
    ]
    early_widths, early_cat = pack_grads([grad_out_t, grad_inner_w, grad_outer_t], late)
    grad_context, early_cat = lax.optimization_barrier((grad_context, early_cat))
    early_strip = reduce_dp(early_cat)
    heads = query.shape[1] // HEAD_DIM
    delta = jnp.sum((grad_context.astype(jnp.float32) * ctx32).reshape(rows, heads, HEAD_DIM), axis=-1)
    delta = delta.T.reshape(heads, rows, 1)
    dk_h, dv_h, dq_h = flash_backward(scaled, key_w, value_w, q_ids, k_ids, lse, delta, grad_context, qlo, qhi, BLOCK, BLOCK, q_steps)
    early_strip, dq_h, dk_h, dv_h = lax.optimization_barrier((early_strip, dq_h, dk_h, dv_h))
    early_sums = reduce_tensor(early_strip, early_widths, 3)
    g_out_t, g_inner, g_outer_t = early_sums[:3]
    late = early_sums[3:]
    grad_query = dq_h.astype(jnp.bfloat16)
    grad_key = dk_h.astype(jnp.bfloat16)
    grad_value = dv_h.astype(jnp.bfloat16)
    grad_query_w = contract_first(x_own, grad_query)
    grad_key_w = contract_first(x_win, grad_key)
    grad_value_w = contract_first(x_win, grad_value)
    grad_win = contract_last(grad_key, wk) + contract_last(grad_value, wv)
    grad_tokens = grad_resid_one + contract_last(grad_query, wq) + return_window(grad_win, takes, count)

    late_widths, late_cat = pack_grads(
        [grad_query_w, grad_key_w, grad_value_w], [column_sum(grad_query), column_sum(grad_value)]
    )
    g_query, g_key, g_value, g_bq, g_bv = reduce_tensor(reduce_dp_by_halves(late_cat), late_widths, 3)
    summed = (g_query, g_key, g_value, g_out_t.T, g_inner, g_outer_t.T)
    small = [g_bq, g_bv] + late
    return (output.astype(jnp.bfloat16), grad_tokens) + summed + tuple(small)


def solution(mesh):
    rows = P(("dp", "tensor"), None)
    vec = P(("dp", "tensor"))
    return jax.shard_map(
        shards,
        mesh=mesh,
        in_specs=(rows, P(), P(), P("dp", "tensor"), P("dp", "tensor"), P("dp", "tensor"), P("tensor", "dp"), P("dp", "tensor"), P("tensor", "dp"), P(), P(), P(), P(), P(), P(), P(), P(), P(), rows),
        out_specs=(rows, rows, P("dp", "tensor"), P("dp", "tensor"), P("dp", "tensor"), P("tensor", "dp"), P("dp", "tensor"), P("tensor", "dp")) + (vec,) * 9,
        check_vma=False,
    )
```

```python
import math

import jax
import jax.numpy as jnp
from jax import lax
from jax.experimental import pallas as pl
from jax.experimental.pallas import tpu as pltpu
from jax.sharding import PartitionSpec as P

HEAD_DIM = 64
LONGEST = 1024
BLOCK = 256

NEG = -1e30
LANES = 128


def _lanes(rows):
    return lax.broadcasted_iota(jnp.int32, (rows, LANES), 1) < LANES // 2


def _pick(first, second, lanes):
    return jnp.where(lanes, first, second)


def _nt(a, b):
    return lax.dot_general(a, b, (((1,), (1,)), ((), ())), preferred_element_type=jnp.float32)


def _tn(a, b):
    return lax.dot_general(a, b, (((0,), (0,)), ((), ())), preferred_element_type=jnp.float32)


def _nn(a, b):
    return lax.dot_general(a, b, (((1,), (0,)), ((), ())), preferred_element_type=jnp.float32)


def _attn_fwd(lo_ref, hi_ref, q_ref, k_ref, v_ref, qs_ref, ks_ref, o_ref, lse_ref, m_sc, l_sc, acc_sc):
    i = pl.program_id(0)
    j = pl.program_id(1)
    kv = lo_ref[i] + j
    pairs = q_ref.shape[1] // LANES
    bq = q_ref.shape[0]

    @pl.when(j == 0)
    def _():
        m_sc[...] = jnp.full_like(m_sc, NEG)
        l_sc[...] = jnp.zeros_like(l_sc)
        acc_sc[...] = jnp.zeros_like(acc_sc)

    @pl.when(kv <= hi_ref[i])
    def _():
        mask = qs_ref[...] == ks_ref[...]
        lanes = _lanes(bq)

        def pair(p, carry):
            cols = pl.ds(p * LANES, LANES)
            q2 = q_ref[:, cols]
            k2 = k_ref[:, cols]
            v2 = v_ref[:, cols]
            zero = jnp.zeros_like(q2)
            alphas, pvs = [], []
            for h in range(2):
                hq = _pick(q2, zero, lanes) if h == 0 else _pick(zero, q2, lanes)
                s = jnp.where(mask, _nt(hq, k2), NEG)
                m_old = m_sc[2 * p + h]
                m_new = jnp.maximum(m_old, jnp.max(s, axis=-1, keepdims=True))
                alpha = jnp.exp(m_old - m_new)
                e = jnp.exp(s - m_new)
                l_sc[2 * p + h] = alpha * l_sc[2 * p + h] + jnp.sum(e, axis=-1, keepdims=True)
                m_sc[2 * p + h] = m_new
                alphas.append(alpha)
                pvs.append(_nn(e.astype(jnp.bfloat16), v2))
            acc_sc[:, cols] = _pick(alphas[0], alphas[1], lanes) * acc_sc[:, cols] + _pick(pvs[0], pvs[1], lanes)
            return carry

        for p in range(pairs):
            pair(p, 0)

    @pl.when(j == pl.num_programs(1) - 1)
    def _():
        lanes = _lanes(bq)

        def pair(p, carry):
            cols = pl.ds(p * LANES, LANES)
            l0, l1 = l_sc[2 * p], l_sc[2 * p + 1]
            o_ref[:, cols] = acc_sc[:, cols] / _pick(l0, l1, lanes)
            lse_ref[2 * p] = m_sc[2 * p] + jnp.log(l0)
            lse_ref[2 * p + 1] = m_sc[2 * p + 1] + jnp.log(l1)
            return carry

        for p in range(pairs):
            pair(p, 0)


def _attn_dq(lo_ref, hi_ref, q_ref, k_ref, v_ref, qs_ref, ks_ref, lse_ref, dl_ref, do_ref, dq_ref, acc_sc):
    i = pl.program_id(0)
    j = pl.program_id(1)
    kv = lo_ref[i] + j
    pairs = q_ref.shape[1] // LANES
    bq = q_ref.shape[0]

    @pl.when(j == 0)
    def _():
        acc_sc[...] = jnp.zeros_like(acc_sc)

    @pl.when(kv <= hi_ref[i])
    def _():
        mask = qs_ref[...] == ks_ref[...]
        lanes = _lanes(bq)

        def pair(p, carry):
            cols = pl.ds(p * LANES, LANES)
            q2 = q_ref[:, cols]
            k2 = k_ref[:, cols]
            v2 = v_ref[:, cols]
            do2 = do_ref[:, cols]
            zero = jnp.zeros_like(q2)
            parts = []
            for h in range(2):
                sel = (lambda a: _pick(a, zero, lanes)) if h == 0 else (lambda a: _pick(zero, a, lanes))
                s = _nt(sel(q2), k2)
                e = jnp.where(mask, jnp.exp(s - lse_ref[2 * p + h]), 0.0)
                dp = _nt(sel(do2), v2)
                ds = (e * (dp - dl_ref[2 * p + h])).astype(jnp.bfloat16)
                parts.append(_nn(ds, k2))
            acc_sc[:, cols] += _pick(parts[0], parts[1], lanes)
            return carry

        for p in range(pairs):
            pair(p, 0)

    @pl.when(j == pl.num_programs(1) - 1)
    def _():
        dq_ref[...] = acc_sc[...] * 0.125


def _attn_dkv(lo_ref, hi_ref, q_ref, k_ref, v_ref, qs_ref, ks_ref, lse_ref, dl_ref, do_ref, dk_ref, dv_ref, dk_sc, dv_sc):
    j = pl.program_id(0)
    i = pl.program_id(1)
    qb = lo_ref[j] + i
    pairs = q_ref.shape[1] // LANES
    bq = q_ref.shape[0]
    bk = k_ref.shape[0]

    @pl.when(i == 0)
    def _():
        dk_sc[...] = jnp.zeros_like(dk_sc)
        dv_sc[...] = jnp.zeros_like(dv_sc)

    @pl.when(qb <= hi_ref[j])
    def _():
        mask = qs_ref[...] == ks_ref[...]
        lanes_q = _lanes(bq)
        lanes_k = _lanes(bk)

        def pair(p, carry):
            cols = pl.ds(p * LANES, LANES)
            q2 = q_ref[:, cols]
            k2 = k_ref[:, cols]
            v2 = v_ref[:, cols]
            do2 = do_ref[:, cols]
            zero = jnp.zeros_like(q2)
            dks, dvs = [], []
            for h in range(2):
                sel = (lambda a: _pick(a, zero, lanes_q)) if h == 0 else (lambda a: _pick(zero, a, lanes_q))
                s = _nt(sel(q2), k2)
                e = jnp.where(mask, jnp.exp(s - lse_ref[2 * p + h]), 0.0)
                dp = _nt(sel(do2), v2)
                ds = (e * (dp - dl_ref[2 * p + h])).astype(jnp.bfloat16)
                dvs.append(_tn(e.astype(jnp.bfloat16), do2))
                dks.append(_tn(ds, q2))
            dv_sc[:, cols] += _pick(dvs[0], dvs[1], lanes_k)
            dk_sc[:, cols] += _pick(dks[0], dks[1], lanes_k)
            return carry

        for p in range(pairs):
            pair(p, 0)

    @pl.when(i == pl.num_programs(1) - 1)
    def _():
        dk_ref[...] = dk_sc[...]
        dv_ref[...] = dv_sc[...]


def _attn_bwd(lo_ref, hi_ref, q_ref, k_ref, v_ref, qs_ref, ks_ref, lse_ref, dl_ref, do_ref, dk_ref, dv_ref, dq_ref, dk_sc, dv_sc):
    j = pl.program_id(0)
    i = pl.program_id(1)
    qb = lo_ref[j] + i
    pairs = q_ref.shape[1] // LANES
    bq = q_ref.shape[0]
    bk = k_ref.shape[0]

    @pl.when((j == 0) & (i == 0))
    def _():
        dq_ref[...] = jnp.zeros_like(dq_ref)

    @pl.when(i == 0)
    def _():
        dk_sc[...] = jnp.zeros_like(dk_sc)
        dv_sc[...] = jnp.zeros_like(dv_sc)

    @pl.when(qb <= hi_ref[j])
    def _():
        mask = qs_ref[...] == ks_ref[...]
        lanes_q = _lanes(bq)
        lanes_k = _lanes(bk)
        rows = pl.ds(pl.multiple_of(qb * bq, bq), bq)
        for p in range(pairs):
            cols = pl.ds(p * LANES, LANES)
            q2 = q_ref[:, cols]
            k2 = k_ref[:, cols]
            v2 = v_ref[:, cols]
            do2 = do_ref[:, cols]
            zero = jnp.zeros_like(q2)
            dks, dvs, dqs = [], [], []
            for h in range(2):
                sel = (lambda a: _pick(a, zero, lanes_q)) if h == 0 else (lambda a: _pick(zero, a, lanes_q))
                s = _nt(sel(q2), k2)
                e = jnp.where(mask, jnp.exp(s - lse_ref[2 * p + h]), 0.0)
                dp = _nt(sel(do2), v2)
                ds = (e * (dp - dl_ref[2 * p + h])).astype(jnp.bfloat16)
                dvs.append(_tn(e.astype(jnp.bfloat16), do2))
                dks.append(_tn(ds, q2))
                dqs.append(_nn(ds, k2))
            dv_sc[:, cols] += _pick(dvs[0], dvs[1], lanes_k)
            dk_sc[:, cols] += _pick(dks[0], dks[1], lanes_k)
            dq_ref[rows, cols] += _pick(dqs[0], dqs[1], lanes_q)

    @pl.when(i == pl.num_programs(1) - 1)
    def _():
        dk_ref[...] = dk_sc[...]
        dv_ref[...] = dv_sc[...]

    @pl.when((i == pl.num_programs(1) - 1) & (j == pl.num_programs(0) - 1))
    def _():
        dq_ref[...] = dq_ref[...] * 0.125


def _clamp(start, step, last):
    return jnp.minimum(start + step, jnp.maximum(last, 0))


def _params():
    return pltpu.CompilerParams(dimension_semantics=("arbitrary", "arbitrary"), vmem_limit_bytes=48 * 1024 * 1024)


def flash_forward(q, k, v, q_ids, k_ids, lo, hi, block_q, block_k, steps):
    nq, width = q.shape
    nk = k.shape[0]
    heads = width // 64
    kv_map = lambda i, j, a, b: (_clamp(a[i], j, b[i]), 0)
    ks_map = lambda i, j, a, b: (0, _clamp(a[i], j, b[i]))
    row = lambda i, j, a, b: (i, 0)
    grid_spec = pltpu.PrefetchScalarGridSpec(
        num_scalar_prefetch=2,
        grid=(nq // block_q, steps),
        in_specs=[
            pl.BlockSpec((block_q, width), row),
            pl.BlockSpec((block_k, width), kv_map),
            pl.BlockSpec((block_k, width), kv_map),
            pl.BlockSpec((block_q, 1), row),
            pl.BlockSpec((1, block_k), ks_map),
        ],
        out_specs=[
            pl.BlockSpec((block_q, width), row),
            pl.BlockSpec((heads, block_q, 1), lambda i, j, a, b: (0, i, 0)),
        ],
        scratch_shapes=[
            pltpu.VMEM((heads, block_q, 1), jnp.float32),
            pltpu.VMEM((heads, block_q, 1), jnp.float32),
            pltpu.VMEM((block_q, width), jnp.float32),
        ],
    )
    return pl.pallas_call(
        _attn_fwd,
        grid_spec=grid_spec,
        cost_estimate=pl.CostEstimate(flops=8 * nq * LONGEST * width, transcendentals=nq * LONGEST * heads, bytes_accessed=2 * (nq + 2 * nk) * width * 2),
        out_shape=[jax.ShapeDtypeStruct((nq, width), jnp.float32), jax.ShapeDtypeStruct((heads, nq, 1), jnp.float32)],
        compiler_params=_params(),
    )(lo, hi, q, k, v, q_ids.reshape(nq, 1), k_ids.reshape(1, nk))


def flash_dq(q, k, v, q_ids, k_ids, lse, delta, do, lo, hi, block_q, block_k, steps):
    nq, width = q.shape
    nk = k.shape[0]
    heads = width // 64
    kv_map = lambda i, j, a, b: (_clamp(a[i], j, b[i]), 0)
    ks_map = lambda i, j, a, b: (0, _clamp(a[i], j, b[i]))
    row = lambda i, j, a, b: (i, 0)
    hrow = lambda i, j, a, b: (0, i, 0)
    grid_spec = pltpu.PrefetchScalarGridSpec(
        num_scalar_prefetch=2,
        grid=(nq // block_q, steps),
        in_specs=[
            pl.BlockSpec((block_q, width), row),
            pl.BlockSpec((block_k, width), kv_map),
            pl.BlockSpec((block_k, width), kv_map),
            pl.BlockSpec((block_q, 1), row),
            pl.BlockSpec((1, block_k), ks_map),
            pl.BlockSpec((heads, block_q, 1), hrow),
            pl.BlockSpec((heads, block_q, 1), hrow),
            pl.BlockSpec((block_q, width), row),
        ],
        out_specs=pl.BlockSpec((block_q, width), row),
        scratch_shapes=[pltpu.VMEM((block_q, width), jnp.float32)],
    )
    return pl.pallas_call(
        _attn_dq,
        grid_spec=grid_spec,
        out_shape=jax.ShapeDtypeStruct((nq, width), jnp.float32),
        compiler_params=_params(),
    )(lo, hi, q, k, v, q_ids.reshape(nq, 1), k_ids.reshape(1, nk), lse, delta, do)


def flash_dkv(q, k, v, q_ids, k_ids, lse, delta, do, qlo, qhi, block_q, block_k, steps):
    nq, width = q.shape
    nk = k.shape[0]
    heads = width // 64
    q_map = lambda j, i, a, b: (_clamp(a[j], i, b[j]), 0)
    h_map = lambda j, i, a, b: (0, _clamp(a[j], i, b[j]), 0)
    col = lambda j, i, a, b: (j, 0)
    grid_spec = pltpu.PrefetchScalarGridSpec(
        num_scalar_prefetch=2,
        grid=(nk // block_k, steps),
        in_specs=[
            pl.BlockSpec((block_q, width), q_map),
            pl.BlockSpec((block_k, width), col),
            pl.BlockSpec((block_k, width), col),
            pl.BlockSpec((block_q, 1), q_map),
            pl.BlockSpec((1, block_k), lambda j, i, a, b: (0, j)),
            pl.BlockSpec((heads, block_q, 1), h_map),
            pl.BlockSpec((heads, block_q, 1), h_map),
            pl.BlockSpec((block_q, width), q_map),
        ],
        out_specs=[pl.BlockSpec((block_k, width), col), pl.BlockSpec((block_k, width), col)],
        scratch_shapes=[pltpu.VMEM((block_k, width), jnp.float32), pltpu.VMEM((block_k, width), jnp.float32)],
    )
    return pl.pallas_call(
        _attn_dkv,
        grid_spec=grid_spec,
        out_shape=[jax.ShapeDtypeStruct((nk, width), jnp.float32), jax.ShapeDtypeStruct((nk, width), jnp.float32)],
        compiler_params=_params(),
    )(qlo, qhi, q, k, v, q_ids.reshape(nq, 1), k_ids.reshape(1, nk), lse, delta, do)


def flash_backward(q, k, v, q_ids, k_ids, lse, delta, do, qlo, qhi, block_q, block_k, steps):
    nq, width = q.shape
    nk = k.shape[0]
    heads = width // 64
    q_map = lambda j, i, a, b: (_clamp(a[j], i, b[j]), 0)
    h_map = lambda j, i, a, b: (0, _clamp(a[j], i, b[j]), 0)
    col = lambda j, i, a, b: (j, 0)
    grid_spec = pltpu.PrefetchScalarGridSpec(
        num_scalar_prefetch=2,
        grid=(nk // block_k, steps),
        in_specs=[
            pl.BlockSpec((block_q, width), q_map),
            pl.BlockSpec((block_k, width), col),
            pl.BlockSpec((block_k, width), col),
            pl.BlockSpec((block_q, 1), q_map),
            pl.BlockSpec((1, block_k), lambda j, i, a, b: (0, j)),
            pl.BlockSpec((heads, block_q, 1), h_map),
            pl.BlockSpec((heads, block_q, 1), h_map),
            pl.BlockSpec((block_q, width), q_map),
        ],
        out_specs=[
            pl.BlockSpec((block_k, width), col),
            pl.BlockSpec((block_k, width), col),
            pl.BlockSpec((nq, width), lambda j, i, a, b: (0, 0)),
        ],
        scratch_shapes=[pltpu.VMEM((block_k, width), jnp.float32), pltpu.VMEM((block_k, width), jnp.float32)],
    )
    return pl.pallas_call(
        _attn_bwd,
        grid_spec=grid_spec,
        cost_estimate=pl.CostEstimate(flops=20 * nq * LONGEST * width, transcendentals=nq * LONGEST * heads, bytes_accessed=4 * (2 * nq + 4 * nk) * width),
        out_shape=[
            jax.ShapeDtypeStruct((nk, width), jnp.float32),
            jax.ShapeDtypeStruct((nk, width), jnp.float32),
            jax.ShapeDtypeStruct((nq, width), jnp.float32),
        ],
        compiler_params=_params(),
    )(qlo, qhi, q, k, v, q_ids.reshape(nq, 1), k_ids.reshape(1, nk), lse, delta, do)


def block_ranges(q_ids, k_ids, q_start, q_end, block_q, block_k):
    nq = q_ids.shape[0]
    nk = k_ids.shape[0]
    nqb, nkb = nq // block_q, nk // block_k
    first = q_start.reshape(nqb, block_q)[:, 0]
    last = q_end.reshape(nqb, block_q)[:, block_q - 1]
    lo = jnp.clip(first // block_k, 0, nkb - 1).astype(jnp.int32)
    hi = jnp.clip((last - 1) // block_k, 0, nkb - 1).astype(jnp.int32)
    kb = jnp.arange(nkb, dtype=jnp.int32)
    qb = jnp.arange(nqb, dtype=jnp.int32)
    cover = (lo[:, None] <= kb[None, :]) & (kb[None, :] <= hi[:, None])
    qlo = jnp.min(jnp.where(cover, qb[:, None], nqb), axis=0).astype(jnp.int32)
    qhi = jnp.max(jnp.where(cover, qb[:, None], -1), axis=0).astype(jnp.int32)
    return lo, hi, qlo, qhi


def norm_forward(values, gain, shift):
    center = jnp.mean(values, axis=-1, keepdims=True)
    offsets = values - center
    spread = jnp.mean(offsets * offsets, axis=-1, keepdims=True)
    inverse = lax.rsqrt(spread + 1e-06)
    normed = offsets * inverse
    return (normed * gain + shift, normed, inverse)


def norm_backward(grad_y, normed, inverse, gain):
    grad_normed = grad_y * gain
    mean_one = jnp.mean(grad_normed, axis=-1, keepdims=True)
    mean_two = jnp.mean(grad_normed * normed, axis=-1, keepdims=True)
    return inverse * (grad_normed - mean_one - normed * mean_two)


def activate(values):
    return jax.nn.gelu(values, approximate=False)


def contract_last(left, right):
    return lax.dot_general(left, right, (((1,), (1,)), ((), ())), preferred_element_type=jnp.float32)


def contract_first(left, right):
    return lax.dot_general(left, right, (((0,), (0,)), ((), ())), preferred_element_type=jnp.float32)


def column_sum(values):
    return jnp.sum(values.astype(jnp.float32), axis=0)


def group_segments(lengths, dealing, group_index, group_rows, per_group):
    picked = lax.dynamic_slice_in_dim(dealing, group_index * per_group, per_group)
    match = picked[:, None] == jnp.arange(lengths.shape[0], dtype=jnp.int32)[None, :]
    chosen = jnp.sum(jnp.where(match, lengths[None, :], 0), axis=1)
    ends = jnp.cumsum(chosen)
    starts = ends - chosen
    places = jnp.arange(group_rows, dtype=jnp.int32)
    segment_ids = jnp.sum((places[:, None] >= ends[None, :]).astype(jnp.int32), axis=1)
    return (segment_ids, starts, ends)


def cyclic_pieces(piece):
    count = lax.axis_size("tensor")
    me = lax.axis_index("tensor")
    got = [piece]
    for k in range(1, count):
        got.append(lax.ppermute(piece, "tensor", [(s, (s + k) % count) for s in range(count)]))
    order = (me - jnp.arange(count, dtype=jnp.int32)) % count
    return jnp.take(jnp.stack(got), order, axis=0)


def gather_weights(blocks):
    count = lax.axis_size("tensor")
    widths = [b.shape[1] for b in blocks]
    piece = jnp.concatenate(blocks, axis=1)
    parts = cyclic_pieces(piece)
    cols, at = [], 0
    for w in widths:
        cols.extend(parts[t, :, at:at + w] for t in range(count))
        at += w
    strip = jnp.concatenate(cols, axis=1)
    full = lax.all_gather(strip, "dp", axis=0, tiled=True)
    out, at = [], 0
    for w in widths:
        out.append(full[:, at:at + w * count])
        at += w * count
    return out


def vector_rows(v, rows):
    dp = lax.axis_size("dp")
    slab = rows // dp
    spread = v.reshape(dp, 1, -1)
    return jnp.pad(spread, ((0, 0), (0, slab - 1), (0, 0))).reshape(rows, -1)


def pack_grads(grads, vectors):
    count = lax.axis_size("tensor")
    me = lax.axis_index("tensor")
    rows = grads[0].shape[0]
    mats = [g.astype(jnp.bfloat16) for g in grads] + [vector_rows(v.astype(jnp.bfloat16), rows) for v in vectors]
    widths = [m.shape[1] // count for m in mats]
    cat = jnp.concatenate(mats, axis=1)
    return widths, cat


def reduce_dp(cat):
    return lax.psum_scatter(cat, "dp", scatter_dimension=0, tiled=True)


def reduce_dp_by_halves(cat):
    dp = lax.axis_size("dp")
    me = lax.axis_index("dp")
    slab = cat.shape[0] // dp
    part = cat.astype(jnp.float32).reshape(dp, slab, cat.shape[1])
    bit = 0
    while (1 << bit) < dp:
        mine = (me >> bit) % 2
        halves = part.reshape(part.shape[0] // 2, 2, slab, cat.shape[1])
        keep = lax.dynamic_index_in_dim(halves, mine, axis=1, keepdims=False)
        send = lax.dynamic_index_in_dim(halves, 1 - mine, axis=1, keepdims=False)
        pairs = [(i, i ^ (1 << bit)) for i in range(dp)]
        part = keep + lax.ppermute(send.astype(jnp.bfloat16), "dp", pairs).astype(jnp.float32)
        bit += 1
    return part.reshape(slab, cat.shape[1])


def reduce_tensor(strip, widths, n_grads):
    count = lax.axis_size("tensor")
    me = lax.axis_index("tensor")
    strip = strip.astype(jnp.float32)
    per_t = []
    for t in range(count):
        at, cols = 0, []
        for w in widths:
            cols.append(strip[:, at + t * w:at + (t + 1) * w])
            at += w * count
        per_t.append(jnp.concatenate(cols, axis=1))
    stacked = jnp.stack(per_t)
    total = jnp.take(stacked, me, axis=0)
    for k in range(1, count):
        send = jnp.take(stacked, (me + k) % count, axis=0)
        total = total + lax.ppermute(send, "tensor", [(s, (s + k) % count) for s in range(count)])
    out, at = [], 0
    for i, w in enumerate(widths):
        block = total[:, at:at + w]
        at += w
        out.append(block if i < n_grads else block[0])
    return out


def halo_plan(rows):
    hops = -(-LONGEST // rows)
    takes = [rows] * (hops - 1) + [LONGEST - rows * (hops - 1)]
    return takes


def shift_rows(values, distance, count):
    if distance >= count:
        return jnp.zeros_like(values)
    if distance > 0:
        pairs = [(s, s + distance) for s in range(count - distance)]
    else:
        pairs = [(s - distance, s) for s in range(count + distance)]
    return lax.ppermute(values, "tensor", pairs)


def build_window(own, takes, count):
    rows = own.shape[0]
    left = [shift_rows(own[rows - take:], d + 1, count) for d, take in enumerate(takes)]
    right = [shift_rows(own[:take], -(d + 1), count) for d, take in enumerate(takes)]
    return jnp.concatenate(left[::-1] + [own] + right, axis=0)


def return_window(values, takes, count):
    rows = values.shape[0] - 2 * LONGEST
    total = values[LONGEST:LONGEST + rows]
    at = LONGEST
    for d, take in enumerate(takes):
        piece = values[at - take:at].astype(jnp.bfloat16)
        at -= take
        back = shift_rows(piece, -(d + 1), count).astype(jnp.float32)
        total = total + jnp.pad(back, ((rows - take, 0), (0, 0)))
    at = LONGEST + rows
    for d, take in enumerate(takes):
        piece = values[at:at + take].astype(jnp.bfloat16)
        at += take
        back = shift_rows(piece, d + 1, count).astype(jnp.float32)
        total = total + jnp.pad(back, ((0, rows - take), (0, 0)))
    return total


def to_heads(values):
    rows, width = values.shape
    return values.reshape(rows, width // HEAD_DIM, HEAD_DIM).transpose(1, 0, 2)


def from_heads(values):
    heads, rows, hd = values.shape
    return values.transpose(1, 0, 2).reshape(rows, heads * hd)


def shards(tokens, lengths, dealing, w_query, w_key, w_value, w_out, w_inner, w_outer, b_query, b_value, b_out, b_inner, b_outer, gain_attn, shift_attn, gain_ffn, shift_ffn, grad_out):
    count = lax.axis_size("tensor")
    tens_index = lax.axis_index("tensor")
    group_index = lax.axis_index("dp")
    rows = tokens.shape[0]
    group_rows = rows * count
    per_group = lengths.shape[0] // lax.axis_size("dp")
    takes = halo_plan(rows)
    window = rows + 2 * LONGEST
    seg, starts, ends = group_segments(lengths, dealing, group_index, group_rows, per_group)
    base = rows * tens_index - LONGEST
    places = base + jnp.arange(window, dtype=jnp.int32)
    valid = (places >= 0) & (places < group_rows)
    k_ids = jnp.where(valid, jnp.sum((places[:, None] >= ends[None, :]).astype(jnp.int32), axis=1), -1).astype(jnp.int32)
    q_ids = lax.dynamic_slice_in_dim(seg, rows * tens_index, rows)
    q_start = jnp.take(starts, q_ids) - base
    q_end = jnp.take(ends, q_ids) - base
    lo, hi, qlo, qhi = block_ranges(q_ids, k_ids, q_start, q_end, BLOCK, BLOCK)
    nkb = window // BLOCK
    kv_steps = min(nkb, (BLOCK + 2 * (LONGEST - 1)) // BLOCK + 2)
    q_steps = rows // BLOCK

    wq, wk, wv = gather_weights([w_query, w_key, w_value])
    wo_t, wi, wf_t = gather_weights([w_out.T, w_inner, w_outer.T])
    gain_one = gain_attn.astype(jnp.float32)
    gain_two = gain_ffn.astype(jnp.float32)

    x_own = tokens
    x_win = build_window(tokens, takes, count)
    query = (jnp.dot(x_own, wq, preferred_element_type=jnp.float32) + b_query.astype(jnp.float32)).astype(jnp.bfloat16)
    key_w = jnp.dot(x_win, wk, preferred_element_type=jnp.float32).astype(jnp.bfloat16)
    value_w = (jnp.dot(x_win, wv, preferred_element_type=jnp.float32) + b_value.astype(jnp.float32)).astype(jnp.bfloat16)
    scaled = query * jnp.asarray(1.0 / math.sqrt(HEAD_DIM), jnp.bfloat16)
    ctx32, lse = flash_forward(scaled, key_w, value_w, q_ids, k_ids, lo, hi, BLOCK, BLOCK, kv_steps)
    context = ctx32.astype(jnp.bfloat16)
    attn = contract_last(context, wo_t) + b_out.astype(jnp.float32)
    hidden, norm_one, inverse_one = norm_forward(tokens.astype(jnp.float32) + attn, gain_one, shift_attn.astype(jnp.float32))
    hidden_low = hidden.astype(jnp.bfloat16)
    pre_act = jnp.dot(hidden_low, wi, preferred_element_type=jnp.float32) + b_inner.astype(jnp.float32)
    act = activate(pre_act).astype(jnp.bfloat16)
    ffn = contract_last(act, wf_t) + b_outer.astype(jnp.float32)
    output, norm_two, inverse_two = norm_forward(hidden + ffn, gain_two, shift_ffn.astype(jnp.float32))

    grad_y = grad_out.astype(jnp.float32)
    grad_resid_two = norm_backward(grad_y, norm_two, inverse_two, gain_two)
    grad_ffn = grad_resid_two.astype(jnp.bfloat16)
    grad_outer_t = contract_first(grad_ffn, act)
    grad_act = jnp.dot(grad_ffn, wf_t, preferred_element_type=jnp.float32)
    unused, gelu_pull = jax.vjp(activate, pre_act)
    grad_pre = gelu_pull(grad_act)[0].astype(jnp.bfloat16)
    grad_inner_w = contract_first(hidden_low, grad_pre)
    grad_hidden = grad_resid_two + contract_last(grad_pre, wi)
    grad_resid_one = norm_backward(grad_hidden, norm_one, inverse_one, gain_one)
    grad_attn = grad_resid_one.astype(jnp.bfloat16)
    grad_out_t = contract_first(grad_attn, context)
    grad_context = jnp.dot(grad_attn, wo_t, preferred_element_type=jnp.float32).astype(jnp.bfloat16)
    late = [
        column_sum(grad_attn),
        column_sum(grad_pre),
        column_sum(grad_ffn),
        jnp.sum(grad_hidden * norm_one, axis=0),
        jnp.sum(grad_hidden, axis=0),
        jnp.sum(grad_y * norm_two, axis=0),
        jnp.sum(grad_y, axis=0),
    ]
    early_widths, early_cat = pack_grads([grad_out_t, grad_inner_w, grad_outer_t], late)
    grad_context, early_cat = lax.optimization_barrier((grad_context, early_cat))
    early_strip = reduce_dp(early_cat)
    heads = query.shape[1] // HEAD_DIM
    delta = jnp.sum((grad_context.astype(jnp.float32) * ctx32).reshape(rows, heads, HEAD_DIM), axis=-1)
    delta = delta.T.reshape(heads, rows, 1)
    dk_h, dv_h, dq_h = flash_backward(scaled, key_w, value_w, q_ids, k_ids, lse, delta, grad_context, qlo, qhi, BLOCK, BLOCK, q_steps)
    early_strip, dq_h, dk_h, dv_h = lax.optimization_barrier((early_strip, dq_h, dk_h, dv_h))
    early_sums = reduce_tensor(early_strip, early_widths, 3)
    g_out_t, g_inner, g_outer_t = early_sums[:3]
    late = early_sums[3:]
    grad_query = dq_h.astype(jnp.bfloat16)
    grad_key = dk_h.astype(jnp.bfloat16)
    grad_value = dv_h.astype(jnp.bfloat16)
    grad_query_w = contract_first(x_own, grad_query)
    grad_key_w = contract_first(x_win, grad_key)
    grad_value_w = contract_first(x_win, grad_value)
    grad_win = contract_last(grad_key, wk) + contract_last(grad_value, wv)
    grad_tokens = grad_resid_one + contract_last(grad_query, wq) + return_window(grad_win, takes, count)

    late_widths, late_cat = pack_grads(
        [grad_query_w, grad_key_w, grad_value_w], [column_sum(grad_query), column_sum(grad_value)]
    )
    g_query, g_key, g_value, g_bq, g_bv = reduce_tensor(reduce_dp_by_halves(late_cat), late_widths, 3)
    summed = (g_query, g_key, g_value, g_out_t.T, g_inner, g_outer_t.T)
    small = [g_bq, g_bv] + late
    return (output.astype(jnp.bfloat16), grad_tokens) + summed + tuple(small)


def solution(mesh):
    rows = P(("dp", "tensor"), None)
    vec = P(("dp", "tensor"))
    return jax.shard_map(
        shards,
        mesh=mesh,
        in_specs=(rows, P(), P(), P("dp", "tensor"), P("dp", "tensor"), P("dp", "tensor"), P("tensor", "dp"), P("dp", "tensor"), P("tensor", "dp"), P(), P(), P(), P(), P(), P(), P(), P(), P(), rows),
        out_specs=(rows, rows, P("dp", "tensor"), P("dp", "tensor"), P("dp", "tensor"), P("tensor", "dp"), P("dp", "tensor"), P("tensor", "dp")) + (vec,) * 9,
        check_vma=False,
    )
```

```python
import math

import jax
import jax.numpy as jnp
from jax import lax
from jax.experimental import pallas as pl
from jax.experimental.pallas import tpu as pltpu
from jax.sharding import PartitionSpec as P

HEAD_DIM = 64
LONGEST = 1024
BLOCK = 256

NEG = -1e30
LANES = 128


def _lanes(rows):
    return lax.broadcasted_iota(jnp.int32, (rows, LANES), 1) < LANES // 2


def _pick(first, second, lanes):
    return jnp.where(lanes, first, second)


def _nt(a, b):
    return lax.dot_general(a, b, (((1,), (1,)), ((), ())), preferred_element_type=jnp.float32)


def _tn(a, b):
    return lax.dot_general(a, b, (((0,), (0,)), ((), ())), preferred_element_type=jnp.float32)


def _nn(a, b):
    return lax.dot_general(a, b, (((1,), (0,)), ((), ())), preferred_element_type=jnp.float32)


def _attn_fwd(lo_ref, hi_ref, q_ref, k_ref, v_ref, qs_ref, ks_ref, o_ref, lse_ref, m_sc, l_sc, acc_sc):
    i = pl.program_id(0)
    j = pl.program_id(1)
    kv = lo_ref[i] + j
    pairs = q_ref.shape[1] // LANES
    bq = q_ref.shape[0]

    @pl.when(j == 0)
    def _():
        m_sc[...] = jnp.full_like(m_sc, NEG)
        l_sc[...] = jnp.zeros_like(l_sc)
        acc_sc[...] = jnp.zeros_like(acc_sc)

    @pl.when(kv <= hi_ref[i])
    def _():
        mask = qs_ref[...] == ks_ref[...]
        lanes = _lanes(bq)

        def pair(p, carry):
            cols = pl.ds(p * LANES, LANES)
            q2 = q_ref[:, cols]
            k2 = k_ref[:, cols]
            v2 = v_ref[:, cols]
            zero = jnp.zeros_like(q2)
            alphas, pvs = [], []
            for h in range(2):
                hq = _pick(q2, zero, lanes) if h == 0 else _pick(zero, q2, lanes)
                s = jnp.where(mask, _nt(hq, k2), NEG)
                m_old = m_sc[2 * p + h]
                m_new = jnp.maximum(m_old, jnp.max(s, axis=-1, keepdims=True))
                alpha = jnp.exp(m_old - m_new)
                e = jnp.exp(s - m_new)
                l_sc[2 * p + h] = alpha * l_sc[2 * p + h] + jnp.sum(e, axis=-1, keepdims=True)
                m_sc[2 * p + h] = m_new
                alphas.append(alpha)
                pvs.append(_nn(e.astype(jnp.bfloat16), v2))
            acc_sc[:, cols] = _pick(alphas[0], alphas[1], lanes) * acc_sc[:, cols] + _pick(pvs[0], pvs[1], lanes)
            return carry

        for p in range(pairs):
            pair(p, 0)

    @pl.when(j == pl.num_programs(1) - 1)
    def _():
        lanes = _lanes(bq)

        def pair(p, carry):
            cols = pl.ds(p * LANES, LANES)
            l0, l1 = l_sc[2 * p], l_sc[2 * p + 1]
            o_ref[:, cols] = acc_sc[:, cols] / _pick(l0, l1, lanes)
            lse_ref[2 * p] = m_sc[2 * p] + jnp.log(l0)
            lse_ref[2 * p + 1] = m_sc[2 * p + 1] + jnp.log(l1)
            return carry

        for p in range(pairs):
            pair(p, 0)


def _attn_dq(lo_ref, hi_ref, q_ref, k_ref, v_ref, qs_ref, ks_ref, lse_ref, dl_ref, do_ref, dq_ref, acc_sc):
    i = pl.program_id(0)
    j = pl.program_id(1)
    kv = lo_ref[i] + j
    pairs = q_ref.shape[1] // LANES
    bq = q_ref.shape[0]

    @pl.when(j == 0)
    def _():
        acc_sc[...] = jnp.zeros_like(acc_sc)

    @pl.when(kv <= hi_ref[i])
    def _():
        mask = qs_ref[...] == ks_ref[...]
        lanes = _lanes(bq)

        def pair(p, carry):
            cols = pl.ds(p * LANES, LANES)
            q2 = q_ref[:, cols]
            k2 = k_ref[:, cols]
            v2 = v_ref[:, cols]
            do2 = do_ref[:, cols]
            zero = jnp.zeros_like(q2)
            parts = []
            for h in range(2):
                sel = (lambda a: _pick(a, zero, lanes)) if h == 0 else (lambda a: _pick(zero, a, lanes))
                s = _nt(sel(q2), k2)
                e = jnp.where(mask, jnp.exp(s - lse_ref[2 * p + h]), 0.0)
                dp = _nt(sel(do2), v2)
                ds = (e * (dp - dl_ref[2 * p + h])).astype(jnp.bfloat16)
                parts.append(_nn(ds, k2))
            acc_sc[:, cols] += _pick(parts[0], parts[1], lanes)
            return carry

        for p in range(pairs):
            pair(p, 0)

    @pl.when(j == pl.num_programs(1) - 1)
    def _():
        dq_ref[...] = acc_sc[...] * 0.125


def _attn_dkv(lo_ref, hi_ref, q_ref, k_ref, v_ref, qs_ref, ks_ref, lse_ref, dl_ref, do_ref, dk_ref, dv_ref, dk_sc, dv_sc):
    j = pl.program_id(0)
    i = pl.program_id(1)
    qb = lo_ref[j] + i
    pairs = q_ref.shape[1] // LANES
    bq = q_ref.shape[0]
    bk = k_ref.shape[0]

    @pl.when(i == 0)
    def _():
        dk_sc[...] = jnp.zeros_like(dk_sc)
        dv_sc[...] = jnp.zeros_like(dv_sc)

    @pl.when(qb <= hi_ref[j])
    def _():
        mask = qs_ref[...] == ks_ref[...]
        lanes_q = _lanes(bq)
        lanes_k = _lanes(bk)

        def pair(p, carry):
            cols = pl.ds(p * LANES, LANES)
            q2 = q_ref[:, cols]
            k2 = k_ref[:, cols]
            v2 = v_ref[:, cols]
            do2 = do_ref[:, cols]
            zero = jnp.zeros_like(q2)
            dks, dvs = [], []
            for h in range(2):
                sel = (lambda a: _pick(a, zero, lanes_q)) if h == 0 else (lambda a: _pick(zero, a, lanes_q))
                s = _nt(sel(q2), k2)
                e = jnp.where(mask, jnp.exp(s - lse_ref[2 * p + h]), 0.0)
                dp = _nt(sel(do2), v2)
                ds = (e * (dp - dl_ref[2 * p + h])).astype(jnp.bfloat16)
                dvs.append(_tn(e.astype(jnp.bfloat16), do2))
                dks.append(_tn(ds, q2))
            dv_sc[:, cols] += _pick(dvs[0], dvs[1], lanes_k)
            dk_sc[:, cols] += _pick(dks[0], dks[1], lanes_k)
            return carry

        for p in range(pairs):
            pair(p, 0)

    @pl.when(i == pl.num_programs(1) - 1)
    def _():
        dk_ref[...] = dk_sc[...]
        dv_ref[...] = dv_sc[...]


def _attn_bwd(lo_ref, hi_ref, q_ref, k_ref, v_ref, qs_ref, ks_ref, lse_ref, dl_ref, do_ref, dk_ref, dv_ref, dq_ref, dk_sc, dv_sc):
    j = pl.program_id(0)
    i = pl.program_id(1)
    qb = lo_ref[j] + i
    pairs = q_ref.shape[1] // LANES
    bq = q_ref.shape[0]
    bk = k_ref.shape[0]

    @pl.when((j == 0) & (i == 0))
    def _():
        dq_ref[...] = jnp.zeros_like(dq_ref)

    @pl.when(i == 0)
    def _():
        dk_sc[...] = jnp.zeros_like(dk_sc)
        dv_sc[...] = jnp.zeros_like(dv_sc)

    @pl.when(qb <= hi_ref[j])
    def _():
        mask = qs_ref[...] == ks_ref[...]
        lanes_q = _lanes(bq)
        lanes_k = _lanes(bk)
        rows = pl.ds(pl.multiple_of(qb * bq, bq), bq)
        for p in range(pairs):
            cols = pl.ds(p * LANES, LANES)
            q2 = q_ref[:, cols]
            k2 = k_ref[:, cols]
            v2 = v_ref[:, cols]
            do2 = do_ref[:, cols]
            zero = jnp.zeros_like(q2)
            dks, dvs, dqs = [], [], []
            for h in range(2):
                sel = (lambda a: _pick(a, zero, lanes_q)) if h == 0 else (lambda a: _pick(zero, a, lanes_q))
                s = _nt(sel(q2), k2)
                e = jnp.where(mask, jnp.exp(s - lse_ref[2 * p + h]), 0.0)
                dp = _nt(sel(do2), v2)
                ds = (e * (dp - dl_ref[2 * p + h])).astype(jnp.bfloat16)
                dvs.append(_tn(e.astype(jnp.bfloat16), do2))
                dks.append(_tn(ds, q2))
                dqs.append(_nn(ds, k2))
            dv_sc[:, cols] += _pick(dvs[0], dvs[1], lanes_k)
            dk_sc[:, cols] += _pick(dks[0], dks[1], lanes_k)
            dq_ref[rows, cols] += _pick(dqs[0], dqs[1], lanes_q)

    @pl.when(i == pl.num_programs(1) - 1)
    def _():
        dk_ref[...] = dk_sc[...]
        dv_ref[...] = dv_sc[...]

    @pl.when((i == pl.num_programs(1) - 1) & (j == pl.num_programs(0) - 1))
    def _():
        dq_ref[...] = dq_ref[...] * 0.125


def _clamp(start, step, last):
    return jnp.minimum(start + step, jnp.maximum(last, 0))


def _params():
    return pltpu.CompilerParams(dimension_semantics=("arbitrary", "arbitrary"), vmem_limit_bytes=48 * 1024 * 1024)


def flash_forward(q, k, v, q_ids, k_ids, lo, hi, block_q, block_k, steps):
    nq, width = q.shape
    nk = k.shape[0]
    heads = width // 64
    kv_map = lambda i, j, a, b: (_clamp(a[i], j, b[i]), 0)
    ks_map = lambda i, j, a, b: (0, _clamp(a[i], j, b[i]))
    row = lambda i, j, a, b: (i, 0)
    grid_spec = pltpu.PrefetchScalarGridSpec(
        num_scalar_prefetch=2,
        grid=(nq // block_q, steps),
        in_specs=[
            pl.BlockSpec((block_q, width), row),
            pl.BlockSpec((block_k, width), kv_map),
            pl.BlockSpec((block_k, width), kv_map),
            pl.BlockSpec((block_q, 1), row),
            pl.BlockSpec((1, block_k), ks_map),
        ],
        out_specs=[
            pl.BlockSpec((block_q, width), row),
            pl.BlockSpec((heads, block_q, 1), lambda i, j, a, b: (0, i, 0)),
        ],
        scratch_shapes=[
            pltpu.VMEM((heads, block_q, 1), jnp.float32),
            pltpu.VMEM((heads, block_q, 1), jnp.float32),
            pltpu.VMEM((block_q, width), jnp.float32),
        ],
    )
    return pl.pallas_call(
        _attn_fwd,
        grid_spec=grid_spec,
        cost_estimate=pl.CostEstimate(flops=8 * nq * LONGEST * width, transcendentals=nq * LONGEST * heads, bytes_accessed=2 * (nq + 2 * nk) * width * 2),
        out_shape=[jax.ShapeDtypeStruct((nq, width), jnp.float32), jax.ShapeDtypeStruct((heads, nq, 1), jnp.float32)],
        compiler_params=_params(),
    )(lo, hi, q, k, v, q_ids.reshape(nq, 1), k_ids.reshape(1, nk))


def flash_dq(q, k, v, q_ids, k_ids, lse, delta, do, lo, hi, block_q, block_k, steps):
    nq, width = q.shape
    nk = k.shape[0]
    heads = width // 64
    kv_map = lambda i, j, a, b: (_clamp(a[i], j, b[i]), 0)
    ks_map = lambda i, j, a, b: (0, _clamp(a[i], j, b[i]))
    row = lambda i, j, a, b: (i, 0)
    hrow = lambda i, j, a, b: (0, i, 0)
    grid_spec = pltpu.PrefetchScalarGridSpec(
        num_scalar_prefetch=2,
        grid=(nq // block_q, steps),
        in_specs=[
            pl.BlockSpec((block_q, width), row),
            pl.BlockSpec((block_k, width), kv_map),
            pl.BlockSpec((block_k, width), kv_map),
            pl.BlockSpec((block_q, 1), row),
            pl.BlockSpec((1, block_k), ks_map),
            pl.BlockSpec((heads, block_q, 1), hrow),
            pl.BlockSpec((heads, block_q, 1), hrow),
            pl.BlockSpec((block_q, width), row),
        ],
        out_specs=pl.BlockSpec((block_q, width), row),
        scratch_shapes=[pltpu.VMEM((block_q, width), jnp.float32)],
    )
    return pl.pallas_call(
        _attn_dq,
        grid_spec=grid_spec,
        out_shape=jax.ShapeDtypeStruct((nq, width), jnp.float32),
        compiler_params=_params(),
    )(lo, hi, q, k, v, q_ids.reshape(nq, 1), k_ids.reshape(1, nk), lse, delta, do)


def flash_dkv(q, k, v, q_ids, k_ids, lse, delta, do, qlo, qhi, block_q, block_k, steps):
    nq, width = q.shape
    nk = k.shape[0]
    heads = width // 64
    q_map = lambda j, i, a, b: (_clamp(a[j], i, b[j]), 0)
    h_map = lambda j, i, a, b: (0, _clamp(a[j], i, b[j]), 0)
    col = lambda j, i, a, b: (j, 0)
    grid_spec = pltpu.PrefetchScalarGridSpec(
        num_scalar_prefetch=2,
        grid=(nk // block_k, steps),
        in_specs=[
            pl.BlockSpec((block_q, width), q_map),
            pl.BlockSpec((block_k, width), col),
            pl.BlockSpec((block_k, width), col),
            pl.BlockSpec((block_q, 1), q_map),
            pl.BlockSpec((1, block_k), lambda j, i, a, b: (0, j)),
            pl.BlockSpec((heads, block_q, 1), h_map),
            pl.BlockSpec((heads, block_q, 1), h_map),
            pl.BlockSpec((block_q, width), q_map),
        ],
        out_specs=[pl.BlockSpec((block_k, width), col), pl.BlockSpec((block_k, width), col)],
        scratch_shapes=[pltpu.VMEM((block_k, width), jnp.float32), pltpu.VMEM((block_k, width), jnp.float32)],
    )
    return pl.pallas_call(
        _attn_dkv,
        grid_spec=grid_spec,
        out_shape=[jax.ShapeDtypeStruct((nk, width), jnp.float32), jax.ShapeDtypeStruct((nk, width), jnp.float32)],
        compiler_params=_params(),
    )(qlo, qhi, q, k, v, q_ids.reshape(nq, 1), k_ids.reshape(1, nk), lse, delta, do)


def flash_backward(q, k, v, q_ids, k_ids, lse, delta, do, qlo, qhi, block_q, block_k, steps):
    nq, width = q.shape
    nk = k.shape[0]
    heads = width // 64
    q_map = lambda j, i, a, b: (_clamp(a[j], i, b[j]), 0)
    h_map = lambda j, i, a, b: (0, _clamp(a[j], i, b[j]), 0)
    col = lambda j, i, a, b: (j, 0)
    grid_spec = pltpu.PrefetchScalarGridSpec(
        num_scalar_prefetch=2,
        grid=(nk // block_k, steps),
        in_specs=[
            pl.BlockSpec((block_q, width), q_map),
            pl.BlockSpec((block_k, width), col),
            pl.BlockSpec((block_k, width), col),
            pl.BlockSpec((block_q, 1), q_map),
            pl.BlockSpec((1, block_k), lambda j, i, a, b: (0, j)),
            pl.BlockSpec((heads, block_q, 1), h_map),
            pl.BlockSpec((heads, block_q, 1), h_map),
            pl.BlockSpec((block_q, width), q_map),
        ],
        out_specs=[
            pl.BlockSpec((block_k, width), col),
            pl.BlockSpec((block_k, width), col),
            pl.BlockSpec((nq, width), lambda j, i, a, b: (0, 0)),
        ],
        scratch_shapes=[pltpu.VMEM((block_k, width), jnp.float32), pltpu.VMEM((block_k, width), jnp.float32)],
    )
    return pl.pallas_call(
        _attn_bwd,
        grid_spec=grid_spec,
        cost_estimate=pl.CostEstimate(flops=20 * nq * LONGEST * width, transcendentals=nq * LONGEST * heads, bytes_accessed=4 * (2 * nq + 4 * nk) * width),
        out_shape=[
            jax.ShapeDtypeStruct((nk, width), jnp.float32),
            jax.ShapeDtypeStruct((nk, width), jnp.float32),
            jax.ShapeDtypeStruct((nq, width), jnp.float32),
        ],
        compiler_params=_params(),
    )(qlo, qhi, q, k, v, q_ids.reshape(nq, 1), k_ids.reshape(1, nk), lse, delta, do)


def block_ranges(q_ids, k_ids, q_start, q_end, block_q, block_k):
    nq = q_ids.shape[0]
    nk = k_ids.shape[0]
    nqb, nkb = nq // block_q, nk // block_k
    first = q_start.reshape(nqb, block_q)[:, 0]
    last = q_end.reshape(nqb, block_q)[:, block_q - 1]
    lo = jnp.clip(first // block_k, 0, nkb - 1).astype(jnp.int32)
    hi = jnp.clip((last - 1) // block_k, 0, nkb - 1).astype(jnp.int32)
    kb = jnp.arange(nkb, dtype=jnp.int32)
    qb = jnp.arange(nqb, dtype=jnp.int32)
    cover = (lo[:, None] <= kb[None, :]) & (kb[None, :] <= hi[:, None])
    qlo = jnp.min(jnp.where(cover, qb[:, None], nqb), axis=0).astype(jnp.int32)
    qhi = jnp.max(jnp.where(cover, qb[:, None], -1), axis=0).astype(jnp.int32)
    return lo, hi, qlo, qhi


def norm_forward(values, gain, shift):
    center = jnp.mean(values, axis=-1, keepdims=True)
    offsets = values - center
    spread = jnp.mean(offsets * offsets, axis=-1, keepdims=True)
    inverse = lax.rsqrt(spread + 1e-06)
    normed = offsets * inverse
    return (normed * gain + shift, normed, inverse)


def norm_backward(grad_y, normed, inverse, gain):
    grad_normed = grad_y * gain
    mean_one = jnp.mean(grad_normed, axis=-1, keepdims=True)
    mean_two = jnp.mean(grad_normed * normed, axis=-1, keepdims=True)
    return inverse * (grad_normed - mean_one - normed * mean_two)


def activate(values):
    return jax.nn.gelu(values, approximate=False)


def contract_last(left, right):
    return lax.dot_general(left, right, (((1,), (1,)), ((), ())), preferred_element_type=jnp.float32)


def contract_first(left, right):
    return lax.dot_general(left, right, (((0,), (0,)), ((), ())), preferred_element_type=jnp.float32)


def column_sum(values):
    return jnp.sum(values.astype(jnp.float32), axis=0)


def group_segments(lengths, dealing, group_index, group_rows, per_group):
    picked = lax.dynamic_slice_in_dim(dealing, group_index * per_group, per_group)
    match = picked[:, None] == jnp.arange(lengths.shape[0], dtype=jnp.int32)[None, :]
    chosen = jnp.sum(jnp.where(match, lengths[None, :], 0), axis=1)
    ends = jnp.cumsum(chosen)
    starts = ends - chosen
    places = jnp.arange(group_rows, dtype=jnp.int32)
    segment_ids = jnp.sum((places[:, None] >= ends[None, :]).astype(jnp.int32), axis=1)
    return (segment_ids, starts, ends)


def cyclic_pieces(piece):
    count = lax.axis_size("tensor")
    me = lax.axis_index("tensor")
    got = [piece]
    for k in range(1, count):
        got.append(lax.ppermute(piece, "tensor", [(s, (s + k) % count) for s in range(count)]))
    order = (me - jnp.arange(count, dtype=jnp.int32)) % count
    return jnp.take(jnp.stack(got), order, axis=0)


def gather_weights(blocks):
    count = lax.axis_size("tensor")
    widths = [b.shape[1] for b in blocks]
    piece = jnp.concatenate(blocks, axis=1)
    parts = cyclic_pieces(piece)
    cols, at = [], 0
    for w in widths:
        cols.extend(parts[t, :, at:at + w] for t in range(count))
        at += w
    strip = jnp.concatenate(cols, axis=1)
    full = lax.all_gather(strip, "dp", axis=0, tiled=True)
    out, at = [], 0
    for w in widths:
        out.append(full[:, at:at + w * count])
        at += w * count
    return out


def vector_rows(v, rows):
    dp = lax.axis_size("dp")
    slab = rows // dp
    spread = v.reshape(dp, 1, -1)
    return jnp.pad(spread, ((0, 0), (0, slab - 1), (0, 0))).reshape(rows, -1)


def pack_grads(grads, vectors):
    count = lax.axis_size("tensor")
    me = lax.axis_index("tensor")
    rows = grads[0].shape[0]
    mats = [g.astype(jnp.bfloat16) for g in grads] + [vector_rows(v.astype(jnp.bfloat16), rows) for v in vectors]
    widths = [m.shape[1] // count for m in mats]
    cat = jnp.concatenate(mats, axis=1)
    return widths, cat


def reduce_dp(cat):
    return lax.psum_scatter(cat, "dp", scatter_dimension=0, tiled=True)


def reduce_dp_by_halves(cat):
    dp = lax.axis_size("dp")
    me = lax.axis_index("dp")
    slab = cat.shape[0] // dp
    part = cat.astype(jnp.float32).reshape(dp, slab, cat.shape[1])
    bit = 0
    while (1 << bit) < dp:
        mine = (me >> bit) % 2
        halves = part.reshape(part.shape[0] // 2, 2, slab, cat.shape[1])
        keep = lax.dynamic_index_in_dim(halves, mine, axis=1, keepdims=False)
        send = lax.dynamic_index_in_dim(halves, 1 - mine, axis=1, keepdims=False)
        pairs = [(i, i ^ (1 << bit)) for i in range(dp)]
        part = keep + lax.ppermute(send.astype(jnp.bfloat16), "dp", pairs).astype(jnp.float32)
        bit += 1
    return part.reshape(slab, cat.shape[1])


def reduce_tensor(strip, widths, n_grads):
    count = lax.axis_size("tensor")
    me = lax.axis_index("tensor")
    strip = strip.astype(jnp.float32)
    per_t = []
    for t in range(count):
        at, cols = 0, []
        for w in widths:
            cols.append(strip[:, at + t * w:at + (t + 1) * w])
            at += w * count
        per_t.append(jnp.concatenate(cols, axis=1))
    stacked = jnp.stack(per_t)
    total = jnp.take(stacked, me, axis=0)
    for k in range(1, count):
        send = jnp.take(stacked, (me + k) % count, axis=0)
        total = total + lax.ppermute(send, "tensor", [(s, (s + k) % count) for s in range(count)])
    out, at = [], 0
    for i, w in enumerate(widths):
        block = total[:, at:at + w]
        at += w
        out.append(block if i < n_grads else block[0])
    return out


def halo_plan(rows):
    hops = -(-LONGEST // rows)
    takes = [rows] * (hops - 1) + [LONGEST - rows * (hops - 1)]
    return takes


def shift_rows(values, distance, count):
    if distance >= count:
        return jnp.zeros_like(values)
    if distance > 0:
        pairs = [(s, s + distance) for s in range(count - distance)]
    else:
        pairs = [(s - distance, s) for s in range(count + distance)]
    return lax.ppermute(values, "tensor", pairs)


def build_window(own, takes, count):
    rows = own.shape[0]
    left = [shift_rows(own[rows - take:], d + 1, count) for d, take in enumerate(takes)]
    right = [shift_rows(own[:take], -(d + 1), count) for d, take in enumerate(takes)]
    return jnp.concatenate(left[::-1] + [own] + right, axis=0)


def return_halo(left_vals, right_vals, takes, count):
    rows = None
    backs = []
    at = left_vals.shape[0]
    for d, take in enumerate(takes):
        piece = left_vals[at - take:at].astype(jnp.bfloat16)
        at -= take
        backs.append(("last", shift_rows(piece, -(d + 1), count)))
    at = 0
    for d, take in enumerate(takes):
        piece = right_vals[at:at + take].astype(jnp.bfloat16)
        at += take
        backs.append(("first", shift_rows(piece, d + 1, count)))
    return backs


def add_backs(total, backs):
    rows = total.shape[0]
    for where_to, got in backs:
        take = got.shape[0]
        got = got.astype(jnp.float32)
        if where_to == "last":
            total = total + jnp.pad(got, ((rows - take, 0), (0, 0)))
        else:
            total = total + jnp.pad(got, ((0, rows - take), (0, 0)))
    return total


def return_window(values, takes, count):
    rows = values.shape[0] - 2 * LONGEST
    total = values[LONGEST:LONGEST + rows]
    at = LONGEST
    for d, take in enumerate(takes):
        piece = values[at - take:at].astype(jnp.bfloat16)
        at -= take
        back = shift_rows(piece, -(d + 1), count).astype(jnp.float32)
        total = total + jnp.pad(back, ((rows - take, 0), (0, 0)))
    at = LONGEST + rows
    for d, take in enumerate(takes):
        piece = values[at:at + take].astype(jnp.bfloat16)
        at += take
        back = shift_rows(piece, d + 1, count).astype(jnp.float32)
        total = total + jnp.pad(back, ((0, rows - take), (0, 0)))
    return total


def to_heads(values):
    rows, width = values.shape
    return values.reshape(rows, width // HEAD_DIM, HEAD_DIM).transpose(1, 0, 2)


def from_heads(values):
    heads, rows, hd = values.shape
    return values.transpose(1, 0, 2).reshape(rows, heads * hd)


def shards(tokens, lengths, dealing, w_query, w_key, w_value, w_out, w_inner, w_outer, b_query, b_value, b_out, b_inner, b_outer, gain_attn, shift_attn, gain_ffn, shift_ffn, grad_out):
    count = lax.axis_size("tensor")
    tens_index = lax.axis_index("tensor")
    group_index = lax.axis_index("dp")
    rows = tokens.shape[0]
    group_rows = rows * count
    per_group = lengths.shape[0] // lax.axis_size("dp")
    takes = halo_plan(rows)
    window = rows + 2 * LONGEST
    seg, starts, ends = group_segments(lengths, dealing, group_index, group_rows, per_group)
    base = rows * tens_index - LONGEST
    places = base + jnp.arange(window, dtype=jnp.int32)
    valid = (places >= 0) & (places < group_rows)
    k_ids = jnp.where(valid, jnp.sum((places[:, None] >= ends[None, :]).astype(jnp.int32), axis=1), -1).astype(jnp.int32)
    q_ids = lax.dynamic_slice_in_dim(seg, rows * tens_index, rows)
    q_start = jnp.take(starts, q_ids) - base
    q_end = jnp.take(ends, q_ids) - base
    lo, hi, qlo, qhi = block_ranges(q_ids, k_ids, q_start, q_end, BLOCK, BLOCK)
    nkb = window // BLOCK
    kv_steps = min(nkb, (BLOCK + 2 * (LONGEST - 1)) // BLOCK + 2)
    q_steps = rows // BLOCK

    wq, wk, wv = gather_weights([w_query, w_key, w_value])
    wo_t, wi, wf_t = gather_weights([w_out.T, w_inner, w_outer.T])
    gain_one = gain_attn.astype(jnp.float32)
    gain_two = gain_ffn.astype(jnp.float32)

    x_own = tokens
    x_win = build_window(tokens, takes, count)
    query = (jnp.dot(x_own, wq, preferred_element_type=jnp.float32) + b_query.astype(jnp.float32)).astype(jnp.bfloat16)
    key_w = jnp.dot(x_win, wk, preferred_element_type=jnp.float32).astype(jnp.bfloat16)
    value_w = (jnp.dot(x_win, wv, preferred_element_type=jnp.float32) + b_value.astype(jnp.float32)).astype(jnp.bfloat16)
    scaled = query * jnp.asarray(1.0 / math.sqrt(HEAD_DIM), jnp.bfloat16)
    ctx32, lse = flash_forward(scaled, key_w, value_w, q_ids, k_ids, lo, hi, BLOCK, BLOCK, kv_steps)
    context = ctx32.astype(jnp.bfloat16)
    attn = contract_last(context, wo_t) + b_out.astype(jnp.float32)
    hidden, norm_one, inverse_one = norm_forward(tokens.astype(jnp.float32) + attn, gain_one, shift_attn.astype(jnp.float32))
    hidden_low = hidden.astype(jnp.bfloat16)
    pre_act = jnp.dot(hidden_low, wi, preferred_element_type=jnp.float32) + b_inner.astype(jnp.float32)
    act = activate(pre_act).astype(jnp.bfloat16)
    ffn = contract_last(act, wf_t) + b_outer.astype(jnp.float32)
    output, norm_two, inverse_two = norm_forward(hidden + ffn, gain_two, shift_ffn.astype(jnp.float32))

    grad_y = grad_out.astype(jnp.float32)
    grad_resid_two = norm_backward(grad_y, norm_two, inverse_two, gain_two)
    grad_ffn = grad_resid_two.astype(jnp.bfloat16)
    grad_outer_t = contract_first(grad_ffn, act)
    grad_act = jnp.dot(grad_ffn, wf_t, preferred_element_type=jnp.float32)
    unused, gelu_pull = jax.vjp(activate, pre_act)
    grad_pre = gelu_pull(grad_act)[0].astype(jnp.bfloat16)
    grad_inner_w = contract_first(hidden_low, grad_pre)
    grad_hidden = grad_resid_two + contract_last(grad_pre, wi)
    grad_resid_one = norm_backward(grad_hidden, norm_one, inverse_one, gain_one)
    grad_attn = grad_resid_one.astype(jnp.bfloat16)
    grad_out_t = contract_first(grad_attn, context)
    grad_context = jnp.dot(grad_attn, wo_t, preferred_element_type=jnp.float32).astype(jnp.bfloat16)
    late = [
        column_sum(grad_attn),
        column_sum(grad_pre),
        column_sum(grad_ffn),
        jnp.sum(grad_hidden * norm_one, axis=0),
        jnp.sum(grad_hidden, axis=0),
        jnp.sum(grad_y * norm_two, axis=0),
        jnp.sum(grad_y, axis=0),
    ]
    early_widths, early_cat = pack_grads([grad_out_t, grad_inner_w, grad_outer_t], late)
    grad_context, early_cat = lax.optimization_barrier((grad_context, early_cat))
    early_strip = reduce_dp(early_cat)
    heads = query.shape[1] // HEAD_DIM
    delta = jnp.sum((grad_context.astype(jnp.float32) * ctx32).reshape(rows, heads, HEAD_DIM), axis=-1)
    delta = delta.T.reshape(heads, rows, 1)
    dk_h, dv_h, dq_h = flash_backward(scaled, key_w, value_w, q_ids, k_ids, lse, delta, grad_context, qlo, qhi, BLOCK, BLOCK, q_steps)
    early_strip, dq_h, dk_h, dv_h = lax.optimization_barrier((early_strip, dq_h, dk_h, dv_h))
    early_sums = reduce_tensor(early_strip, early_widths, 3)
    g_out_t, g_inner, g_outer_t = early_sums[:3]
    late = early_sums[3:]
    grad_query = dq_h.astype(jnp.bfloat16)
    grad_key = dk_h.astype(jnp.bfloat16)
    grad_value = dv_h.astype(jnp.bfloat16)
    grad_query_w = contract_first(x_own, grad_query)
    grad_key_w = contract_first(x_win, grad_key)
    grad_value_w = contract_first(x_win, grad_value)
    halo = sum(takes)
    def win_grad(lo_row, hi_row):
        return contract_last(grad_key[lo_row:hi_row], wk) + contract_last(grad_value[lo_row:hi_row], wv)
    back = return_halo(win_grad(0, halo), win_grad(halo + rows, 2 * halo + rows), takes, count)
    grad_tokens = add_backs(grad_resid_one + contract_last(grad_query, wq) + win_grad(halo, halo + rows), back)

    late_widths, late_cat = pack_grads(
        [grad_query_w, grad_key_w, grad_value_w], [column_sum(grad_query), column_sum(grad_value)]
    )
    g_query, g_key, g_value, g_bq, g_bv = reduce_tensor(reduce_dp_by_halves(late_cat), late_widths, 3)
    summed = (g_query, g_key, g_value, g_out_t.T, g_inner, g_outer_t.T)
    small = [g_bq, g_bv] + late
    return (output.astype(jnp.bfloat16), grad_tokens) + summed + tuple(small)


def solution(mesh):
    rows = P(("dp", "tensor"), None)
    vec = P(("dp", "tensor"))
    return jax.shard_map(
        shards,
        mesh=mesh,
        in_specs=(rows, P(), P(), P("dp", "tensor"), P("dp", "tensor"), P("dp", "tensor"), P("tensor", "dp"), P("dp", "tensor"), P("tensor", "dp"), P(), P(), P(), P(), P(), P(), P(), P(), P(), rows),
        out_specs=(rows, rows, P("dp", "tensor"), P("dp", "tensor"), P("dp", "tensor"), P("tensor", "dp"), P("dp", "tensor"), P("tensor", "dp")) + (vec,) * 9,
        check_vma=False,
    )
```

```python
import math

import jax
import jax.numpy as jnp
from jax import lax
from jax.experimental import pallas as pl
from jax.experimental.pallas import tpu as pltpu
from jax.sharding import PartitionSpec as P

HEAD_DIM = 64
LONGEST = 1024
BLOCK = 256

NEG = -1e30
LANES = 128


def _lanes(rows):
    return lax.broadcasted_iota(jnp.int32, (rows, LANES), 1) < LANES // 2


def _pick(first, second, lanes):
    return jnp.where(lanes, first, second)


def _nt(a, b):
    return lax.dot_general(a, b, (((1,), (1,)), ((), ())), preferred_element_type=jnp.float32)


def _tn(a, b):
    return lax.dot_general(a, b, (((0,), (0,)), ((), ())), preferred_element_type=jnp.float32)


def _nn(a, b):
    return lax.dot_general(a, b, (((1,), (0,)), ((), ())), preferred_element_type=jnp.float32)


def _attn_fwd(lo_ref, hi_ref, q_ref, k_ref, v_ref, qs_ref, ks_ref, o_ref, lse_ref, m_sc, l_sc, acc_sc):
    i = pl.program_id(0)
    j = pl.program_id(1)
    kv = lo_ref[i] + j
    pairs = q_ref.shape[1] // LANES
    bq = q_ref.shape[0]

    @pl.when(j == 0)
    def _():
        m_sc[...] = jnp.full_like(m_sc, NEG)
        l_sc[...] = jnp.zeros_like(l_sc)
        acc_sc[...] = jnp.zeros_like(acc_sc)

    @pl.when(kv <= hi_ref[i])
    def _():
        mask = qs_ref[...] == ks_ref[...]
        lanes = _lanes(bq)

        def pair(p, carry):
            cols = pl.ds(p * LANES, LANES)
            q2 = q_ref[:, cols]
            k2 = k_ref[:, cols]
            v2 = v_ref[:, cols]
            zero = jnp.zeros_like(q2)
            alphas, pvs = [], []
            for h in range(2):
                hq = _pick(q2, zero, lanes) if h == 0 else _pick(zero, q2, lanes)
                s = jnp.where(mask, _nt(hq, k2), NEG)
                m_old = m_sc[2 * p + h]
                m_new = jnp.maximum(m_old, jnp.max(s, axis=-1, keepdims=True))
                alpha = jnp.exp(m_old - m_new)
                e = jnp.exp(s - m_new)
                l_sc[2 * p + h] = alpha * l_sc[2 * p + h] + jnp.sum(e, axis=-1, keepdims=True)
                m_sc[2 * p + h] = m_new
                alphas.append(alpha)
                pvs.append(_nn(e.astype(jnp.bfloat16), v2))
            acc_sc[:, cols] = _pick(alphas[0], alphas[1], lanes) * acc_sc[:, cols] + _pick(pvs[0], pvs[1], lanes)
            return carry

        for p in range(pairs):
            pair(p, 0)

    @pl.when(j == pl.num_programs(1) - 1)
    def _():
        lanes = _lanes(bq)

        def pair(p, carry):
            cols = pl.ds(p * LANES, LANES)
            l0, l1 = l_sc[2 * p], l_sc[2 * p + 1]
            o_ref[:, cols] = acc_sc[:, cols] / _pick(l0, l1, lanes)
            lse_ref[2 * p] = m_sc[2 * p] + jnp.log(l0)
            lse_ref[2 * p + 1] = m_sc[2 * p + 1] + jnp.log(l1)
            return carry

        for p in range(pairs):
            pair(p, 0)


def _attn_dq(lo_ref, hi_ref, q_ref, k_ref, v_ref, qs_ref, ks_ref, lse_ref, dl_ref, do_ref, dq_ref, acc_sc):
    i = pl.program_id(0)
    j = pl.program_id(1)
    kv = lo_ref[i] + j
    pairs = q_ref.shape[1] // LANES
    bq = q_ref.shape[0]

    @pl.when(j == 0)
    def _():
        acc_sc[...] = jnp.zeros_like(acc_sc)

    @pl.when(kv <= hi_ref[i])
    def _():
        mask = qs_ref[...] == ks_ref[...]
        lanes = _lanes(bq)

        def pair(p, carry):
            cols = pl.ds(p * LANES, LANES)
            q2 = q_ref[:, cols]
            k2 = k_ref[:, cols]
            v2 = v_ref[:, cols]
            do2 = do_ref[:, cols]
            zero = jnp.zeros_like(q2)
            parts = []
            for h in range(2):
                sel = (lambda a: _pick(a, zero, lanes)) if h == 0 else (lambda a: _pick(zero, a, lanes))
                s = _nt(sel(q2), k2)
                e = jnp.where(mask, jnp.exp(s - lse_ref[2 * p + h]), 0.0)
                dp = _nt(sel(do2), v2)
                ds = (e * (dp - dl_ref[2 * p + h])).astype(jnp.bfloat16)
                parts.append(_nn(ds, k2))
            acc_sc[:, cols] += _pick(parts[0], parts[1], lanes)
            return carry

        for p in range(pairs):
            pair(p, 0)

    @pl.when(j == pl.num_programs(1) - 1)
    def _():
        dq_ref[...] = acc_sc[...] * 0.125


def _attn_dkv(lo_ref, hi_ref, q_ref, k_ref, v_ref, qs_ref, ks_ref, lse_ref, dl_ref, do_ref, dk_ref, dv_ref, dk_sc, dv_sc):
    j = pl.program_id(0)
    i = pl.program_id(1)
    qb = lo_ref[j] + i
    pairs = q_ref.shape[1] // LANES
    bq = q_ref.shape[0]
    bk = k_ref.shape[0]

    @pl.when(i == 0)
    def _():
        dk_sc[...] = jnp.zeros_like(dk_sc)
        dv_sc[...] = jnp.zeros_like(dv_sc)

    @pl.when(qb <= hi_ref[j])
    def _():
        mask = qs_ref[...] == ks_ref[...]
        lanes_q = _lanes(bq)
        lanes_k = _lanes(bk)

        def pair(p, carry):
            cols = pl.ds(p * LANES, LANES)
            q2 = q_ref[:, cols]
            k2 = k_ref[:, cols]
            v2 = v_ref[:, cols]
            do2 = do_ref[:, cols]
            zero = jnp.zeros_like(q2)
            dks, dvs = [], []
            for h in range(2):
                sel = (lambda a: _pick(a, zero, lanes_q)) if h == 0 else (lambda a: _pick(zero, a, lanes_q))
                s = _nt(sel(q2), k2)
                e = jnp.where(mask, jnp.exp(s - lse_ref[2 * p + h]), 0.0)
                dp = _nt(sel(do2), v2)
                ds = (e * (dp - dl_ref[2 * p + h])).astype(jnp.bfloat16)
                dvs.append(_tn(e.astype(jnp.bfloat16), do2))
                dks.append(_tn(ds, q2))
            dv_sc[:, cols] += _pick(dvs[0], dvs[1], lanes_k)
            dk_sc[:, cols] += _pick(dks[0], dks[1], lanes_k)
            return carry

        for p in range(pairs):
            pair(p, 0)

    @pl.when(i == pl.num_programs(1) - 1)
    def _():
        dk_ref[...] = dk_sc[...]
        dv_ref[...] = dv_sc[...]


def _attn_bwd(lo_ref, hi_ref, q_ref, k_ref, v_ref, qs_ref, ks_ref, lse_ref, dl_ref, do_ref, dk_ref, dv_ref, dq_ref, dk_sc, dv_sc):
    j = pl.program_id(0)
    i = pl.program_id(1)
    qb = lo_ref[j] + i
    pairs = q_ref.shape[1] // LANES
    bq = q_ref.shape[0]
    bk = k_ref.shape[0]

    @pl.when((j == 0) & (i == 0))
    def _():
        dq_ref[...] = jnp.zeros_like(dq_ref)

    @pl.when(i == 0)
    def _():
        dk_sc[...] = jnp.zeros_like(dk_sc)
        dv_sc[...] = jnp.zeros_like(dv_sc)

    @pl.when(qb <= hi_ref[j])
    def _():
        mask = qs_ref[...] == ks_ref[...]
        lanes_q = _lanes(bq)
        lanes_k = _lanes(bk)
        rows = pl.ds(pl.multiple_of(qb * bq, bq), bq)
        for p in range(pairs):
            cols = pl.ds(p * LANES, LANES)
            q2 = q_ref[:, cols]
            k2 = k_ref[:, cols]
            v2 = v_ref[:, cols]
            do2 = do_ref[:, cols]
            zero = jnp.zeros_like(q2)
            dks, dvs, dqs = [], [], []
            for h in range(2):
                sel = (lambda a: _pick(a, zero, lanes_q)) if h == 0 else (lambda a: _pick(zero, a, lanes_q))
                s = _nt(sel(q2), k2)
                e = jnp.where(mask, jnp.exp(s - lse_ref[2 * p + h]), 0.0)
                dp = _nt(sel(do2), v2)
                ds = (e * (dp - dl_ref[2 * p + h])).astype(jnp.bfloat16)
                dvs.append(_tn(e.astype(jnp.bfloat16), do2))
                dks.append(_tn(ds, q2))
                dqs.append(_nn(ds, k2))
            dv_sc[:, cols] += _pick(dvs[0], dvs[1], lanes_k)
            dk_sc[:, cols] += _pick(dks[0], dks[1], lanes_k)
            dq_ref[rows, cols] += _pick(dqs[0], dqs[1], lanes_q)

    @pl.when(i == pl.num_programs(1) - 1)
    def _():
        dk_ref[...] = dk_sc[...]
        dv_ref[...] = dv_sc[...]

    @pl.when((i == pl.num_programs(1) - 1) & (j == pl.num_programs(0) - 1))
    def _():
        dq_ref[...] = dq_ref[...] * 0.125


def _clamp(start, step, last):
    return jnp.minimum(start + step, jnp.maximum(last, 0))


def _params():
    return pltpu.CompilerParams(dimension_semantics=("arbitrary", "arbitrary"), vmem_limit_bytes=48 * 1024 * 1024)


def flash_forward(q, k, v, q_ids, k_ids, lo, hi, block_q, block_k, steps):
    nq, width = q.shape
    nk = k.shape[0]
    heads = width // 64
    kv_map = lambda i, j, a, b: (_clamp(a[i], j, b[i]), 0)
    ks_map = lambda i, j, a, b: (0, _clamp(a[i], j, b[i]))
    row = lambda i, j, a, b: (i, 0)
    grid_spec = pltpu.PrefetchScalarGridSpec(
        num_scalar_prefetch=2,
        grid=(nq // block_q, steps),
        in_specs=[
            pl.BlockSpec((block_q, width), row),
            pl.BlockSpec((block_k, width), kv_map),
            pl.BlockSpec((block_k, width), kv_map),
            pl.BlockSpec((block_q, 1), row),
            pl.BlockSpec((1, block_k), ks_map),
        ],
        out_specs=[
            pl.BlockSpec((block_q, width), row),
            pl.BlockSpec((heads, block_q, 1), lambda i, j, a, b: (0, i, 0)),
        ],
        scratch_shapes=[
            pltpu.VMEM((heads, block_q, 1), jnp.float32),
            pltpu.VMEM((heads, block_q, 1), jnp.float32),
            pltpu.VMEM((block_q, width), jnp.float32),
        ],
    )
    return pl.pallas_call(
        _attn_fwd,
        grid_spec=grid_spec,
        cost_estimate=pl.CostEstimate(flops=8 * nq * LONGEST * width, transcendentals=nq * LONGEST * heads, bytes_accessed=2 * (nq + 2 * nk) * width * 2),
        out_shape=[jax.ShapeDtypeStruct((nq, width), jnp.float32), jax.ShapeDtypeStruct((heads, nq, 1), jnp.float32)],
        compiler_params=_params(),
    )(lo, hi, q, k, v, q_ids.reshape(nq, 1), k_ids.reshape(1, nk))


def flash_dq(q, k, v, q_ids, k_ids, lse, delta, do, lo, hi, block_q, block_k, steps):
    nq, width = q.shape
    nk = k.shape[0]
    heads = width // 64
    kv_map = lambda i, j, a, b: (_clamp(a[i], j, b[i]), 0)
    ks_map = lambda i, j, a, b: (0, _clamp(a[i], j, b[i]))
    row = lambda i, j, a, b: (i, 0)
    hrow = lambda i, j, a, b: (0, i, 0)
    grid_spec = pltpu.PrefetchScalarGridSpec(
        num_scalar_prefetch=2,
        grid=(nq // block_q, steps),
        in_specs=[
            pl.BlockSpec((block_q, width), row),
            pl.BlockSpec((block_k, width), kv_map),
            pl.BlockSpec((block_k, width), kv_map),
            pl.BlockSpec((block_q, 1), row),
            pl.BlockSpec((1, block_k), ks_map),
            pl.BlockSpec((heads, block_q, 1), hrow),
            pl.BlockSpec((heads, block_q, 1), hrow),
            pl.BlockSpec((block_q, width), row),
        ],
        out_specs=pl.BlockSpec((block_q, width), row),
        scratch_shapes=[pltpu.VMEM((block_q, width), jnp.float32)],
    )
    return pl.pallas_call(
        _attn_dq,
        grid_spec=grid_spec,
        out_shape=jax.ShapeDtypeStruct((nq, width), jnp.float32),
        compiler_params=_params(),
    )(lo, hi, q, k, v, q_ids.reshape(nq, 1), k_ids.reshape(1, nk), lse, delta, do)


def flash_dkv(q, k, v, q_ids, k_ids, lse, delta, do, qlo, qhi, block_q, block_k, steps):
    nq, width = q.shape
    nk = k.shape[0]
    heads = width // 64
    q_map = lambda j, i, a, b: (_clamp(a[j], i, b[j]), 0)
    h_map = lambda j, i, a, b: (0, _clamp(a[j], i, b[j]), 0)
    col = lambda j, i, a, b: (j, 0)
    grid_spec = pltpu.PrefetchScalarGridSpec(
        num_scalar_prefetch=2,
        grid=(nk // block_k, steps),
        in_specs=[
            pl.BlockSpec((block_q, width), q_map),
            pl.BlockSpec((block_k, width), col),
            pl.BlockSpec((block_k, width), col),
            pl.BlockSpec((block_q, 1), q_map),
            pl.BlockSpec((1, block_k), lambda j, i, a, b: (0, j)),
            pl.BlockSpec((heads, block_q, 1), h_map),
            pl.BlockSpec((heads, block_q, 1), h_map),
            pl.BlockSpec((block_q, width), q_map),
        ],
        out_specs=[pl.BlockSpec((block_k, width), col), pl.BlockSpec((block_k, width), col)],
        scratch_shapes=[pltpu.VMEM((block_k, width), jnp.float32), pltpu.VMEM((block_k, width), jnp.float32)],
    )
    return pl.pallas_call(
        _attn_dkv,
        grid_spec=grid_spec,
        out_shape=[jax.ShapeDtypeStruct((nk, width), jnp.float32), jax.ShapeDtypeStruct((nk, width), jnp.float32)],
        compiler_params=_params(),
    )(qlo, qhi, q, k, v, q_ids.reshape(nq, 1), k_ids.reshape(1, nk), lse, delta, do)


def flash_backward(q, k, v, q_ids, k_ids, lse, delta, do, qlo, qhi, block_q, block_k, steps):
    nq, width = q.shape
    nk = k.shape[0]
    heads = width // 64
    q_map = lambda j, i, a, b: (_clamp(a[j], i, b[j]), 0)
    h_map = lambda j, i, a, b: (0, _clamp(a[j], i, b[j]), 0)
    col = lambda j, i, a, b: (j, 0)
    grid_spec = pltpu.PrefetchScalarGridSpec(
        num_scalar_prefetch=2,
        grid=(nk // block_k, steps),
        in_specs=[
            pl.BlockSpec((block_q, width), q_map),
            pl.BlockSpec((block_k, width), col),
            pl.BlockSpec((block_k, width), col),
            pl.BlockSpec((block_q, 1), q_map),
            pl.BlockSpec((1, block_k), lambda j, i, a, b: (0, j)),
            pl.BlockSpec((heads, block_q, 1), h_map),
            pl.BlockSpec((heads, block_q, 1), h_map),
            pl.BlockSpec((block_q, width), q_map),
        ],
        out_specs=[
            pl.BlockSpec((block_k, width), col),
            pl.BlockSpec((block_k, width), col),
            pl.BlockSpec((nq, width), lambda j, i, a, b: (0, 0)),
        ],
        scratch_shapes=[pltpu.VMEM((block_k, width), jnp.float32), pltpu.VMEM((block_k, width), jnp.float32)],
    )
    return pl.pallas_call(
        _attn_bwd,
        grid_spec=grid_spec,
        cost_estimate=pl.CostEstimate(flops=20 * nq * LONGEST * width, transcendentals=nq * LONGEST * heads, bytes_accessed=4 * (2 * nq + 4 * nk) * width),
        out_shape=[
            jax.ShapeDtypeStruct((nk, width), jnp.float32),
            jax.ShapeDtypeStruct((nk, width), jnp.float32),
            jax.ShapeDtypeStruct((nq, width), jnp.float32),
        ],
        compiler_params=_params(),
    )(qlo, qhi, q, k, v, q_ids.reshape(nq, 1), k_ids.reshape(1, nk), lse, delta, do)


def block_ranges(q_ids, k_ids, q_start, q_end, block_q, block_k):
    nq = q_ids.shape[0]
    nk = k_ids.shape[0]
    nqb, nkb = nq // block_q, nk // block_k
    first = q_start.reshape(nqb, block_q)[:, 0]
    last = q_end.reshape(nqb, block_q)[:, block_q - 1]
    lo = jnp.clip(first // block_k, 0, nkb - 1).astype(jnp.int32)
    hi = jnp.clip((last - 1) // block_k, 0, nkb - 1).astype(jnp.int32)
    kb = jnp.arange(nkb, dtype=jnp.int32)
    qb = jnp.arange(nqb, dtype=jnp.int32)
    cover = (lo[:, None] <= kb[None, :]) & (kb[None, :] <= hi[:, None])
    qlo = jnp.min(jnp.where(cover, qb[:, None], nqb), axis=0).astype(jnp.int32)
    qhi = jnp.max(jnp.where(cover, qb[:, None], -1), axis=0).astype(jnp.int32)
    return lo, hi, qlo, qhi


def norm_forward(values, gain, shift):
    center = jnp.mean(values, axis=-1, keepdims=True)
    offsets = values - center
    spread = jnp.mean(offsets * offsets, axis=-1, keepdims=True)
    inverse = lax.rsqrt(spread + 1e-06)
    normed = offsets * inverse
    return (normed * gain + shift, normed, inverse)


def norm_backward(grad_y, normed, inverse, gain):
    grad_normed = grad_y * gain
    mean_one = jnp.mean(grad_normed, axis=-1, keepdims=True)
    mean_two = jnp.mean(grad_normed * normed, axis=-1, keepdims=True)
    return inverse * (grad_normed - mean_one - normed * mean_two)


def activate(values):
    return jax.nn.gelu(values, approximate=False)


def contract_last(left, right):
    return lax.dot_general(left, right, (((1,), (1,)), ((), ())), preferred_element_type=jnp.float32)


def contract_first(left, right):
    return lax.dot_general(left, right, (((0,), (0,)), ((), ())), preferred_element_type=jnp.float32)


def column_sum(values):
    return jnp.sum(values.astype(jnp.float32), axis=0)


def group_segments(lengths, dealing, group_index, group_rows, per_group):
    picked = lax.dynamic_slice_in_dim(dealing, group_index * per_group, per_group)
    match = picked[:, None] == jnp.arange(lengths.shape[0], dtype=jnp.int32)[None, :]
    chosen = jnp.sum(jnp.where(match, lengths[None, :], 0), axis=1)
    ends = jnp.cumsum(chosen)
    starts = ends - chosen
    places = jnp.arange(group_rows, dtype=jnp.int32)
    segment_ids = jnp.sum((places[:, None] >= ends[None, :]).astype(jnp.int32), axis=1)
    return (segment_ids, starts, ends)


def cyclic_pieces(piece):
    count = lax.axis_size("tensor")
    me = lax.axis_index("tensor")
    got = [piece]
    for k in range(1, count):
        got.append(lax.ppermute(piece, "tensor", [(s, (s + k) % count) for s in range(count)]))
    order = (me - jnp.arange(count, dtype=jnp.int32)) % count
    return jnp.take(jnp.stack(got), order, axis=0)


def gather_weights(blocks):
    count = lax.axis_size("tensor")
    widths = [b.shape[1] for b in blocks]
    piece = jnp.concatenate(blocks, axis=1)
    parts = cyclic_pieces(piece)
    cols, at = [], 0
    for w in widths:
        cols.extend(parts[t, :, at:at + w] for t in range(count))
        at += w
    strip = jnp.concatenate(cols, axis=1)
    full = lax.all_gather(strip, "dp", axis=0, tiled=True)
    out, at = [], 0
    for w in widths:
        out.append(full[:, at:at + w * count])
        at += w * count
    return out


def vector_rows(v, rows):
    dp = lax.axis_size("dp")
    slab = rows // dp
    spread = v.reshape(dp, 1, -1)
    return jnp.pad(spread, ((0, 0), (0, slab - 1), (0, 0))).reshape(rows, -1)


def pack_grads(grads, vectors):
    count = lax.axis_size("tensor")
    me = lax.axis_index("tensor")
    rows = grads[0].shape[0]
    mats = [g.astype(jnp.bfloat16) for g in grads] + [vector_rows(v.astype(jnp.bfloat16), rows) for v in vectors]
    widths = [m.shape[1] // count for m in mats]
    cat = jnp.concatenate(mats, axis=1)
    return widths, cat


def reduce_dp(cat):
    return lax.psum_scatter(cat, "dp", scatter_dimension=0, tiled=True)


def reduce_dp_by_halves(cat):
    dp = lax.axis_size("dp")
    me = lax.axis_index("dp")
    slab = cat.shape[0] // dp
    part = cat.astype(jnp.float32).reshape(dp, slab, cat.shape[1])
    bit = 0
    while (1 << bit) < dp:
        mine = (me >> bit) % 2
        halves = part.reshape(part.shape[0] // 2, 2, slab, cat.shape[1])
        keep = lax.dynamic_index_in_dim(halves, mine, axis=1, keepdims=False)
        send = lax.dynamic_index_in_dim(halves, 1 - mine, axis=1, keepdims=False)
        pairs = [(i, i ^ (1 << bit)) for i in range(dp)]
        part = keep + lax.ppermute(send.astype(jnp.bfloat16), "dp", pairs).astype(jnp.float32)
        bit += 1
    return part.reshape(slab, cat.shape[1])


def reduce_tensor(strip, widths, n_grads):
    count = lax.axis_size("tensor")
    me = lax.axis_index("tensor")
    strip = strip.astype(jnp.float32)
    per_t = []
    for t in range(count):
        at, cols = 0, []
        for w in widths:
            cols.append(strip[:, at + t * w:at + (t + 1) * w])
            at += w * count
        per_t.append(jnp.concatenate(cols, axis=1))
    stacked = jnp.stack(per_t)
    total = jnp.take(stacked, me, axis=0)
    for k in range(1, count):
        send = jnp.take(stacked, (me + k) % count, axis=0)
        total = total + lax.ppermute(send, "tensor", [(s, (s + k) % count) for s in range(count)])
    out, at = [], 0
    for i, w in enumerate(widths):
        block = total[:, at:at + w]
        at += w
        out.append(block if i < n_grads else block[0])
    return out


def halo_plan(rows):
    hops = -(-LONGEST // rows)
    takes = [rows] * (hops - 1) + [LONGEST - rows * (hops - 1)]
    return takes


def shift_rows(values, distance, count):
    if distance >= count:
        return jnp.zeros_like(values)
    if distance > 0:
        pairs = [(s, s + distance) for s in range(count - distance)]
    else:
        pairs = [(s - distance, s) for s in range(count + distance)]
    return lax.ppermute(values, "tensor", pairs)


def build_window(own, takes, count):
    rows = own.shape[0]
    left = [shift_rows(own[rows - take:], d + 1, count) for d, take in enumerate(takes)]
    right = [shift_rows(own[:take], -(d + 1), count) for d, take in enumerate(takes)]
    return jnp.concatenate(left[::-1] + [own] + right, axis=0)


def return_window(values, takes, count):
    rows = values.shape[0] - 2 * LONGEST
    total = values[LONGEST:LONGEST + rows]
    at = LONGEST
    for d, take in enumerate(takes):
        piece = values[at - take:at].astype(jnp.bfloat16)
        at -= take
        back = shift_rows(piece, -(d + 1), count).astype(jnp.float32)
        total = total + jnp.pad(back, ((rows - take, 0), (0, 0)))
    at = LONGEST + rows
    for d, take in enumerate(takes):
        piece = values[at:at + take].astype(jnp.bfloat16)
        at += take
        back = shift_rows(piece, d + 1, count).astype(jnp.float32)
        total = total + jnp.pad(back, ((0, rows - take), (0, 0)))
    return total


def to_heads(values):
    rows, width = values.shape
    return values.reshape(rows, width // HEAD_DIM, HEAD_DIM).transpose(1, 0, 2)


def from_heads(values):
    heads, rows, hd = values.shape
    return values.transpose(1, 0, 2).reshape(rows, heads * hd)


def shards(tokens, lengths, dealing, w_query, w_key, w_value, w_out, w_inner, w_outer, b_query, b_value, b_out, b_inner, b_outer, gain_attn, shift_attn, gain_ffn, shift_ffn, grad_out):
    count = lax.axis_size("tensor")
    tens_index = lax.axis_index("tensor")
    group_index = lax.axis_index("dp")
    rows = tokens.shape[0]
    group_rows = rows * count
    per_group = lengths.shape[0] // lax.axis_size("dp")
    takes = halo_plan(rows)
    window = rows + 2 * LONGEST
    seg, starts, ends = group_segments(lengths, dealing, group_index, group_rows, per_group)
    base = rows * tens_index - LONGEST
    places = base + jnp.arange(window, dtype=jnp.int32)
    valid = (places >= 0) & (places < group_rows)
    k_ids = jnp.where(valid, jnp.sum((places[:, None] >= ends[None, :]).astype(jnp.int32), axis=1), -1).astype(jnp.int32)
    q_ids = lax.dynamic_slice_in_dim(seg, rows * tens_index, rows)
    q_start = jnp.take(starts, q_ids) - base
    q_end = jnp.take(ends, q_ids) - base
    lo, hi, qlo, qhi = block_ranges(q_ids, k_ids, q_start, q_end, BLOCK, BLOCK)
    nkb = window // BLOCK
    kv_steps = min(nkb, (BLOCK + 2 * (LONGEST - 1)) // BLOCK + 2)
    q_steps = rows // BLOCK

    wq, wk, wv = gather_weights([w_query, w_key, w_value])
    wo_t, wi, wf_t = gather_weights([w_out.T, w_inner, w_outer.T])
    gain_one = gain_attn.astype(jnp.float32)
    gain_two = gain_ffn.astype(jnp.float32)

    x_own = tokens
    x_win = build_window(tokens, takes, count)
    query = (jnp.dot(x_own, wq, preferred_element_type=jnp.float32) + b_query.astype(jnp.float32)).astype(jnp.bfloat16)
    key_w = jnp.dot(x_win, wk, preferred_element_type=jnp.float32).astype(jnp.bfloat16)
    value_w = (jnp.dot(x_win, wv, preferred_element_type=jnp.float32) + b_value.astype(jnp.float32)).astype(jnp.bfloat16)
    scaled = query * jnp.asarray(1.0 / math.sqrt(HEAD_DIM), jnp.bfloat16)
    ctx32, lse = flash_forward(scaled, key_w, value_w, q_ids, k_ids, lo, hi, BLOCK, BLOCK, kv_steps)
    context = ctx32.astype(jnp.bfloat16)
    attn = contract_last(context, wo_t) + b_out.astype(jnp.float32)
    hidden, norm_one, inverse_one = norm_forward(tokens.astype(jnp.float32) + attn, gain_one, shift_attn.astype(jnp.float32))
    hidden_low = hidden.astype(jnp.bfloat16)
    pre_act = jnp.dot(hidden_low, wi, preferred_element_type=jnp.float32) + b_inner.astype(jnp.float32)
    act = activate(pre_act).astype(jnp.bfloat16)
    ffn = contract_last(act, wf_t) + b_outer.astype(jnp.float32)
    output, norm_two, inverse_two = norm_forward(hidden + ffn, gain_two, shift_ffn.astype(jnp.float32))

    grad_y = grad_out.astype(jnp.float32)
    grad_resid_two = norm_backward(grad_y, norm_two, inverse_two, gain_two)
    grad_ffn = grad_resid_two.astype(jnp.bfloat16)
    grad_outer_t = contract_first(grad_ffn, act)
    grad_act = jnp.dot(grad_ffn, wf_t, preferred_element_type=jnp.float32)
    unused, gelu_pull = jax.vjp(activate, pre_act)
    grad_pre = gelu_pull(grad_act)[0].astype(jnp.bfloat16)
    grad_inner_w = contract_first(hidden_low, grad_pre)
    grad_hidden = grad_resid_two + contract_last(grad_pre, wi)
    grad_resid_one = norm_backward(grad_hidden, norm_one, inverse_one, gain_one)
    grad_attn = grad_resid_one.astype(jnp.bfloat16)
    grad_out_t = contract_first(grad_attn, context)
    grad_context = jnp.dot(grad_attn, wo_t, preferred_element_type=jnp.float32).astype(jnp.bfloat16)
    late = [
        column_sum(grad_attn),
        column_sum(grad_pre),
        column_sum(grad_ffn),
        jnp.sum(grad_hidden * norm_one, axis=0),
        jnp.sum(grad_hidden, axis=0),
        jnp.sum(grad_y * norm_two, axis=0),
        jnp.sum(grad_y, axis=0),
    ]
    early_widths, early_cat = pack_grads([grad_out_t, grad_inner_w, grad_outer_t], late)
    grad_context, early_cat = lax.optimization_barrier((grad_context, early_cat))
    early_strip = reduce_dp(early_cat)
    heads = query.shape[1] // HEAD_DIM
    delta = jnp.sum((grad_context.astype(jnp.float32) * ctx32).reshape(rows, heads, HEAD_DIM), axis=-1)
    delta = delta.T.reshape(heads, rows, 1)
    dk_h, dv_h, dq_h = flash_backward(scaled, key_w, value_w, q_ids, k_ids, lse, delta, grad_context, qlo, qhi, BLOCK, BLOCK, q_steps)
    early_sums = reduce_tensor(early_strip, early_widths, 3)
    g_out_t, g_inner, g_outer_t = early_sums[:3]
    late = early_sums[3:]
    grad_query = dq_h.astype(jnp.bfloat16)
    grad_key = dk_h.astype(jnp.bfloat16)
    grad_value = dv_h.astype(jnp.bfloat16)
    grad_query_w = contract_first(x_own, grad_query)
    grad_key_w = contract_first(x_win, grad_key)
    grad_value_w = contract_first(x_win, grad_value)
    grad_win = contract_last(grad_key, wk) + contract_last(grad_value, wv)
    grad_tokens = grad_resid_one + contract_last(grad_query, wq) + return_window(grad_win, takes, count)

    late_widths, late_cat = pack_grads(
        [grad_query_w, grad_key_w, grad_value_w], [column_sum(grad_query), column_sum(grad_value)]
    )
    g_query, g_key, g_value, g_bq, g_bv = reduce_tensor(reduce_dp_by_halves(late_cat), late_widths, 3)
    summed = (g_query, g_key, g_value, g_out_t.T, g_inner, g_outer_t.T)
    small = [g_bq, g_bv] + late
    return (output.astype(jnp.bfloat16), grad_tokens) + summed + tuple(small)


def solution(mesh):
    rows = P(("dp", "tensor"), None)
    vec = P(("dp", "tensor"))
    return jax.shard_map(
        shards,
        mesh=mesh,
        in_specs=(rows, P(), P(), P("dp", "tensor"), P("dp", "tensor"), P("dp", "tensor"), P("tensor", "dp"), P("dp", "tensor"), P("tensor", "dp"), P(), P(), P(), P(), P(), P(), P(), P(), P(), rows),
        out_specs=(rows, rows, P("dp", "tensor"), P("dp", "tensor"), P("dp", "tensor"), P("tensor", "dp"), P("dp", "tensor"), P("tensor", "dp")) + (vec,) * 9,
        check_vma=False,
    )
```
